32 devices in a mesh: group: 2 (over x), strip: 16 (over z, y, core).
Axes of the slice: x: 2, y: 2, z: 4, core: 2. Of those that a mesh axis runs over, the one named last changes fastest.
Arguments:
- strip_fields: float32 [3, 64, 128, 128], P(None, ('group', 'strip')), may hold values from -18 to 18
- strip_riser: int32 [64, 1], P('group'), may hold values from 0 to 3; in each aligned block of 2 rows (0 to 1, 2 to 3, ...) at most 2 rows name the same one
- strip_node: int32 [64], P('group'), may hold values from 0 to 1023
- riser_owner: int32 [2, 4], P('group'), may hold values from 0 to 15, as said below
- pivot_inv: float32 [32, 8, 128, 128], P(('group', 'strip')), may hold values from -0.2 to 1
- lower_block: float32 [32, 7, 128, 128], P(('group', 'strip')), may hold values from -0.109375 to 0.109375
- upper_block: float32 [32, 7, 128, 128], P(('group', 'strip')), may hold values from -0.109375 to 0.109375
Outputs:
- vorticity: float32 [64, 128, 128], P(('group', 'strip'))
- displacement: float32 [32, 16, 1024], P(('group', 'strip'))
The draws below stay inside these ranges and needn't reach their ends.
Inputs may be any that keep to these rules, and one draw needn't show every extreme that they name: `strip_riser`: in each aligned block of 2 strips (the strips of one device) no riser is named more than 2 times, and some block names one riser exactly 2 times. `riser_owner`: the 4 owners in a row are distinct devices.
All inputs are finite; a program needn't handle non-finite values.
Results may differ from the reference program's by a relative error of at most 0.0003.
Values sent between devices are 32-bit elements; how exact they have to be, the bound alone decides.
No kernel may reach another device: no remote copies, remote signals or barrier semaphores. Data moves between devices by JAX's collectives and lax.ppermute only.
A program may use at most 64 MiB of HBM per device.

```python
import math
import jax
import jax.numpy as jnp
import numpy as np
from jax import lax

CELLS = 128
S_DEV = 2
NSUB = 8
COUPLED = 2
RISERS = 4
NODES = 1024
BS = 128
NB = 8
CAP = 2
STRIPS = 64
SLOTS = 32
N_GROUP = 2
N_STRIP = 16


def draw_strip_fields(key, part):
    key_amp, key_vortex, key_flowx, key_flowy = jax.random.split(key, 4)
    strip_rank = jnp.arange(STRIPS, dtype=jnp.float32) / max(STRIPS - 1, 1)
    spread = jnp.exp(jax.random.uniform(key_amp, (STRIPS, 1, 1), jnp.float32, 0.0, 1.0986))
    amplitude = (0.5 + strip_rank)[:, None, None] * spread
    shape = (STRIPS, CELLS, CELLS)
    vortex_field = amplitude * jnp.clip(jax.random.normal(key_vortex, shape, jnp.float32), -4.0, 4.0)
    flow_x = 0.6 + 0.12 * jnp.clip(jax.random.normal(key_flowx, shape, jnp.float32), -3.3, 3.3)
    flow_y = 0.12 * jnp.clip(jax.random.normal(key_flowy, shape, jnp.float32), -3.3, 3.3)
    return jnp.stack([vortex_field, flow_x, flow_y])


def draw_riser_owner(key, part):
    key_rows, key_first, key_order = jax.random.split(jax.random.fold_in(key, 31), 3)
    group_keys = jax.random.split(key_rows, N_GROUP)
    rows = jax.vmap(lambda row_key: jax.random.permutation(row_key, N_STRIP)[:RISERS])(group_keys)
    middle = jax.random.permutation(key_first, jnp.arange(1, N_STRIP - 1, dtype=jnp.int32))[:RISERS - 2]
    first_row = jnp.concatenate([jnp.array([0, N_STRIP - 1], jnp.int32), middle.astype(jnp.int32)])
    first_row = jax.random.permutation(key_order, first_row)
    return rows.astype(jnp.int32).at[0].set(first_row)


def draw_pivot_inv(key, part):
    key_diag, key_off = jax.random.split(key)
    identity = (jnp.arange(BS)[:, None] == jnp.arange(BS)[None, :]).astype(jnp.float32)
    diagonal = jax.random.uniform(key_diag, (SLOTS, NB, 1, BS), jnp.float32, 0.5, 1.0)
    shape = (SLOTS, NB, BS, BS)
    off_diagonal = jnp.clip(0.5 * BS ** (-0.5) * jax.random.normal(key_off, shape, jnp.float32), -0.2, 0.2)
    return identity * diagonal + (1.0 - identity) * off_diagonal


def with_ends(entries, rng, low, high):
    longest = entries.shape.index(max(entries.shape))
    spots = []
    for shift in (0, 1):
        where = [jax.random.randint(jax.random.fold_in(rng, axis), (), 0, length) for axis, length in enumerate(entries.shape)]
        where[longest] = (where[longest] + shift) % entries.shape[longest]
        spots.append(tuple(where))
    return entries.at[spots[0]].set(low).at[spots[1]].set(high)


def shard_levels(stream_key, extent, cuts, smallest, high):
    def one(position, blocks):
        steps = jax.random.uniform(jax.random.fold_in(jax.random.fold_in(stream_key, 6), position), (blocks,), jnp.float32, smallest / len(cuts), high / len(cuts))
        return jnp.repeat(jnp.exp(steps), extent[position] // blocks).reshape((-1,) + (1,) * (len(extent) - position - 1))

    gain = one(*cuts[0])
    for cut in cuts[1:]:
        gain = gain * one(*cut)
    return gain


def shared_out(key, own, number, rows, count, top, reach, lean):
    ranking = jax.random.permutation(key, count)
    crowded, usual = portions_of(count, rows * top, reach, lean, True), portions_of(count, rows * top, reach, lean, False)
    places = jnp.arange(count)

    def named(tallies, turn):
        used = int((tallies > 0).sum())
        fixed = max(1, used // 4)
        moved = fixed + (places - fixed + turn * (used - fixed)) % max(1, count - fixed)
        return jnp.zeros((count,), jnp.int32).at[ranking[jnp.where(places < fixed, places, moved)]].set(jnp.asarray(tallies, jnp.int32))

    tallies = jnp.where(number % 4 == 0, named(crowded, number // 4), named(usual, number - number // 4 - 1))
    mixed = jax.random.permutation(jax.random.fold_in(own, 3), count)
    giver, receiver = mixed[0:count // 2 * 2:2], mixed[1:count // 2 * 2:2]
    room = jnp.minimum(tallies[giver] - 1, reach - tallies[receiver]) // 2
    room = jnp.where((giver == ranking[0]) | (receiver == ranking[0]) | (tallies[receiver] == 0), 0, jnp.maximum(room, 0))
    moved = jax.random.randint(jax.random.fold_in(own, 4), (count // 2,), 0, 1 << 20) % (room + 1)
    tallies = tallies.at[giver].add(-moved).at[receiver].add(moved)
    labels = jnp.searchsorted(jnp.cumsum(tallies), jnp.arange(rows * top), side="right").astype(jnp.int32)
    table = labels.reshape(top, rows).T
    table = table[jax.random.permutation(jax.random.fold_in(own, 1), rows)]
    turn = jax.random.randint(jax.random.fold_in(own, 2), (rows, 1), 0, top)
    return jnp.take_along_axis(table, (jnp.arange(top)[None, :] + turn) % top, axis=1)


def portions_of(amount, total, reach, lean, full):
    loads = [(1 << 20) // math.isqrt(standing ** lean) + 1 for standing in range(1, amount + 1)]
    largest = reach if full else min(reach, max(-(-total // amount), total * loads[0] // sum(loads)))
    least = 1 if total - largest >= amount - 1 else 0
    counts, spare = [largest] + [least] * (amount - 1), total - largest - least * (amount - 1)
    while spare > 0:
        movable = [i for i in range(1, amount) if counts[i] < largest] or [i for i in range(1, amount) if counts[i] < reach]
        pool, budget = sum([loads[i] for i in movable]), spare
        for i in movable:
            more = min(reach - counts[i], max(1, budget * loads[i] // pool), spare)
            counts[i] = counts[i] + more
            spare = spare - more
    return np.array(counts)


def normal_values(own_key, extent, deviation, most, pieces=(), held_as=jnp.bfloat16):
    values = deviation * jax.random.normal(own_key, extent, jnp.float32)
    if pieces:
        values = values * shard_levels(own_key, extent, pieces, -0.22, 0.18)
    return jnp.clip(values, -most, most).astype(held_as)


def setup_inputs(seed: int = 0) -> dict:
    arg_keys = jax.random.split(jax.random.key(seed), 8)
    strip_fields = draw_strip_fields(jax.random.fold_in(arg_keys[7], 71), 0)
    strip_riser_keys = jax.random.split(jax.random.fold_in(arg_keys[1], 1), STRIPS // S_DEV)
    strip_riser_turns = jax.random.permutation(jax.random.fold_in(arg_keys[1], 3), STRIPS // S_DEV)
    strip_riser = jax.vmap(lambda own, number: shared_out(jax.random.fold_in(arg_keys[1], 2), own, number, S_DEV, RISERS, 1, CAP, 2))(strip_riser_keys, strip_riser_turns).reshape((STRIPS, 1))
    strip_node = with_ends(jax.random.randint(arg_keys[2], (STRIPS,), 0, NODES), jax.random.fold_in(arg_keys[2], 1), 0, NODES - 1).astype(jnp.int32)
    riser_owner = draw_riser_owner(jax.random.fold_in(arg_keys[7], 71), 0)
    pivot_inv = draw_pivot_inv(jax.random.fold_in(arg_keys[7], 71), 0)
    lower_block = normal_values(arg_keys[5], (SLOTS, NB - 1, BS, BS), (25 * BS) ** -0.5, 0.109375, ((0, 32),), jnp.float32)
    upper_block = normal_values(arg_keys[6], (SLOTS, NB - 1, BS, BS), (25 * BS) ** -0.5, 0.109375, ((0, 32),), jnp.float32)
    return {"strip_fields": strip_fields, "strip_riser": strip_riser, "strip_node": strip_node, "riser_owner": riser_owner, "pivot_inv": pivot_inv, "lower_block": lower_block, "upper_block": upper_block}


TIME_STEP = 0.25
VISCOSITY = 0.05
COUPLING = 0.5
EXACT_DOT = lax.Precision.HIGHEST

def make_kernels(grid_cells):
    centre = jnp.arange(grid_cells, dtype=jnp.float32) - grid_cells / 2.0 + 0.5
    near_x = (centre / (grid_cells / 16.0))[None, :]
    near_y = (centre / (grid_cells / 16.0))[:, None]
    bell_near = jnp.exp(-(near_x * near_x + near_y * near_y) / 2.0)
    source_x = -near_x * bell_near
    source_y = -near_y * bell_near
    wide_x = (centre / (grid_cells / 8.0))[None, :]
    wide_y = (centre / (grid_cells / 8.0))[:, None]
    bell_wide = jnp.exp(-(wide_x * wide_x + wide_y * wide_y) / 2.0)
    lift_kernel = -wide_x * bell_wide
    drag_kernel = wide_y * bell_wide
    lift_kernel = lift_kernel / jnp.sqrt(jnp.sum(lift_kernel * lift_kernel))
    drag_kernel = drag_kernel / jnp.sqrt(jnp.sum(drag_kernel * drag_kernel))
    return (source_x, source_y, lift_kernel, drag_kernel)

def strip_step(vorticity, flow_x, flow_y, motion, kernels, substeps):
    source_x, source_y, lift_kernel, drag_kernel = kernels
    halves = motion.reshape(motion.shape[0], 2, substeps)
    earlier = jnp.concatenate([jnp.zeros_like(halves[:, :, :1]), halves[:, :, :-1]], axis=2)
    velocity = halves - earlier
    lift_rows = []
    drag_rows = []
    for substep in range(substeps):
        right_cell = jnp.roll(vorticity, -1, axis=2)
        left_cell = jnp.roll(vorticity, 1, axis=2)
        upper_cell = jnp.roll(vorticity, -1, axis=1)
        lower_cell = jnp.roll(vorticity, 1, axis=1)
        laplacian = right_cell + left_cell + upper_cell + lower_cell - 4.0 * vorticity
        tendency = VISCOSITY * laplacian - flow_x * (0.5 * (right_cell - left_cell)) - flow_y * (0.5 * (upper_cell - lower_cell))
        forcing = velocity[:, 0, substep][:, None, None] * source_x - velocity[:, 1, substep][:, None, None] * source_y
        vorticity = vorticity + TIME_STEP * tendency + COUPLING * forcing
        lift_rows.append(lax.optimization_barrier(jnp.sum(vorticity * lift_kernel, axis=(1, 2))))
        drag_rows.append(lax.optimization_barrier(jnp.sum(vorticity * drag_kernel, axis=(1, 2))))
    return (vorticity, jnp.stack(lift_rows + drag_rows, axis=1))

def apply_block(vectors, matrix):
    return lax.dot_general(vectors, matrix, (((1,), (1,)), ((), ())), precision=EXACT_DOT)

def beam_solve(beam_load, pivot_inv, lower_block, upper_block):
    block_count = pivot_inv.shape[0]
    block_size = pivot_inv.shape[1]
    blocks = beam_load.reshape(beam_load.shape[0], block_count, block_size)
    carried = [blocks[:, 0]]
    for block_index in range(1, block_count):
        pivoted = apply_block(carried[-1], pivot_inv[block_index - 1])
        carried.append(blocks[:, block_index] - apply_block(pivoted, lower_block[block_index - 1]))
    solved = [apply_block(carried[-1], pivot_inv[block_count - 1])]
    for block_index in range(block_count - 2, -1, -1):
        remainder = carried[block_index] - apply_block(solved[0], upper_block[block_index])
        solved.insert(0, apply_block(remainder, pivot_inv[block_index]))
    return jnp.concatenate(solved, axis=1)

def reference(strip_fields, strip_riser, strip_node, riser_owner, pivot_inv, lower_block, upper_block):
    kernels = make_kernels(CELLS)
    per_group = S_DEV * N_STRIP
    group_of = jnp.arange(STRIPS, dtype=jnp.int32) // per_group
    owner_index = riser_owner[group_of, strip_riser[:, 0]].astype(jnp.int32)
    slot_index = (group_of * N_STRIP + owner_index).astype(jnp.int32)
    top_taper = 1.0 - jnp.arange(NODES, dtype=jnp.float32) / NODES
    shaped = strip_fields.reshape(3, N_GROUP, per_group, CELLS, CELLS)
    vorticity = shaped[0]
    motion = jnp.zeros((N_GROUP, per_group, 2 * NSUB), jnp.float32)
    displacement = jnp.zeros((SLOTS, 2 * NSUB, NODES), jnp.float32)
    for coupled_step in range(COUPLED):

        def one_group(group_inputs):
            return strip_step(group_inputs[0], group_inputs[1], group_inputs[2], group_inputs[3], kernels, NSUB)
        vorticity, force_rows = lax.map(one_group, (vorticity, shaped[1], shaped[2], motion))
        flat_rows = force_rows.reshape(STRIPS, 2 * NSUB)
        offset = lax.optimization_barrier(jnp.sum(flat_rows[:, NSUB:], axis=0)) / jnp.sqrt(jnp.float32(STRIPS))
        beam_load = jnp.zeros((SLOTS, 2 * NSUB, NODES), jnp.float32).at[slot_index, :, strip_node].add(flat_rows)
        displacement = lax.map(lambda solve_inputs: beam_solve(solve_inputs[0], solve_inputs[1], solve_inputs[2], solve_inputs[3]), (beam_load, pivot_inv, lower_block, upper_block))
        displacement = displacement.at[:, NSUB:, :].add(offset[None, :, None] * top_taper[None, None, :])
        if coupled_step + 1 < COUPLED:
            motion = displacement[slot_index, :, strip_node].reshape(N_GROUP, per_group, 2 * NSUB)
    return (vorticity.reshape(STRIPS, CELLS, CELLS), displacement)
```

```python
import jax
import jax.numpy as jnp
from jax import lax
from jax.sharding import PartitionSpec as P

NSUB = 8
COUPLED = 2


TIME_STEP = 0.25
VISCOSITY = 0.05
COUPLING = 0.5
EXACT_DOT = lax.Precision.HIGHEST


def make_kernels(grid_cells):
    centre = jnp.arange(grid_cells, dtype=jnp.float32) - grid_cells / 2.0 + 0.5
    near_x = (centre / (grid_cells / 16.0))[None, :]
    near_y = (centre / (grid_cells / 16.0))[:, None]
    bell_near = jnp.exp(-(near_x * near_x + near_y * near_y) / 2.0)
    source_x = -near_x * bell_near
    source_y = -near_y * bell_near
    wide_x = (centre / (grid_cells / 8.0))[None, :]
    wide_y = (centre / (grid_cells / 8.0))[:, None]
    bell_wide = jnp.exp(-(wide_x * wide_x + wide_y * wide_y) / 2.0)
    lift_kernel = -wide_x * bell_wide
    drag_kernel = wide_y * bell_wide
    lift_kernel = lift_kernel / jnp.sqrt(jnp.sum(lift_kernel * lift_kernel))
    drag_kernel = drag_kernel / jnp.sqrt(jnp.sum(drag_kernel * drag_kernel))
    return (source_x, source_y, lift_kernel, drag_kernel)


def strip_step(vorticity, flow_x, flow_y, motion, kernels, substeps):
    source_x, source_y, lift_kernel, drag_kernel = kernels
    halves = motion.reshape(motion.shape[0], 2, substeps)
    earlier = jnp.concatenate([jnp.zeros_like(halves[:, :, :1]), halves[:, :, :-1]], axis=2)
    velocity = halves - earlier
    lift_rows = []
    drag_rows = []
    for substep in range(substeps):
        right_cell = jnp.roll(vorticity, -1, axis=2)
        left_cell = jnp.roll(vorticity, 1, axis=2)
        upper_cell = jnp.roll(vorticity, -1, axis=1)
        lower_cell = jnp.roll(vorticity, 1, axis=1)
        laplacian = right_cell + left_cell + upper_cell + lower_cell - 4.0 * vorticity
        tendency = (
            VISCOSITY * laplacian
            - flow_x * (0.5 * (right_cell - left_cell))
            - flow_y * (0.5 * (upper_cell - lower_cell))
        )
        forcing = (
            velocity[:, 0, substep][:, None, None] * source_x
            - velocity[:, 1, substep][:, None, None] * source_y
        )
        vorticity = vorticity + TIME_STEP * tendency + COUPLING * forcing
        lift_rows.append(jnp.sum(vorticity * lift_kernel, axis=(1, 2)))
        drag_rows.append(jnp.sum(vorticity * drag_kernel, axis=(1, 2)))
    return (vorticity, jnp.stack(lift_rows + drag_rows, axis=1))


def apply_block(vectors, matrix):
    return lax.dot_general(vectors, matrix, (((1,), (1,)), ((), ())), precision=EXACT_DOT)


def first_contract(left_side, right_side):
    return lax.dot_general(left_side, right_side, (((0,), (0,)), ((), ())), precision=EXACT_DOT)


def beam_solve(beam_load, pivot_inv, lower_block, upper_block):
    block_count = pivot_inv.shape[0]
    block_size = pivot_inv.shape[1]
    blocks = beam_load.reshape(beam_load.shape[0], block_count, block_size)
    carried = [blocks[:, 0]]
    for block_index in range(1, block_count):
        pivoted = apply_block(carried[-1], pivot_inv[block_index - 1])
        carried.append(blocks[:, block_index] - apply_block(pivoted, lower_block[block_index - 1]))
    solved = [apply_block(carried[-1], pivot_inv[block_count - 1])]
    for block_index in range(block_count - 2, -1, -1):
        remainder = carried[block_index] - apply_block(solved[0], upper_block[block_index])
        solved.insert(0, apply_block(remainder, pivot_inv[block_index]))
    return jnp.concatenate(solved, axis=1)


def local(strip_fields, strip_riser, strip_node, riser_owner, pivot_inv, lower_block, upper_block):
    position = lax.axis_index("strip")
    group_position = lax.axis_index("group")
    group_count = lax.axis_size("group")
    devices = lax.axis_size("strip") * group_count
    per_device = strip_fields.shape[1]
    grid_cells = strip_fields.shape[2]
    node_count = pivot_inv.shape[1] * pivot_inv.shape[2]
    riser_count = riser_owner.shape[1]
    group_strips = strip_node.shape[0]
    substeps = NSUB
    total_strips = per_device * devices
    kernels = make_kernels(grid_cells)
    riser_match = (
        strip_riser[:, 0][:, None] == jnp.arange(riser_count, dtype=jnp.int32)[None, :]
    ).astype(jnp.int32)
    owner_index = jnp.sum(riser_match * riser_owner[0][None, :], axis=1)
    owned_here = (owner_index == position).astype(jnp.float32)
    node_onehot = (
        strip_node[:, None] == jnp.arange(node_count, dtype=jnp.int32)[None, :]
    ).astype(jnp.float32)
    local_node = lax.dynamic_slice_in_dim(strip_node, position * per_device, per_device)
    top_taper = 1.0 - jnp.arange(node_count, dtype=jnp.float32) / node_count
    local_taper = 1.0 - local_node.astype(jnp.float32) / node_count

    unit_response = beam_solve(
        node_onehot * owned_here[:, None], pivot_inv[0], lower_block[0], upper_block[0]
    )
    coupling = apply_block(node_onehot, unit_response) * owned_here[:, None]
    coupling_out = jnp.where(
        jnp.arange(group_count)[:, None, None] == group_position, coupling[None], 0.0
    ).reshape(group_count * group_strips, group_strips)

    vorticity = strip_fields[0]
    flow_x = strip_fields[1]
    flow_y = strip_fields[2]
    motion = jnp.zeros((per_device, 2 * substeps), jnp.float32)
    for coupled_step in range(COUPLED):
        vorticity, force_rows = strip_step(vorticity, flow_x, flow_y, motion, kernels, substeps)
        sent = jnp.tile(force_rows, (devices, 1))
        if coupled_step + 1 < COUPLED:
            sent = jnp.concatenate([sent, coupling_out], axis=1)
        received = lax.all_to_all(sent, ("group", "strip"), 0, 0, tiled=True)
        every_force = received[:, : 2 * substeps]
        offset = jnp.sum(every_force[:, substeps:], axis=0) / jnp.sqrt(jnp.float32(total_strips))
        group_force = lax.dynamic_slice_in_dim(every_force, group_position * group_strips, group_strips)
        if coupled_step + 1 < COUPLED:
            my_coupling = jnp.sum(
                received[:, 2 * substeps :].reshape(devices, per_device, group_strips), axis=0
            )
            motion = lax.dot_general(
                my_coupling, group_force, (((1,), (0,)), ((), ())), precision=EXACT_DOT
            )
            motion = motion.at[:, substeps:].add(local_taper[:, None] * offset[None, :])
        else:
            displacement = first_contract(group_force * owned_here[:, None], unit_response)
            displacement = displacement.at[substeps:, :].add(offset[:, None] * top_taper[None, :])
    return (vorticity, displacement[None])


def solution(mesh):
    in_specs = (
        P(None, ("group", "strip"), None, None),
        P("group", None),
        P("group"),
        P("group", None),
        P(("group", "strip"), None, None, None),
        P(("group", "strip"), None, None, None),
        P(("group", "strip"), None, None, None),
    )
    out_specs = (P(("group", "strip"), None, None), P(("group", "strip"), None, None))
    return jax.shard_map(local, mesh=mesh, in_specs=in_specs, out_specs=out_specs, check_vma=False)
```

```python
import jax
import jax.numpy as jnp
from jax import lax
from jax.sharding import PartitionSpec as P

NSUB = 8
COUPLED = 2


TIME_STEP = 0.25
VISCOSITY = 0.05
COUPLING = 0.5
EXACT_DOT = lax.Precision.HIGHEST


def make_kernels(grid_cells):
    centre = jnp.arange(grid_cells, dtype=jnp.float32) - grid_cells / 2.0 + 0.5
    near_x = (centre / (grid_cells / 16.0))[None, :]
    near_y = (centre / (grid_cells / 16.0))[:, None]
    bell_near = jnp.exp(-(near_x * near_x + near_y * near_y) / 2.0)
    source_x = -near_x * bell_near
    source_y = -near_y * bell_near
    wide_x = (centre / (grid_cells / 8.0))[None, :]
    wide_y = (centre / (grid_cells / 8.0))[:, None]
    bell_wide = jnp.exp(-(wide_x * wide_x + wide_y * wide_y) / 2.0)
    lift_kernel = -wide_x * bell_wide
    drag_kernel = wide_y * bell_wide
    lift_kernel = lift_kernel / jnp.sqrt(jnp.sum(lift_kernel * lift_kernel))
    drag_kernel = drag_kernel / jnp.sqrt(jnp.sum(drag_kernel * drag_kernel))
    return (source_x, source_y, lift_kernel, drag_kernel)


def advance(vorticity, flow_x, flow_y):
    right_cell = jnp.roll(vorticity, -1, axis=2)
    left_cell = jnp.roll(vorticity, 1, axis=2)
    upper_cell = jnp.roll(vorticity, -1, axis=1)
    lower_cell = jnp.roll(vorticity, 1, axis=1)
    laplacian = right_cell + left_cell + upper_cell + lower_cell - 4.0 * vorticity
    tendency = (
        VISCOSITY * laplacian
        - flow_x * (0.5 * (right_cell - left_cell))
        - flow_y * (0.5 * (upper_cell - lower_cell))
    )
    return vorticity + TIME_STEP * tendency


def kernel_sums(fields, lift_kernel, drag_kernel):
    stacked = jnp.stack(fields, axis=0)
    lift = jnp.sum(stacked * lift_kernel, axis=(2, 3))
    drag = jnp.sum(stacked * drag_kernel, axis=(2, 3))
    return lift, drag


def free_run(vorticity, flow_x, flow_y, kernels, substeps):
    _, _, lift_kernel, drag_kernel = kernels
    fields = []
    for substep in range(substeps):
        vorticity = advance(vorticity, flow_x, flow_y)
        fields.append(vorticity)
    lift, drag = kernel_sums(fields, lift_kernel, drag_kernel)
    return vorticity, jnp.concatenate([lift.T, drag.T], axis=1)


def source_responses(flow_x, flow_y, kernels, substeps):
    source_x, source_y, lift_kernel, drag_kernel = kernels
    shape = flow_x.shape
    carried_x = [jnp.broadcast_to(source_x, shape)]
    carried_y = [jnp.broadcast_to(source_y, shape)]
    for _ in range(substeps - 1):
        carried_x.append(advance(carried_x[-1], flow_x, flow_y))
        carried_y.append(advance(carried_y[-1], flow_x, flow_y))
    lift, drag = kernel_sums(carried_x + carried_y, lift_kernel, drag_kernel)
    return carried_x, carried_y, lift, drag


def forced_rows(free_rows, motion, response_lift, response_drag, substeps):
    halves = motion.reshape(motion.shape[0], 2, substeps)
    earlier = jnp.concatenate([jnp.zeros_like(halves[:, :, :1]), halves[:, :, :-1]], axis=2)
    velocity = halves - earlier
    later = jnp.arange(substeps)[:, None] - jnp.arange(substeps)[None, :]
    reach = jnp.clip(later, 0, substeps - 1)
    mask = (later >= 0).astype(jnp.float32)
    rows = []
    for response in (response_lift, response_drag):
        toeplitz_x = response[:substeps][reach] * mask[:, :, None]
        toeplitz_y = response[substeps:][reach] * mask[:, :, None]
        gain = jnp.sum(
            toeplitz_x * velocity[:, 0, :].T[None, :, :] - toeplitz_y * velocity[:, 1, :].T[None, :, :],
            axis=1,
        )
        rows.append(COUPLING * gain.T)
    return free_rows + jnp.concatenate(rows, axis=1), velocity


def forced_field(free_field, velocity, carried_x, carried_y, substeps):
    field = free_field
    for substep in range(substeps):
        field = field + COUPLING * (
            velocity[:, 0, substep][:, None, None] * carried_x[substeps - 1 - substep]
            - velocity[:, 1, substep][:, None, None] * carried_y[substeps - 1 - substep]
        )
    return field


def apply_block(vectors, matrix):
    return lax.dot_general(vectors, matrix, (((1,), (1,)), ((), ())), precision=EXACT_DOT)


def first_contract(left_side, right_side):
    return lax.dot_general(left_side, right_side, (((0,), (0,)), ((), ())), precision=EXACT_DOT)


def beam_solve(beam_load, pivot_inv, lower_block, upper_block):
    block_count = pivot_inv.shape[0]
    block_size = pivot_inv.shape[1]
    blocks = beam_load.reshape(beam_load.shape[0], block_count, block_size)
    carried = [blocks[:, 0]]
    for block_index in range(1, block_count):
        pivoted = apply_block(carried[-1], pivot_inv[block_index - 1])
        carried.append(blocks[:, block_index] - apply_block(pivoted, lower_block[block_index - 1]))
    solved = [apply_block(carried[-1], pivot_inv[block_count - 1])]
    for block_index in range(block_count - 2, -1, -1):
        remainder = carried[block_index] - apply_block(solved[0], upper_block[block_index])
        solved.insert(0, apply_block(remainder, pivot_inv[block_index]))
    return jnp.concatenate(solved, axis=1)


def local(strip_fields, strip_riser, strip_node, riser_owner, pivot_inv, lower_block, upper_block):
    position = lax.axis_index("strip")
    group_position = lax.axis_index("group")
    group_count = lax.axis_size("group")
    devices = lax.axis_size("strip") * group_count
    per_device = strip_fields.shape[1]
    grid_cells = strip_fields.shape[2]
    node_count = pivot_inv.shape[1] * pivot_inv.shape[2]
    riser_count = riser_owner.shape[1]
    group_strips = strip_node.shape[0]
    substeps = NSUB
    total_strips = per_device * devices
    kernels = make_kernels(grid_cells)
    riser_match = (
        strip_riser[:, 0][:, None] == jnp.arange(riser_count, dtype=jnp.int32)[None, :]
    ).astype(jnp.int32)
    owner_index = jnp.sum(riser_match * riser_owner[0][None, :], axis=1)
    owned_here = (owner_index == position).astype(jnp.float32)
    node_onehot = (
        strip_node[:, None] == jnp.arange(node_count, dtype=jnp.int32)[None, :]
    ).astype(jnp.float32)
    local_node = lax.dynamic_slice_in_dim(strip_node, position * per_device, per_device)
    top_taper = 1.0 - jnp.arange(node_count, dtype=jnp.float32) / node_count
    local_taper = 1.0 - local_node.astype(jnp.float32) / node_count

    unit_response = beam_solve(
        node_onehot * owned_here[:, None], pivot_inv[0], lower_block[0], upper_block[0]
    )
    coupling = apply_block(node_onehot, unit_response) * owned_here[:, None]
    coupling_out = jnp.where(
        jnp.arange(group_count)[:, None, None] == group_position, coupling[None], 0.0
    ).reshape(group_count * group_strips, group_strips)

    vorticity = strip_fields[0]
    flow_x = strip_fields[1]
    flow_y = strip_fields[2]
    vorticity, force_rows = free_run(vorticity, flow_x, flow_y, kernels, substeps)
    sent = jnp.concatenate([jnp.tile(force_rows, (devices, 1)), coupling_out], axis=1)
    received = lax.all_to_all(sent, ("group", "strip"), 0, 0, tiled=True)
    free_field, free_rows = free_run(vorticity, flow_x, flow_y, kernels, substeps)
    carried_x, carried_y, response_lift, response_drag = source_responses(flow_x, flow_y, kernels, substeps)
    every_force = received[:, : 2 * substeps]
    offset = jnp.sum(every_force[:, substeps:], axis=0) / jnp.sqrt(jnp.float32(total_strips))
    group_force = lax.dynamic_slice_in_dim(every_force, group_position * group_strips, group_strips)
    my_coupling = jnp.sum(received[:, 2 * substeps :].reshape(devices, per_device, group_strips), axis=0)
    motion = lax.dot_general(my_coupling, group_force, (((1,), (0,)), ((), ())), precision=EXACT_DOT)
    motion = motion.at[:, substeps:].add(local_taper[:, None] * offset[None, :])
    force_rows, velocity = forced_rows(free_rows, motion, response_lift, response_drag, substeps)
    received = lax.all_to_all(jnp.tile(force_rows, (devices, 1)), ("group", "strip"), 0, 0, tiled=True)
    vorticity = forced_field(free_field, velocity, carried_x, carried_y, substeps)
    offset = jnp.sum(received[:, substeps:], axis=0) / jnp.sqrt(jnp.float32(total_strips))
    group_force = lax.dynamic_slice_in_dim(received, group_position * group_strips, group_strips)
    displacement = first_contract(group_force * owned_here[:, None], unit_response)
    displacement = displacement.at[substeps:, :].add(offset[:, None] * top_taper[None, :])
    return (vorticity, displacement[None])


def solution(mesh):
    in_specs = (
        P(None, ("group", "strip"), None, None),
        P("group", None),
        P("group"),
        P("group", None),
        P(("group", "strip"), None, None, None),
        P(("group", "strip"), None, None, None),
        P(("group", "strip"), None, None, None),
    )
    out_specs = (P(("group", "strip"), None, None), P(("group", "strip"), None, None))
    return jax.shard_map(local, mesh=mesh, in_specs=in_specs, out_specs=out_specs, check_vma=False)
```

```python
import jax
import jax.numpy as jnp
from jax import lax
from jax.sharding import PartitionSpec as P
from jax.experimental import pallas as pl
from jax.experimental.pallas import tpu as pltpu

NSUB = 8
COUPLED = 2


TIME_STEP = 0.25
VISCOSITY = 0.05
COUPLING = 0.5
EXACT_DOT = lax.Precision.HIGHEST


def make_kernels(grid_cells):
    centre = jnp.arange(grid_cells, dtype=jnp.float32) - grid_cells / 2.0 + 0.5
    near_x = (centre / (grid_cells / 16.0))[None, :]
    near_y = (centre / (grid_cells / 16.0))[:, None]
    bell_near = jnp.exp(-(near_x * near_x + near_y * near_y) / 2.0)
    source_x = -near_x * bell_near
    source_y = -near_y * bell_near
    wide_x = (centre / (grid_cells / 8.0))[None, :]
    wide_y = (centre / (grid_cells / 8.0))[:, None]
    bell_wide = jnp.exp(-(wide_x * wide_x + wide_y * wide_y) / 2.0)
    lift_kernel = -wide_x * bell_wide
    drag_kernel = wide_y * bell_wide
    lift_kernel = lift_kernel / jnp.sqrt(jnp.sum(lift_kernel * lift_kernel))
    drag_kernel = drag_kernel / jnp.sqrt(jnp.sum(drag_kernel * drag_kernel))
    return (source_x, source_y, lift_kernel, drag_kernel)


def strip_step(vorticity, flow_x, flow_y, motion, kernels, substeps):
    source_x, source_y, lift_kernel, drag_kernel = kernels
    halves = motion.reshape(motion.shape[0], 2, substeps)
    earlier = jnp.concatenate([jnp.zeros_like(halves[:, :, :1]), halves[:, :, :-1]], axis=2)
    velocity = halves - earlier
    lift_rows = []
    drag_rows = []
    for substep in range(substeps):
        right_cell = jnp.roll(vorticity, -1, axis=2)
        left_cell = jnp.roll(vorticity, 1, axis=2)
        upper_cell = jnp.roll(vorticity, -1, axis=1)
        lower_cell = jnp.roll(vorticity, 1, axis=1)
        laplacian = right_cell + left_cell + upper_cell + lower_cell - 4.0 * vorticity
        tendency = (
            VISCOSITY * laplacian
            - flow_x * (0.5 * (right_cell - left_cell))
            - flow_y * (0.5 * (upper_cell - lower_cell))
        )
        forcing = (
            velocity[:, 0, substep][:, None, None] * source_x
            - velocity[:, 1, substep][:, None, None] * source_y
        )
        vorticity = vorticity + TIME_STEP * tendency + COUPLING * forcing
        lift_rows.append(jnp.sum(vorticity * lift_kernel, axis=(1, 2)))
        drag_rows.append(jnp.sum(vorticity * drag_kernel, axis=(1, 2)))
    return (vorticity, jnp.stack(lift_rows + drag_rows, axis=1))


def stencil_kernel(velocity_ref, vorticity_ref, flow_x_ref, flow_y_ref, source_x_ref, source_y_ref, lift_ref, drag_ref, out_ref, rows_ref, *, substeps):
    strip = pl.program_id(0)
    vorticity = vorticity_ref[0, 0]
    flow_x = flow_x_ref[0, 0]
    flow_y = flow_y_ref[0, 0]
    rows_across, cols_across = vorticity.shape
    lane = lax.broadcasted_iota(jnp.int32, (1, 2 * substeps), 1)
    row = jnp.zeros((1, 2 * substeps), jnp.float32)
    for substep in range(substeps):
        right_cell = pltpu.roll(vorticity, cols_across - 1, 1)
        left_cell = pltpu.roll(vorticity, 1, 1)
        upper_cell = pltpu.roll(vorticity, rows_across - 1, 0)
        lower_cell = pltpu.roll(vorticity, 1, 0)
        laplacian = right_cell + left_cell + upper_cell + lower_cell - 4.0 * vorticity
        tendency = (
            VISCOSITY * laplacian
            - flow_x * (0.5 * (right_cell - left_cell))
            - flow_y * (0.5 * (upper_cell - lower_cell))
        )
        forcing = (
            velocity_ref[strip, substep] * source_x_ref[...]
            - velocity_ref[strip, substeps + substep] * source_y_ref[...]
        )
        vorticity = vorticity + TIME_STEP * tendency + COUPLING * forcing
        lift = jnp.sum(jnp.sum(vorticity * lift_ref[...], axis=0, keepdims=True), axis=1, keepdims=True)
        drag = jnp.sum(jnp.sum(vorticity * drag_ref[...], axis=0, keepdims=True), axis=1, keepdims=True)
        row = row + jnp.where(lane == substep, lift, 0.0) + jnp.where(lane == substeps + substep, drag, 0.0)
    out_ref[0] = vorticity
    rows_ref[0] = row


def strip_step_kernel(strip_fields, vorticity, motion, kernels, substeps):
    source_x, source_y, lift_kernel, drag_kernel = kernels
    strips, cells_y, cells_x = strip_fields.shape[1:]
    halves = motion.reshape(strips, 2, substeps)
    earlier = jnp.concatenate([jnp.zeros_like(halves[:, :, :1]), halves[:, :, :-1]], axis=2)
    velocity = (halves - earlier).reshape(strips, 2 * substeps)
    plane = pl.BlockSpec((cells_y, cells_x), lambda s: (0, 0))

    def field(index):
        return pl.BlockSpec((1, 1, cells_y, cells_x), lambda s: (index, s, 0, 0))

    new_vorticity, rows = pl.pallas_call(
        lambda *refs: stencil_kernel(*refs, substeps=substeps),
        grid=(strips,),
        in_specs=[
            pl.BlockSpec(memory_space=pltpu.SMEM),
            field(0), field(1), field(2),
            plane, plane, plane, plane,
        ],
        out_specs=[
            pl.BlockSpec((1, cells_y, cells_x), lambda s: (s, 0, 0)),
            pl.BlockSpec((1, 1, 2 * substeps), lambda s: (s, 0, 0)),
        ],
        out_shape=[
            jax.ShapeDtypeStruct((strips, cells_y, cells_x), jnp.float32),
            jax.ShapeDtypeStruct((strips, 1, 2 * substeps), jnp.float32),
        ],
        name="strip_stencil",
    )(velocity, vorticity, strip_fields, strip_fields, source_x, source_y, lift_kernel, drag_kernel)
    return new_vorticity, rows[:, 0, :]


def apply_block(vectors, matrix):
    return lax.dot_general(vectors, matrix, (((1,), (1,)), ((), ())), precision=EXACT_DOT)


def first_contract(left_side, right_side):
    return lax.dot_general(left_side, right_side, (((0,), (0,)), ((), ())), precision=EXACT_DOT)


def beam_solve(beam_load, pivot_inv, lower_block, upper_block):
    block_count = pivot_inv.shape[0]
    block_size = pivot_inv.shape[1]
    blocks = beam_load.reshape(beam_load.shape[0], block_count, block_size)
    carried = [blocks[:, 0]]
    for block_index in range(1, block_count):
        pivoted = apply_block(carried[-1], pivot_inv[block_index - 1])
        carried.append(blocks[:, block_index] - apply_block(pivoted, lower_block[block_index - 1]))
    solved = [apply_block(carried[-1], pivot_inv[block_count - 1])]
    for block_index in range(block_count - 2, -1, -1):
        remainder = carried[block_index] - apply_block(solved[0], upper_block[block_index])
        solved.insert(0, apply_block(remainder, pivot_inv[block_index]))
    return jnp.concatenate(solved, axis=1)


def local(strip_fields, strip_riser, strip_node, riser_owner, pivot_inv, lower_block, upper_block):
    position = lax.axis_index("strip")
    group_position = lax.axis_index("group")
    group_count = lax.axis_size("group")
    devices = lax.axis_size("strip") * group_count
    per_device = strip_fields.shape[1]
    grid_cells = strip_fields.shape[2]
    node_count = pivot_inv.shape[1] * pivot_inv.shape[2]
    riser_count = riser_owner.shape[1]
    group_strips = strip_node.shape[0]
    substeps = NSUB
    total_strips = per_device * devices
    kernels = make_kernels(grid_cells)
    riser_match = (
        strip_riser[:, 0][:, None] == jnp.arange(riser_count, dtype=jnp.int32)[None, :]
    ).astype(jnp.int32)
    owner_index = jnp.sum(riser_match * riser_owner[0][None, :], axis=1)
    owned_here = (owner_index == position).astype(jnp.float32)
    node_onehot = (
        strip_node[:, None] == jnp.arange(node_count, dtype=jnp.int32)[None, :]
    ).astype(jnp.float32)
    local_node = lax.dynamic_slice_in_dim(strip_node, position * per_device, per_device)
    top_taper = 1.0 - jnp.arange(node_count, dtype=jnp.float32) / node_count
    local_taper = 1.0 - local_node.astype(jnp.float32) / node_count

    unit_response = beam_solve(
        node_onehot * owned_here[:, None], pivot_inv[0], lower_block[0], upper_block[0]
    )
    coupling = apply_block(node_onehot, unit_response) * owned_here[:, None]
    coupling_out = jnp.where(
        jnp.arange(group_count)[:, None, None] == group_position, coupling[None], 0.0
    ).reshape(group_count * group_strips, group_strips)

    vorticity = strip_fields
    motion = jnp.zeros((per_device, 2 * substeps), jnp.float32)
    for coupled_step in range(COUPLED):
        vorticity, force_rows = strip_step_kernel(strip_fields, vorticity, motion, kernels, substeps)
        sent = jnp.tile(force_rows, (devices, 1))
        if coupled_step + 1 < COUPLED:
            sent = jnp.concatenate([sent, coupling_out], axis=1)
        received = lax.all_to_all(sent, ("group", "strip"), 0, 0, tiled=True)
        every_force = received[:, : 2 * substeps]
        offset = jnp.sum(every_force[:, substeps:], axis=0) / jnp.sqrt(jnp.float32(total_strips))
        group_force = lax.dynamic_slice_in_dim(every_force, group_position * group_strips, group_strips)
        if coupled_step + 1 < COUPLED:
            my_coupling = jnp.sum(
                received[:, 2 * substeps :].reshape(devices, per_device, group_strips), axis=0
            )
            motion = lax.dot_general(
                my_coupling, group_force, (((1,), (0,)), ((), ())), precision=EXACT_DOT
            )
            motion = motion.at[:, substeps:].add(local_taper[:, None] * offset[None, :])
            vorticity = vorticity[None]
        else:
            displacement = first_contract(group_force * owned_here[:, None], unit_response)
            displacement = displacement.at[substeps:, :].add(offset[:, None] * top_taper[None, :])
    return (vorticity, displacement[None])


def solution(mesh):
    in_specs = (
        P(None, ("group", "strip"), None, None),
        P("group", None),
        P("group"),
        P("group", None),
        P(("group", "strip"), None, None, None),
        P(("group", "strip"), None, None, None),
        P(("group", "strip"), None, None, None),
    )
    out_specs = (P(("group", "strip"), None, None), P(("group", "strip"), None, None))
    return jax.shard_map(local, mesh=mesh, in_specs=in_specs, out_specs=out_specs, check_vma=False)
```

```python
import jax
import jax.numpy as jnp
from jax import lax
from jax.sharding import PartitionSpec as P
from jax.experimental import pallas as pl
from jax.experimental.pallas import tpu as pltpu

NSUB = 8
COUPLED = 2


TIME_STEP = 0.25
VISCOSITY = 0.05
COUPLING = 0.5
EXACT_DOT = lax.Precision.HIGHEST


def make_kernels(grid_cells):
    centre = jnp.arange(grid_cells, dtype=jnp.float32) - grid_cells / 2.0 + 0.5
    near_x = (centre / (grid_cells / 16.0))[None, :]
    near_y = (centre / (grid_cells / 16.0))[:, None]
    bell_near = jnp.exp(-(near_x * near_x + near_y * near_y) / 2.0)
    source_x = -near_x * bell_near
    source_y = -near_y * bell_near
    wide_x = (centre / (grid_cells / 8.0))[None, :]
    wide_y = (centre / (grid_cells / 8.0))[:, None]
    bell_wide = jnp.exp(-(wide_x * wide_x + wide_y * wide_y) / 2.0)
    lift_kernel = -wide_x * bell_wide
    drag_kernel = wide_y * bell_wide
    lift_kernel = lift_kernel / jnp.sqrt(jnp.sum(lift_kernel * lift_kernel))
    drag_kernel = drag_kernel / jnp.sqrt(jnp.sum(drag_kernel * drag_kernel))
    return (source_x, source_y, lift_kernel, drag_kernel)


def strip_step(vorticity, flow_x, flow_y, motion, kernels, substeps):
    source_x, source_y, lift_kernel, drag_kernel = kernels
    halves = motion.reshape(motion.shape[0], 2, substeps)
    earlier = jnp.concatenate([jnp.zeros_like(halves[:, :, :1]), halves[:, :, :-1]], axis=2)
    velocity = halves - earlier
    lift_rows = []
    drag_rows = []
    for substep in range(substeps):
        right_cell = jnp.roll(vorticity, -1, axis=2)
        left_cell = jnp.roll(vorticity, 1, axis=2)
        upper_cell = jnp.roll(vorticity, -1, axis=1)
        lower_cell = jnp.roll(vorticity, 1, axis=1)
        laplacian = right_cell + left_cell + upper_cell + lower_cell - 4.0 * vorticity
        tendency = (
            VISCOSITY * laplacian
            - flow_x * (0.5 * (right_cell - left_cell))
            - flow_y * (0.5 * (upper_cell - lower_cell))
        )
        forcing = (
            velocity[:, 0, substep][:, None, None] * source_x
            - velocity[:, 1, substep][:, None, None] * source_y
        )
        vorticity = vorticity + TIME_STEP * tendency + COUPLING * forcing
        lift_rows.append(jnp.sum(vorticity * lift_kernel, axis=(1, 2)))
        drag_rows.append(jnp.sum(vorticity * drag_kernel, axis=(1, 2)))
    return (vorticity, jnp.stack(lift_rows + drag_rows, axis=1))


def stencil_kernel(velocity_ref, vorticity_ref, flow_x_ref, flow_y_ref, source_x_ref, source_y_ref, lift_ref, drag_ref, out_ref, rows_ref, *, substeps):
    strip = pl.program_id(0)
    vorticity = vorticity_ref[0, 0]
    flow_x = flow_x_ref[0, 0]
    flow_y = flow_y_ref[0, 0]
    rows_across, cols_across = vorticity.shape
    lane = lax.broadcasted_iota(jnp.int32, (1, 2 * substeps), 1)
    row = jnp.zeros((1, 2 * substeps), jnp.float32)
    for substep in range(substeps):
        right_cell = pltpu.roll(vorticity, cols_across - 1, 1)
        left_cell = pltpu.roll(vorticity, 1, 1)
        upper_cell = pltpu.roll(vorticity, rows_across - 1, 0)
        lower_cell = pltpu.roll(vorticity, 1, 0)
        laplacian = right_cell + left_cell + upper_cell + lower_cell - 4.0 * vorticity
        tendency = (
            VISCOSITY * laplacian
            - flow_x * (0.5 * (right_cell - left_cell))
            - flow_y * (0.5 * (upper_cell - lower_cell))
        )
        forcing = (
            velocity_ref[strip, substep] * source_x_ref[...]
            - velocity_ref[strip, substeps + substep] * source_y_ref[...]
        )
        vorticity = vorticity + TIME_STEP * tendency + COUPLING * forcing
        lift = jnp.sum(jnp.sum(vorticity * lift_ref[...], axis=0, keepdims=True), axis=1, keepdims=True)
        drag = jnp.sum(jnp.sum(vorticity * drag_ref[...], axis=0, keepdims=True), axis=1, keepdims=True)
        row = row + jnp.where(lane == substep, lift, 0.0) + jnp.where(lane == substeps + substep, drag, 0.0)
    out_ref[0] = vorticity
    rows_ref[0] = row


def strip_step_kernel(strip_fields, vorticity, motion, kernels, substeps):
    source_x, source_y, lift_kernel, drag_kernel = kernels
    strips, cells_y, cells_x = strip_fields.shape[1:]
    halves = motion.reshape(strips, 2, substeps)
    earlier = jnp.concatenate([jnp.zeros_like(halves[:, :, :1]), halves[:, :, :-1]], axis=2)
    velocity = (halves - earlier).reshape(strips, 2 * substeps)
    plane = pl.BlockSpec((cells_y, cells_x), lambda s: (0, 0))

    def field(index):
        return pl.BlockSpec((1, 1, cells_y, cells_x), lambda s: (index, s, 0, 0))

    new_vorticity, rows = pl.pallas_call(
        lambda *refs: stencil_kernel(*refs, substeps=substeps),
        grid=(strips,),
        in_specs=[
            pl.BlockSpec(memory_space=pltpu.SMEM),
            field(0), field(1), field(2),
            plane, plane, plane, plane,
        ],
        out_specs=[
            pl.BlockSpec((1, cells_y, cells_x), lambda s: (s, 0, 0)),
            pl.BlockSpec((1, 1, 2 * substeps), lambda s: (s, 0, 0)),
        ],
        out_shape=[
            jax.ShapeDtypeStruct((strips, cells_y, cells_x), jnp.float32),
            jax.ShapeDtypeStruct((strips, 1, 2 * substeps), jnp.float32),
        ],
        name="strip_stencil",
    )(velocity, vorticity, strip_fields, strip_fields, source_x, source_y, lift_kernel, drag_kernel)
    return new_vorticity, rows[:, 0, :]


def apply_block(vectors, matrix):
    return lax.dot_general(vectors, matrix, (((1,), (1,)), ((), ())), precision=EXACT_DOT)


def first_contract(left_side, right_side):
    return lax.dot_general(left_side, right_side, (((0,), (0,)), ((), ())), precision=EXACT_DOT)


def beam_solve(beam_load, pivot_inv, lower_block, upper_block):
    block_count = pivot_inv.shape[0]
    block_size = pivot_inv.shape[1]
    blocks = beam_load.reshape(beam_load.shape[0], block_count, block_size)
    carried = [blocks[:, 0]]
    for block_index in range(1, block_count):
        pivoted = apply_block(carried[-1], pivot_inv[block_index - 1])
        carried.append(blocks[:, block_index] - apply_block(pivoted, lower_block[block_index - 1]))
    solved = [apply_block(carried[-1], pivot_inv[block_count - 1])]
    for block_index in range(block_count - 2, -1, -1):
        remainder = carried[block_index] - apply_block(solved[0], upper_block[block_index])
        solved.insert(0, apply_block(remainder, pivot_inv[block_index]))
    return jnp.concatenate(solved, axis=1)


def solve_kernel(load_ref, pivot_ref, lower_ref, upper_ref, out_ref):
    block_count = pivot_ref.shape[1]
    block_size = pivot_ref.shape[2]

    def apply(vectors, matrix):
        return lax.dot_general(
            vectors, matrix, (((1,), (1,)), ((), ())),
            precision=EXACT_DOT, preferred_element_type=jnp.float32,
        )

    carried = [load_ref[:, 0:block_size]]
    for block_index in range(1, block_count):
        pivoted = apply(carried[-1], pivot_ref[0, block_index - 1])
        carried.append(
            load_ref[:, block_index * block_size:(block_index + 1) * block_size]
            - apply(pivoted, lower_ref[0, block_index - 1])
        )
    solved = apply(carried[-1], pivot_ref[0, block_count - 1])
    out_ref[:, (block_count - 1) * block_size:] = solved
    for block_index in range(block_count - 2, -1, -1):
        remainder = carried[block_index] - apply(solved, upper_ref[0, block_index])
        solved = apply(remainder, pivot_ref[0, block_index])
        out_ref[:, block_index * block_size:(block_index + 1) * block_size] = solved


def beam_solve_kernel(beam_load, pivot_inv, lower_block, upper_block):
    return pl.pallas_call(
        solve_kernel,
        out_shape=jax.ShapeDtypeStruct(beam_load.shape, jnp.float32),
        name="beam_solve",
    )(beam_load, pivot_inv, lower_block, upper_block)


def local(strip_fields, strip_riser, strip_node, riser_owner, pivot_inv, lower_block, upper_block):
    position = lax.axis_index("strip")
    group_position = lax.axis_index("group")
    group_count = lax.axis_size("group")
    devices = lax.axis_size("strip") * group_count
    per_device = strip_fields.shape[1]
    grid_cells = strip_fields.shape[2]
    node_count = pivot_inv.shape[1] * pivot_inv.shape[2]
    riser_count = riser_owner.shape[1]
    group_strips = strip_node.shape[0]
    substeps = NSUB
    total_strips = per_device * devices
    kernels = make_kernels(grid_cells)
    riser_match = (
        strip_riser[:, 0][:, None] == jnp.arange(riser_count, dtype=jnp.int32)[None, :]
    ).astype(jnp.int32)
    owner_index = jnp.sum(riser_match * riser_owner[0][None, :], axis=1)
    owned_here = (owner_index == position).astype(jnp.float32)
    node_onehot = (
        strip_node[:, None] == jnp.arange(node_count, dtype=jnp.int32)[None, :]
    ).astype(jnp.float32)
    local_node = lax.dynamic_slice_in_dim(strip_node, position * per_device, per_device)
    top_taper = 1.0 - jnp.arange(node_count, dtype=jnp.float32) / node_count
    local_taper = 1.0 - local_node.astype(jnp.float32) / node_count

    unit_response = beam_solve_kernel(
        node_onehot * owned_here[:, None], pivot_inv, lower_block, upper_block
    )
    coupling = apply_block(node_onehot, unit_response) * owned_here[:, None]
    coupling_out = jnp.where(
        jnp.arange(group_count)[:, None, None] == group_position, coupling[None], 0.0
    ).reshape(group_count * group_strips, group_strips)

    vorticity = strip_fields
    motion = jnp.zeros((per_device, 2 * substeps), jnp.float32)
    for coupled_step in range(COUPLED):
        vorticity, force_rows = strip_step_kernel(strip_fields, vorticity, motion, kernels, substeps)
        sent = jnp.tile(force_rows, (devices, 1))
        if coupled_step + 1 < COUPLED:
            sent = jnp.concatenate([sent, coupling_out], axis=1)
        received = lax.all_to_all(sent, ("group", "strip"), 0, 0, tiled=True)
        every_force = received[:, : 2 * substeps]
        offset = jnp.sum(every_force[:, substeps:], axis=0) / jnp.sqrt(jnp.float32(total_strips))
        group_force = lax.dynamic_slice_in_dim(every_force, group_position * group_strips, group_strips)
        if coupled_step + 1 < COUPLED:
            my_coupling = jnp.sum(
                received[:, 2 * substeps :].reshape(devices, per_device, group_strips), axis=0
            )
            motion = lax.dot_general(
                my_coupling, group_force, (((1,), (0,)), ((), ())), precision=EXACT_DOT
            )
            motion = motion.at[:, substeps:].add(local_taper[:, None] * offset[None, :])
            vorticity = vorticity[None]
        else:
            displacement = first_contract(group_force * owned_here[:, None], unit_response)
            displacement = displacement.at[substeps:, :].add(offset[:, None] * top_taper[None, :])
    return (vorticity, displacement[None])


def solution(mesh):
    in_specs = (
        P(None, ("group", "strip"), None, None),
        P("group", None),
        P("group"),
        P("group", None),
        P(("group", "strip"), None, None, None),
        P(("group", "strip"), None, None, None),
        P(("group", "strip"), None, None, None),
    )
    out_specs = (P(("group", "strip"), None, None), P(("group", "strip"), None, None))
    return jax.shard_map(local, mesh=mesh, in_specs=in_specs, out_specs=out_specs, check_vma=False)
```

```python
import jax
import jax.numpy as jnp
from jax import lax
from jax.sharding import PartitionSpec as P
from jax.experimental import pallas as pl
from jax.experimental.pallas import tpu as pltpu

NSUB = 8
COUPLED = 2


TIME_STEP = 0.25
VISCOSITY = 0.05
COUPLING = 0.5
EXACT_DOT = lax.Precision.HIGHEST


def make_kernels(grid_cells):
    centre = jnp.arange(grid_cells, dtype=jnp.float32) - grid_cells / 2.0 + 0.5
    near_x = (centre / (grid_cells / 16.0))[None, :]
    near_y = (centre / (grid_cells / 16.0))[:, None]
    bell_near = jnp.exp(-(near_x * near_x + near_y * near_y) / 2.0)
    source_x = -near_x * bell_near
    source_y = -near_y * bell_near
    wide_x = (centre / (grid_cells / 8.0))[None, :]
    wide_y = (centre / (grid_cells / 8.0))[:, None]
    bell_wide = jnp.exp(-(wide_x * wide_x + wide_y * wide_y) / 2.0)
    lift_kernel = -wide_x * bell_wide
    drag_kernel = wide_y * bell_wide
    lift_kernel = lift_kernel / jnp.sqrt(jnp.sum(lift_kernel * lift_kernel))
    drag_kernel = drag_kernel / jnp.sqrt(jnp.sum(drag_kernel * drag_kernel))
    return (source_x, source_y, lift_kernel, drag_kernel)


def strip_step(vorticity, flow_x, flow_y, motion, kernels, substeps):
    source_x, source_y, lift_kernel, drag_kernel = kernels
    halves = motion.reshape(motion.shape[0], 2, substeps)
    earlier = jnp.concatenate([jnp.zeros_like(halves[:, :, :1]), halves[:, :, :-1]], axis=2)
    velocity = halves - earlier
    lift_rows = []
    drag_rows = []
    for substep in range(substeps):
        right_cell = jnp.roll(vorticity, -1, axis=2)
        left_cell = jnp.roll(vorticity, 1, axis=2)
        upper_cell = jnp.roll(vorticity, -1, axis=1)
        lower_cell = jnp.roll(vorticity, 1, axis=1)
        laplacian = right_cell + left_cell + upper_cell + lower_cell - 4.0 * vorticity
        tendency = (
            VISCOSITY * laplacian
            - flow_x * (0.5 * (right_cell - left_cell))
            - flow_y * (0.5 * (upper_cell - lower_cell))
        )
        forcing = (
            velocity[:, 0, substep][:, None, None] * source_x
            - velocity[:, 1, substep][:, None, None] * source_y
        )
        vorticity = vorticity + TIME_STEP * tendency + COUPLING * forcing
        lift_rows.append(jnp.sum(vorticity * lift_kernel, axis=(1, 2)))
        drag_rows.append(jnp.sum(vorticity * drag_kernel, axis=(1, 2)))
    return (vorticity, jnp.stack(lift_rows + drag_rows, axis=1))


def stencil_kernel(velocity_ref, vorticity_ref, flow_x_ref, flow_y_ref, source_x_ref, source_y_ref, lift_ref, drag_ref, out_ref, rows_ref, *, substeps):
    strip = pl.program_id(0)
    vorticity = vorticity_ref[0, 0]
    flow_x = flow_x_ref[0, 0]
    flow_y = flow_y_ref[0, 0]
    rows_across, cols_across = vorticity.shape
    lane = lax.broadcasted_iota(jnp.int32, (1, 2 * substeps), 1)
    row = jnp.zeros((1, 2 * substeps), jnp.float32)
    for substep in range(substeps):
        right_cell = pltpu.roll(vorticity, cols_across - 1, 1)
        left_cell = pltpu.roll(vorticity, 1, 1)
        upper_cell = pltpu.roll(vorticity, rows_across - 1, 0)
        lower_cell = pltpu.roll(vorticity, 1, 0)
        laplacian = right_cell + left_cell + upper_cell + lower_cell - 4.0 * vorticity
        tendency = (
            VISCOSITY * laplacian
            - flow_x * (0.5 * (right_cell - left_cell))
            - flow_y * (0.5 * (upper_cell - lower_cell))
        )
        forcing = (
            velocity_ref[strip, substep] * source_x_ref[...]
            - velocity_ref[strip, substeps + substep] * source_y_ref[...]
        )
        vorticity = vorticity + TIME_STEP * tendency + COUPLING * forcing
        lift = jnp.sum(jnp.sum(vorticity * lift_ref[...], axis=0, keepdims=True), axis=1, keepdims=True)
        drag = jnp.sum(jnp.sum(vorticity * drag_ref[...], axis=0, keepdims=True), axis=1, keepdims=True)
        row = row + jnp.where(lane == substep, lift, 0.0) + jnp.where(lane == substeps + substep, drag, 0.0)
    out_ref[0] = vorticity
    rows_ref[0] = row


def strip_step_kernel(strip_fields, vorticity, motion, kernels, substeps):
    source_x, source_y, lift_kernel, drag_kernel = kernels
    strips, cells_y, cells_x = strip_fields.shape[1:]
    halves = motion.reshape(strips, 2, substeps)
    earlier = jnp.concatenate([jnp.zeros_like(halves[:, :, :1]), halves[:, :, :-1]], axis=2)
    velocity = (halves - earlier).reshape(strips, 2 * substeps)
    plane = pl.BlockSpec((cells_y, cells_x), lambda s: (0, 0))

    def field(index):
        return pl.BlockSpec((1, 1, cells_y, cells_x), lambda s: (index, s, 0, 0))

    new_vorticity, rows = pl.pallas_call(
        lambda *refs: stencil_kernel(*refs, substeps=substeps),
        grid=(strips,),
        in_specs=[
            pl.BlockSpec(memory_space=pltpu.SMEM),
            field(0), field(1), field(2),
            plane, plane, plane, plane,
        ],
        out_specs=[
            pl.BlockSpec((1, cells_y, cells_x), lambda s: (s, 0, 0)),
            pl.BlockSpec((1, 1, 2 * substeps), lambda s: (s, 0, 0)),
        ],
        out_shape=[
            jax.ShapeDtypeStruct((strips, cells_y, cells_x), jnp.float32),
            jax.ShapeDtypeStruct((strips, 1, 2 * substeps), jnp.float32),
        ],
        name="strip_stencil",
    )(velocity, vorticity, strip_fields, strip_fields, source_x, source_y, lift_kernel, drag_kernel)
    return new_vorticity, rows[:, 0, :]


def apply_block(vectors, matrix):
    return lax.dot_general(vectors, matrix, (((1,), (1,)), ((), ())), precision=EXACT_DOT)


def first_contract(left_side, right_side):
    return lax.dot_general(left_side, right_side, (((0,), (0,)), ((), ())), precision=EXACT_DOT)


def beam_solve(beam_load, pivot_inv, lower_block, upper_block):
    block_count = pivot_inv.shape[0]
    block_size = pivot_inv.shape[1]
    blocks = beam_load.reshape(beam_load.shape[0], block_count, block_size)
    carried = [blocks[:, 0]]
    for block_index in range(1, block_count):
        pivoted = apply_block(carried[-1], pivot_inv[block_index - 1])
        carried.append(blocks[:, block_index] - apply_block(pivoted, lower_block[block_index - 1]))
    solved = [apply_block(carried[-1], pivot_inv[block_count - 1])]
    for block_index in range(block_count - 2, -1, -1):
        remainder = carried[block_index] - apply_block(solved[0], upper_block[block_index])
        solved.insert(0, apply_block(remainder, pivot_inv[block_index]))
    return jnp.concatenate(solved, axis=1)


def solve_kernel(load_ref, pivot_ref, lower_ref, upper_ref, out_ref):
    block_count = pivot_ref.shape[1]
    block_size = pivot_ref.shape[2]

    def apply(matrix, vectors):
        return jnp.dot(matrix, vectors, precision=EXACT_DOT, preferred_element_type=jnp.float32)

    carried = [load_ref[0:block_size, :]]
    for block_index in range(1, block_count):
        pivoted = apply(pivot_ref[0, block_index - 1], carried[-1])
        carried.append(
            load_ref[block_index * block_size:(block_index + 1) * block_size, :]
            - apply(lower_ref[0, block_index - 1], pivoted)
        )
    solved = apply(pivot_ref[0, block_count - 1], carried[-1])
    out_ref[(block_count - 1) * block_size:, :] = solved
    for block_index in range(block_count - 2, -1, -1):
        remainder = carried[block_index] - apply(upper_ref[0, block_index], solved)
        solved = apply(pivot_ref[0, block_index], remainder)
        out_ref[block_index * block_size:(block_index + 1) * block_size, :] = solved


def beam_solve_kernel(load_t, pivot_inv, lower_block, upper_block):
    return pl.pallas_call(
        solve_kernel,
        out_shape=jax.ShapeDtypeStruct(load_t.shape, jnp.float32),
        name="beam_solve",
    )(load_t, pivot_inv, lower_block, upper_block)


def local(strip_fields, strip_riser, strip_node, riser_owner, pivot_inv, lower_block, upper_block):
    position = lax.axis_index("strip")
    group_position = lax.axis_index("group")
    group_count = lax.axis_size("group")
    devices = lax.axis_size("strip") * group_count
    per_device = strip_fields.shape[1]
    grid_cells = strip_fields.shape[2]
    node_count = pivot_inv.shape[1] * pivot_inv.shape[2]
    riser_count = riser_owner.shape[1]
    group_strips = strip_node.shape[0]
    substeps = NSUB
    total_strips = per_device * devices
    kernels = make_kernels(grid_cells)
    riser_match = (
        strip_riser[:, 0][:, None] == jnp.arange(riser_count, dtype=jnp.int32)[None, :]
    ).astype(jnp.int32)
    owner_index = jnp.sum(riser_match * riser_owner[0][None, :], axis=1)
    owned_here = (owner_index == position).astype(jnp.float32)
    node_onehot = (
        strip_node[:, None] == jnp.arange(node_count, dtype=jnp.int32)[None, :]
    ).astype(jnp.float32)
    local_node = lax.dynamic_slice_in_dim(strip_node, position * per_device, per_device)
    top_taper = 1.0 - jnp.arange(node_count, dtype=jnp.float32) / node_count
    local_taper = 1.0 - local_node.astype(jnp.float32) / node_count

    unit_response = beam_solve_kernel(
        node_onehot.T * owned_here[None, :], pivot_inv, lower_block, upper_block
    )
    coupling = jnp.dot(node_onehot, unit_response, precision=EXACT_DOT) * owned_here[:, None]
    coupling_out = jnp.where(
        jnp.arange(group_count)[:, None, None] == group_position, coupling[None], 0.0
    ).reshape(group_count * group_strips, group_strips)

    vorticity = strip_fields
    motion = jnp.zeros((per_device, 2 * substeps), jnp.float32)
    for coupled_step in range(COUPLED):
        vorticity, force_rows = strip_step_kernel(strip_fields, vorticity, motion, kernels, substeps)
        sent = jnp.tile(force_rows, (devices, 1))
        if coupled_step + 1 < COUPLED:
            sent = jnp.concatenate([sent, coupling_out], axis=1)
        received = lax.all_to_all(sent, ("group", "strip"), 0, 0, tiled=True)
        every_force = received[:, : 2 * substeps]
        offset = jnp.sum(every_force[:, substeps:], axis=0) / jnp.sqrt(jnp.float32(total_strips))
        group_force = lax.dynamic_slice_in_dim(every_force, group_position * group_strips, group_strips)
        if coupled_step + 1 < COUPLED:
            my_coupling = jnp.sum(
                received[:, 2 * substeps :].reshape(devices, per_device, group_strips), axis=0
            )
            motion = lax.dot_general(
                my_coupling, group_force, (((1,), (0,)), ((), ())), precision=EXACT_DOT
            )
            motion = motion.at[:, substeps:].add(local_taper[:, None] * offset[None, :])
            vorticity = vorticity[None]
        else:
            displacement = lax.dot_general(
                group_force * owned_here[:, None], unit_response, (((0,), (1,)), ((), ())), precision=EXACT_DOT
            )
            displacement = displacement.at[substeps:, :].add(offset[:, None] * top_taper[None, :])
    return (vorticity, displacement[None])


def solution(mesh):
    in_specs = (
        P(None, ("group", "strip"), None, None),
        P("group", None),
        P("group"),
        P("group", None),
        P(("group", "strip"), None, None, None),
        P(("group", "strip"), None, None, None),
        P(("group", "strip"), None, None, None),
    )
    out_specs = (P(("group", "strip"), None, None), P(("group", "strip"), None, None))
    return jax.shard_map(local, mesh=mesh, in_specs=in_specs, out_specs=out_specs, check_vma=False)
```

```python
import jax
import jax.numpy as jnp
from jax import lax
from jax.sharding import PartitionSpec as P
from jax.experimental import pallas as pl
from jax.experimental.pallas import tpu as pltpu

NSUB = 8
COUPLED = 2


TIME_STEP = 0.25
VISCOSITY = 0.05
COUPLING = 0.5
EXACT_DOT = lax.Precision.HIGHEST


def make_kernels(grid_cells):
    centre = jnp.arange(grid_cells, dtype=jnp.float32) - grid_cells / 2.0 + 0.5
    near_x = (centre / (grid_cells / 16.0))[None, :]
    near_y = (centre / (grid_cells / 16.0))[:, None]
    bell_near = jnp.exp(-(near_x * near_x + near_y * near_y) / 2.0)
    source_x = -near_x * bell_near
    source_y = -near_y * bell_near
    wide_x = (centre / (grid_cells / 8.0))[None, :]
    wide_y = (centre / (grid_cells / 8.0))[:, None]
    bell_wide = jnp.exp(-(wide_x * wide_x + wide_y * wide_y) / 2.0)
    lift_kernel = -wide_x * bell_wide
    drag_kernel = wide_y * bell_wide
    lift_kernel = lift_kernel / jnp.sqrt(jnp.sum(lift_kernel * lift_kernel))
    drag_kernel = drag_kernel / jnp.sqrt(jnp.sum(drag_kernel * drag_kernel))
    return (source_x, source_y, lift_kernel, drag_kernel)


def strip_step(vorticity, flow_x, flow_y, motion, kernels, substeps):
    source_x, source_y, lift_kernel, drag_kernel = kernels
    halves = motion.reshape(motion.shape[0], 2, substeps)
    earlier = jnp.concatenate([jnp.zeros_like(halves[:, :, :1]), halves[:, :, :-1]], axis=2)
    velocity = halves - earlier
    lift_rows = []
    drag_rows = []
    for substep in range(substeps):
        right_cell = jnp.roll(vorticity, -1, axis=2)
        left_cell = jnp.roll(vorticity, 1, axis=2)
        upper_cell = jnp.roll(vorticity, -1, axis=1)
        lower_cell = jnp.roll(vorticity, 1, axis=1)
        laplacian = right_cell + left_cell + upper_cell + lower_cell - 4.0 * vorticity
        tendency = (
            VISCOSITY * laplacian
            - flow_x * (0.5 * (right_cell - left_cell))
            - flow_y * (0.5 * (upper_cell - lower_cell))
        )
        forcing = (
            velocity[:, 0, substep][:, None, None] * source_x
            - velocity[:, 1, substep][:, None, None] * source_y
        )
        vorticity = vorticity + TIME_STEP * tendency + COUPLING * forcing
        lift_rows.append(jnp.sum(vorticity * lift_kernel, axis=(1, 2)))
        drag_rows.append(jnp.sum(vorticity * drag_kernel, axis=(1, 2)))
    return (vorticity, jnp.stack(lift_rows + drag_rows, axis=1))


def stencil_kernel(velocity_ref, vorticity_ref, flow_x_ref, flow_y_ref, source_x_ref, source_y_ref, lift_ref, drag_ref, out_ref, rows_ref, *, substeps):
    strip = pl.program_id(0)
    vorticity = vorticity_ref[0, 0]
    flow_x = flow_x_ref[0, 0]
    flow_y = flow_y_ref[0, 0]
    rows_across, cols_across = vorticity.shape
    lane = lax.broadcasted_iota(jnp.int32, (1, 2 * substeps), 1)
    row = jnp.zeros((1, 2 * substeps), jnp.float32)
    for substep in range(substeps):
        right_cell = pltpu.roll(vorticity, cols_across - 1, 1)
        left_cell = pltpu.roll(vorticity, 1, 1)
        upper_cell = pltpu.roll(vorticity, rows_across - 1, 0)
        lower_cell = pltpu.roll(vorticity, 1, 0)
        laplacian = right_cell + left_cell + upper_cell + lower_cell - 4.0 * vorticity
        tendency = (
            VISCOSITY * laplacian
            - flow_x * (0.5 * (right_cell - left_cell))
            - flow_y * (0.5 * (upper_cell - lower_cell))
        )
        forcing = (
            velocity_ref[strip, substep] * source_x_ref[...]
            - velocity_ref[strip, substeps + substep] * source_y_ref[...]
        )
        vorticity = vorticity + TIME_STEP * tendency + COUPLING * forcing
        lift = jnp.sum(jnp.sum(vorticity * lift_ref[...], axis=0, keepdims=True), axis=1, keepdims=True)
        drag = jnp.sum(jnp.sum(vorticity * drag_ref[...], axis=0, keepdims=True), axis=1, keepdims=True)
        row = row + jnp.where(lane == substep, lift, 0.0) + jnp.where(lane == substeps + substep, drag, 0.0)
    out_ref[0] = vorticity
    rows_ref[0] = row


def strip_step_kernel(strip_fields, vorticity, motion, kernels, substeps):
    source_x, source_y, lift_kernel, drag_kernel = kernels
    strips, cells_y, cells_x = strip_fields.shape[1:]
    halves = motion.reshape(strips, 2, substeps)
    earlier = jnp.concatenate([jnp.zeros_like(halves[:, :, :1]), halves[:, :, :-1]], axis=2)
    velocity = (halves - earlier).reshape(strips, 2 * substeps)
    plane = pl.BlockSpec((cells_y, cells_x), lambda s: (0, 0))

    def field(index):
        return pl.BlockSpec((1, 1, cells_y, cells_x), lambda s: (index, s, 0, 0))

    new_vorticity, rows = pl.pallas_call(
        lambda *refs: stencil_kernel(*refs, substeps=substeps),
        grid=(strips,),
        in_specs=[
            pl.BlockSpec(memory_space=pltpu.SMEM),
            field(0), field(1), field(2),
            plane, plane, plane, plane,
        ],
        out_specs=[
            pl.BlockSpec((1, cells_y, cells_x), lambda s: (s, 0, 0)),
            pl.BlockSpec((1, 1, 2 * substeps), lambda s: (s, 0, 0)),
        ],
        out_shape=[
            jax.ShapeDtypeStruct((strips, cells_y, cells_x), jnp.float32),
            jax.ShapeDtypeStruct((strips, 1, 2 * substeps), jnp.float32),
        ],
        name="strip_stencil",
    )(velocity, vorticity, strip_fields, strip_fields, source_x, source_y, lift_kernel, drag_kernel)
    return new_vorticity, rows[:, 0, :]


def apply_block(vectors, matrix):
    return lax.dot_general(vectors, matrix, (((1,), (1,)), ((), ())), precision=EXACT_DOT)


def first_contract(left_side, right_side):
    return lax.dot_general(left_side, right_side, (((0,), (0,)), ((), ())), precision=EXACT_DOT)


def beam_solve(beam_load, pivot_inv, lower_block, upper_block):
    block_count = pivot_inv.shape[0]
    block_size = pivot_inv.shape[1]
    blocks = beam_load.reshape(beam_load.shape[0], block_count, block_size)
    carried = [blocks[:, 0]]
    for block_index in range(1, block_count):
        pivoted = apply_block(carried[-1], pivot_inv[block_index - 1])
        carried.append(blocks[:, block_index] - apply_block(pivoted, lower_block[block_index - 1]))
    solved = [apply_block(carried[-1], pivot_inv[block_count - 1])]
    for block_index in range(block_count - 2, -1, -1):
        remainder = carried[block_index] - apply_block(solved[0], upper_block[block_index])
        solved.insert(0, apply_block(remainder, pivot_inv[block_index]))
    return jnp.concatenate(solved, axis=1)


def solve_kernel(load_ref, pivot_ref, lower_ref, upper_ref, out_ref):
    block_count = pivot_ref.shape[1]
    block_size = pivot_ref.shape[2]

    def apply(matrix, vectors):
        return jnp.dot(matrix, vectors, precision=lax.Precision.HIGH, preferred_element_type=jnp.float32)

    carried = [load_ref[0:block_size, :]]
    for block_index in range(1, block_count):
        pivoted = apply(pivot_ref[0, block_index - 1], carried[-1])
        carried.append(
            load_ref[block_index * block_size:(block_index + 1) * block_size, :]
            - apply(lower_ref[0, block_index - 1], pivoted)
        )
    solved = apply(pivot_ref[0, block_count - 1], carried[-1])
    out_ref[(block_count - 1) * block_size:, :] = solved
    for block_index in range(block_count - 2, -1, -1):
        remainder = carried[block_index] - apply(upper_ref[0, block_index], solved)
        solved = apply(pivot_ref[0, block_index], remainder)
        out_ref[block_index * block_size:(block_index + 1) * block_size, :] = solved


def beam_solve_kernel(load_t, pivot_inv, lower_block, upper_block):
    return pl.pallas_call(
        solve_kernel,
        out_shape=jax.ShapeDtypeStruct(load_t.shape, jnp.float32),
        name="beam_solve",
    )(load_t, pivot_inv, lower_block, upper_block)


def local(strip_fields, strip_riser, strip_node, riser_owner, pivot_inv, lower_block, upper_block):
    position = lax.axis_index("strip")
    group_position = lax.axis_index("group")
    group_count = lax.axis_size("group")
    devices = lax.axis_size("strip") * group_count
    per_device = strip_fields.shape[1]
    grid_cells = strip_fields.shape[2]
    node_count = pivot_inv.shape[1] * pivot_inv.shape[2]
    riser_count = riser_owner.shape[1]
    group_strips = strip_node.shape[0]
    substeps = NSUB
    total_strips = per_device * devices
    kernels = make_kernels(grid_cells)
    riser_match = (
        strip_riser[:, 0][:, None] == jnp.arange(riser_count, dtype=jnp.int32)[None, :]
    ).astype(jnp.int32)
    owner_index = jnp.sum(riser_match * riser_owner[0][None, :], axis=1)
    owned_here = (owner_index == position).astype(jnp.float32)
    node_onehot = (
        strip_node[:, None] == jnp.arange(node_count, dtype=jnp.int32)[None, :]
    ).astype(jnp.float32)
    local_node = lax.dynamic_slice_in_dim(strip_node, position * per_device, per_device)
    top_taper = 1.0 - jnp.arange(node_count, dtype=jnp.float32) / node_count
    local_taper = 1.0 - local_node.astype(jnp.float32) / node_count

    unit_response = beam_solve_kernel(
        node_onehot.T * owned_here[None, :], pivot_inv, lower_block, upper_block
    )
    coupling = jnp.dot(node_onehot, unit_response, precision=EXACT_DOT) * owned_here[:, None]
    coupling_out = jnp.where(
        jnp.arange(group_count)[:, None, None] == group_position, coupling[None], 0.0
    ).reshape(group_count * group_strips, group_strips)

    vorticity = strip_fields
    motion = jnp.zeros((per_device, 2 * substeps), jnp.float32)
    for coupled_step in range(COUPLED):
        vorticity, force_rows = strip_step_kernel(strip_fields, vorticity, motion, kernels, substeps)
        sent = jnp.tile(force_rows, (devices, 1))
        if coupled_step + 1 < COUPLED:
            sent = jnp.concatenate([sent, coupling_out], axis=1)
        received = lax.all_to_all(sent, ("group", "strip"), 0, 0, tiled=True)
        every_force = received[:, : 2 * substeps]
        offset = jnp.sum(every_force[:, substeps:], axis=0) / jnp.sqrt(jnp.float32(total_strips))
        group_force = lax.dynamic_slice_in_dim(every_force, group_position * group_strips, group_strips)
        if coupled_step + 1 < COUPLED:
            my_coupling = jnp.sum(
                received[:, 2 * substeps :].reshape(devices, per_device, group_strips), axis=0
            )
            motion = lax.dot_general(
                my_coupling, group_force, (((1,), (0,)), ((), ())), precision=EXACT_DOT
            )
            motion = motion.at[:, substeps:].add(local_taper[:, None] * offset[None, :])
            vorticity = vorticity[None]
        else:
            displacement = lax.dot_general(
                group_force * owned_here[:, None], unit_response, (((0,), (1,)), ((), ())), precision=EXACT_DOT
            )
            displacement = displacement.at[substeps:, :].add(offset[:, None] * top_taper[None, :])
    return (vorticity, displacement[None])


def solution(mesh):
    in_specs = (
        P(None, ("group", "strip"), None, None),
        P("group", None),
        P("group"),
        P("group", None),
        P(("group", "strip"), None, None, None),
        P(("group", "strip"), None, None, None),
        P(("group", "strip"), None, None, None),
    )
    out_specs = (P(("group", "strip"), None, None), P(("group", "strip"), None, None))
    return jax.shard_map(local, mesh=mesh, in_specs=in_specs, out_specs=out_specs, check_vma=False)
```

```python
import jax
import jax.numpy as jnp
from jax import lax
from jax.sharding import PartitionSpec as P
from jax.experimental import pallas as pl
from jax.experimental.pallas import tpu as pltpu

NSUB = 8
COUPLED = 2


TIME_STEP = 0.25
VISCOSITY = 0.05
COUPLING = 0.5
EXACT_DOT = lax.Precision.HIGHEST


def make_kernels(grid_cells):
    centre = jnp.arange(grid_cells, dtype=jnp.float32) - grid_cells / 2.0 + 0.5
    near_x = (centre / (grid_cells / 16.0))[None, :]
    near_y = (centre / (grid_cells / 16.0))[:, None]
    bell_near = jnp.exp(-(near_x * near_x + near_y * near_y) / 2.0)
    source_x = -near_x * bell_near
    source_y = -near_y * bell_near
    wide_x = (centre / (grid_cells / 8.0))[None, :]
    wide_y = (centre / (grid_cells / 8.0))[:, None]
    bell_wide = jnp.exp(-(wide_x * wide_x + wide_y * wide_y) / 2.0)
    lift_kernel = -wide_x * bell_wide
    drag_kernel = wide_y * bell_wide
    lift_kernel = lift_kernel / jnp.sqrt(jnp.sum(lift_kernel * lift_kernel))
    drag_kernel = drag_kernel / jnp.sqrt(jnp.sum(drag_kernel * drag_kernel))
    return (source_x, source_y, lift_kernel, drag_kernel)


def strip_step(vorticity, flow_x, flow_y, motion, kernels, substeps):
    source_x, source_y, lift_kernel, drag_kernel = kernels
    halves = motion.reshape(motion.shape[0], 2, substeps)
    earlier = jnp.concatenate([jnp.zeros_like(halves[:, :, :1]), halves[:, :, :-1]], axis=2)
    velocity = halves - earlier
    lift_rows = []
    drag_rows = []
    for substep in range(substeps):
        right_cell = jnp.roll(vorticity, -1, axis=2)
        left_cell = jnp.roll(vorticity, 1, axis=2)
        upper_cell = jnp.roll(vorticity, -1, axis=1)
        lower_cell = jnp.roll(vorticity, 1, axis=1)
        laplacian = right_cell + left_cell + upper_cell + lower_cell - 4.0 * vorticity
        tendency = (
            VISCOSITY * laplacian
            - flow_x * (0.5 * (right_cell - left_cell))
            - flow_y * (0.5 * (upper_cell - lower_cell))
        )
        forcing = (
            velocity[:, 0, substep][:, None, None] * source_x
            - velocity[:, 1, substep][:, None, None] * source_y
        )
        vorticity = vorticity + TIME_STEP * tendency + COUPLING * forcing
        lift_rows.append(jnp.sum(vorticity * lift_kernel, axis=(1, 2)))
        drag_rows.append(jnp.sum(vorticity * drag_kernel, axis=(1, 2)))
    return (vorticity, jnp.stack(lift_rows + drag_rows, axis=1))


def run_substeps(vorticity, flow_x, flow_y, forcing_of, lift_kernel, drag_kernel, substeps):
    rows_across, cols_across = vorticity.shape
    lane = lax.broadcasted_iota(jnp.int32, (1, 2 * substeps), 1)
    row = jnp.zeros((1, 2 * substeps), jnp.float32)
    for substep in range(substeps):
        right_cell = pltpu.roll(vorticity, cols_across - 1, 1)
        left_cell = pltpu.roll(vorticity, 1, 1)
        upper_cell = pltpu.roll(vorticity, rows_across - 1, 0)
        lower_cell = pltpu.roll(vorticity, 1, 0)
        laplacian = right_cell + left_cell + upper_cell + lower_cell - 4.0 * vorticity
        tendency = (
            VISCOSITY * laplacian
            - flow_x * (0.5 * (right_cell - left_cell))
            - flow_y * (0.5 * (upper_cell - lower_cell))
        )
        if forcing_of is None:
            vorticity = vorticity + TIME_STEP * tendency
        else:
            vorticity = vorticity + TIME_STEP * tendency + COUPLING * forcing_of(substep)
        lift = jnp.sum(jnp.sum(vorticity * lift_kernel, axis=0, keepdims=True), axis=1, keepdims=True)
        drag = jnp.sum(jnp.sum(vorticity * drag_kernel, axis=0, keepdims=True), axis=1, keepdims=True)
        row = row + jnp.where(lane == substep, lift, 0.0) + jnp.where(lane == substeps + substep, drag, 0.0)
    return vorticity, row


def stencil_kernel(velocity_ref, vorticity_ref, flow_x_ref, flow_y_ref, source_x_ref, source_y_ref, lift_ref, drag_ref, out_ref, rows_ref, *, substeps):
    strip = pl.program_id(0)

    def forcing_of(substep):
        return (
            velocity_ref[strip, substep] * source_x_ref[...]
            - velocity_ref[strip, substeps + substep] * source_y_ref[...]
        )

    vorticity, row = run_substeps(
        vorticity_ref[0, 0], flow_x_ref[0, 0], flow_y_ref[0, 0], forcing_of,
        lift_ref[...], drag_ref[...], substeps,
    )
    out_ref[0] = vorticity
    rows_ref[0] = row


def strip_step_kernel(strip_fields, vorticity, motion, kernels, substeps):
    source_x, source_y, lift_kernel, drag_kernel = kernels
    strips, cells_y, cells_x = strip_fields.shape[1:]
    halves = motion.reshape(strips, 2, substeps)
    earlier = jnp.concatenate([jnp.zeros_like(halves[:, :, :1]), halves[:, :, :-1]], axis=2)
    velocity = (halves - earlier).reshape(strips, 2 * substeps)
    plane = pl.BlockSpec((cells_y, cells_x), lambda s: (0, 0))

    def field(index):
        return pl.BlockSpec((1, 1, cells_y, cells_x), lambda s: (index, s, 0, 0))

    new_vorticity, rows = pl.pallas_call(
        lambda *refs: stencil_kernel(*refs, substeps=substeps),
        grid=(strips,),
        in_specs=[
            pl.BlockSpec(memory_space=pltpu.SMEM),
            field(0), field(1), field(2),
            plane, plane, plane, plane,
        ],
        out_specs=[
            pl.BlockSpec((1, cells_y, cells_x), lambda s: (s, 0, 0)),
            pl.BlockSpec((1, 1, 2 * substeps), lambda s: (s, 0, 0)),
        ],
        out_shape=[
            jax.ShapeDtypeStruct((strips, cells_y, cells_x), jnp.float32),
            jax.ShapeDtypeStruct((strips, 1, 2 * substeps), jnp.float32),
        ],
        name="strip_stencil",
    )(velocity, vorticity, strip_fields, strip_fields, source_x, source_y, lift_kernel, drag_kernel)
    return new_vorticity, rows[:, 0, :]


def apply_block(vectors, matrix):
    return lax.dot_general(vectors, matrix, (((1,), (1,)), ((), ())), precision=EXACT_DOT)


def first_contract(left_side, right_side):
    return lax.dot_general(left_side, right_side, (((0,), (0,)), ((), ())), precision=EXACT_DOT)


def beam_solve(beam_load, pivot_inv, lower_block, upper_block):
    block_count = pivot_inv.shape[0]
    block_size = pivot_inv.shape[1]
    blocks = beam_load.reshape(beam_load.shape[0], block_count, block_size)
    carried = [blocks[:, 0]]
    for block_index in range(1, block_count):
        pivoted = apply_block(carried[-1], pivot_inv[block_index - 1])
        carried.append(blocks[:, block_index] - apply_block(pivoted, lower_block[block_index - 1]))
    solved = [apply_block(carried[-1], pivot_inv[block_count - 1])]
    for block_index in range(block_count - 2, -1, -1):
        remainder = carried[block_index] - apply_block(solved[0], upper_block[block_index])
        solved.insert(0, apply_block(remainder, pivot_inv[block_index]))
    return jnp.concatenate(solved, axis=1)


def start_kernel(node_col_ref, node_row_ref, owned_col_ref, owned_row_ref, pivot_ref, lower_ref, upper_ref,
                 fields_ref, lift_ref, drag_ref, response_ref, coupling_ref, vorticity_ref, rows_ref, *, substeps):
    block_count = pivot_ref.shape[1]
    block_size = pivot_ref.shape[2]
    node_count = block_count * block_size
    strips = node_col_ref.shape[0]

    def apply(matrix, vectors):
        return jnp.dot(matrix, vectors, precision=lax.Precision.HIGH, preferred_element_type=jnp.float32)

    def unit_load(block_index):
        node = block_index * block_size + lax.broadcasted_iota(jnp.int32, (block_size, strips), 0)
        return (node == node_row_ref[...]).astype(jnp.float32) * owned_row_ref[...]

    carried = [unit_load(0)]
    for block_index in range(1, block_count):
        pivoted = apply(pivot_ref[0, block_index - 1], carried[-1])
        carried.append(unit_load(block_index) - apply(lower_ref[0, block_index - 1], pivoted))
    solved = apply(pivot_ref[0, block_count - 1], carried[-1])
    response_ref[(block_count - 1) * block_size:, :] = solved
    for block_index in range(block_count - 2, -1, -1):
        remainder = carried[block_index] - apply(upper_ref[0, block_index], solved)
        solved = apply(pivot_ref[0, block_index], remainder)
        response_ref[block_index * block_size:(block_index + 1) * block_size, :] = solved

    for strip in range(fields_ref.shape[1]):
        vorticity, row = run_substeps(
            fields_ref[0, strip], fields_ref[1, strip], fields_ref[2, strip], None,
            lift_ref[...], drag_ref[...], substeps,
        )
        vorticity_ref[strip] = vorticity
        rows_ref[strip:strip + 1, :] = row

    node_onehot = (
        node_col_ref[...] == lax.broadcasted_iota(jnp.int32, (strips, node_count), 1)
    ).astype(jnp.float32)
    coupling = jnp.dot(node_onehot, response_ref[...], precision=EXACT_DOT, preferred_element_type=jnp.float32)
    coupling_ref[...] = coupling * owned_col_ref[...]


def start_step(strip_node, owned_here, pivot_inv, lower_block, upper_block, strip_fields, kernels, substeps):
    _, _, lift_kernel, drag_kernel = kernels
    strips = strip_node.shape[0]
    node_count = pivot_inv.shape[1] * pivot_inv.shape[2]
    _, per_device, cells_y, cells_x = strip_fields.shape
    return pl.pallas_call(
        lambda *refs: start_kernel(*refs, substeps=substeps),
        out_shape=[
            jax.ShapeDtypeStruct((node_count, strips), jnp.float32),
            jax.ShapeDtypeStruct((strips, strips), jnp.float32),
            jax.ShapeDtypeStruct((per_device, cells_y, cells_x), jnp.float32),
            jax.ShapeDtypeStruct((per_device, 2 * substeps), jnp.float32),
        ],
        name="start_step",
    )(
        strip_node[:, None], strip_node[None, :], owned_here[:, None], owned_here[None, :],
        pivot_inv, lower_block, upper_block, strip_fields, lift_kernel, drag_kernel,
    )


def local(strip_fields, strip_riser, strip_node, riser_owner, pivot_inv, lower_block, upper_block):
    position = lax.axis_index("strip")
    group_position = lax.axis_index("group")
    group_count = lax.axis_size("group")
    devices = lax.axis_size("strip") * group_count
    per_device = strip_fields.shape[1]
    grid_cells = strip_fields.shape[2]
    node_count = pivot_inv.shape[1] * pivot_inv.shape[2]
    riser_count = riser_owner.shape[1]
    group_strips = strip_node.shape[0]
    substeps = NSUB
    total_strips = per_device * devices
    kernels = make_kernels(grid_cells)
    riser_match = (
        strip_riser[:, 0][:, None] == jnp.arange(riser_count, dtype=jnp.int32)[None, :]
    ).astype(jnp.int32)
    owner_index = jnp.sum(riser_match * riser_owner[0][None, :], axis=1)
    owned_here = (owner_index == position).astype(jnp.float32)
    node_onehot = (
        strip_node[:, None] == jnp.arange(node_count, dtype=jnp.int32)[None, :]
    ).astype(jnp.float32)
    local_node = lax.dynamic_slice_in_dim(strip_node, position * per_device, per_device)
    top_taper = 1.0 - jnp.arange(node_count, dtype=jnp.float32) / node_count
    local_taper = 1.0 - local_node.astype(jnp.float32) / node_count

    unit_response, coupling, first_vorticity, first_rows = start_step(
        strip_node, owned_here, pivot_inv, lower_block, upper_block, strip_fields, kernels, substeps
    )
    coupling_out = jnp.where(
        jnp.arange(group_count)[:, None, None] == group_position, coupling[None], 0.0
    ).reshape(group_count * group_strips, group_strips)

    vorticity = strip_fields
    motion = jnp.zeros((per_device, 2 * substeps), jnp.float32)
    for coupled_step in range(COUPLED):
        if coupled_step == 0:
            vorticity, force_rows = first_vorticity[None], first_rows
        else:
            vorticity, force_rows = strip_step_kernel(strip_fields, vorticity, motion, kernels, substeps)
        sent = jnp.tile(force_rows, (devices, 1))
        if coupled_step + 1 < COUPLED:
            sent = jnp.concatenate([sent, coupling_out], axis=1)
        received = lax.all_to_all(sent, ("group", "strip"), 0, 0, tiled=True)
        every_force = received[:, : 2 * substeps]
        offset = jnp.sum(every_force[:, substeps:], axis=0) / jnp.sqrt(jnp.float32(total_strips))
        group_force = lax.dynamic_slice_in_dim(every_force, group_position * group_strips, group_strips)
        if coupled_step + 1 < COUPLED:
            my_coupling = jnp.sum(
                received[:, 2 * substeps :].reshape(devices, per_device, group_strips), axis=0
            )
            motion = lax.dot_general(
                my_coupling, group_force, (((1,), (0,)), ((), ())), precision=EXACT_DOT
            )
            motion = motion.at[:, substeps:].add(local_taper[:, None] * offset[None, :])
        else:
            displacement = lax.dot_general(
                group_force * owned_here[:, None], unit_response, (((0,), (1,)), ((), ())), precision=EXACT_DOT
            )
            displacement = displacement.at[substeps:, :].add(offset[:, None] * top_taper[None, :])
    return (vorticity, displacement[None])


def solution(mesh):
    in_specs = (
        P(None, ("group", "strip"), None, None),
        P("group", None),
        P("group"),
        P("group", None),
        P(("group", "strip"), None, None, None),
        P(("group", "strip"), None, None, None),
        P(("group", "strip"), None, None, None),
    )
    out_specs = (P(("group", "strip"), None, None), P(("group", "strip"), None, None))
    return jax.shard_map(local, mesh=mesh, in_specs=in_specs, out_specs=out_specs, check_vma=False)
```

```python
import jax
import jax.numpy as jnp
from jax import lax
from jax.sharding import PartitionSpec as P
from jax.experimental import pallas as pl
from jax.experimental.pallas import tpu as pltpu

NSUB = 8
COUPLED = 2


TIME_STEP = 0.25
VISCOSITY = 0.05
COUPLING = 0.5
EXACT_DOT = lax.Precision.HIGHEST


def make_kernels(grid_cells):
    centre = jnp.arange(grid_cells, dtype=jnp.float32) - grid_cells / 2.0 + 0.5
    near_x = (centre / (grid_cells / 16.0))[None, :]
    near_y = (centre / (grid_cells / 16.0))[:, None]
    bell_near = jnp.exp(-(near_x * near_x + near_y * near_y) / 2.0)
    source_x = -near_x * bell_near
    source_y = -near_y * bell_near
    wide_x = (centre / (grid_cells / 8.0))[None, :]
    wide_y = (centre / (grid_cells / 8.0))[:, None]
    bell_wide = jnp.exp(-(wide_x * wide_x + wide_y * wide_y) / 2.0)
    lift_kernel = -wide_x * bell_wide
    drag_kernel = wide_y * bell_wide
    lift_kernel = lift_kernel / jnp.sqrt(jnp.sum(lift_kernel * lift_kernel))
    drag_kernel = drag_kernel / jnp.sqrt(jnp.sum(drag_kernel * drag_kernel))
    return (source_x, source_y, lift_kernel, drag_kernel)


def strip_step(vorticity, flow_x, flow_y, motion, kernels, substeps):
    source_x, source_y, lift_kernel, drag_kernel = kernels
    halves = motion.reshape(motion.shape[0], 2, substeps)
    earlier = jnp.concatenate([jnp.zeros_like(halves[:, :, :1]), halves[:, :, :-1]], axis=2)
    velocity = halves - earlier
    lift_rows = []
    drag_rows = []
    for substep in range(substeps):
        right_cell = jnp.roll(vorticity, -1, axis=2)
        left_cell = jnp.roll(vorticity, 1, axis=2)
        upper_cell = jnp.roll(vorticity, -1, axis=1)
        lower_cell = jnp.roll(vorticity, 1, axis=1)
        laplacian = right_cell + left_cell + upper_cell + lower_cell - 4.0 * vorticity
        tendency = (
            VISCOSITY * laplacian
            - flow_x * (0.5 * (right_cell - left_cell))
            - flow_y * (0.5 * (upper_cell - lower_cell))
        )
        forcing = (
            velocity[:, 0, substep][:, None, None] * source_x
            - velocity[:, 1, substep][:, None, None] * source_y
        )
        vorticity = vorticity + TIME_STEP * tendency + COUPLING * forcing
        lift_rows.append(jnp.sum(vorticity * lift_kernel, axis=(1, 2)))
        drag_rows.append(jnp.sum(vorticity * drag_kernel, axis=(1, 2)))
    return (vorticity, jnp.stack(lift_rows + drag_rows, axis=1))


def kernel_planes(cells):
    centre_x = lax.broadcasted_iota(jnp.int32, (cells, cells), 1).astype(jnp.float32) - cells / 2.0 + 0.5
    centre_y = lax.broadcasted_iota(jnp.int32, (cells, cells), 0).astype(jnp.float32) - cells / 2.0 + 0.5
    near_x = centre_x / (cells / 16.0)
    near_y = centre_y / (cells / 16.0)
    bell_near = jnp.exp(-(near_x * near_x + near_y * near_y) / 2.0)
    source_x = -near_x * bell_near
    source_y = -near_y * bell_near
    wide_x = centre_x / (cells / 8.0)
    wide_y = centre_y / (cells / 8.0)
    bell_wide = jnp.exp(-(wide_x * wide_x + wide_y * wide_y) / 2.0)
    lift_kernel = -wide_x * bell_wide
    drag_kernel = wide_y * bell_wide

    def total(plane):
        return jnp.sum(jnp.sum(plane, axis=0, keepdims=True), axis=1, keepdims=True)

    lift_kernel = lift_kernel / jnp.sqrt(total(lift_kernel * lift_kernel))
    drag_kernel = drag_kernel / jnp.sqrt(total(drag_kernel * drag_kernel))
    return (source_x, source_y, lift_kernel, drag_kernel)


def run_substeps(vorticity, flow_x, flow_y, forcing_of, lift_kernel, drag_kernel, substeps):
    rows_across, cols_across = vorticity.shape
    lane = lax.broadcasted_iota(jnp.int32, (1, 2 * substeps), 1)
    row = jnp.zeros((1, 2 * substeps), jnp.float32)
    for substep in range(substeps):
        right_cell = pltpu.roll(vorticity, cols_across - 1, 1)
        left_cell = pltpu.roll(vorticity, 1, 1)
        upper_cell = pltpu.roll(vorticity, rows_across - 1, 0)
        lower_cell = pltpu.roll(vorticity, 1, 0)
        laplacian = right_cell + left_cell + upper_cell + lower_cell - 4.0 * vorticity
        tendency = (
            VISCOSITY * laplacian
            - flow_x * (0.5 * (right_cell - left_cell))
            - flow_y * (0.5 * (upper_cell - lower_cell))
        )
        if forcing_of is None:
            vorticity = vorticity + TIME_STEP * tendency
        else:
            vorticity = vorticity + TIME_STEP * tendency + COUPLING * forcing_of(substep)
        lift = jnp.sum(jnp.sum(vorticity * lift_kernel, axis=0, keepdims=True), axis=1, keepdims=True)
        drag = jnp.sum(jnp.sum(vorticity * drag_kernel, axis=0, keepdims=True), axis=1, keepdims=True)
        row = row + jnp.where(lane == substep, lift, 0.0) + jnp.where(lane == substeps + substep, drag, 0.0)
    return vorticity, row


def stencil_kernel(velocity_ref, vorticity_ref, flow_x_ref, flow_y_ref, out_ref, rows_ref, *, substeps):
    strip = pl.program_id(0)
    source_x, source_y, lift_kernel, drag_kernel = kernel_planes(vorticity_ref.shape[-1])

    def forcing_of(substep):
        return (
            velocity_ref[strip, substep] * source_x
            - velocity_ref[strip, substeps + substep] * source_y
        )

    vorticity, row = run_substeps(
        vorticity_ref[0, 0], flow_x_ref[0, 0], flow_y_ref[0, 0], forcing_of,
        lift_kernel, drag_kernel, substeps,
    )
    out_ref[0] = vorticity
    rows_ref[0] = row


def strip_step_kernel(strip_fields, vorticity, motion, kernels, substeps):
    strips, cells_y, cells_x = strip_fields.shape[1:]
    halves = motion.reshape(strips, 2, substeps)
    earlier = jnp.concatenate([jnp.zeros_like(halves[:, :, :1]), halves[:, :, :-1]], axis=2)
    velocity = (halves - earlier).reshape(strips, 2 * substeps)
    def field(index):
        return pl.BlockSpec((1, 1, cells_y, cells_x), lambda s: (index, s, 0, 0))

    new_vorticity, rows = pl.pallas_call(
        lambda *refs: stencil_kernel(*refs, substeps=substeps),
        grid=(strips,),
        in_specs=[
            pl.BlockSpec(memory_space=pltpu.SMEM),
            field(0), field(1), field(2),
        ],
        out_specs=[
            pl.BlockSpec((1, cells_y, cells_x), lambda s: (s, 0, 0)),
            pl.BlockSpec((1, 1, 2 * substeps), lambda s: (s, 0, 0)),
        ],
        out_shape=[
            jax.ShapeDtypeStruct((strips, cells_y, cells_x), jnp.float32),
            jax.ShapeDtypeStruct((strips, 1, 2 * substeps), jnp.float32),
        ],
        name="strip_stencil",
    )(velocity, vorticity, strip_fields, strip_fields)
    return new_vorticity, rows[:, 0, :]


def apply_block(vectors, matrix):
    return lax.dot_general(vectors, matrix, (((1,), (1,)), ((), ())), precision=EXACT_DOT)


def first_contract(left_side, right_side):
    return lax.dot_general(left_side, right_side, (((0,), (0,)), ((), ())), precision=EXACT_DOT)


def beam_solve(beam_load, pivot_inv, lower_block, upper_block):
    block_count = pivot_inv.shape[0]
    block_size = pivot_inv.shape[1]
    blocks = beam_load.reshape(beam_load.shape[0], block_count, block_size)
    carried = [blocks[:, 0]]
    for block_index in range(1, block_count):
        pivoted = apply_block(carried[-1], pivot_inv[block_index - 1])
        carried.append(blocks[:, block_index] - apply_block(pivoted, lower_block[block_index - 1]))
    solved = [apply_block(carried[-1], pivot_inv[block_count - 1])]
    for block_index in range(block_count - 2, -1, -1):
        remainder = carried[block_index] - apply_block(solved[0], upper_block[block_index])
        solved.insert(0, apply_block(remainder, pivot_inv[block_index]))
    return jnp.concatenate(solved, axis=1)


def start_kernel(owner_ref, riser_ref, node_ref, spread_ref, pivot_ref, lower_ref, upper_ref, fields_ref,
                 response_ref, vorticity_ref, sent_ref, *, substeps):
    block_count = pivot_ref.shape[1]
    block_size = pivot_ref.shape[2]
    node_count = block_count * block_size
    strips = node_ref.shape[1]
    per_device = fields_ref.shape[1]
    position = lax.axis_index("strip")
    group_position = lax.axis_index("group")

    riser = riser_ref[...]
    owner = jnp.zeros(riser.shape, jnp.int32)
    for riser_index in range(owner_ref.shape[1]):
        owner = jnp.where(riser == riser_index, owner_ref[0, riser_index], owner)
    owned_col = (owner == position).astype(jnp.float32)
    diagonal = lax.broadcasted_iota(jnp.int32, (strips, strips), 0) == lax.broadcasted_iota(jnp.int32, (strips, strips), 1)
    owned_row = jnp.sum(jnp.where(diagonal, owned_col, 0.0), axis=0, keepdims=True)
    node_row = node_ref[...]
    node_col = jnp.sum(jnp.where(diagonal, node_row.astype(jnp.float32), 0.0), axis=1, keepdims=True)

    def apply(matrix, vectors):
        return jnp.dot(matrix, vectors, precision=lax.Precision.HIGH, preferred_element_type=jnp.float32)

    def unit_load(block_index):
        node = block_index * block_size + lax.broadcasted_iota(jnp.int32, (block_size, strips), 0)
        return (node == node_row).astype(jnp.float32) * owned_row

    carried = [unit_load(0)]
    for block_index in range(1, block_count):
        pivoted = apply(pivot_ref[0, block_index - 1], carried[-1])
        carried.append(unit_load(block_index) - apply(lower_ref[0, block_index - 1], pivoted))
    solved = apply(pivot_ref[0, block_count - 1], carried[-1])
    response_ref[(block_count - 1) * block_size:, :] = solved
    for block_index in range(block_count - 2, -1, -1):
        remainder = carried[block_index] - apply(upper_ref[0, block_index], solved)
        solved = apply(pivot_ref[0, block_index], remainder)
        response_ref[block_index * block_size:(block_index + 1) * block_size, :] = solved

    _, _, lift_kernel, drag_kernel = kernel_planes(fields_ref.shape[-1])
    strip_of_row = lax.broadcasted_iota(jnp.int32, (per_device, 2 * substeps), 0)
    rows = jnp.zeros((per_device, 2 * substeps), jnp.float32)
    for strip in range(per_device):
        vorticity, row = run_substeps(
            fields_ref[0, strip], fields_ref[1, strip], fields_ref[2, strip], None,
            lift_kernel, drag_kernel, substeps,
        )
        vorticity_ref[strip] = vorticity
        rows = jnp.where(strip_of_row == strip, row, rows)

    node_onehot = (
        node_col == lax.broadcasted_iota(jnp.int32, (strips, node_count), 1).astype(jnp.float32)
    ).astype(jnp.float32)
    coupling = jnp.dot(node_onehot, response_ref[...], precision=EXACT_DOT, preferred_element_type=jnp.float32)
    coupling = coupling * owned_col
    sent_rows = sent_ref.shape[0]
    place = lax.broadcasted_iota(jnp.int32, (sent_rows, strips), 0) - group_position * strips
    pick = (place == lax.broadcasted_iota(jnp.int32, (sent_rows, strips), 1)).astype(jnp.float32)
    sent_ref[:, 0:2 * substeps] = jnp.dot(spread_ref[...], rows, precision=EXACT_DOT, preferred_element_type=jnp.float32)
    sent_ref[:, 2 * substeps:] = jnp.dot(pick, coupling, precision=EXACT_DOT, preferred_element_type=jnp.float32)


def spread_matrix(devices, per_device):
    return (
        jnp.arange(devices * per_device)[:, None] % per_device == jnp.arange(per_device)[None, :]
    ).astype(jnp.float32)


def start_step(riser_owner, strip_riser, strip_node, pivot_inv, lower_block, upper_block, strip_fields, devices, substeps):
    strips = strip_node.shape[0]
    node_count = pivot_inv.shape[1] * pivot_inv.shape[2]
    _, per_device, cells_y, cells_x = strip_fields.shape
    vmem = pl.BlockSpec(memory_space=pltpu.VMEM)
    return pl.pallas_call(
        lambda *refs: start_kernel(*refs, substeps=substeps),
        in_specs=[pl.BlockSpec(memory_space=pltpu.SMEM)] + [vmem] * 7,
        out_shape=[
            jax.ShapeDtypeStruct((node_count, strips), jnp.float32),
            jax.ShapeDtypeStruct((per_device, cells_y, cells_x), jnp.float32),
            jax.ShapeDtypeStruct((devices * per_device, 2 * substeps + strips), jnp.float32),
        ],
        name="start_step",
    )(
        riser_owner, strip_riser, strip_node[None, :], spread_matrix(devices, per_device),
        pivot_inv, lower_block, upper_block, strip_fields,
    )


def local(strip_fields, strip_riser, strip_node, riser_owner, pivot_inv, lower_block, upper_block):
    position = lax.axis_index("strip")
    group_position = lax.axis_index("group")
    group_count = lax.axis_size("group")
    devices = lax.axis_size("strip") * group_count
    per_device = strip_fields.shape[1]
    grid_cells = strip_fields.shape[2]
    node_count = pivot_inv.shape[1] * pivot_inv.shape[2]
    riser_count = riser_owner.shape[1]
    group_strips = strip_node.shape[0]
    substeps = NSUB
    total_strips = per_device * devices
    kernels = None
    local_node = lax.dynamic_slice_in_dim(strip_node, position * per_device, per_device)
    top_taper = 1.0 - jnp.arange(node_count, dtype=jnp.float32) / node_count
    local_taper = 1.0 - local_node.astype(jnp.float32) / node_count

    unit_response, first_vorticity, first_sent = start_step(
        riser_owner, strip_riser, strip_node, pivot_inv, lower_block, upper_block, strip_fields, devices, substeps
    )

    vorticity = strip_fields
    motion = jnp.zeros((per_device, 2 * substeps), jnp.float32)
    for coupled_step in range(COUPLED):
        if coupled_step == 0:
            vorticity, sent = first_vorticity[None], first_sent
        else:
            vorticity, force_rows = strip_step_kernel(strip_fields, vorticity, motion, kernels, substeps)
            sent = jnp.tile(force_rows, (devices, 1))
        received = lax.all_to_all(sent, ("group", "strip"), 0, 0, tiled=True)
        every_force = received[:, : 2 * substeps]
        offset = jnp.sum(every_force[:, substeps:], axis=0) / jnp.sqrt(jnp.float32(total_strips))
        group_force = lax.dynamic_slice_in_dim(every_force, group_position * group_strips, group_strips)
        if coupled_step + 1 < COUPLED:
            my_coupling = jnp.sum(
                received[:, 2 * substeps :].reshape(devices, per_device, group_strips), axis=0
            )
            motion = lax.dot_general(
                my_coupling, group_force, (((1,), (0,)), ((), ())), precision=EXACT_DOT
            )
            motion = motion.at[:, substeps:].add(local_taper[:, None] * offset[None, :])
        else:
            displacement = lax.dot_general(
                group_force, unit_response, (((0,), (1,)), ((), ())), precision=EXACT_DOT
            )
            displacement = displacement.at[substeps:, :].add(offset[:, None] * top_taper[None, :])
    return (vorticity, displacement[None])


def solution(mesh):
    in_specs = (
        P(None, ("group", "strip"), None, None),
        P("group", None),
        P("group"),
        P("group", None),
        P(("group", "strip"), None, None, None),
        P(("group", "strip"), None, None, None),
        P(("group", "strip"), None, None, None),
    )
    out_specs = (P(("group", "strip"), None, None), P(("group", "strip"), None, None))
    return jax.shard_map(local, mesh=mesh, in_specs=in_specs, out_specs=out_specs, check_vma=False)
```

```python
import numpy as np
import jax
import jax.numpy as jnp
from jax import lax
from jax.sharding import PartitionSpec as P
from jax.experimental import pallas as pl
from jax.experimental.pallas import tpu as pltpu

NSUB = 8
COUPLED = 2


TIME_STEP = 0.25
VISCOSITY = 0.05
COUPLING = 0.5
EXACT_DOT = lax.Precision.HIGHEST


def make_kernels(grid_cells):
    centre = jnp.arange(grid_cells, dtype=jnp.float32) - grid_cells / 2.0 + 0.5
    near_x = (centre / (grid_cells / 16.0))[None, :]
    near_y = (centre / (grid_cells / 16.0))[:, None]
    bell_near = jnp.exp(-(near_x * near_x + near_y * near_y) / 2.0)
    source_x = -near_x * bell_near
    source_y = -near_y * bell_near
    wide_x = (centre / (grid_cells / 8.0))[None, :]
    wide_y = (centre / (grid_cells / 8.0))[:, None]
    bell_wide = jnp.exp(-(wide_x * wide_x + wide_y * wide_y) / 2.0)
    lift_kernel = -wide_x * bell_wide
    drag_kernel = wide_y * bell_wide
    lift_kernel = lift_kernel / jnp.sqrt(jnp.sum(lift_kernel * lift_kernel))
    drag_kernel = drag_kernel / jnp.sqrt(jnp.sum(drag_kernel * drag_kernel))
    return (source_x, source_y, lift_kernel, drag_kernel)


def strip_step(vorticity, flow_x, flow_y, motion, kernels, substeps):
    source_x, source_y, lift_kernel, drag_kernel = kernels
    halves = motion.reshape(motion.shape[0], 2, substeps)
    earlier = jnp.concatenate([jnp.zeros_like(halves[:, :, :1]), halves[:, :, :-1]], axis=2)
    velocity = halves - earlier
    lift_rows = []
    drag_rows = []
    for substep in range(substeps):
        right_cell = jnp.roll(vorticity, -1, axis=2)
        left_cell = jnp.roll(vorticity, 1, axis=2)
        upper_cell = jnp.roll(vorticity, -1, axis=1)
        lower_cell = jnp.roll(vorticity, 1, axis=1)
        laplacian = right_cell + left_cell + upper_cell + lower_cell - 4.0 * vorticity
        tendency = (
            VISCOSITY * laplacian
            - flow_x * (0.5 * (right_cell - left_cell))
            - flow_y * (0.5 * (upper_cell - lower_cell))
        )
        forcing = (
            velocity[:, 0, substep][:, None, None] * source_x
            - velocity[:, 1, substep][:, None, None] * source_y
        )
        vorticity = vorticity + TIME_STEP * tendency + COUPLING * forcing
        lift_rows.append(jnp.sum(vorticity * lift_kernel, axis=(1, 2)))
        drag_rows.append(jnp.sum(vorticity * drag_kernel, axis=(1, 2)))
    return (vorticity, jnp.stack(lift_rows + drag_rows, axis=1))


def kernel_planes(cells):
    centre_x = lax.broadcasted_iota(jnp.int32, (cells, cells), 1).astype(jnp.float32) - cells / 2.0 + 0.5
    centre_y = lax.broadcasted_iota(jnp.int32, (cells, cells), 0).astype(jnp.float32) - cells / 2.0 + 0.5
    near_x = centre_x / (cells / 16.0)
    near_y = centre_y / (cells / 16.0)
    bell_near = jnp.exp(-(near_x * near_x + near_y * near_y) / 2.0)
    source_x = -near_x * bell_near
    source_y = -near_y * bell_near
    wide_x = centre_x / (cells / 8.0)
    wide_y = centre_y / (cells / 8.0)
    bell_wide = jnp.exp(-(wide_x * wide_x + wide_y * wide_y) / 2.0)
    lift_kernel = -wide_x * bell_wide
    drag_kernel = wide_y * bell_wide

    def total(plane):
        return jnp.sum(jnp.sum(plane, axis=0, keepdims=True), axis=1, keepdims=True)

    lift_kernel = lift_kernel / jnp.sqrt(total(lift_kernel * lift_kernel))
    drag_kernel = drag_kernel / jnp.sqrt(total(drag_kernel * drag_kernel))
    return (source_x, source_y, lift_kernel, drag_kernel)


def run_substeps(vorticity, flow_x, flow_y, forcing_of, lift_kernel, drag_kernel, substeps):
    rows_across, cols_across = vorticity.shape
    lane = lax.broadcasted_iota(jnp.int32, (1, 2 * substeps), 1)
    row = jnp.zeros((1, 2 * substeps), jnp.float32)
    for substep in range(substeps):
        right_cell = pltpu.roll(vorticity, cols_across - 1, 1)
        left_cell = pltpu.roll(vorticity, 1, 1)
        upper_cell = pltpu.roll(vorticity, rows_across - 1, 0)
        lower_cell = pltpu.roll(vorticity, 1, 0)
        laplacian = right_cell + left_cell + upper_cell + lower_cell - 4.0 * vorticity
        tendency = (
            VISCOSITY * laplacian
            - flow_x * (0.5 * (right_cell - left_cell))
            - flow_y * (0.5 * (upper_cell - lower_cell))
        )
        if forcing_of is None:
            vorticity = vorticity + TIME_STEP * tendency
        else:
            vorticity = vorticity + TIME_STEP * tendency + COUPLING * forcing_of(substep)
        lift = jnp.sum(jnp.sum(vorticity * lift_kernel, axis=0, keepdims=True), axis=1, keepdims=True)
        drag = jnp.sum(jnp.sum(vorticity * drag_kernel, axis=0, keepdims=True), axis=1, keepdims=True)
        row = row + jnp.where(lane == substep, lift, 0.0) + jnp.where(lane == substeps + substep, drag, 0.0)
    return vorticity, row


def stencil_kernel(velocity_ref, vorticity_ref, flow_x_ref, flow_y_ref, out_ref, rows_ref, *, substeps):
    strip = pl.program_id(0)
    source_x, source_y, lift_kernel, drag_kernel = kernel_planes(vorticity_ref.shape[-1])

    def forcing_of(substep):
        return (
            velocity_ref[strip, substep] * source_x
            - velocity_ref[strip, substeps + substep] * source_y
        )

    vorticity, row = run_substeps(
        vorticity_ref[0, 0], flow_x_ref[0, 0], flow_y_ref[0, 0], forcing_of,
        lift_kernel, drag_kernel, substeps,
    )
    out_ref[0] = vorticity
    rows_ref[0] = row


def strip_step_kernel(strip_fields, vorticity, motion, kernels, substeps):
    strips, cells_y, cells_x = strip_fields.shape[1:]
    halves = motion.reshape(strips, 2, substeps)
    earlier = jnp.concatenate([jnp.zeros_like(halves[:, :, :1]), halves[:, :, :-1]], axis=2)
    velocity = (halves - earlier).reshape(strips, 2 * substeps)
    def field(index):
        return pl.BlockSpec((1, 1, cells_y, cells_x), lambda s: (index, s, 0, 0))

    new_vorticity, rows = pl.pallas_call(
        lambda *refs: stencil_kernel(*refs, substeps=substeps),
        grid=(strips,),
        in_specs=[
            pl.BlockSpec(memory_space=pltpu.SMEM),
            field(0), field(1), field(2),
        ],
        out_specs=[
            pl.BlockSpec((1, cells_y, cells_x), lambda s: (s, 0, 0)),
            pl.BlockSpec((1, 1, 2 * substeps), lambda s: (s, 0, 0)),
        ],
        out_shape=[
            jax.ShapeDtypeStruct((strips, cells_y, cells_x), jnp.float32),
            jax.ShapeDtypeStruct((strips, 1, 2 * substeps), jnp.float32),
        ],
        name="strip_stencil",
    )(velocity, vorticity, strip_fields, strip_fields)
    return new_vorticity, rows[:, 0, :]


def apply_block(vectors, matrix):
    return lax.dot_general(vectors, matrix, (((1,), (1,)), ((), ())), precision=EXACT_DOT)


def first_contract(left_side, right_side):
    return lax.dot_general(left_side, right_side, (((0,), (0,)), ((), ())), precision=EXACT_DOT)


def beam_solve(beam_load, pivot_inv, lower_block, upper_block):
    block_count = pivot_inv.shape[0]
    block_size = pivot_inv.shape[1]
    blocks = beam_load.reshape(beam_load.shape[0], block_count, block_size)
    carried = [blocks[:, 0]]
    for block_index in range(1, block_count):
        pivoted = apply_block(carried[-1], pivot_inv[block_index - 1])
        carried.append(blocks[:, block_index] - apply_block(pivoted, lower_block[block_index - 1]))
    solved = [apply_block(carried[-1], pivot_inv[block_count - 1])]
    for block_index in range(block_count - 2, -1, -1):
        remainder = carried[block_index] - apply_block(solved[0], upper_block[block_index])
        solved.insert(0, apply_block(remainder, pivot_inv[block_index]))
    return jnp.concatenate(solved, axis=1)


def start_kernel(owner_ref, riser_ref, node_ref, spread_ref, pivot_ref, lower_ref, upper_ref, fields_ref,
                 response_ref, vorticity_ref, sent_ref, *, substeps):
    block_count = pivot_ref.shape[1]
    block_size = pivot_ref.shape[2]
    node_count = block_count * block_size
    strips = node_ref.shape[1]
    per_device = fields_ref.shape[1]
    position = lax.axis_index("strip")
    group_position = lax.axis_index("group")

    strip_lane = lax.broadcasted_iota(jnp.int32, (1, strips), 1)
    strip_sublane = lax.broadcasted_iota(jnp.int32, (strips, 1), 0)
    owned_row = jnp.zeros((1, strips), jnp.float32)
    owned_col = jnp.zeros((strips, 1), jnp.float32)
    for strip in range(strips):
        held = jnp.where(owner_ref[0, riser_ref[strip, 0]] == position, 1.0, 0.0)
        owned_row = jnp.where(strip_lane == strip, held, owned_row)
        owned_col = jnp.where(strip_sublane == strip, held, owned_col)
    diagonal = lax.broadcasted_iota(jnp.int32, (strips, strips), 0) == lax.broadcasted_iota(jnp.int32, (strips, strips), 1)
    node_row = node_ref[...]
    node_col = jnp.sum(jnp.where(diagonal, node_row.astype(jnp.float32), 0.0), axis=1, keepdims=True)

    def apply(matrix, vectors):
        return jnp.dot(matrix, vectors, precision=lax.Precision.HIGH, preferred_element_type=jnp.float32)

    def unit_load(block_index):
        node = block_index * block_size + lax.broadcasted_iota(jnp.int32, (block_size, strips), 0)
        return (node == node_row).astype(jnp.float32) * owned_row

    carried = [unit_load(0)]
    for block_index in range(1, block_count):
        pivoted = apply(pivot_ref[0, block_index - 1], carried[-1])
        carried.append(unit_load(block_index) - apply(lower_ref[0, block_index - 1], pivoted))
    solved = apply(pivot_ref[0, block_count - 1], carried[-1])
    response_ref[(block_count - 1) * block_size:, :] = solved
    for block_index in range(block_count - 2, -1, -1):
        remainder = carried[block_index] - apply(upper_ref[0, block_index], solved)
        solved = apply(pivot_ref[0, block_index], remainder)
        response_ref[block_index * block_size:(block_index + 1) * block_size, :] = solved

    _, _, lift_kernel, drag_kernel = kernel_planes(fields_ref.shape[-1])
    strip_of_row = lax.broadcasted_iota(jnp.int32, (per_device, 2 * substeps), 0)
    rows = jnp.zeros((per_device, 2 * substeps), jnp.float32)
    for strip in range(per_device):
        vorticity, row = run_substeps(
            fields_ref[0, strip], fields_ref[1, strip], fields_ref[2, strip], None,
            lift_kernel, drag_kernel, substeps,
        )
        vorticity_ref[strip] = vorticity
        rows = jnp.where(strip_of_row == strip, row, rows)

    node_onehot = (
        node_col == lax.broadcasted_iota(jnp.int32, (strips, node_count), 1).astype(jnp.float32)
    ).astype(jnp.float32)
    coupling = jnp.dot(node_onehot, response_ref[...], precision=EXACT_DOT, preferred_element_type=jnp.float32)
    coupling = coupling * owned_col
    sent_rows = sent_ref.shape[0]
    place = lax.broadcasted_iota(jnp.int32, (sent_rows, strips), 0) - group_position * strips
    pick = (place == lax.broadcasted_iota(jnp.int32, (sent_rows, strips), 1)).astype(jnp.float32)
    sent_ref[:, 0:2 * substeps] = jnp.dot(spread_ref[...], rows, precision=EXACT_DOT, preferred_element_type=jnp.float32)
    sent_ref[:, 2 * substeps:] = jnp.dot(pick, coupling, precision=EXACT_DOT, preferred_element_type=jnp.float32)


def spread_matrix(devices, per_device):
    return (
        np.arange(devices * per_device)[:, None] % per_device == np.arange(per_device)[None, :]
    ).astype(np.float32)


def start_step(riser_owner, strip_riser, strip_node, pivot_inv, lower_block, upper_block, strip_fields, devices, substeps):
    strips = strip_node.shape[0]
    node_count = pivot_inv.shape[1] * pivot_inv.shape[2]
    _, per_device, cells_y, cells_x = strip_fields.shape
    vmem = pl.BlockSpec(memory_space=pltpu.VMEM)
    return pl.pallas_call(
        lambda *refs: start_kernel(*refs, substeps=substeps),
        in_specs=[pl.BlockSpec(memory_space=pltpu.SMEM)] * 2 + [vmem] * 6,
        out_shape=[
            jax.ShapeDtypeStruct((node_count, strips), jnp.float32),
            jax.ShapeDtypeStruct((per_device, cells_y, cells_x), jnp.float32),
            jax.ShapeDtypeStruct((devices * per_device, 2 * substeps + strips), jnp.float32),
        ],
        name="start_step",
    )(
        riser_owner, strip_riser, strip_node[None, :], spread_matrix(devices, per_device),
        pivot_inv, lower_block, upper_block, strip_fields,
    )


def second_kernel(received_ref, node_ref, spread_ref, gather_ref, difference_ref, fields_ref, vorticity_ref,
                  out_ref, sent_ref, *, substeps, node_count):
    position = lax.axis_index("strip")
    group_position = lax.axis_index("group")
    total_strips, _ = received_ref.shape
    strips = node_ref.shape[1]
    per_device = fields_ref.shape[1]
    every_force = received_ref[:, 0:2 * substeps]
    offset = jnp.sum(every_force, axis=0, keepdims=True) / jnp.sqrt(jnp.float32(total_strips))
    group_force = received_ref[pl.ds(group_position * strips, strips), 0:2 * substeps]
    my_coupling = jnp.dot(
        gather_ref[...], received_ref[:, 2 * substeps:], precision=EXACT_DOT, preferred_element_type=jnp.float32
    )
    motion = jnp.dot(my_coupling, group_force, precision=EXACT_DOT, preferred_element_type=jnp.float32)
    mine = (
        lax.broadcasted_iota(jnp.int32, (per_device, strips), 1)
        == position * per_device + lax.broadcasted_iota(jnp.int32, (per_device, strips), 0)
    )
    local_node = jnp.sum(jnp.where(mine, node_ref[...].astype(jnp.float32), 0.0), axis=1, keepdims=True)
    local_taper = 1.0 - local_node / node_count
    lane = lax.broadcasted_iota(jnp.int32, (per_device, 2 * substeps), 1)
    sublane = lax.broadcasted_iota(jnp.int32, (per_device, 2 * substeps), 0)
    motion = motion + jnp.where(lane >= substeps, local_taper * offset, 0.0)
    velocity = jnp.dot(motion, difference_ref[...], precision=EXACT_DOT, preferred_element_type=jnp.float32)

    source_x, source_y, lift_kernel, drag_kernel = kernel_planes(fields_ref.shape[-1])
    rows = jnp.zeros((per_device, 2 * substeps), jnp.float32)
    for strip in range(per_device):
        picks = [
            jnp.sum(jnp.sum(jnp.where((sublane == strip) & (lane == column), velocity, 0.0), axis=0, keepdims=True), axis=1, keepdims=True)
            for column in range(2 * substeps)
        ]

        def forcing_of(substep, picks=picks):
            return picks[substep] * source_x - picks[substeps + substep] * source_y

        vorticity, row = run_substeps(
            vorticity_ref[strip], fields_ref[1, strip], fields_ref[2, strip], forcing_of,
            lift_kernel, drag_kernel, substeps,
        )
        out_ref[strip] = vorticity
        rows = jnp.where(sublane == strip, row, rows)
    sent_ref[...] = jnp.dot(spread_ref[...], rows, precision=EXACT_DOT, preferred_element_type=jnp.float32)


def difference_matrix(substeps):
    columns = np.arange(2 * substeps)
    same = columns[:, None] == columns[None, :]
    before = (columns[:, None] + 1 == columns[None, :]) & (columns[None, :] % substeps != 0)
    return same.astype(np.float32) - before.astype(np.float32)


def second_step(received, strip_node, strip_fields, vorticity, devices, node_count, substeps):
    _, per_device, cells_y, cells_x = strip_fields.shape
    spread = spread_matrix(devices, per_device)
    vmem = pl.BlockSpec(memory_space=pltpu.VMEM)
    return pl.pallas_call(
        lambda *refs: second_kernel(*refs, substeps=substeps, node_count=node_count),
        in_specs=[vmem] * 7,
        out_shape=[
            jax.ShapeDtypeStruct((per_device, cells_y, cells_x), jnp.float32),
            jax.ShapeDtypeStruct((devices * per_device, 2 * substeps), jnp.float32),
        ],
        name="second_step",
    )(received, strip_node[None, :], spread, np.ascontiguousarray(spread.T), difference_matrix(substeps), strip_fields, vorticity)


def local(strip_fields, strip_riser, strip_node, riser_owner, pivot_inv, lower_block, upper_block):
    position = lax.axis_index("strip")
    group_position = lax.axis_index("group")
    group_count = lax.axis_size("group")
    devices = lax.axis_size("strip") * group_count
    per_device = strip_fields.shape[1]
    grid_cells = strip_fields.shape[2]
    node_count = pivot_inv.shape[1] * pivot_inv.shape[2]
    riser_count = riser_owner.shape[1]
    group_strips = strip_node.shape[0]
    substeps = NSUB
    total_strips = per_device * devices
    kernels = None
    local_node = lax.dynamic_slice_in_dim(strip_node, position * per_device, per_device)
    top_taper = 1.0 - jnp.arange(node_count, dtype=jnp.float32) / node_count
    local_taper = 1.0 - local_node.astype(jnp.float32) / node_count

    unit_response, first_vorticity, first_sent = start_step(
        riser_owner, strip_riser, strip_node, pivot_inv, lower_block, upper_block, strip_fields, devices, substeps
    )

    received = lax.all_to_all(first_sent, ("group", "strip"), 0, 0, tiled=True)
    vorticity, sent = second_step(received, strip_node, strip_fields, first_vorticity, devices, node_count, substeps)
    received = lax.all_to_all(sent, ("group", "strip"), 0, 0, tiled=True)
    offset = jnp.sum(received[:, substeps:], axis=0) / jnp.sqrt(jnp.float32(total_strips))
    group_force = lax.dynamic_slice_in_dim(received, group_position * group_strips, group_strips)
    displacement = lax.dot_general(
        group_force, unit_response, (((0,), (1,)), ((), ())), precision=EXACT_DOT
    )
    displacement = displacement.at[substeps:, :].add(offset[:, None] * top_taper[None, :])
    return (vorticity, displacement[None])


def solution(mesh):
    in_specs = (
        P(None, ("group", "strip"), None, None),
        P("group", None),
        P("group"),
        P("group", None),
        P(("group", "strip"), None, None, None),
        P(("group", "strip"), None, None, None),
        P(("group", "strip"), None, None, None),
    )
    out_specs = (P(("group", "strip"), None, None), P(("group", "strip"), None, None))
    return jax.shard_map(local, mesh=mesh, in_specs=in_specs, out_specs=out_specs, check_vma=False)
```

```python
import numpy as np
import jax
import jax.numpy as jnp
from jax import lax
from jax.sharding import PartitionSpec as P
from jax.experimental import pallas as pl
from jax.experimental.pallas import tpu as pltpu

NSUB = 8
COUPLED = 2


TIME_STEP = 0.25
VISCOSITY = 0.05
COUPLING = 0.5
EXACT_DOT = lax.Precision.HIGHEST


def make_kernels(grid_cells):
    centre = jnp.arange(grid_cells, dtype=jnp.float32) - grid_cells / 2.0 + 0.5
    near_x = (centre / (grid_cells / 16.0))[None, :]
    near_y = (centre / (grid_cells / 16.0))[:, None]
    bell_near = jnp.exp(-(near_x * near_x + near_y * near_y) / 2.0)
    source_x = -near_x * bell_near
    source_y = -near_y * bell_near
    wide_x = (centre / (grid_cells / 8.0))[None, :]
    wide_y = (centre / (grid_cells / 8.0))[:, None]
    bell_wide = jnp.exp(-(wide_x * wide_x + wide_y * wide_y) / 2.0)
    lift_kernel = -wide_x * bell_wide
    drag_kernel = wide_y * bell_wide
    lift_kernel = lift_kernel / jnp.sqrt(jnp.sum(lift_kernel * lift_kernel))
    drag_kernel = drag_kernel / jnp.sqrt(jnp.sum(drag_kernel * drag_kernel))
    return (source_x, source_y, lift_kernel, drag_kernel)


def strip_step(vorticity, flow_x, flow_y, motion, kernels, substeps):
    source_x, source_y, lift_kernel, drag_kernel = kernels
    halves = motion.reshape(motion.shape[0], 2, substeps)
    earlier = jnp.concatenate([jnp.zeros_like(halves[:, :, :1]), halves[:, :, :-1]], axis=2)
    velocity = halves - earlier
    lift_rows = []
    drag_rows = []
    for substep in range(substeps):
        right_cell = jnp.roll(vorticity, -1, axis=2)
        left_cell = jnp.roll(vorticity, 1, axis=2)
        upper_cell = jnp.roll(vorticity, -1, axis=1)
        lower_cell = jnp.roll(vorticity, 1, axis=1)
        laplacian = right_cell + left_cell + upper_cell + lower_cell - 4.0 * vorticity
        tendency = (
            VISCOSITY * laplacian
            - flow_x * (0.5 * (right_cell - left_cell))
            - flow_y * (0.5 * (upper_cell - lower_cell))
        )
        forcing = (
            velocity[:, 0, substep][:, None, None] * source_x
            - velocity[:, 1, substep][:, None, None] * source_y
        )
        vorticity = vorticity + TIME_STEP * tendency + COUPLING * forcing
        lift_rows.append(jnp.sum(vorticity * lift_kernel, axis=(1, 2)))
        drag_rows.append(jnp.sum(vorticity * drag_kernel, axis=(1, 2)))
    return (vorticity, jnp.stack(lift_rows + drag_rows, axis=1))


def kernel_planes(cells):
    centre_x = lax.broadcasted_iota(jnp.int32, (cells, cells), 1).astype(jnp.float32) - cells / 2.0 + 0.5
    centre_y = lax.broadcasted_iota(jnp.int32, (cells, cells), 0).astype(jnp.float32) - cells / 2.0 + 0.5
    near_x = centre_x / (cells / 16.0)
    near_y = centre_y / (cells / 16.0)
    bell_near = jnp.exp(-(near_x * near_x + near_y * near_y) / 2.0)
    source_x = -near_x * bell_near
    source_y = -near_y * bell_near
    wide_x = centre_x / (cells / 8.0)
    wide_y = centre_y / (cells / 8.0)
    bell_wide = jnp.exp(-(wide_x * wide_x + wide_y * wide_y) / 2.0)
    lift_kernel = -wide_x * bell_wide
    drag_kernel = wide_y * bell_wide

    def total(plane):
        return jnp.sum(jnp.sum(plane, axis=0, keepdims=True), axis=1, keepdims=True)

    lift_kernel = lift_kernel / jnp.sqrt(total(lift_kernel * lift_kernel))
    drag_kernel = drag_kernel / jnp.sqrt(total(drag_kernel * drag_kernel))
    return (source_x, source_y, lift_kernel, drag_kernel)


def run_substeps(vorticity, flow_x, flow_y, forcing_of, lift_kernel, drag_kernel, substeps):
    rows_across, cols_across = vorticity.shape
    lane = lax.broadcasted_iota(jnp.int32, (1, 2 * substeps), 1)
    row = jnp.zeros((1, 2 * substeps), jnp.float32)
    for substep in range(substeps):
        right_cell = pltpu.roll(vorticity, cols_across - 1, 1)
        left_cell = pltpu.roll(vorticity, 1, 1)
        upper_cell = pltpu.roll(vorticity, rows_across - 1, 0)
        lower_cell = pltpu.roll(vorticity, 1, 0)
        laplacian = right_cell + left_cell + upper_cell + lower_cell - 4.0 * vorticity
        tendency = (
            VISCOSITY * laplacian
            - flow_x * (0.5 * (right_cell - left_cell))
            - flow_y * (0.5 * (upper_cell - lower_cell))
        )
        if forcing_of is None:
            vorticity = vorticity + TIME_STEP * tendency
        else:
            vorticity = vorticity + TIME_STEP * tendency + COUPLING * forcing_of(substep)
        lift = jnp.sum(jnp.sum(vorticity * lift_kernel, axis=0, keepdims=True), axis=1, keepdims=True)
        drag = jnp.sum(jnp.sum(vorticity * drag_kernel, axis=0, keepdims=True), axis=1, keepdims=True)
        row = row + jnp.where(lane == substep, lift, 0.0) + jnp.where(lane == substeps + substep, drag, 0.0)
    return vorticity, row


def stencil_kernel(velocity_ref, vorticity_ref, flow_x_ref, flow_y_ref, out_ref, rows_ref, *, substeps):
    strip = pl.program_id(0)
    source_x, source_y, lift_kernel, drag_kernel = kernel_planes(vorticity_ref.shape[-1])

    def forcing_of(substep):
        return (
            velocity_ref[strip, substep] * source_x
            - velocity_ref[strip, substeps + substep] * source_y
        )

    vorticity, row = run_substeps(
        vorticity_ref[0, 0], flow_x_ref[0, 0], flow_y_ref[0, 0], forcing_of,
        lift_kernel, drag_kernel, substeps,
    )
    out_ref[0] = vorticity
    rows_ref[0] = row


def strip_step_kernel(strip_fields, vorticity, motion, kernels, substeps):
    strips, cells_y, cells_x = strip_fields.shape[1:]
    halves = motion.reshape(strips, 2, substeps)
    earlier = jnp.concatenate([jnp.zeros_like(halves[:, :, :1]), halves[:, :, :-1]], axis=2)
    velocity = (halves - earlier).reshape(strips, 2 * substeps)
    def field(index):
        return pl.BlockSpec((1, 1, cells_y, cells_x), lambda s: (index, s, 0, 0))

    new_vorticity, rows = pl.pallas_call(
        lambda *refs: stencil_kernel(*refs, substeps=substeps),
        grid=(strips,),
        in_specs=[
            pl.BlockSpec(memory_space=pltpu.SMEM),
            field(0), field(1), field(2),
        ],
        out_specs=[
            pl.BlockSpec((1, cells_y, cells_x), lambda s: (s, 0, 0)),
            pl.BlockSpec((1, 1, 2 * substeps), lambda s: (s, 0, 0)),
        ],
        out_shape=[
            jax.ShapeDtypeStruct((strips, cells_y, cells_x), jnp.float32),
            jax.ShapeDtypeStruct((strips, 1, 2 * substeps), jnp.float32),
        ],
        name="strip_stencil",
    )(velocity, vorticity, strip_fields, strip_fields)
    return new_vorticity, rows[:, 0, :]


def apply_block(vectors, matrix):
    return lax.dot_general(vectors, matrix, (((1,), (1,)), ((), ())), precision=EXACT_DOT)


def first_contract(left_side, right_side):
    return lax.dot_general(left_side, right_side, (((0,), (0,)), ((), ())), precision=EXACT_DOT)


def beam_solve(beam_load, pivot_inv, lower_block, upper_block):
    block_count = pivot_inv.shape[0]
    block_size = pivot_inv.shape[1]
    blocks = beam_load.reshape(beam_load.shape[0], block_count, block_size)
    carried = [blocks[:, 0]]
    for block_index in range(1, block_count):
        pivoted = apply_block(carried[-1], pivot_inv[block_index - 1])
        carried.append(blocks[:, block_index] - apply_block(pivoted, lower_block[block_index - 1]))
    solved = [apply_block(carried[-1], pivot_inv[block_count - 1])]
    for block_index in range(block_count - 2, -1, -1):
        remainder = carried[block_index] - apply_block(solved[0], upper_block[block_index])
        solved.insert(0, apply_block(remainder, pivot_inv[block_index]))
    return jnp.concatenate(solved, axis=1)


def start_kernel(owner_ref, riser_ref, node_ref, spread_ref, pivot_ref, lower_ref, upper_ref, fields_ref,
                 response_ref, vorticity_ref, sent_ref, *, substeps):
    block_count = pivot_ref.shape[1]
    block_size = pivot_ref.shape[2]
    node_count = block_count * block_size
    strips = node_ref.shape[1]
    per_device = fields_ref.shape[1]
    position = lax.axis_index("strip")
    group_position = lax.axis_index("group")

    strip_lane = lax.broadcasted_iota(jnp.int32, (1, strips), 1)
    strip_sublane = lax.broadcasted_iota(jnp.int32, (strips, 1), 0)
    owned_row = jnp.zeros((1, strips), jnp.float32)
    owned_col = jnp.zeros((strips, 1), jnp.float32)
    for strip in range(strips):
        held = jnp.where(owner_ref[0, riser_ref[strip]] == position, 1.0, 0.0)
        owned_row = jnp.where(strip_lane == strip, held, owned_row)
        owned_col = jnp.where(strip_sublane == strip, held, owned_col)
    diagonal = lax.broadcasted_iota(jnp.int32, (strips, strips), 0) == lax.broadcasted_iota(jnp.int32, (strips, strips), 1)
    node_row = node_ref[...]
    node_col = jnp.sum(jnp.where(diagonal, node_row.astype(jnp.float32), 0.0), axis=1, keepdims=True)

    def apply(matrix, vectors):
        return jnp.dot(matrix, vectors, precision=lax.Precision.HIGH, preferred_element_type=jnp.float32)

    def unit_load(block_index):
        node = block_index * block_size + lax.broadcasted_iota(jnp.int32, (block_size, strips), 0)
        return (node == node_row).astype(jnp.float32) * owned_row

    carried = [unit_load(0)]
    for block_index in range(1, block_count):
        pivoted = apply(pivot_ref[0, block_index - 1], carried[-1])
        carried.append(unit_load(block_index) - apply(lower_ref[0, block_index - 1], pivoted))
    solved = apply(pivot_ref[0, block_count - 1], carried[-1])
    response_ref[(block_count - 1) * block_size:, :] = solved
    for block_index in range(block_count - 2, -1, -1):
        remainder = carried[block_index] - apply(upper_ref[0, block_index], solved)
        solved = apply(pivot_ref[0, block_index], remainder)
        response_ref[block_index * block_size:(block_index + 1) * block_size, :] = solved

    _, _, lift_kernel, drag_kernel = kernel_planes(fields_ref.shape[-1])
    strip_of_row = lax.broadcasted_iota(jnp.int32, (per_device, 2 * substeps), 0)
    rows = jnp.zeros((per_device, 2 * substeps), jnp.float32)
    for strip in range(per_device):
        vorticity, row = run_substeps(
            fields_ref[0, strip], fields_ref[1, strip], fields_ref[2, strip], None,
            lift_kernel, drag_kernel, substeps,
        )
        vorticity_ref[strip] = vorticity
        rows = jnp.where(strip_of_row == strip, row, rows)

    node_onehot = (
        node_col == lax.broadcasted_iota(jnp.int32, (strips, node_count), 1).astype(jnp.float32)
    ).astype(jnp.float32)
    coupling = jnp.dot(node_onehot, response_ref[...], precision=EXACT_DOT, preferred_element_type=jnp.float32)
    coupling = coupling * owned_col
    sent_rows = sent_ref.shape[0]
    place = lax.broadcasted_iota(jnp.int32, (sent_rows, strips), 0) - group_position * strips
    pick = (place == lax.broadcasted_iota(jnp.int32, (sent_rows, strips), 1)).astype(jnp.float32)
    sent_ref[:, 0:2 * substeps] = jnp.dot(spread_ref[...], rows, precision=EXACT_DOT, preferred_element_type=jnp.float32)
    sent_ref[:, 2 * substeps:] = jnp.dot(pick, coupling, precision=EXACT_DOT, preferred_element_type=jnp.float32)


def spread_matrix(devices, per_device):
    return (
        np.arange(devices * per_device)[:, None] % per_device == np.arange(per_device)[None, :]
    ).astype(np.float32)


def start_step(riser_owner, strip_riser, strip_node, pivot_inv, lower_block, upper_block, strip_fields, devices, substeps):
    strips = strip_node.shape[0]
    node_count = pivot_inv.shape[1] * pivot_inv.shape[2]
    _, per_device, cells_y, cells_x = strip_fields.shape
    vmem = pl.BlockSpec(memory_space=pltpu.VMEM)
    return pl.pallas_call(
        lambda *refs: start_kernel(*refs, substeps=substeps),
        in_specs=[pl.BlockSpec(memory_space=pltpu.SMEM)] * 2 + [vmem] * 6,
        out_shape=[
            jax.ShapeDtypeStruct((node_count, strips), jnp.float32),
            jax.ShapeDtypeStruct((per_device, cells_y, cells_x), jnp.float32),
            jax.ShapeDtypeStruct((devices * per_device, 2 * substeps + strips), jnp.float32),
        ],
        name="start_step",
    )(
        riser_owner, strip_riser.reshape(strips), strip_node[None, :], spread_matrix(devices, per_device),
        pivot_inv, lower_block, upper_block, strip_fields,
    )


def second_kernel(received_ref, node_ref, spread_ref, gather_ref, difference_ref, fields_ref, vorticity_ref,
                  out_ref, sent_ref, *, substeps, node_count):
    position = lax.axis_index("strip")
    group_position = lax.axis_index("group")
    total_strips, _ = received_ref.shape
    strips = node_ref.shape[1]
    per_device = fields_ref.shape[1]
    every_force = received_ref[:, 0:2 * substeps]
    offset = jnp.sum(every_force, axis=0, keepdims=True) / jnp.sqrt(jnp.float32(total_strips))
    group_force = received_ref[pl.ds(group_position * strips, strips), 0:2 * substeps]
    my_coupling = jnp.dot(
        gather_ref[...], received_ref[:, 2 * substeps:], precision=EXACT_DOT, preferred_element_type=jnp.float32
    )
    motion = jnp.dot(my_coupling, group_force, precision=EXACT_DOT, preferred_element_type=jnp.float32)
    mine = (
        lax.broadcasted_iota(jnp.int32, (per_device, strips), 1)
        == position * per_device + lax.broadcasted_iota(jnp.int32, (per_device, strips), 0)
    )
    local_node = jnp.sum(jnp.where(mine, node_ref[...].astype(jnp.float32), 0.0), axis=1, keepdims=True)
    local_taper = 1.0 - local_node / node_count
    lane = lax.broadcasted_iota(jnp.int32, (per_device, 2 * substeps), 1)
    sublane = lax.broadcasted_iota(jnp.int32, (per_device, 2 * substeps), 0)
    motion = motion + jnp.where(lane >= substeps, local_taper * offset, 0.0)
    velocity = jnp.dot(motion, difference_ref[...], precision=EXACT_DOT, preferred_element_type=jnp.float32)

    source_x, source_y, lift_kernel, drag_kernel = kernel_planes(fields_ref.shape[-1])
    rows = jnp.zeros((per_device, 2 * substeps), jnp.float32)
    for strip in range(per_device):
        picks = [
            jnp.sum(jnp.sum(jnp.where((sublane == strip) & (lane == column), velocity, 0.0), axis=0, keepdims=True), axis=1, keepdims=True)
            for column in range(2 * substeps)
        ]

        def forcing_of(substep, picks=picks):
            return picks[substep] * source_x - picks[substeps + substep] * source_y

        vorticity, row = run_substeps(
            vorticity_ref[strip], fields_ref[1, strip], fields_ref[2, strip], forcing_of,
            lift_kernel, drag_kernel, substeps,
        )
        out_ref[strip] = vorticity
        rows = jnp.where(sublane == strip, row, rows)
    sent_ref[...] = jnp.dot(spread_ref[...], rows, precision=EXACT_DOT, preferred_element_type=jnp.float32)


def difference_matrix(substeps):
    columns = np.arange(2 * substeps)
    same = columns[:, None] == columns[None, :]
    before = (columns[:, None] + 1 == columns[None, :]) & (columns[None, :] % substeps != 0)
    return same.astype(np.float32) - before.astype(np.float32)


def second_step(received, strip_node, strip_fields, vorticity, devices, node_count, substeps):
    _, per_device, cells_y, cells_x = strip_fields.shape
    spread = spread_matrix(devices, per_device)
    vmem = pl.BlockSpec(memory_space=pltpu.VMEM)
    return pl.pallas_call(
        lambda *refs: second_kernel(*refs, substeps=substeps, node_count=node_count),
        in_specs=[vmem] * 7,
        out_shape=[
            jax.ShapeDtypeStruct((per_device, cells_y, cells_x), jnp.float32),
            jax.ShapeDtypeStruct((devices * per_device, 2 * substeps), jnp.float32),
        ],
        name="second_step",
    )(received, strip_node[None, :], spread, np.ascontiguousarray(spread.T), difference_matrix(substeps), strip_fields, vorticity)


def local(strip_fields, strip_riser, strip_node, riser_owner, pivot_inv, lower_block, upper_block):
    position = lax.axis_index("strip")
    group_position = lax.axis_index("group")
    group_count = lax.axis_size("group")
    devices = lax.axis_size("strip") * group_count
    per_device = strip_fields.shape[1]
    grid_cells = strip_fields.shape[2]
    node_count = pivot_inv.shape[1] * pivot_inv.shape[2]
    riser_count = riser_owner.shape[1]
    group_strips = strip_node.shape[0]
    substeps = NSUB
    total_strips = per_device * devices
    top_taper = 1.0 - jnp.arange(node_count, dtype=jnp.float32) / node_count

    unit_response, first_vorticity, first_sent = start_step(
        riser_owner, strip_riser, strip_node, pivot_inv, lower_block, upper_block, strip_fields, devices, substeps
    )

    received = lax.all_to_all(first_sent, ("group", "strip"), 0, 0, tiled=True)
    vorticity, sent = second_step(received, strip_node, strip_fields, first_vorticity, devices, node_count, substeps)
    received = lax.all_to_all(sent, ("group", "strip"), 0, 0, tiled=True)
    offset = jnp.sum(received[:, substeps:], axis=0) / jnp.sqrt(jnp.float32(total_strips))
    group_force = lax.dynamic_slice_in_dim(received, group_position * group_strips, group_strips)
    displacement = lax.dot_general(
        group_force, unit_response, (((0,), (1,)), ((), ())), precision=EXACT_DOT
    )
    displacement = displacement.at[substeps:, :].add(offset[:, None] * top_taper[None, :])
    return (vorticity, displacement[None])


def solution(mesh):
    in_specs = (
        P(None, ("group", "strip"), None, None),
        P("group", None),
        P("group"),
        P("group", None),
        P(("group", "strip"), None, None, None),
        P(("group", "strip"), None, None, None),
        P(("group", "strip"), None, None, None),
    )
    out_specs = (P(("group", "strip"), None, None), P(("group", "strip"), None, None))
    return jax.shard_map(local, mesh=mesh, in_specs=in_specs, out_specs=out_specs, check_vma=False)
```

```python
import numpy as np
import jax
import jax.numpy as jnp
from jax import lax
from jax.sharding import PartitionSpec as P
from jax.experimental import pallas as pl
from jax.experimental.pallas import tpu as pltpu

NSUB = 8
COUPLED = 2


TIME_STEP = 0.25
VISCOSITY = 0.05
COUPLING = 0.5
EXACT_DOT = lax.Precision.HIGHEST


def make_kernels(grid_cells):
    centre = jnp.arange(grid_cells, dtype=jnp.float32) - grid_cells / 2.0 + 0.5
    near_x = (centre / (grid_cells / 16.0))[None, :]
    near_y = (centre / (grid_cells / 16.0))[:, None]
    bell_near = jnp.exp(-(near_x * near_x + near_y * near_y) / 2.0)
    source_x = -near_x * bell_near
    source_y = -near_y * bell_near
    wide_x = (centre / (grid_cells / 8.0))[None, :]
    wide_y = (centre / (grid_cells / 8.0))[:, None]
    bell_wide = jnp.exp(-(wide_x * wide_x + wide_y * wide_y) / 2.0)
    lift_kernel = -wide_x * bell_wide
    drag_kernel = wide_y * bell_wide
    lift_kernel = lift_kernel / jnp.sqrt(jnp.sum(lift_kernel * lift_kernel))
    drag_kernel = drag_kernel / jnp.sqrt(jnp.sum(drag_kernel * drag_kernel))
    return (source_x, source_y, lift_kernel, drag_kernel)


def strip_step(vorticity, flow_x, flow_y, motion, kernels, substeps):
    source_x, source_y, lift_kernel, drag_kernel = kernels
    halves = motion.reshape(motion.shape[0], 2, substeps)
    earlier = jnp.concatenate([jnp.zeros_like(halves[:, :, :1]), halves[:, :, :-1]], axis=2)
    velocity = halves - earlier
    lift_rows = []
    drag_rows = []
    for substep in range(substeps):
        right_cell = jnp.roll(vorticity, -1, axis=2)
        left_cell = jnp.roll(vorticity, 1, axis=2)
        upper_cell = jnp.roll(vorticity, -1, axis=1)
        lower_cell = jnp.roll(vorticity, 1, axis=1)
        laplacian = right_cell + left_cell + upper_cell + lower_cell - 4.0 * vorticity
        tendency = (
            VISCOSITY * laplacian
            - flow_x * (0.5 * (right_cell - left_cell))
            - flow_y * (0.5 * (upper_cell - lower_cell))
        )
        forcing = (
            velocity[:, 0, substep][:, None, None] * source_x
            - velocity[:, 1, substep][:, None, None] * source_y
        )
        vorticity = vorticity + TIME_STEP * tendency + COUPLING * forcing
        lift_rows.append(jnp.sum(vorticity * lift_kernel, axis=(1, 2)))
        drag_rows.append(jnp.sum(vorticity * drag_kernel, axis=(1, 2)))
    return (vorticity, jnp.stack(lift_rows + drag_rows, axis=1))


def kernel_planes(cells):
    centre_x = lax.broadcasted_iota(jnp.int32, (cells, cells), 1).astype(jnp.float32) - cells / 2.0 + 0.5
    centre_y = lax.broadcasted_iota(jnp.int32, (cells, cells), 0).astype(jnp.float32) - cells / 2.0 + 0.5
    near_x = centre_x / (cells / 16.0)
    near_y = centre_y / (cells / 16.0)
    bell_near = jnp.exp(-(near_x * near_x + near_y * near_y) / 2.0)
    source_x = -near_x * bell_near
    source_y = -near_y * bell_near
    wide_x = centre_x / (cells / 8.0)
    wide_y = centre_y / (cells / 8.0)
    bell_wide = jnp.exp(-(wide_x * wide_x + wide_y * wide_y) / 2.0)
    lift_kernel = -wide_x * bell_wide
    drag_kernel = wide_y * bell_wide

    def total(plane):
        return jnp.sum(jnp.sum(plane, axis=0, keepdims=True), axis=1, keepdims=True)

    lift_kernel = lift_kernel / jnp.sqrt(total(lift_kernel * lift_kernel))
    drag_kernel = drag_kernel / jnp.sqrt(total(drag_kernel * drag_kernel))
    return (source_x, source_y, lift_kernel, drag_kernel)


def run_substeps(vorticity, flow_x, flow_y, forcing_of, lift_kernel, drag_kernel, substeps):
    rows_across, cols_across = vorticity.shape
    lane = lax.broadcasted_iota(jnp.int32, (1, 2 * substeps), 1)
    row = jnp.zeros((1, 2 * substeps), jnp.float32)
    for substep in range(substeps):
        right_cell = pltpu.roll(vorticity, cols_across - 1, 1)
        left_cell = pltpu.roll(vorticity, 1, 1)
        upper_cell = pltpu.roll(vorticity, rows_across - 1, 0)
        lower_cell = pltpu.roll(vorticity, 1, 0)
        laplacian = right_cell + left_cell + upper_cell + lower_cell - 4.0 * vorticity
        tendency = (
            VISCOSITY * laplacian
            - flow_x * (0.5 * (right_cell - left_cell))
            - flow_y * (0.5 * (upper_cell - lower_cell))
        )
        if forcing_of is None:
            vorticity = vorticity + TIME_STEP * tendency
        else:
            vorticity = vorticity + TIME_STEP * tendency + COUPLING * forcing_of(substep)
        lift = jnp.sum(jnp.sum(vorticity * lift_kernel, axis=0, keepdims=True), axis=1, keepdims=True)
        drag = jnp.sum(jnp.sum(vorticity * drag_kernel, axis=0, keepdims=True), axis=1, keepdims=True)
        row = row + jnp.where(lane == substep, lift, 0.0) + jnp.where(lane == substeps + substep, drag, 0.0)
    return vorticity, row


def stencil_kernel(velocity_ref, vorticity_ref, flow_x_ref, flow_y_ref, out_ref, rows_ref, *, substeps):
    strip = pl.program_id(0)
    source_x, source_y, lift_kernel, drag_kernel = kernel_planes(vorticity_ref.shape[-1])

    def forcing_of(substep):
        return (
            velocity_ref[strip, substep] * source_x
            - velocity_ref[strip, substeps + substep] * source_y
        )

    vorticity, row = run_substeps(
        vorticity_ref[0, 0], flow_x_ref[0, 0], flow_y_ref[0, 0], forcing_of,
        lift_kernel, drag_kernel, substeps,
    )
    out_ref[0] = vorticity
    rows_ref[0] = row


def strip_step_kernel(strip_fields, vorticity, motion, kernels, substeps):
    strips, cells_y, cells_x = strip_fields.shape[1:]
    halves = motion.reshape(strips, 2, substeps)
    earlier = jnp.concatenate([jnp.zeros_like(halves[:, :, :1]), halves[:, :, :-1]], axis=2)
    velocity = (halves - earlier).reshape(strips, 2 * substeps)
    def field(index):
        return pl.BlockSpec((1, 1, cells_y, cells_x), lambda s: (index, s, 0, 0))

    new_vorticity, rows = pl.pallas_call(
        lambda *refs: stencil_kernel(*refs, substeps=substeps),
        grid=(strips,),
        in_specs=[
            pl.BlockSpec(memory_space=pltpu.SMEM),
            field(0), field(1), field(2),
        ],
        out_specs=[
            pl.BlockSpec((1, cells_y, cells_x), lambda s: (s, 0, 0)),
            pl.BlockSpec((1, 1, 2 * substeps), lambda s: (s, 0, 0)),
        ],
        out_shape=[
            jax.ShapeDtypeStruct((strips, cells_y, cells_x), jnp.float32),
            jax.ShapeDtypeStruct((strips, 1, 2 * substeps), jnp.float32),
        ],
        name="strip_stencil",
    )(velocity, vorticity, strip_fields, strip_fields)
    return new_vorticity, rows[:, 0, :]


def apply_block(vectors, matrix):
    return lax.dot_general(vectors, matrix, (((1,), (1,)), ((), ())), precision=EXACT_DOT)


def first_contract(left_side, right_side):
    return lax.dot_general(left_side, right_side, (((0,), (0,)), ((), ())), precision=EXACT_DOT)


def beam_solve(beam_load, pivot_inv, lower_block, upper_block):
    block_count = pivot_inv.shape[0]
    block_size = pivot_inv.shape[1]
    blocks = beam_load.reshape(beam_load.shape[0], block_count, block_size)
    carried = [blocks[:, 0]]
    for block_index in range(1, block_count):
        pivoted = apply_block(carried[-1], pivot_inv[block_index - 1])
        carried.append(blocks[:, block_index] - apply_block(pivoted, lower_block[block_index - 1]))
    solved = [apply_block(carried[-1], pivot_inv[block_count - 1])]
    for block_index in range(block_count - 2, -1, -1):
        remainder = carried[block_index] - apply_block(solved[0], upper_block[block_index])
        solved.insert(0, apply_block(remainder, pivot_inv[block_index]))
    return jnp.concatenate(solved, axis=1)


def start_kernel(owner_ref, riser_ref, node_ref, spread_ref, pivot_hbm, lower_hbm, upper_hbm, fields_ref,
                 response_ref, vorticity_ref, sent_ref, pivot_ref, lower_ref, upper_ref, copy_sems, *, substeps):
    block_count = pivot_hbm.shape[1]
    block_size = pivot_hbm.shape[2]
    pending = {}

    def fetch(name, source, target, block_index):
        copy = pltpu.make_async_copy(source.at[0, block_index], target.at[block_index], copy_sems.at[len(pending)])
        copy.start()
        pending[(name, block_index)] = copy

    for block_index in range(block_count - 1):
        fetch("pivot", pivot_hbm, pivot_ref, block_index)
        fetch("lower", lower_hbm, lower_ref, block_index)
    fetch("pivot", pivot_hbm, pivot_ref, block_count - 1)
    for block_index in range(block_count - 2, -1, -1):
        fetch("upper", upper_hbm, upper_ref, block_index)

    def block(name, ref, block_index):
        pending.pop((name, block_index)).wait()
        return ref[block_index]

    node_count = block_count * block_size
    strips = node_ref.shape[1]
    per_device = fields_ref.shape[1]
    position = lax.axis_index("strip")
    group_position = lax.axis_index("group")

    strip_lane = lax.broadcasted_iota(jnp.int32, (1, strips), 1)
    strip_sublane = lax.broadcasted_iota(jnp.int32, (strips, 1), 0)
    owned_row = jnp.zeros((1, strips), jnp.float32)
    owned_col = jnp.zeros((strips, 1), jnp.float32)
    for strip in range(strips):
        held = jnp.where(owner_ref[0, riser_ref[strip]] == position, 1.0, 0.0)
        owned_row = jnp.where(strip_lane == strip, held, owned_row)
        owned_col = jnp.where(strip_sublane == strip, held, owned_col)
    diagonal = lax.broadcasted_iota(jnp.int32, (strips, strips), 0) == lax.broadcasted_iota(jnp.int32, (strips, strips), 1)
    node_row = node_ref[...]
    node_col = jnp.sum(jnp.where(diagonal, node_row.astype(jnp.float32), 0.0), axis=1, keepdims=True)

    def apply(matrix, vectors):
        return jnp.dot(matrix, vectors, precision=lax.Precision.HIGH, preferred_element_type=jnp.float32)

    def unit_load(block_index):
        node = block_index * block_size + lax.broadcasted_iota(jnp.int32, (block_size, strips), 0)
        return (node == node_row).astype(jnp.float32) * owned_row

    carried = [unit_load(0)]
    for block_index in range(1, block_count):
        pivoted = apply(block("pivot", pivot_ref, block_index - 1), carried[-1])
        carried.append(unit_load(block_index) - apply(block("lower", lower_ref, block_index - 1), pivoted))
    solved = apply(block("pivot", pivot_ref, block_count - 1), carried[-1])
    response_ref[(block_count - 1) * block_size:, :] = solved
    for block_index in range(block_count - 2, -1, -1):
        remainder = carried[block_index] - apply(block("upper", upper_ref, block_index), solved)
        solved = apply(pivot_ref[block_index], remainder)
        response_ref[block_index * block_size:(block_index + 1) * block_size, :] = solved

    _, _, lift_kernel, drag_kernel = kernel_planes(fields_ref.shape[-1])
    strip_of_row = lax.broadcasted_iota(jnp.int32, (per_device, 2 * substeps), 0)
    rows = jnp.zeros((per_device, 2 * substeps), jnp.float32)
    for strip in range(per_device):
        vorticity, row = run_substeps(
            fields_ref[0, strip], fields_ref[1, strip], fields_ref[2, strip], None,
            lift_kernel, drag_kernel, substeps,
        )
        vorticity_ref[strip] = vorticity
        rows = jnp.where(strip_of_row == strip, row, rows)

    node_onehot = (
        node_col == lax.broadcasted_iota(jnp.int32, (strips, node_count), 1).astype(jnp.float32)
    ).astype(jnp.float32)
    coupling = jnp.dot(node_onehot, response_ref[...], precision=EXACT_DOT, preferred_element_type=jnp.float32)
    coupling = coupling * owned_col
    sent_rows = sent_ref.shape[0]
    place = lax.broadcasted_iota(jnp.int32, (sent_rows, strips), 0) - group_position * strips
    pick = (place == lax.broadcasted_iota(jnp.int32, (sent_rows, strips), 1)).astype(jnp.float32)
    sent_ref[:, 0:2 * substeps] = jnp.dot(spread_ref[...], rows, precision=EXACT_DOT, preferred_element_type=jnp.float32)
    sent_ref[:, 2 * substeps:] = jnp.dot(pick, coupling, precision=EXACT_DOT, preferred_element_type=jnp.float32)


def spread_matrix(devices, per_device):
    return (
        np.arange(devices * per_device)[:, None] % per_device == np.arange(per_device)[None, :]
    ).astype(np.float32)


def start_step(riser_owner, strip_riser, strip_node, pivot_inv, lower_block, upper_block, strip_fields, devices, substeps):
    strips = strip_node.shape[0]
    node_count = pivot_inv.shape[1] * pivot_inv.shape[2]
    _, per_device, cells_y, cells_x = strip_fields.shape
    vmem = pl.BlockSpec(memory_space=pltpu.VMEM)
    hbm = pl.BlockSpec(memory_space=pl.ANY)
    block_count, block_size = pivot_inv.shape[1], pivot_inv.shape[2]
    return pl.pallas_call(
        lambda *refs: start_kernel(*refs, substeps=substeps),
        in_specs=[pl.BlockSpec(memory_space=pltpu.SMEM)] * 2 + [vmem] * 2 + [hbm] * 3 + [vmem],
        scratch_shapes=[
            pltpu.VMEM((block_count, block_size, block_size), jnp.float32),
            pltpu.VMEM((block_count - 1, block_size, block_size), jnp.float32),
            pltpu.VMEM((block_count - 1, block_size, block_size), jnp.float32),
            pltpu.SemaphoreType.DMA((3 * block_count - 2,)),
        ],
        out_shape=[
            jax.ShapeDtypeStruct((node_count, strips), jnp.float32),
            jax.ShapeDtypeStruct((per_device, cells_y, cells_x), jnp.float32),
            jax.ShapeDtypeStruct((devices * per_device, 2 * substeps + strips), jnp.float32),
        ],
        name="start_step",
    )(
        riser_owner, strip_riser.reshape(strips), strip_node[None, :], spread_matrix(devices, per_device),
        pivot_inv, lower_block, upper_block, strip_fields,
    )


def second_kernel(received_ref, node_ref, spread_ref, gather_ref, difference_ref, fields_ref, vorticity_ref,
                  out_ref, sent_ref, *, substeps, node_count):
    position = lax.axis_index("strip")
    group_position = lax.axis_index("group")
    total_strips, _ = received_ref.shape
    strips = node_ref.shape[1]
    per_device = fields_ref.shape[1]
    every_force = received_ref[:, 0:2 * substeps]
    offset = jnp.sum(every_force, axis=0, keepdims=True) / jnp.sqrt(jnp.float32(total_strips))
    group_force = received_ref[pl.ds(group_position * strips, strips), 0:2 * substeps]
    my_coupling = jnp.dot(
        gather_ref[...], received_ref[:, 2 * substeps:], precision=EXACT_DOT, preferred_element_type=jnp.float32
    )
    motion = jnp.dot(my_coupling, group_force, precision=EXACT_DOT, preferred_element_type=jnp.float32)
    mine = (
        lax.broadcasted_iota(jnp.int32, (per_device, strips), 1)
        == position * per_device + lax.broadcasted_iota(jnp.int32, (per_device, strips), 0)
    )
    local_node = jnp.sum(jnp.where(mine, node_ref[...].astype(jnp.float32), 0.0), axis=1, keepdims=True)
    local_taper = 1.0 - local_node / node_count
    lane = lax.broadcasted_iota(jnp.int32, (per_device, 2 * substeps), 1)
    sublane = lax.broadcasted_iota(jnp.int32, (per_device, 2 * substeps), 0)
    motion = motion + jnp.where(lane >= substeps, local_taper * offset, 0.0)
    velocity = jnp.dot(motion, difference_ref[...], precision=EXACT_DOT, preferred_element_type=jnp.float32)

    source_x, source_y, lift_kernel, drag_kernel = kernel_planes(fields_ref.shape[-1])
    rows = jnp.zeros((per_device, 2 * substeps), jnp.float32)
    for strip in range(per_device):
        picks = [
            jnp.sum(jnp.sum(jnp.where((sublane == strip) & (lane == column), velocity, 0.0), axis=0, keepdims=True), axis=1, keepdims=True)
            for column in range(2 * substeps)
        ]

        def forcing_of(substep, picks=picks):
            return picks[substep] * source_x - picks[substeps + substep] * source_y

        vorticity, row = run_substeps(
            vorticity_ref[strip], fields_ref[1, strip], fields_ref[2, strip], forcing_of,
            lift_kernel, drag_kernel, substeps,
        )
        out_ref[strip] = vorticity
        rows = jnp.where(sublane == strip, row, rows)
    sent_ref[...] = jnp.dot(spread_ref[...], rows, precision=EXACT_DOT, preferred_element_type=jnp.float32)


def difference_matrix(substeps):
    columns = np.arange(2 * substeps)
    same = columns[:, None] == columns[None, :]
    before = (columns[:, None] + 1 == columns[None, :]) & (columns[None, :] % substeps != 0)
    return same.astype(np.float32) - before.astype(np.float32)


def second_step(received, strip_node, strip_fields, vorticity, devices, node_count, substeps):
    _, per_device, cells_y, cells_x = strip_fields.shape
    spread = spread_matrix(devices, per_device)
    vmem = pl.BlockSpec(memory_space=pltpu.VMEM)
    return pl.pallas_call(
        lambda *refs: second_kernel(*refs, substeps=substeps, node_count=node_count),
        in_specs=[vmem] * 7,
        out_shape=[
            jax.ShapeDtypeStruct((per_device, cells_y, cells_x), jnp.float32),
            jax.ShapeDtypeStruct((devices * per_device, 2 * substeps), jnp.float32),
        ],
        name="second_step",
    )(received, strip_node[None, :], spread, np.ascontiguousarray(spread.T), difference_matrix(substeps), strip_fields, vorticity)


def local(strip_fields, strip_riser, strip_node, riser_owner, pivot_inv, lower_block, upper_block):
    position = lax.axis_index("strip")
    group_position = lax.axis_index("group")
    group_count = lax.axis_size("group")
    devices = lax.axis_size("strip") * group_count
    per_device = strip_fields.shape[1]
    grid_cells = strip_fields.shape[2]
    node_count = pivot_inv.shape[1] * pivot_inv.shape[2]
    riser_count = riser_owner.shape[1]
    group_strips = strip_node.shape[0]
    substeps = NSUB
    total_strips = per_device * devices
    top_taper = 1.0 - jnp.arange(node_count, dtype=jnp.float32) / node_count

    unit_response, first_vorticity, first_sent = start_step(
        riser_owner, strip_riser, strip_node, pivot_inv, lower_block, upper_block, strip_fields, devices, substeps
    )

    received = lax.all_to_all(first_sent, ("group", "strip"), 0, 0, tiled=True)
    vorticity, sent = second_step(received, strip_node, strip_fields, first_vorticity, devices, node_count, substeps)
    received = lax.all_to_all(sent, ("group", "strip"), 0, 0, tiled=True)
    offset = jnp.sum(received[:, substeps:], axis=0) / jnp.sqrt(jnp.float32(total_strips))
    group_force = lax.dynamic_slice_in_dim(received, group_position * group_strips, group_strips)
    displacement = lax.dot_general(
        group_force, unit_response, (((0,), (1,)), ((), ())), precision=EXACT_DOT
    )
    displacement = displacement.at[substeps:, :].add(offset[:, None] * top_taper[None, :])
    return (vorticity, displacement[None])


def solution(mesh):
    in_specs = (
        P(None, ("group", "strip"), None, None),
        P("group", None),
        P("group"),
        P("group", None),
        P(("group", "strip"), None, None, None),
        P(("group", "strip"), None, None, None),
        P(("group", "strip"), None, None, None),
    )
    out_specs = (P(("group", "strip"), None, None), P(("group", "strip"), None, None))
    return jax.shard_map(local, mesh=mesh, in_specs=in_specs, out_specs=out_specs, check_vma=False)
```

```python
import numpy as np
import jax
import jax.numpy as jnp
from jax import lax
from jax.sharding import PartitionSpec as P
from jax.experimental import pallas as pl
from jax.experimental.pallas import tpu as pltpu

NSUB = 8
COUPLED = 2


TIME_STEP = 0.25
VISCOSITY = 0.05
COUPLING = 0.5
EXACT_DOT = lax.Precision.HIGHEST


def make_kernels(grid_cells):
    centre = jnp.arange(grid_cells, dtype=jnp.float32) - grid_cells / 2.0 + 0.5
    near_x = (centre / (grid_cells / 16.0))[None, :]
    near_y = (centre / (grid_cells / 16.0))[:, None]
    bell_near = jnp.exp(-(near_x * near_x + near_y * near_y) / 2.0)
    source_x = -near_x * bell_near
    source_y = -near_y * bell_near
    wide_x = (centre / (grid_cells / 8.0))[None, :]
    wide_y = (centre / (grid_cells / 8.0))[:, None]
    bell_wide = jnp.exp(-(wide_x * wide_x + wide_y * wide_y) / 2.0)
    lift_kernel = -wide_x * bell_wide
    drag_kernel = wide_y * bell_wide
    lift_kernel = lift_kernel / jnp.sqrt(jnp.sum(lift_kernel * lift_kernel))
    drag_kernel = drag_kernel / jnp.sqrt(jnp.sum(drag_kernel * drag_kernel))
    return (source_x, source_y, lift_kernel, drag_kernel)


def strip_step(vorticity, flow_x, flow_y, motion, kernels, substeps):
    source_x, source_y, lift_kernel, drag_kernel = kernels
    halves = motion.reshape(motion.shape[0], 2, substeps)
    earlier = jnp.concatenate([jnp.zeros_like(halves[:, :, :1]), halves[:, :, :-1]], axis=2)
    velocity = halves - earlier
    lift_rows = []
    drag_rows = []
    for substep in range(substeps):
        right_cell = jnp.roll(vorticity, -1, axis=2)
        left_cell = jnp.roll(vorticity, 1, axis=2)
        upper_cell = jnp.roll(vorticity, -1, axis=1)
        lower_cell = jnp.roll(vorticity, 1, axis=1)
        laplacian = right_cell + left_cell + upper_cell + lower_cell - 4.0 * vorticity
        tendency = (
            VISCOSITY * laplacian
            - flow_x * (0.5 * (right_cell - left_cell))
            - flow_y * (0.5 * (upper_cell - lower_cell))
        )
        forcing = (
            velocity[:, 0, substep][:, None, None] * source_x
            - velocity[:, 1, substep][:, None, None] * source_y
        )
        vorticity = vorticity + TIME_STEP * tendency + COUPLING * forcing
        lift_rows.append(jnp.sum(vorticity * lift_kernel, axis=(1, 2)))
        drag_rows.append(jnp.sum(vorticity * drag_kernel, axis=(1, 2)))
    return (vorticity, jnp.stack(lift_rows + drag_rows, axis=1))


def kernel_planes(cells):
    centre_x = lax.broadcasted_iota(jnp.int32, (cells, cells), 1).astype(jnp.float32) - cells / 2.0 + 0.5
    centre_y = lax.broadcasted_iota(jnp.int32, (cells, cells), 0).astype(jnp.float32) - cells / 2.0 + 0.5
    near_x = centre_x / (cells / 16.0)
    near_y = centre_y / (cells / 16.0)
    bell_near = jnp.exp(-(near_x * near_x + near_y * near_y) / 2.0)
    source_x = -near_x * bell_near
    source_y = -near_y * bell_near
    wide_x = centre_x / (cells / 8.0)
    wide_y = centre_y / (cells / 8.0)
    bell_wide = jnp.exp(-(wide_x * wide_x + wide_y * wide_y) / 2.0)
    lift_kernel = -wide_x * bell_wide
    drag_kernel = wide_y * bell_wide

    def total(plane):
        return jnp.sum(jnp.sum(plane, axis=0, keepdims=True), axis=1, keepdims=True)

    lift_kernel = lift_kernel / jnp.sqrt(total(lift_kernel * lift_kernel))
    drag_kernel = drag_kernel / jnp.sqrt(total(drag_kernel * drag_kernel))
    return (source_x, source_y, lift_kernel, drag_kernel)


def run_substeps(vorticity, flow_x, flow_y, forcing_of, lift_kernel, drag_kernel, substeps):
    rows_across, cols_across = vorticity.shape
    lane = lax.broadcasted_iota(jnp.int32, (1, 2 * substeps), 1)
    row = jnp.zeros((1, 2 * substeps), jnp.float32)
    for substep in range(substeps):
        right_cell = pltpu.roll(vorticity, cols_across - 1, 1)
        left_cell = pltpu.roll(vorticity, 1, 1)
        upper_cell = pltpu.roll(vorticity, rows_across - 1, 0)
        lower_cell = pltpu.roll(vorticity, 1, 0)
        laplacian = right_cell + left_cell + upper_cell + lower_cell - 4.0 * vorticity
        tendency = (
            VISCOSITY * laplacian
            - flow_x * (0.5 * (right_cell - left_cell))
            - flow_y * (0.5 * (upper_cell - lower_cell))
        )
        if forcing_of is None:
            vorticity = vorticity + TIME_STEP * tendency
        else:
            vorticity = vorticity + TIME_STEP * tendency + COUPLING * forcing_of(substep)
        lift = jnp.sum(jnp.sum(vorticity * lift_kernel, axis=0, keepdims=True), axis=1, keepdims=True)
        drag = jnp.sum(jnp.sum(vorticity * drag_kernel, axis=0, keepdims=True), axis=1, keepdims=True)
        row = row + jnp.where(lane == substep, lift, 0.0) + jnp.where(lane == substeps + substep, drag, 0.0)
    return vorticity, row


def stencil_kernel(velocity_ref, vorticity_ref, flow_x_ref, flow_y_ref, out_ref, rows_ref, *, substeps):
    strip = pl.program_id(0)
    source_x, source_y, lift_kernel, drag_kernel = kernel_planes(vorticity_ref.shape[-1])

    def forcing_of(substep):
        return (
            velocity_ref[strip, substep] * source_x
            - velocity_ref[strip, substeps + substep] * source_y
        )

    vorticity, row = run_substeps(
        vorticity_ref[0, 0], flow_x_ref[0, 0], flow_y_ref[0, 0], forcing_of,
        lift_kernel, drag_kernel, substeps,
    )
    out_ref[0] = vorticity
    rows_ref[0] = row


def strip_step_kernel(strip_fields, vorticity, motion, kernels, substeps):
    strips, cells_y, cells_x = strip_fields.shape[1:]
    halves = motion.reshape(strips, 2, substeps)
    earlier = jnp.concatenate([jnp.zeros_like(halves[:, :, :1]), halves[:, :, :-1]], axis=2)
    velocity = (halves - earlier).reshape(strips, 2 * substeps)
    def field(index):
        return pl.BlockSpec((1, 1, cells_y, cells_x), lambda s: (index, s, 0, 0))

    new_vorticity, rows = pl.pallas_call(
        lambda *refs: stencil_kernel(*refs, substeps=substeps),
        grid=(strips,),
        in_specs=[
            pl.BlockSpec(memory_space=pltpu.SMEM),
            field(0), field(1), field(2),
        ],
        out_specs=[
            pl.BlockSpec((1, cells_y, cells_x), lambda s: (s, 0, 0)),
            pl.BlockSpec((1, 1, 2 * substeps), lambda s: (s, 0, 0)),
        ],
        out_shape=[
            jax.ShapeDtypeStruct((strips, cells_y, cells_x), jnp.float32),
            jax.ShapeDtypeStruct((strips, 1, 2 * substeps), jnp.float32),
        ],
        name="strip_stencil",
    )(velocity, vorticity, strip_fields, strip_fields)
    return new_vorticity, rows[:, 0, :]


def apply_block(vectors, matrix):
    return lax.dot_general(vectors, matrix, (((1,), (1,)), ((), ())), precision=EXACT_DOT)


def first_contract(left_side, right_side):
    return lax.dot_general(left_side, right_side, (((0,), (0,)), ((), ())), precision=EXACT_DOT)


def beam_solve(beam_load, pivot_inv, lower_block, upper_block):
    block_count = pivot_inv.shape[0]
    block_size = pivot_inv.shape[1]
    blocks = beam_load.reshape(beam_load.shape[0], block_count, block_size)
    carried = [blocks[:, 0]]
    for block_index in range(1, block_count):
        pivoted = apply_block(carried[-1], pivot_inv[block_index - 1])
        carried.append(blocks[:, block_index] - apply_block(pivoted, lower_block[block_index - 1]))
    solved = [apply_block(carried[-1], pivot_inv[block_count - 1])]
    for block_index in range(block_count - 2, -1, -1):
        remainder = carried[block_index] - apply_block(solved[0], upper_block[block_index])
        solved.insert(0, apply_block(remainder, pivot_inv[block_index]))
    return jnp.concatenate(solved, axis=1)


def start_kernel(owner_ref, riser_ref, node_ref, spread_ref, pivot_ref, lower_ref, upper_ref, fields_ref,
                 response_ref, vorticity_ref, sent_ref, *, substeps):
    block_count = pivot_ref.shape[1]
    block_size = pivot_ref.shape[2]
    node_count = block_count * block_size
    strips = node_ref.shape[1]
    per_device = fields_ref.shape[1]
    position = lax.axis_index("strip")
    group_position = lax.axis_index("group")

    strip_lane = lax.broadcasted_iota(jnp.int32, (1, strips), 1)
    strip_sublane = lax.broadcasted_iota(jnp.int32, (strips, 1), 0)
    owned_row = jnp.zeros((1, strips), jnp.float32)
    owned_col = jnp.zeros((strips, 1), jnp.float32)
    for strip in range(strips):
        held = jnp.where(owner_ref[0, riser_ref[strip]] == position, 1.0, 0.0)
        owned_row = jnp.where(strip_lane == strip, held, owned_row)
        owned_col = jnp.where(strip_sublane == strip, held, owned_col)
    diagonal = lax.broadcasted_iota(jnp.int32, (strips, strips), 0) == lax.broadcasted_iota(jnp.int32, (strips, strips), 1)
    node_row = node_ref[...]
    node_col = jnp.sum(jnp.where(diagonal, node_row.astype(jnp.float32), 0.0), axis=1, keepdims=True)

    def apply(matrix, vectors):
        return jnp.dot(matrix, vectors, precision=lax.Precision.HIGH, preferred_element_type=jnp.float32)

    def unit_load(block_index):
        node = block_index * block_size + lax.broadcasted_iota(jnp.int32, (block_size, strips), 0)
        return (node == node_row).astype(jnp.float32) * owned_row

    def product(left, right):
        return jnp.dot(left, right, precision=EXACT_DOT, preferred_element_type=jnp.float32)

    forward = [None] + [product(lower_ref[0, i - 1], pivot_ref[0, i - 1]) for i in range(1, block_count)]
    backward = [product(pivot_ref[0, i], upper_ref[0, i]) for i in range(block_count - 1)]
    carried = [unit_load(0)]
    for block_index in range(1, block_count):
        carried.append(unit_load(block_index) - apply(forward[block_index], carried[-1]))
    pivoted = [apply(pivot_ref[0, i], carried[i]) for i in range(block_count)]
    solved = pivoted[block_count - 1]
    response_ref[(block_count - 1) * block_size:, :] = solved
    for block_index in range(block_count - 2, -1, -1):
        solved = pivoted[block_index] - apply(backward[block_index], solved)
        response_ref[block_index * block_size:(block_index + 1) * block_size, :] = solved

    _, _, lift_kernel, drag_kernel = kernel_planes(fields_ref.shape[-1])
    strip_of_row = lax.broadcasted_iota(jnp.int32, (per_device, 2 * substeps), 0)
    rows = jnp.zeros((per_device, 2 * substeps), jnp.float32)
    for strip in range(per_device):
        vorticity, row = run_substeps(
            fields_ref[0, strip], fields_ref[1, strip], fields_ref[2, strip], None,
            lift_kernel, drag_kernel, substeps,
        )
        vorticity_ref[strip] = vorticity
        rows = jnp.where(strip_of_row == strip, row, rows)

    node_onehot = (
        node_col == lax.broadcasted_iota(jnp.int32, (strips, node_count), 1).astype(jnp.float32)
    ).astype(jnp.float32)
    coupling = jnp.dot(node_onehot, response_ref[...], precision=EXACT_DOT, preferred_element_type=jnp.float32)
    coupling = coupling * owned_col
    sent_rows = sent_ref.shape[0]
    place = lax.broadcasted_iota(jnp.int32, (sent_rows, strips), 0) - group_position * strips
    pick = (place == lax.broadcasted_iota(jnp.int32, (sent_rows, strips), 1)).astype(jnp.float32)
    sent_ref[:, 0:2 * substeps] = jnp.dot(spread_ref[...], rows, precision=EXACT_DOT, preferred_element_type=jnp.float32)
    sent_ref[:, 2 * substeps:] = jnp.dot(pick, coupling, precision=EXACT_DOT, preferred_element_type=jnp.float32)


def spread_matrix(devices, per_device):
    return (
        np.arange(devices * per_device)[:, None] % per_device == np.arange(per_device)[None, :]
    ).astype(np.float32)


def start_step(riser_owner, strip_riser, strip_node, pivot_inv, lower_block, upper_block, strip_fields, devices, substeps):
    strips = strip_node.shape[0]
    node_count = pivot_inv.shape[1] * pivot_inv.shape[2]
    _, per_device, cells_y, cells_x = strip_fields.shape
    vmem = pl.BlockSpec(memory_space=pltpu.VMEM)
    return pl.pallas_call(
        lambda *refs: start_kernel(*refs, substeps=substeps),
        in_specs=[pl.BlockSpec(memory_space=pltpu.SMEM)] * 2 + [vmem] * 6,
        out_shape=[
            jax.ShapeDtypeStruct((node_count, strips), jnp.float32),
            jax.ShapeDtypeStruct((per_device, cells_y, cells_x), jnp.float32),
            jax.ShapeDtypeStruct((devices * per_device, 2 * substeps + strips), jnp.float32),
        ],
        name="start_step",
    )(
        riser_owner, strip_riser.reshape(strips), strip_node[None, :], spread_matrix(devices, per_device),
        pivot_inv, lower_block, upper_block, strip_fields,
    )


def second_kernel(received_ref, node_ref, spread_ref, gather_ref, difference_ref, fields_ref, vorticity_ref,
                  out_ref, sent_ref, *, substeps, node_count):
    position = lax.axis_index("strip")
    group_position = lax.axis_index("group")
    total_strips, _ = received_ref.shape
    strips = node_ref.shape[1]
    per_device = fields_ref.shape[1]
    every_force = received_ref[:, 0:2 * substeps]
    offset = jnp.sum(every_force, axis=0, keepdims=True) / jnp.sqrt(jnp.float32(total_strips))
    group_force = received_ref[pl.ds(group_position * strips, strips), 0:2 * substeps]
    my_coupling = jnp.dot(
        gather_ref[...], received_ref[:, 2 * substeps:], precision=EXACT_DOT, preferred_element_type=jnp.float32
    )
    motion = jnp.dot(my_coupling, group_force, precision=EXACT_DOT, preferred_element_type=jnp.float32)
    mine = (
        lax.broadcasted_iota(jnp.int32, (per_device, strips), 1)
        == position * per_device + lax.broadcasted_iota(jnp.int32, (per_device, strips), 0)
    )
    local_node = jnp.sum(jnp.where(mine, node_ref[...].astype(jnp.float32), 0.0), axis=1, keepdims=True)
    local_taper = 1.0 - local_node / node_count
    lane = lax.broadcasted_iota(jnp.int32, (per_device, 2 * substeps), 1)
    sublane = lax.broadcasted_iota(jnp.int32, (per_device, 2 * substeps), 0)
    motion = motion + jnp.where(lane >= substeps, local_taper * offset, 0.0)
    velocity = jnp.dot(motion, difference_ref[...], precision=EXACT_DOT, preferred_element_type=jnp.float32)

    source_x, source_y, lift_kernel, drag_kernel = kernel_planes(fields_ref.shape[-1])
    rows = jnp.zeros((per_device, 2 * substeps), jnp.float32)
    for strip in range(per_device):
        picks = [
            jnp.sum(jnp.sum(jnp.where((sublane == strip) & (lane == column), velocity, 0.0), axis=0, keepdims=True), axis=1, keepdims=True)
            for column in range(2 * substeps)
        ]

        def forcing_of(substep, picks=picks):
            return picks[substep] * source_x - picks[substeps + substep] * source_y

        vorticity, row = run_substeps(
            vorticity_ref[strip], fields_ref[1, strip], fields_ref[2, strip], forcing_of,
            lift_kernel, drag_kernel, substeps,
        )
        out_ref[strip] = vorticity
        rows = jnp.where(sublane == strip, row, rows)
    sent_ref[...] = jnp.dot(spread_ref[...], rows, precision=EXACT_DOT, preferred_element_type=jnp.float32)


def difference_matrix(substeps):
    columns = np.arange(2 * substeps)
    same = columns[:, None] == columns[None, :]
    before = (columns[:, None] + 1 == columns[None, :]) & (columns[None, :] % substeps != 0)
    return same.astype(np.float32) - before.astype(np.float32)


def second_step(received, strip_node, strip_fields, vorticity, devices, node_count, substeps):
    _, per_device, cells_y, cells_x = strip_fields.shape
    spread = spread_matrix(devices, per_device)
    vmem = pl.BlockSpec(memory_space=pltpu.VMEM)
    return pl.pallas_call(
        lambda *refs: second_kernel(*refs, substeps=substeps, node_count=node_count),
        in_specs=[vmem] * 7,
        out_shape=[
            jax.ShapeDtypeStruct((per_device, cells_y, cells_x), jnp.float32),
            jax.ShapeDtypeStruct((devices * per_device, 2 * substeps), jnp.float32),
        ],
        name="second_step",
    )(received, strip_node[None, :], spread, np.ascontiguousarray(spread.T), difference_matrix(substeps), strip_fields, vorticity)


def local(strip_fields, strip_riser, strip_node, riser_owner, pivot_inv, lower_block, upper_block):
    position = lax.axis_index("strip")
    group_position = lax.axis_index("group")
    group_count = lax.axis_size("group")
    devices = lax.axis_size("strip") * group_count
    per_device = strip_fields.shape[1]
    grid_cells = strip_fields.shape[2]
    node_count = pivot_inv.shape[1] * pivot_inv.shape[2]
    riser_count = riser_owner.shape[1]
    group_strips = strip_node.shape[0]
    substeps = NSUB
    total_strips = per_device * devices
    top_taper = 1.0 - jnp.arange(node_count, dtype=jnp.float32) / node_count

    unit_response, first_vorticity, first_sent = start_step(
        riser_owner, strip_riser, strip_node, pivot_inv, lower_block, upper_block, strip_fields, devices, substeps
    )

    received = lax.all_to_all(first_sent, ("group", "strip"), 0, 0, tiled=True)
    vorticity, sent = second_step(received, strip_node, strip_fields, first_vorticity, devices, node_count, substeps)
    received = lax.all_to_all(sent, ("group", "strip"), 0, 0, tiled=True)
    offset = jnp.sum(received[:, substeps:], axis=0) / jnp.sqrt(jnp.float32(total_strips))
    group_force = lax.dynamic_slice_in_dim(received, group_position * group_strips, group_strips)
    displacement = lax.dot_general(
        group_force, unit_response, (((0,), (1,)), ((), ())), precision=EXACT_DOT
    )
    displacement = displacement.at[substeps:, :].add(offset[:, None] * top_taper[None, :])
    return (vorticity, displacement[None])


def solution(mesh):
    in_specs = (
        P(None, ("group", "strip"), None, None),
        P("group", None),
        P("group"),
        P("group", None),
        P(("group", "strip"), None, None, None),
        P(("group", "strip"), None, None, None),
        P(("group", "strip"), None, None, None),
    )
    out_specs = (P(("group", "strip"), None, None), P(("group", "strip"), None, None))
    return jax.shard_map(local, mesh=mesh, in_specs=in_specs, out_specs=out_specs, check_vma=False)
```

```python
import numpy as np
import jax
import jax.numpy as jnp
from jax import lax
from jax.sharding import PartitionSpec as P
from jax.experimental import pallas as pl
from jax.experimental.pallas import tpu as pltpu

NSUB = 8
COUPLED = 2


TIME_STEP = 0.25
VISCOSITY = 0.05
COUPLING = 0.5
EXACT_DOT = lax.Precision.HIGHEST


def make_kernels(grid_cells):
    centre = jnp.arange(grid_cells, dtype=jnp.float32) - grid_cells / 2.0 + 0.5
    near_x = (centre / (grid_cells / 16.0))[None, :]
    near_y = (centre / (grid_cells / 16.0))[:, None]
    bell_near = jnp.exp(-(near_x * near_x + near_y * near_y) / 2.0)
    source_x = -near_x * bell_near
    source_y = -near_y * bell_near
    wide_x = (centre / (grid_cells / 8.0))[None, :]
    wide_y = (centre / (grid_cells / 8.0))[:, None]
    bell_wide = jnp.exp(-(wide_x * wide_x + wide_y * wide_y) / 2.0)
    lift_kernel = -wide_x * bell_wide
    drag_kernel = wide_y * bell_wide
    lift_kernel = lift_kernel / jnp.sqrt(jnp.sum(lift_kernel * lift_kernel))
    drag_kernel = drag_kernel / jnp.sqrt(jnp.sum(drag_kernel * drag_kernel))
    return (source_x, source_y, lift_kernel, drag_kernel)


def strip_step(vorticity, flow_x, flow_y, motion, kernels, substeps):
    source_x, source_y, lift_kernel, drag_kernel = kernels
    halves = motion.reshape(motion.shape[0], 2, substeps)
    earlier = jnp.concatenate([jnp.zeros_like(halves[:, :, :1]), halves[:, :, :-1]], axis=2)
    velocity = halves - earlier
    lift_rows = []
    drag_rows = []
    for substep in range(substeps):
        right_cell = jnp.roll(vorticity, -1, axis=2)
        left_cell = jnp.roll(vorticity, 1, axis=2)
        upper_cell = jnp.roll(vorticity, -1, axis=1)
        lower_cell = jnp.roll(vorticity, 1, axis=1)
        laplacian = right_cell + left_cell + upper_cell + lower_cell - 4.0 * vorticity
        tendency = (
            VISCOSITY * laplacian
            - flow_x * (0.5 * (right_cell - left_cell))
            - flow_y * (0.5 * (upper_cell - lower_cell))
        )
        forcing = (
            velocity[:, 0, substep][:, None, None] * source_x
            - velocity[:, 1, substep][:, None, None] * source_y
        )
        vorticity = vorticity + TIME_STEP * tendency + COUPLING * forcing
        lift_rows.append(jnp.sum(vorticity * lift_kernel, axis=(1, 2)))
        drag_rows.append(jnp.sum(vorticity * drag_kernel, axis=(1, 2)))
    return (vorticity, jnp.stack(lift_rows + drag_rows, axis=1))


def kernel_planes(cells):
    centre_x = lax.broadcasted_iota(jnp.int32, (cells, cells), 1).astype(jnp.float32) - cells / 2.0 + 0.5
    centre_y = lax.broadcasted_iota(jnp.int32, (cells, cells), 0).astype(jnp.float32) - cells / 2.0 + 0.5
    near_x = centre_x / (cells / 16.0)
    near_y = centre_y / (cells / 16.0)
    bell_near = jnp.exp(-(near_x * near_x + near_y * near_y) / 2.0)
    source_x = -near_x * bell_near
    source_y = -near_y * bell_near
    wide_x = centre_x / (cells / 8.0)
    wide_y = centre_y / (cells / 8.0)
    bell_wide = jnp.exp(-(wide_x * wide_x + wide_y * wide_y) / 2.0)
    lift_kernel = -wide_x * bell_wide
    drag_kernel = wide_y * bell_wide

    def total(plane):
        return jnp.sum(jnp.sum(plane, axis=0, keepdims=True), axis=1, keepdims=True)

    lift_kernel = lift_kernel / jnp.sqrt(total(lift_kernel * lift_kernel))
    drag_kernel = drag_kernel / jnp.sqrt(total(drag_kernel * drag_kernel))
    return (source_x, source_y, lift_kernel, drag_kernel)


def run_substeps(vorticity, flow_x, flow_y, forcing_of, lift_kernel, drag_kernel, substeps):
    rows_across, cols_across = vorticity.shape
    lane = lax.broadcasted_iota(jnp.int32, (1, 2 * substeps), 1)
    row = jnp.zeros((1, 2 * substeps), jnp.float32)
    for substep in range(substeps):
        right_cell = pltpu.roll(vorticity, cols_across - 1, 1)
        left_cell = pltpu.roll(vorticity, 1, 1)
        upper_cell = pltpu.roll(vorticity, rows_across - 1, 0)
        lower_cell = pltpu.roll(vorticity, 1, 0)
        laplacian = right_cell + left_cell + upper_cell + lower_cell - 4.0 * vorticity
        tendency = (
            VISCOSITY * laplacian
            - flow_x * (0.5 * (right_cell - left_cell))
            - flow_y * (0.5 * (upper_cell - lower_cell))
        )
        if forcing_of is None:
            vorticity = vorticity + TIME_STEP * tendency
        else:
            vorticity = vorticity + TIME_STEP * tendency + COUPLING * forcing_of(substep)
        lift = jnp.sum(jnp.sum(vorticity * lift_kernel, axis=0, keepdims=True), axis=1, keepdims=True)
        drag = jnp.sum(jnp.sum(vorticity * drag_kernel, axis=0, keepdims=True), axis=1, keepdims=True)
        row = row + jnp.where(lane == substep, lift, 0.0) + jnp.where(lane == substeps + substep, drag, 0.0)
    return vorticity, row


def stencil_kernel(velocity_ref, vorticity_ref, flow_x_ref, flow_y_ref, out_ref, rows_ref, *, substeps):
    strip = pl.program_id(0)
    source_x, source_y, lift_kernel, drag_kernel = kernel_planes(vorticity_ref.shape[-1])

    def forcing_of(substep):
        return (
            velocity_ref[strip, substep] * source_x
            - velocity_ref[strip, substeps + substep] * source_y
        )

    vorticity, row = run_substeps(
        vorticity_ref[0, 0], flow_x_ref[0, 0], flow_y_ref[0, 0], forcing_of,
        lift_kernel, drag_kernel, substeps,
    )
    out_ref[0] = vorticity
    rows_ref[0] = row


def strip_step_kernel(strip_fields, vorticity, motion, kernels, substeps):
    strips, cells_y, cells_x = strip_fields.shape[1:]
    halves = motion.reshape(strips, 2, substeps)
    earlier = jnp.concatenate([jnp.zeros_like(halves[:, :, :1]), halves[:, :, :-1]], axis=2)
    velocity = (halves - earlier).reshape(strips, 2 * substeps)
    def field(index):
        return pl.BlockSpec((1, 1, cells_y, cells_x), lambda s: (index, s, 0, 0))

    new_vorticity, rows = pl.pallas_call(
        lambda *refs: stencil_kernel(*refs, substeps=substeps),
        grid=(strips,),
        in_specs=[
            pl.BlockSpec(memory_space=pltpu.SMEM),
            field(0), field(1), field(2),
        ],
        out_specs=[
            pl.BlockSpec((1, cells_y, cells_x), lambda s: (s, 0, 0)),
            pl.BlockSpec((1, 1, 2 * substeps), lambda s: (s, 0, 0)),
        ],
        out_shape=[
            jax.ShapeDtypeStruct((strips, cells_y, cells_x), jnp.float32),
            jax.ShapeDtypeStruct((strips, 1, 2 * substeps), jnp.float32),
        ],
        name="strip_stencil",
    )(velocity, vorticity, strip_fields, strip_fields)
    return new_vorticity, rows[:, 0, :]


def apply_block(vectors, matrix):
    return lax.dot_general(vectors, matrix, (((1,), (1,)), ((), ())), precision=EXACT_DOT)


def first_contract(left_side, right_side):
    return lax.dot_general(left_side, right_side, (((0,), (0,)), ((), ())), precision=EXACT_DOT)


def beam_solve(beam_load, pivot_inv, lower_block, upper_block):
    block_count = pivot_inv.shape[0]
    block_size = pivot_inv.shape[1]
    blocks = beam_load.reshape(beam_load.shape[0], block_count, block_size)
    carried = [blocks[:, 0]]
    for block_index in range(1, block_count):
        pivoted = apply_block(carried[-1], pivot_inv[block_index - 1])
        carried.append(blocks[:, block_index] - apply_block(pivoted, lower_block[block_index - 1]))
    solved = [apply_block(carried[-1], pivot_inv[block_count - 1])]
    for block_index in range(block_count - 2, -1, -1):
        remainder = carried[block_index] - apply_block(solved[0], upper_block[block_index])
        solved.insert(0, apply_block(remainder, pivot_inv[block_index]))
    return jnp.concatenate(solved, axis=1)


def start_kernel(owner_ref, riser_ref, node_ref, spread_ref, pivot_ref, lower_ref, upper_ref, fields_ref,
                 response_ref, vorticity_ref, sent_ref, *, substeps):
    block_count = pivot_ref.shape[1]
    block_size = pivot_ref.shape[2]
    node_count = block_count * block_size
    strips = node_ref.shape[1]
    per_device = fields_ref.shape[1]
    position = lax.axis_index("strip")
    group_position = lax.axis_index("group")

    strip_lane = lax.broadcasted_iota(jnp.int32, (1, strips), 1)
    strip_sublane = lax.broadcasted_iota(jnp.int32, (strips, 1), 0)
    owned_row = jnp.zeros((1, strips), jnp.float32)
    owned_col = jnp.zeros((strips, 1), jnp.float32)
    for strip in range(strips):
        held = jnp.where(owner_ref[0, riser_ref[strip]] == position, 1.0, 0.0)
        owned_row = jnp.where(strip_lane == strip, held, owned_row)
        owned_col = jnp.where(strip_sublane == strip, held, owned_col)
    diagonal = lax.broadcasted_iota(jnp.int32, (strips, strips), 0) == lax.broadcasted_iota(jnp.int32, (strips, strips), 1)
    node_row = node_ref[...]
    node_col = jnp.sum(jnp.where(diagonal, node_row.astype(jnp.float32), 0.0), axis=1, keepdims=True)

    def apply(matrix, vectors):
        return jnp.dot(matrix, vectors, precision=lax.Precision.HIGH, preferred_element_type=jnp.float32)

    def unit_load(block_index):
        node = block_index * block_size + lax.broadcasted_iota(jnp.int32, (block_size, strips), 0)
        return (node == node_row).astype(jnp.float32) * owned_row

    def product(left, right):
        return jnp.dot(left, right, precision=EXACT_DOT, preferred_element_type=jnp.float32)

    forward = [None] + [product(lower_ref[0, i - 1], pivot_ref[0, i - 1]) for i in range(1, block_count)]
    backward = [product(pivot_ref[0, i], upper_ref[0, i]) for i in range(block_count - 1)]
    carried = [unit_load(0)]
    for block_index in range(1, block_count):
        carried.append(unit_load(block_index) - apply(forward[block_index], carried[-1]))
    pivoted = [apply(pivot_ref[0, i], carried[i]) for i in range(block_count)]
    solved = pivoted[block_count - 1]
    response_ref[(block_count - 1) * block_size:, :] = solved
    for block_index in range(block_count - 2, -1, -1):
        solved = pivoted[block_index] - apply(backward[block_index], solved)
        response_ref[block_index * block_size:(block_index + 1) * block_size, :] = solved

    _, _, lift_kernel, drag_kernel = kernel_planes(fields_ref.shape[-1])
    strip_of_row = lax.broadcasted_iota(jnp.int32, (per_device, 2 * substeps), 0)
    rows = jnp.zeros((per_device, 2 * substeps), jnp.float32)
    for strip in range(per_device):
        vorticity, row = run_substeps(
            fields_ref[0, strip], fields_ref[1, strip], fields_ref[2, strip], None,
            lift_kernel, drag_kernel, substeps,
        )
        vorticity_ref[strip] = vorticity
        rows = jnp.where(strip_of_row == strip, row, rows)

    node_onehot = (
        node_col == lax.broadcasted_iota(jnp.int32, (strips, node_count), 1).astype(jnp.float32)
    ).astype(jnp.float32)
    coupling = jnp.dot(node_onehot, response_ref[...], precision=EXACT_DOT, preferred_element_type=jnp.float32)
    coupling = coupling * owned_col
    sent_rows = sent_ref.shape[0]
    place = lax.broadcasted_iota(jnp.int32, (sent_rows, strips), 0) - group_position * strips
    pick = (place == lax.broadcasted_iota(jnp.int32, (sent_rows, strips), 1)).astype(jnp.float32)
    sent_ref[:, 0:2 * substeps] = jnp.dot(spread_ref[...], rows, precision=EXACT_DOT, preferred_element_type=jnp.float32)
    sent_ref[:, 2 * substeps:] = jnp.dot(pick, coupling, precision=EXACT_DOT, preferred_element_type=jnp.float32)


def spread_matrix(devices, per_device):
    return (
        np.arange(devices * per_device)[:, None] % per_device == np.arange(per_device)[None, :]
    ).astype(np.float32)


def start_step(riser_owner, strip_riser, strip_node, pivot_inv, lower_block, upper_block, strip_fields, devices, substeps):
    strips = strip_node.shape[0]
    node_count = pivot_inv.shape[1] * pivot_inv.shape[2]
    _, per_device, cells_y, cells_x = strip_fields.shape
    vmem = pl.BlockSpec(memory_space=pltpu.VMEM)
    return pl.pallas_call(
        lambda *refs: start_kernel(*refs, substeps=substeps),
        in_specs=[pl.BlockSpec(memory_space=pltpu.SMEM)] * 2 + [vmem] * 6,
        out_shape=[
            jax.ShapeDtypeStruct((node_count, strips), jnp.float32),
            jax.ShapeDtypeStruct((per_device, cells_y, cells_x), jnp.float32),
            jax.ShapeDtypeStruct((devices * per_device, 2 * substeps + strips), jnp.float32),
        ],
        name="start_step",
    )(
        riser_owner, strip_riser.reshape(strips), strip_node[None, :], spread_matrix(devices, per_device),
        pivot_inv, lower_block, upper_block, strip_fields,
    )


def second_kernel(received_ref, node_ref, spread_ref, gather_ref, difference_ref, fields_ref, vorticity_ref,
                  out_ref, sent_ref, *, substeps, node_count):
    position = lax.axis_index("strip")
    group_position = lax.axis_index("group")
    total_strips, _ = received_ref.shape
    strips = node_ref.shape[1]
    per_device = fields_ref.shape[1]
    every_force = received_ref[:, 0:2 * substeps]
    offset = jnp.sum(every_force, axis=0, keepdims=True) / jnp.sqrt(jnp.float32(total_strips))
    group_force = received_ref[pl.ds(group_position * strips, strips), 0:2 * substeps]
    my_coupling = jnp.dot(
        gather_ref[...], received_ref[:, 2 * substeps:], precision=EXACT_DOT, preferred_element_type=jnp.float32
    )
    motion = jnp.dot(my_coupling, group_force, precision=EXACT_DOT, preferred_element_type=jnp.float32)
    mine = (
        lax.broadcasted_iota(jnp.int32, (per_device, strips), 1)
        == position * per_device + lax.broadcasted_iota(jnp.int32, (per_device, strips), 0)
    )
    local_node = jnp.sum(jnp.where(mine, node_ref[...].astype(jnp.float32), 0.0), axis=1, keepdims=True)
    local_taper = 1.0 - local_node / node_count
    lane = lax.broadcasted_iota(jnp.int32, (per_device, 2 * substeps), 1)
    sublane = lax.broadcasted_iota(jnp.int32, (per_device, 2 * substeps), 0)
    motion = motion + jnp.where(lane >= substeps, local_taper * offset, 0.0)
    velocity = jnp.dot(motion, difference_ref[...], precision=EXACT_DOT, preferred_element_type=jnp.float32)

    source_x, source_y, lift_kernel, drag_kernel = kernel_planes(fields_ref.shape[-1])
    rows = jnp.zeros((per_device, 2 * substeps), jnp.float32)
    for strip in range(per_device):
        picks = [
            jnp.sum(jnp.sum(jnp.where((sublane == strip) & (lane == column), velocity, 0.0), axis=0, keepdims=True), axis=1, keepdims=True)
            for column in range(2 * substeps)
        ]

        def forcing_of(substep, picks=picks):
            return picks[substep] * source_x - picks[substeps + substep] * source_y

        vorticity, row = run_substeps(
            vorticity_ref[strip], fields_ref[1, strip], fields_ref[2, strip], forcing_of,
            lift_kernel, drag_kernel, substeps,
        )
        out_ref[strip] = vorticity
        rows = jnp.where(sublane == strip, row, rows)
    sent_ref[...] = jnp.dot(spread_ref[...], rows, precision=EXACT_DOT, preferred_element_type=jnp.float32)


def difference_matrix(substeps):
    columns = np.arange(2 * substeps)
    same = columns[:, None] == columns[None, :]
    before = (columns[:, None] + 1 == columns[None, :]) & (columns[None, :] % substeps != 0)
    return same.astype(np.float32) - before.astype(np.float32)


def second_step(received, strip_node, strip_fields, vorticity, devices, node_count, substeps):
    _, per_device, cells_y, cells_x = strip_fields.shape
    spread = spread_matrix(devices, per_device)
    vmem = pl.BlockSpec(memory_space=pltpu.VMEM)
    return pl.pallas_call(
        lambda *refs: second_kernel(*refs, substeps=substeps, node_count=node_count),
        in_specs=[vmem] * 7,
        out_shape=[
            jax.ShapeDtypeStruct((per_device, cells_y, cells_x), jnp.float32),
            jax.ShapeDtypeStruct((devices * per_device, 2 * substeps), jnp.float32),
        ],
        name="second_step",
    )(received, strip_node[None, :], spread, np.ascontiguousarray(spread.T), difference_matrix(substeps), strip_fields, vorticity)


def finish_kernel(received_ref, response_ref, out_ref, *, substeps):
    group_position = lax.axis_index("group")
    total_strips = received_ref.shape[0]
    node_count, strips = response_ref.shape
    rows = 2 * substeps
    offset = jnp.sum(received_ref[...], axis=0, keepdims=True) / jnp.sqrt(jnp.float32(total_strips))
    group_force = received_ref[pl.ds(group_position * strips, strips), :]
    displacement = lax.dot_general(
        group_force, response_ref[...], (((0,), (1,)), ((), ())),
        precision=EXACT_DOT, preferred_element_type=jnp.float32,
    )
    diagonal = lax.broadcasted_iota(jnp.int32, (rows, rows), 0) == lax.broadcasted_iota(jnp.int32, (rows, rows), 1)
    offset_col = jnp.sum(jnp.where(diagonal, offset, 0.0), axis=1, keepdims=True)
    taper = 1.0 - lax.broadcasted_iota(jnp.int32, (1, node_count), 1).astype(jnp.float32) / node_count
    row = lax.broadcasted_iota(jnp.int32, (rows, node_count), 0)
    out_ref[0] = displacement + jnp.where(row >= substeps, offset_col * taper, 0.0)


def finish_step(received, unit_response, substeps):
    node_count = unit_response.shape[0]
    return pl.pallas_call(
        lambda *refs: finish_kernel(*refs, substeps=substeps),
        out_shape=jax.ShapeDtypeStruct((1, 2 * substeps, node_count), jnp.float32),
        name="finish_step",
    )(received, unit_response)


def local(strip_fields, strip_riser, strip_node, riser_owner, pivot_inv, lower_block, upper_block):
    position = lax.axis_index("strip")
    group_position = lax.axis_index("group")
    group_count = lax.axis_size("group")
    devices = lax.axis_size("strip") * group_count
    per_device = strip_fields.shape[1]
    grid_cells = strip_fields.shape[2]
    node_count = pivot_inv.shape[1] * pivot_inv.shape[2]
    riser_count = riser_owner.shape[1]
    group_strips = strip_node.shape[0]
    substeps = NSUB
    total_strips = per_device * devices
    top_taper = 1.0 - jnp.arange(node_count, dtype=jnp.float32) / node_count

    unit_response, first_vorticity, first_sent = start_step(
        riser_owner, strip_riser, strip_node, pivot_inv, lower_block, upper_block, strip_fields, devices, substeps
    )

    received = lax.all_to_all(first_sent, ("group", "strip"), 0, 0, tiled=True)
    vorticity, sent = second_step(received, strip_node, strip_fields, first_vorticity, devices, node_count, substeps)
    received = lax.all_to_all(sent, ("group", "strip"), 0, 0, tiled=True)
    displacement = finish_step(received, unit_response, substeps)
    return (vorticity, displacement)


def solution(mesh):
    in_specs = (
        P(None, ("group", "strip"), None, None),
        P("group", None),
        P("group"),
        P("group", None),
        P(("group", "strip"), None, None, None),
        P(("group", "strip"), None, None, None),
        P(("group", "strip"), None, None, None),
    )
    out_specs = (P(("group", "strip"), None, None), P(("group", "strip"), None, None))
    return jax.shard_map(local, mesh=mesh, in_specs=in_specs, out_specs=out_specs, check_vma=False)
```

```python
import numpy as np
import jax
import jax.numpy as jnp
from jax import lax
from jax.sharding import PartitionSpec as P
from jax.experimental import pallas as pl
from jax.experimental.pallas import tpu as pltpu

NSUB = 8
COUPLED = 2


TIME_STEP = 0.25
VISCOSITY = 0.05
COUPLING = 0.5
EXACT_DOT = lax.Precision.HIGHEST


def make_kernels(grid_cells):
    centre = jnp.arange(grid_cells, dtype=jnp.float32) - grid_cells / 2.0 + 0.5
    near_x = (centre / (grid_cells / 16.0))[None, :]
    near_y = (centre / (grid_cells / 16.0))[:, None]
    bell_near = jnp.exp(-(near_x * near_x + near_y * near_y) / 2.0)
    source_x = -near_x * bell_near
    source_y = -near_y * bell_near
    wide_x = (centre / (grid_cells / 8.0))[None, :]
    wide_y = (centre / (grid_cells / 8.0))[:, None]
    bell_wide = jnp.exp(-(wide_x * wide_x + wide_y * wide_y) / 2.0)
    lift_kernel = -wide_x * bell_wide
    drag_kernel = wide_y * bell_wide
    lift_kernel = lift_kernel / jnp.sqrt(jnp.sum(lift_kernel * lift_kernel))
    drag_kernel = drag_kernel / jnp.sqrt(jnp.sum(drag_kernel * drag_kernel))
    return (source_x, source_y, lift_kernel, drag_kernel)


def strip_step(vorticity, flow_x, flow_y, motion, kernels, substeps):
    source_x, source_y, lift_kernel, drag_kernel = kernels
    halves = motion.reshape(motion.shape[0], 2, substeps)
    earlier = jnp.concatenate([jnp.zeros_like(halves[:, :, :1]), halves[:, :, :-1]], axis=2)
    velocity = halves - earlier
    lift_rows = []
    drag_rows = []
    for substep in range(substeps):
        right_cell = jnp.roll(vorticity, -1, axis=2)
        left_cell = jnp.roll(vorticity, 1, axis=2)
        upper_cell = jnp.roll(vorticity, -1, axis=1)
        lower_cell = jnp.roll(vorticity, 1, axis=1)
        laplacian = right_cell + left_cell + upper_cell + lower_cell - 4.0 * vorticity
        tendency = (
            VISCOSITY * laplacian
            - flow_x * (0.5 * (right_cell - left_cell))
            - flow_y * (0.5 * (upper_cell - lower_cell))
        )
        forcing = (
            velocity[:, 0, substep][:, None, None] * source_x
            - velocity[:, 1, substep][:, None, None] * source_y
        )
        vorticity = vorticity + TIME_STEP * tendency + COUPLING * forcing
        lift_rows.append(jnp.sum(vorticity * lift_kernel, axis=(1, 2)))
        drag_rows.append(jnp.sum(vorticity * drag_kernel, axis=(1, 2)))
    return (vorticity, jnp.stack(lift_rows + drag_rows, axis=1))


def kernel_planes(cells):
    centre_x = lax.broadcasted_iota(jnp.int32, (cells, cells), 1).astype(jnp.float32) - cells / 2.0 + 0.5
    centre_y = lax.broadcasted_iota(jnp.int32, (cells, cells), 0).astype(jnp.float32) - cells / 2.0 + 0.5
    near_x = centre_x / (cells / 16.0)
    near_y = centre_y / (cells / 16.0)
    bell_near = jnp.exp(-(near_x * near_x + near_y * near_y) / 2.0)
    source_x = -near_x * bell_near
    source_y = -near_y * bell_near
    wide_x = centre_x / (cells / 8.0)
    wide_y = centre_y / (cells / 8.0)
    bell_wide = jnp.exp(-(wide_x * wide_x + wide_y * wide_y) / 2.0)
    lift_kernel = -wide_x * bell_wide
    drag_kernel = wide_y * bell_wide

    def total(plane):
        return jnp.sum(jnp.sum(plane, axis=0, keepdims=True), axis=1, keepdims=True)

    lift_kernel = lift_kernel / jnp.sqrt(total(lift_kernel * lift_kernel))
    drag_kernel = drag_kernel / jnp.sqrt(total(drag_kernel * drag_kernel))
    return (source_x, source_y, lift_kernel, drag_kernel)


def run_substeps(vorticity, flow_x, flow_y, forcing_of, lift_kernel, drag_kernel, substeps):
    rows_across, cols_across = vorticity.shape
    lane = lax.broadcasted_iota(jnp.int32, (1, 2 * substeps), 1)
    row = jnp.zeros((1, 2 * substeps), jnp.float32)
    along_x = (TIME_STEP * 0.5) * flow_x
    along_y = (TIME_STEP * 0.5) * flow_y
    for substep in range(substeps):
        right_cell = pltpu.roll(vorticity, cols_across - 1, 1)
        left_cell = pltpu.roll(vorticity, 1, 1)
        upper_cell = pltpu.roll(vorticity, rows_across - 1, 0)
        lower_cell = pltpu.roll(vorticity, 1, 0)
        laplacian = (right_cell + left_cell) + (upper_cell + lower_cell) - 4.0 * vorticity
        step = (
            (TIME_STEP * VISCOSITY) * laplacian
            - along_x * (right_cell - left_cell)
            - along_y * (upper_cell - lower_cell)
        )
        if forcing_of is None:
            vorticity = vorticity + step
        else:
            vorticity = vorticity + step + forcing_of(substep)
        lift = jnp.sum(jnp.sum(vorticity * lift_kernel, axis=0, keepdims=True), axis=1, keepdims=True)
        drag = jnp.sum(jnp.sum(vorticity * drag_kernel, axis=0, keepdims=True), axis=1, keepdims=True)
        row = row + jnp.where(lane == substep, lift, 0.0) + jnp.where(lane == substeps + substep, drag, 0.0)
    return vorticity, row


def stencil_kernel(velocity_ref, vorticity_ref, flow_x_ref, flow_y_ref, out_ref, rows_ref, *, substeps):
    strip = pl.program_id(0)
    source_x, source_y, lift_kernel, drag_kernel = kernel_planes(vorticity_ref.shape[-1])

    def forcing_of(substep):
        return COUPLING * (
            velocity_ref[strip, substep] * source_x
            - velocity_ref[strip, substeps + substep] * source_y
        )

    vorticity, row = run_substeps(
        vorticity_ref[0, 0], flow_x_ref[0, 0], flow_y_ref[0, 0], forcing_of,
        lift_kernel, drag_kernel, substeps,
    )
    out_ref[0] = vorticity
    rows_ref[0] = row


def strip_step_kernel(strip_fields, vorticity, motion, kernels, substeps):
    strips, cells_y, cells_x = strip_fields.shape[1:]
    halves = motion.reshape(strips, 2, substeps)
    earlier = jnp.concatenate([jnp.zeros_like(halves[:, :, :1]), halves[:, :, :-1]], axis=2)
    velocity = (halves - earlier).reshape(strips, 2 * substeps)
    def field(index):
        return pl.BlockSpec((1, 1, cells_y, cells_x), lambda s: (index, s, 0, 0))

    new_vorticity, rows = pl.pallas_call(
        lambda *refs: stencil_kernel(*refs, substeps=substeps),
        grid=(strips,),
        in_specs=[
            pl.BlockSpec(memory_space=pltpu.SMEM),
            field(0), field(1), field(2),
        ],
        out_specs=[
            pl.BlockSpec((1, cells_y, cells_x), lambda s: (s, 0, 0)),
            pl.BlockSpec((1, 1, 2 * substeps), lambda s: (s, 0, 0)),
        ],
        out_shape=[
            jax.ShapeDtypeStruct((strips, cells_y, cells_x), jnp.float32),
            jax.ShapeDtypeStruct((strips, 1, 2 * substeps), jnp.float32),
        ],
        name="strip_stencil",
    )(velocity, vorticity, strip_fields, strip_fields)
    return new_vorticity, rows[:, 0, :]


def apply_block(vectors, matrix):
    return lax.dot_general(vectors, matrix, (((1,), (1,)), ((), ())), precision=EXACT_DOT)


def first_contract(left_side, right_side):
    return lax.dot_general(left_side, right_side, (((0,), (0,)), ((), ())), precision=EXACT_DOT)


def beam_solve(beam_load, pivot_inv, lower_block, upper_block):
    block_count = pivot_inv.shape[0]
    block_size = pivot_inv.shape[1]
    blocks = beam_load.reshape(beam_load.shape[0], block_count, block_size)
    carried = [blocks[:, 0]]
    for block_index in range(1, block_count):
        pivoted = apply_block(carried[-1], pivot_inv[block_index - 1])
        carried.append(blocks[:, block_index] - apply_block(pivoted, lower_block[block_index - 1]))
    solved = [apply_block(carried[-1], pivot_inv[block_count - 1])]
    for block_index in range(block_count - 2, -1, -1):
        remainder = carried[block_index] - apply_block(solved[0], upper_block[block_index])
        solved.insert(0, apply_block(remainder, pivot_inv[block_index]))
    return jnp.concatenate(solved, axis=1)


def start_kernel(owner_ref, riser_ref, node_ref, spread_ref, pivot_ref, lower_ref, upper_ref, fields_ref,
                 response_ref, vorticity_ref, sent_ref, *, substeps):
    block_count = pivot_ref.shape[1]
    block_size = pivot_ref.shape[2]
    node_count = block_count * block_size
    strips = node_ref.shape[1]
    per_device = fields_ref.shape[1]
    position = lax.axis_index("strip")
    group_position = lax.axis_index("group")

    strip_lane = lax.broadcasted_iota(jnp.int32, (1, strips), 1)
    strip_sublane = lax.broadcasted_iota(jnp.int32, (strips, 1), 0)
    owned_row = jnp.zeros((1, strips), jnp.float32)
    owned_col = jnp.zeros((strips, 1), jnp.float32)
    for strip in range(strips):
        held = jnp.where(owner_ref[0, riser_ref[strip]] == position, 1.0, 0.0)
        owned_row = jnp.where(strip_lane == strip, held, owned_row)
        owned_col = jnp.where(strip_sublane == strip, held, owned_col)
    diagonal = lax.broadcasted_iota(jnp.int32, (strips, strips), 0) == lax.broadcasted_iota(jnp.int32, (strips, strips), 1)
    node_row = node_ref[...]
    node_col = jnp.sum(jnp.where(diagonal, node_row.astype(jnp.float32), 0.0), axis=1, keepdims=True)

    def apply(matrix, vectors):
        return jnp.dot(matrix, vectors, precision=lax.Precision.HIGH, preferred_element_type=jnp.float32)

    def unit_load(block_index):
        node = block_index * block_size + lax.broadcasted_iota(jnp.int32, (block_size, strips), 0)
        return (node == node_row).astype(jnp.float32) * owned_row

    def product(left, right):
        return jnp.dot(left, right, precision=EXACT_DOT, preferred_element_type=jnp.float32)

    forward = [None] + [product(lower_ref[0, i - 1], pivot_ref[0, i - 1]) for i in range(1, block_count)]
    backward = [product(pivot_ref[0, i], upper_ref[0, i]) for i in range(block_count - 1)]
    carried = [unit_load(0)]
    for block_index in range(1, block_count):
        carried.append(unit_load(block_index) - apply(forward[block_index], carried[-1]))
    pivoted = [apply(pivot_ref[0, i], carried[i]) for i in range(block_count)]
    solved = pivoted[block_count - 1]
    response_ref[(block_count - 1) * block_size:, :] = solved
    for block_index in range(block_count - 2, -1, -1):
        solved = pivoted[block_index] - apply(backward[block_index], solved)
        response_ref[block_index * block_size:(block_index + 1) * block_size, :] = solved

    _, _, lift_kernel, drag_kernel = kernel_planes(fields_ref.shape[-1])
    strip_of_row = lax.broadcasted_iota(jnp.int32, (per_device, 2 * substeps), 0)
    rows = jnp.zeros((per_device, 2 * substeps), jnp.float32)
    for strip in range(per_device):
        vorticity, row = run_substeps(
            fields_ref[0, strip], fields_ref[1, strip], fields_ref[2, strip], None,
            lift_kernel, drag_kernel, substeps,
        )
        vorticity_ref[strip] = vorticity
        rows = jnp.where(strip_of_row == strip, row, rows)

    node_onehot = (
        node_col == lax.broadcasted_iota(jnp.int32, (strips, node_count), 1).astype(jnp.float32)
    ).astype(jnp.float32)
    coupling = jnp.dot(node_onehot, response_ref[...], precision=EXACT_DOT, preferred_element_type=jnp.float32)
    coupling = coupling * owned_col
    sent_rows = sent_ref.shape[0]
    place = lax.broadcasted_iota(jnp.int32, (sent_rows, strips), 0) - group_position * strips
    pick = (place == lax.broadcasted_iota(jnp.int32, (sent_rows, strips), 1)).astype(jnp.float32)
    sent_ref[:, 0:2 * substeps] = jnp.dot(spread_ref[...], rows, precision=EXACT_DOT, preferred_element_type=jnp.float32)
    sent_ref[:, 2 * substeps:] = jnp.dot(pick, coupling, precision=EXACT_DOT, preferred_element_type=jnp.float32)


def spread_matrix(devices, per_device):
    return (
        np.arange(devices * per_device)[:, None] % per_device == np.arange(per_device)[None, :]
    ).astype(np.float32)


def start_step(riser_owner, strip_riser, strip_node, pivot_inv, lower_block, upper_block, strip_fields, devices, substeps):
    strips = strip_node.shape[0]
    node_count = pivot_inv.shape[1] * pivot_inv.shape[2]
    _, per_device, cells_y, cells_x = strip_fields.shape
    vmem = pl.BlockSpec(memory_space=pltpu.VMEM)
    return pl.pallas_call(
        lambda *refs: start_kernel(*refs, substeps=substeps),
        in_specs=[pl.BlockSpec(memory_space=pltpu.SMEM)] * 2 + [vmem] * 6,
        out_shape=[
            jax.ShapeDtypeStruct((node_count, strips), jnp.float32),
            jax.ShapeDtypeStruct((per_device, cells_y, cells_x), jnp.float32),
            jax.ShapeDtypeStruct((devices * per_device, 2 * substeps + strips), jnp.float32),
        ],
        name="start_step",
    )(
        riser_owner, strip_riser.reshape(strips), strip_node[None, :], spread_matrix(devices, per_device),
        pivot_inv, lower_block, upper_block, strip_fields,
    )


def second_kernel(received_ref, node_ref, spread_ref, gather_ref, difference_ref, fields_ref, vorticity_ref,
                  out_ref, sent_ref, *, substeps, node_count):
    position = lax.axis_index("strip")
    group_position = lax.axis_index("group")
    total_strips, _ = received_ref.shape
    strips = node_ref.shape[1]
    per_device = fields_ref.shape[1]
    every_force = received_ref[:, 0:2 * substeps]
    offset = jnp.sum(every_force, axis=0, keepdims=True) / jnp.sqrt(jnp.float32(total_strips))
    group_force = received_ref[pl.ds(group_position * strips, strips), 0:2 * substeps]
    my_coupling = jnp.dot(
        gather_ref[...], received_ref[:, 2 * substeps:], precision=EXACT_DOT, preferred_element_type=jnp.float32
    )
    motion = jnp.dot(my_coupling, group_force, precision=EXACT_DOT, preferred_element_type=jnp.float32)
    mine = (
        lax.broadcasted_iota(jnp.int32, (per_device, strips), 1)
        == position * per_device + lax.broadcasted_iota(jnp.int32, (per_device, strips), 0)
    )
    local_node = jnp.sum(jnp.where(mine, node_ref[...].astype(jnp.float32), 0.0), axis=1, keepdims=True)
    local_taper = 1.0 - local_node / node_count
    lane = lax.broadcasted_iota(jnp.int32, (per_device, 2 * substeps), 1)
    sublane = lax.broadcasted_iota(jnp.int32, (per_device, 2 * substeps), 0)
    motion = motion + jnp.where(lane >= substeps, local_taper * offset, 0.0)
    velocity = jnp.dot(motion, difference_ref[...], precision=EXACT_DOT, preferred_element_type=jnp.float32)

    source_x, source_y, lift_kernel, drag_kernel = kernel_planes(fields_ref.shape[-1])
    coupled_x = COUPLING * source_x
    coupled_y = COUPLING * source_y
    rows = jnp.zeros((per_device, 2 * substeps), jnp.float32)
    for strip in range(per_device):
        picks = [
            jnp.sum(jnp.sum(jnp.where((sublane == strip) & (lane == column), velocity, 0.0), axis=0, keepdims=True), axis=1, keepdims=True)
            for column in range(2 * substeps)
        ]

        def forcing_of(substep, picks=picks):
            return picks[substep] * coupled_x - picks[substeps + substep] * coupled_y

        vorticity, row = run_substeps(
            vorticity_ref[strip], fields_ref[1, strip], fields_ref[2, strip], forcing_of,
            lift_kernel, drag_kernel, substeps,
        )
        out_ref[strip] = vorticity
        rows = jnp.where(sublane == strip, row, rows)
    sent_ref[...] = jnp.dot(spread_ref[...], rows, precision=EXACT_DOT, preferred_element_type=jnp.float32)


def difference_matrix(substeps):
    columns = np.arange(2 * substeps)
    same = columns[:, None] == columns[None, :]
    before = (columns[:, None] + 1 == columns[None, :]) & (columns[None, :] % substeps != 0)
    return same.astype(np.float32) - before.astype(np.float32)


def second_step(received, strip_node, strip_fields, vorticity, devices, node_count, substeps):
    _, per_device, cells_y, cells_x = strip_fields.shape
    spread = spread_matrix(devices, per_device)
    vmem = pl.BlockSpec(memory_space=pltpu.VMEM)
    return pl.pallas_call(
        lambda *refs: second_kernel(*refs, substeps=substeps, node_count=node_count),
        in_specs=[vmem] * 7,
        out_shape=[
            jax.ShapeDtypeStruct((per_device, cells_y, cells_x), jnp.float32),
            jax.ShapeDtypeStruct((devices * per_device, 2 * substeps), jnp.float32),
        ],
        name="second_step",
    )(received, strip_node[None, :], spread, np.ascontiguousarray(spread.T), difference_matrix(substeps), strip_fields, vorticity)


def local(strip_fields, strip_riser, strip_node, riser_owner, pivot_inv, lower_block, upper_block):
    position = lax.axis_index("strip")
    group_position = lax.axis_index("group")
    group_count = lax.axis_size("group")
    devices = lax.axis_size("strip") * group_count
    per_device = strip_fields.shape[1]
    grid_cells = strip_fields.shape[2]
    node_count = pivot_inv.shape[1] * pivot_inv.shape[2]
    riser_count = riser_owner.shape[1]
    group_strips = strip_node.shape[0]
    substeps = NSUB
    total_strips = per_device * devices
    top_taper = 1.0 - jnp.arange(node_count, dtype=jnp.float32) / node_count

    unit_response, first_vorticity, first_sent = start_step(
        riser_owner, strip_riser, strip_node, pivot_inv, lower_block, upper_block, strip_fields, devices, substeps
    )

    received = lax.all_to_all(first_sent, ("group", "strip"), 0, 0, tiled=True)
    vorticity, sent = second_step(received, strip_node, strip_fields, first_vorticity, devices, node_count, substeps)
    received = lax.all_to_all(sent, ("group", "strip"), 0, 0, tiled=True)
    offset = jnp.sum(received[:, substeps:], axis=0) / jnp.sqrt(jnp.float32(total_strips))
    group_force = lax.dynamic_slice_in_dim(received, group_position * group_strips, group_strips)
    displacement = lax.dot_general(
        group_force, unit_response, (((0,), (1,)), ((), ())), precision=EXACT_DOT
    )
    displacement = displacement.at[substeps:, :].add(offset[:, None] * top_taper[None, :])
    return (vorticity, displacement[None])


def solution(mesh):
    in_specs = (
        P(None, ("group", "strip"), None, None),
        P("group", None),
        P("group"),
        P("group", None),
        P(("group", "strip"), None, None, None),
        P(("group", "strip"), None, None, None),
        P(("group", "strip"), None, None, None),
    )
    out_specs = (P(("group", "strip"), None, None), P(("group", "strip"), None, None))
    return jax.shard_map(local, mesh=mesh, in_specs=in_specs, out_specs=out_specs, check_vma=False)
```

```python
import numpy as np
import jax
import jax.numpy as jnp
from jax import lax
from jax.sharding import PartitionSpec as P
from jax.experimental import pallas as pl
from jax.experimental.pallas import tpu as pltpu

NSUB = 8
COUPLED = 2


TIME_STEP = 0.25
VISCOSITY = 0.05
COUPLING = 0.5
EXACT_DOT = lax.Precision.HIGHEST


def make_kernels(grid_cells):
    centre = jnp.arange(grid_cells, dtype=jnp.float32) - grid_cells / 2.0 + 0.5
    near_x = (centre / (grid_cells / 16.0))[None, :]
    near_y = (centre / (grid_cells / 16.0))[:, None]
    bell_near = jnp.exp(-(near_x * near_x + near_y * near_y) / 2.0)
    source_x = -near_x * bell_near
    source_y = -near_y * bell_near
    wide_x = (centre / (grid_cells / 8.0))[None, :]
    wide_y = (centre / (grid_cells / 8.0))[:, None]
    bell_wide = jnp.exp(-(wide_x * wide_x + wide_y * wide_y) / 2.0)
    lift_kernel = -wide_x * bell_wide
    drag_kernel = wide_y * bell_wide
    lift_kernel = lift_kernel / jnp.sqrt(jnp.sum(lift_kernel * lift_kernel))
    drag_kernel = drag_kernel / jnp.sqrt(jnp.sum(drag_kernel * drag_kernel))
    return (source_x, source_y, lift_kernel, drag_kernel)


def strip_step(vorticity, flow_x, flow_y, motion, kernels, substeps):
    source_x, source_y, lift_kernel, drag_kernel = kernels
    halves = motion.reshape(motion.shape[0], 2, substeps)
    earlier = jnp.concatenate([jnp.zeros_like(halves[:, :, :1]), halves[:, :, :-1]], axis=2)
    velocity = halves - earlier
    lift_rows = []
    drag_rows = []
    for substep in range(substeps):
        right_cell = jnp.roll(vorticity, -1, axis=2)
        left_cell = jnp.roll(vorticity, 1, axis=2)
        upper_cell = jnp.roll(vorticity, -1, axis=1)
        lower_cell = jnp.roll(vorticity, 1, axis=1)
        laplacian = right_cell + left_cell + upper_cell + lower_cell - 4.0 * vorticity
        tendency = (
            VISCOSITY * laplacian
            - flow_x * (0.5 * (right_cell - left_cell))
            - flow_y * (0.5 * (upper_cell - lower_cell))
        )
        forcing = (
            velocity[:, 0, substep][:, None, None] * source_x
            - velocity[:, 1, substep][:, None, None] * source_y
        )
        vorticity = vorticity + TIME_STEP * tendency + COUPLING * forcing
        lift_rows.append(jnp.sum(vorticity * lift_kernel, axis=(1, 2)))
        drag_rows.append(jnp.sum(vorticity * drag_kernel, axis=(1, 2)))
    return (vorticity, jnp.stack(lift_rows + drag_rows, axis=1))


def kernel_planes(cells):
    centre_x = lax.broadcasted_iota(jnp.int32, (cells, cells), 1).astype(jnp.float32) - cells / 2.0 + 0.5
    centre_y = lax.broadcasted_iota(jnp.int32, (cells, cells), 0).astype(jnp.float32) - cells / 2.0 + 0.5
    near_x = centre_x / (cells / 16.0)
    near_y = centre_y / (cells / 16.0)
    bell_near = jnp.exp(-(near_x * near_x + near_y * near_y) / 2.0)
    source_x = -near_x * bell_near
    source_y = -near_y * bell_near
    wide_x = centre_x / (cells / 8.0)
    wide_y = centre_y / (cells / 8.0)
    bell_wide = jnp.exp(-(wide_x * wide_x + wide_y * wide_y) / 2.0)
    lift_kernel = -wide_x * bell_wide
    drag_kernel = wide_y * bell_wide

    def total(plane):
        return jnp.sum(jnp.sum(plane, axis=0, keepdims=True), axis=1, keepdims=True)

    lift_kernel = lift_kernel / jnp.sqrt(total(lift_kernel * lift_kernel))
    drag_kernel = drag_kernel / jnp.sqrt(total(drag_kernel * drag_kernel))
    return (source_x, source_y, lift_kernel, drag_kernel)


def run_substeps(vorticity, flow_x, flow_y, forcing_of, lift_kernel, drag_kernel, substeps):
    rows_across, cols_across = vorticity.shape
    lane = lax.broadcasted_iota(jnp.int32, (1, 2 * substeps), 1)
    row = jnp.zeros((1, 2 * substeps), jnp.float32)
    along_x = (TIME_STEP * 0.5) * flow_x
    along_y = (TIME_STEP * 0.5) * flow_y
    for substep in range(substeps):
        right_cell = pltpu.roll(vorticity, cols_across - 1, 1)
        left_cell = pltpu.roll(vorticity, 1, 1)
        upper_cell = pltpu.roll(vorticity, rows_across - 1, 0)
        lower_cell = pltpu.roll(vorticity, 1, 0)
        laplacian = (right_cell + left_cell) + (upper_cell + lower_cell) - 4.0 * vorticity
        step = (
            (TIME_STEP * VISCOSITY) * laplacian
            - along_x * (right_cell - left_cell)
            - along_y * (upper_cell - lower_cell)
        )
        if forcing_of is None:
            vorticity = vorticity + step
        else:
            vorticity = vorticity + step + forcing_of(substep)
        lift = jnp.sum(jnp.sum(vorticity * lift_kernel, axis=0, keepdims=True), axis=1, keepdims=True)
        drag = jnp.sum(jnp.sum(vorticity * drag_kernel, axis=0, keepdims=True), axis=1, keepdims=True)
        row = row + jnp.where(lane == substep, lift, 0.0) + jnp.where(lane == substeps + substep, drag, 0.0)
    return vorticity, row


def stencil_kernel(velocity_ref, vorticity_ref, flow_x_ref, flow_y_ref, out_ref, rows_ref, *, substeps):
    strip = pl.program_id(0)
    source_x, source_y, lift_kernel, drag_kernel = kernel_planes(vorticity_ref.shape[-1])

    def forcing_of(substep):
        return COUPLING * (
            velocity_ref[strip, substep] * source_x
            - velocity_ref[strip, substeps + substep] * source_y
        )

    vorticity, row = run_substeps(
        vorticity_ref[0, 0], flow_x_ref[0, 0], flow_y_ref[0, 0], forcing_of,
        lift_kernel, drag_kernel, substeps,
    )
    out_ref[0] = vorticity
    rows_ref[0] = row


def strip_step_kernel(strip_fields, vorticity, motion, kernels, substeps):
    strips, cells_y, cells_x = strip_fields.shape[1:]
    halves = motion.reshape(strips, 2, substeps)
    earlier = jnp.concatenate([jnp.zeros_like(halves[:, :, :1]), halves[:, :, :-1]], axis=2)
    velocity = (halves - earlier).reshape(strips, 2 * substeps)
    def field(index):
        return pl.BlockSpec((1, 1, cells_y, cells_x), lambda s: (index, s, 0, 0))

    new_vorticity, rows = pl.pallas_call(
        lambda *refs: stencil_kernel(*refs, substeps=substeps),
        grid=(strips,),
        in_specs=[
            pl.BlockSpec(memory_space=pltpu.SMEM),
            field(0), field(1), field(2),
        ],
        out_specs=[
            pl.BlockSpec((1, cells_y, cells_x), lambda s: (s, 0, 0)),
            pl.BlockSpec((1, 1, 2 * substeps), lambda s: (s, 0, 0)),
        ],
        out_shape=[
            jax.ShapeDtypeStruct((strips, cells_y, cells_x), jnp.float32),
            jax.ShapeDtypeStruct((strips, 1, 2 * substeps), jnp.float32),
        ],
        name="strip_stencil",
    )(velocity, vorticity, strip_fields, strip_fields)
    return new_vorticity, rows[:, 0, :]


def apply_block(vectors, matrix):
    return lax.dot_general(vectors, matrix, (((1,), (1,)), ((), ())), precision=EXACT_DOT)


def first_contract(left_side, right_side):
    return lax.dot_general(left_side, right_side, (((0,), (0,)), ((), ())), precision=EXACT_DOT)


def beam_solve(beam_load, pivot_inv, lower_block, upper_block):
    block_count = pivot_inv.shape[0]
    block_size = pivot_inv.shape[1]
    blocks = beam_load.reshape(beam_load.shape[0], block_count, block_size)
    carried = [blocks[:, 0]]
    for block_index in range(1, block_count):
        pivoted = apply_block(carried[-1], pivot_inv[block_index - 1])
        carried.append(blocks[:, block_index] - apply_block(pivoted, lower_block[block_index - 1]))
    solved = [apply_block(carried[-1], pivot_inv[block_count - 1])]
    for block_index in range(block_count - 2, -1, -1):
        remainder = carried[block_index] - apply_block(solved[0], upper_block[block_index])
        solved.insert(0, apply_block(remainder, pivot_inv[block_index]))
    return jnp.concatenate(solved, axis=1)


def start_kernel(owner_ref, riser_ref, node_ref, spread_ref, pivot_ref, lower_ref, upper_ref, fields_ref,
                 response_ref, vorticity_ref, sent_ref, *, substeps):
    block_count = pivot_ref.shape[1]
    block_size = pivot_ref.shape[2]
    node_count = block_count * block_size
    strips = node_ref.shape[1]
    per_device = fields_ref.shape[1]
    position = lax.axis_index("strip")
    group_position = lax.axis_index("group")

    strip_lane = lax.broadcasted_iota(jnp.int32, (1, strips), 1)
    strip_sublane = lax.broadcasted_iota(jnp.int32, (strips, 1), 0)
    owned_row = jnp.zeros((1, strips), jnp.float32)
    owned_col = jnp.zeros((strips, 1), jnp.float32)
    for strip in range(strips):
        held = jnp.where(owner_ref[0, riser_ref[strip]] == position, 1.0, 0.0)
        owned_row = jnp.where(strip_lane == strip, held, owned_row)
        owned_col = jnp.where(strip_sublane == strip, held, owned_col)
    diagonal = lax.broadcasted_iota(jnp.int32, (strips, strips), 0) == lax.broadcasted_iota(jnp.int32, (strips, strips), 1)
    node_row = node_ref[...]
    node_col = jnp.sum(jnp.where(diagonal, node_row.astype(jnp.float32), 0.0), axis=1, keepdims=True)

    def apply(matrix, vectors):
        return jnp.dot(matrix, vectors, precision=lax.Precision.HIGH, preferred_element_type=jnp.float32)

    def unit_load(block_index):
        node = block_index * block_size + lax.broadcasted_iota(jnp.int32, (block_size, strips), 0)
        return (node == node_row).astype(jnp.float32) * owned_row

    def product(left, right):
        return jnp.dot(left, right, precision=lax.Precision.HIGH, preferred_element_type=jnp.float32)

    forward = [None] + [product(lower_ref[0, i - 1], pivot_ref[0, i - 1]) for i in range(1, block_count)]
    backward = [product(pivot_ref[0, i], upper_ref[0, i]) for i in range(block_count - 1)]
    carried = [unit_load(0)]
    for block_index in range(1, block_count):
        carried.append(unit_load(block_index) - apply(forward[block_index], carried[-1]))
    pivoted = [apply(pivot_ref[0, i], carried[i]) for i in range(block_count)]
    solved = pivoted[block_count - 1]
    response_ref[(block_count - 1) * block_size:, :] = solved
    for block_index in range(block_count - 2, -1, -1):
        solved = pivoted[block_index] - apply(backward[block_index], solved)
        response_ref[block_index * block_size:(block_index + 1) * block_size, :] = solved

    _, _, lift_kernel, drag_kernel = kernel_planes(fields_ref.shape[-1])
    strip_of_row = lax.broadcasted_iota(jnp.int32, (per_device, 2 * substeps), 0)
    rows = jnp.zeros((per_device, 2 * substeps), jnp.float32)
    for strip in range(per_device):
        vorticity, row = run_substeps(
            fields_ref[0, strip], fields_ref[1, strip], fields_ref[2, strip], None,
            lift_kernel, drag_kernel, substeps,
        )
        vorticity_ref[strip] = vorticity
        rows = jnp.where(strip_of_row == strip, row, rows)

    node_onehot = (
        node_col == lax.broadcasted_iota(jnp.int32, (strips, node_count), 1).astype(jnp.float32)
    ).astype(jnp.float32)
    coupling = jnp.dot(node_onehot, response_ref[...], precision=EXACT_DOT, preferred_element_type=jnp.float32)
    coupling = coupling * owned_col
    sent_rows = sent_ref.shape[0]
    place = lax.broadcasted_iota(jnp.int32, (sent_rows, strips), 0) - group_position * strips
    pick = (place == lax.broadcasted_iota(jnp.int32, (sent_rows, strips), 1)).astype(jnp.float32)
    sent_ref[:, 0:2 * substeps] = jnp.dot(spread_ref[...], rows, precision=EXACT_DOT, preferred_element_type=jnp.float32)
    sent_ref[:, 2 * substeps:] = jnp.dot(pick, coupling, precision=EXACT_DOT, preferred_element_type=jnp.float32)


def spread_matrix(devices, per_device):
    return (
        np.arange(devices * per_device)[:, None] % per_device == np.arange(per_device)[None, :]
    ).astype(np.float32)


def start_step(riser_owner, strip_riser, strip_node, pivot_inv, lower_block, upper_block, strip_fields, devices, substeps):
    strips = strip_node.shape[0]
    node_count = pivot_inv.shape[1] * pivot_inv.shape[2]
    _, per_device, cells_y, cells_x = strip_fields.shape
    vmem = pl.BlockSpec(memory_space=pltpu.VMEM)
    return pl.pallas_call(
        lambda *refs: start_kernel(*refs, substeps=substeps),
        in_specs=[pl.BlockSpec(memory_space=pltpu.SMEM)] * 2 + [vmem] * 6,
        out_shape=[
            jax.ShapeDtypeStruct((node_count, strips), jnp.float32),
            jax.ShapeDtypeStruct((per_device, cells_y, cells_x), jnp.float32),
            jax.ShapeDtypeStruct((devices * per_device, 2 * substeps + strips), jnp.float32),
        ],
        name="start_step",
    )(
        riser_owner, strip_riser.reshape(strips), strip_node[None, :], spread_matrix(devices, per_device),
        pivot_inv, lower_block, upper_block, strip_fields,
    )


def second_kernel(received_ref, node_ref, spread_ref, gather_ref, difference_ref, fields_ref, vorticity_ref,
                  out_ref, sent_ref, *, substeps, node_count):
    position = lax.axis_index("strip")
    group_position = lax.axis_index("group")
    total_strips, _ = received_ref.shape
    strips = node_ref.shape[1]
    per_device = fields_ref.shape[1]
    every_force = received_ref[:, 0:2 * substeps]
    offset = jnp.sum(every_force, axis=0, keepdims=True) / jnp.sqrt(jnp.float32(total_strips))
    group_force = received_ref[pl.ds(group_position * strips, strips), 0:2 * substeps]
    my_coupling = jnp.dot(
        gather_ref[...], received_ref[:, 2 * substeps:], precision=EXACT_DOT, preferred_element_type=jnp.float32
    )
    motion = jnp.dot(my_coupling, group_force, precision=EXACT_DOT, preferred_element_type=jnp.float32)
    mine = (
        lax.broadcasted_iota(jnp.int32, (per_device, strips), 1)
        == position * per_device + lax.broadcasted_iota(jnp.int32, (per_device, strips), 0)
    )
    local_node = jnp.sum(jnp.where(mine, node_ref[...].astype(jnp.float32), 0.0), axis=1, keepdims=True)
    local_taper = 1.0 - local_node / node_count
    lane = lax.broadcasted_iota(jnp.int32, (per_device, 2 * substeps), 1)
    sublane = lax.broadcasted_iota(jnp.int32, (per_device, 2 * substeps), 0)
    motion = motion + jnp.where(lane >= substeps, local_taper * offset, 0.0)
    velocity = jnp.dot(motion, difference_ref[...], precision=EXACT_DOT, preferred_element_type=jnp.float32)

    source_x, source_y, lift_kernel, drag_kernel = kernel_planes(fields_ref.shape[-1])
    coupled_x = COUPLING * source_x
    coupled_y = COUPLING * source_y
    rows = jnp.zeros((per_device, 2 * substeps), jnp.float32)
    for strip in range(per_device):
        picks = [
            jnp.sum(jnp.sum(jnp.where((sublane == strip) & (lane == column), velocity, 0.0), axis=0, keepdims=True), axis=1, keepdims=True)
            for column in range(2 * substeps)
        ]

        def forcing_of(substep, picks=picks):
            return picks[substep] * coupled_x - picks[substeps + substep] * coupled_y

        vorticity, row = run_substeps(
            vorticity_ref[strip], fields_ref[1, strip], fields_ref[2, strip], forcing_of,
            lift_kernel, drag_kernel, substeps,
        )
        out_ref[strip] = vorticity
        rows = jnp.where(sublane == strip, row, rows)
    sent_ref[...] = jnp.dot(spread_ref[...], rows, precision=EXACT_DOT, preferred_element_type=jnp.float32)


def difference_matrix(substeps):
    columns = np.arange(2 * substeps)
    same = columns[:, None] == columns[None, :]
    before = (columns[:, None] + 1 == columns[None, :]) & (columns[None, :] % substeps != 0)
    return same.astype(np.float32) - before.astype(np.float32)


def second_step(received, strip_node, strip_fields, vorticity, devices, node_count, substeps):
    _, per_device, cells_y, cells_x = strip_fields.shape
    spread = spread_matrix(devices, per_device)
    vmem = pl.BlockSpec(memory_space=pltpu.VMEM)
    return pl.pallas_call(
        lambda *refs: second_kernel(*refs, substeps=substeps, node_count=node_count),
        in_specs=[vmem] * 7,
        out_shape=[
            jax.ShapeDtypeStruct((per_device, cells_y, cells_x), jnp.float32),
            jax.ShapeDtypeStruct((devices * per_device, 2 * substeps), jnp.float32),
        ],
        name="second_step",
    )(received, strip_node[None, :], spread, np.ascontiguousarray(spread.T), difference_matrix(substeps), strip_fields, vorticity)


def local(strip_fields, strip_riser, strip_node, riser_owner, pivot_inv, lower_block, upper_block):
    position = lax.axis_index("strip")
    group_position = lax.axis_index("group")
    group_count = lax.axis_size("group")
    devices = lax.axis_size("strip") * group_count
    per_device = strip_fields.shape[1]
    grid_cells = strip_fields.shape[2]
    node_count = pivot_inv.shape[1] * pivot_inv.shape[2]
    riser_count = riser_owner.shape[1]
    group_strips = strip_node.shape[0]
    substeps = NSUB
    total_strips = per_device * devices
    top_taper = 1.0 - jnp.arange(node_count, dtype=jnp.float32) / node_count

    unit_response, first_vorticity, first_sent = start_step(
        riser_owner, strip_riser, strip_node, pivot_inv, lower_block, upper_block, strip_fields, devices, substeps
    )

    received = lax.all_to_all(first_sent, ("group", "strip"), 0, 0, tiled=True)
    vorticity, sent = second_step(received, strip_node, strip_fields, first_vorticity, devices, node_count, substeps)
    received = lax.all_to_all(sent, ("group", "strip"), 0, 0, tiled=True)
    offset = jnp.sum(received[:, substeps:], axis=0) / jnp.sqrt(jnp.float32(total_strips))
    group_force = lax.dynamic_slice_in_dim(received, group_position * group_strips, group_strips)
    displacement = lax.dot_general(
        group_force, unit_response, (((0,), (1,)), ((), ())), precision=EXACT_DOT
    )
    displacement = displacement.at[substeps:, :].add(offset[:, None] * top_taper[None, :])
    return (vorticity, displacement[None])


def solution(mesh):
    in_specs = (
        P(None, ("group", "strip"), None, None),
        P("group", None),
        P("group"),
        P("group", None),
        P(("group", "strip"), None, None, None),
        P(("group", "strip"), None, None, None),
        P(("group", "strip"), None, None, None),
    )
    out_specs = (P(("group", "strip"), None, None), P(("group", "strip"), None, None))
    return jax.shard_map(local, mesh=mesh, in_specs=in_specs, out_specs=out_specs, check_vma=False)
```

```python
import numpy as np
import jax
import jax.numpy as jnp
from jax import lax
from jax.sharding import PartitionSpec as P
from jax.experimental import pallas as pl
from jax.experimental.pallas import tpu as pltpu

NSUB = 8
COUPLED = 2


TIME_STEP = 0.25
VISCOSITY = 0.05
COUPLING = 0.5
EXACT_DOT = lax.Precision.HIGHEST


def make_kernels(grid_cells):
    centre = jnp.arange(grid_cells, dtype=jnp.float32) - grid_cells / 2.0 + 0.5
    near_x = (centre / (grid_cells / 16.0))[None, :]
    near_y = (centre / (grid_cells / 16.0))[:, None]
    bell_near = jnp.exp(-(near_x * near_x + near_y * near_y) / 2.0)
    source_x = -near_x * bell_near
    source_y = -near_y * bell_near
    wide_x = (centre / (grid_cells / 8.0))[None, :]
    wide_y = (centre / (grid_cells / 8.0))[:, None]
    bell_wide = jnp.exp(-(wide_x * wide_x + wide_y * wide_y) / 2.0)
    lift_kernel = -wide_x * bell_wide
    drag_kernel = wide_y * bell_wide
    lift_kernel = lift_kernel / jnp.sqrt(jnp.sum(lift_kernel * lift_kernel))
    drag_kernel = drag_kernel / jnp.sqrt(jnp.sum(drag_kernel * drag_kernel))
    return (source_x, source_y, lift_kernel, drag_kernel)


def strip_step(vorticity, flow_x, flow_y, motion, kernels, substeps):
    source_x, source_y, lift_kernel, drag_kernel = kernels
    halves = motion.reshape(motion.shape[0], 2, substeps)
    earlier = jnp.concatenate([jnp.zeros_like(halves[:, :, :1]), halves[:, :, :-1]], axis=2)
    velocity = halves - earlier
    lift_rows = []
    drag_rows = []
    for substep in range(substeps):
        right_cell = jnp.roll(vorticity, -1, axis=2)
        left_cell = jnp.roll(vorticity, 1, axis=2)
        upper_cell = jnp.roll(vorticity, -1, axis=1)
        lower_cell = jnp.roll(vorticity, 1, axis=1)
        laplacian = right_cell + left_cell + upper_cell + lower_cell - 4.0 * vorticity
        tendency = (
            VISCOSITY * laplacian
            - flow_x * (0.5 * (right_cell - left_cell))
            - flow_y * (0.5 * (upper_cell - lower_cell))
        )
        forcing = (
            velocity[:, 0, substep][:, None, None] * source_x
            - velocity[:, 1, substep][:, None, None] * source_y
        )
        vorticity = vorticity + TIME_STEP * tendency + COUPLING * forcing
        lift_rows.append(jnp.sum(vorticity * lift_kernel, axis=(1, 2)))
        drag_rows.append(jnp.sum(vorticity * drag_kernel, axis=(1, 2)))
    return (vorticity, jnp.stack(lift_rows + drag_rows, axis=1))


def kernel_planes(cells):
    centre_x = lax.broadcasted_iota(jnp.int32, (cells, cells), 1).astype(jnp.float32) - cells / 2.0 + 0.5
    centre_y = lax.broadcasted_iota(jnp.int32, (cells, cells), 0).astype(jnp.float32) - cells / 2.0 + 0.5
    near_x = centre_x / (cells / 16.0)
    near_y = centre_y / (cells / 16.0)
    bell_near = jnp.exp(-(near_x * near_x + near_y * near_y) / 2.0)
    source_x = -near_x * bell_near
    source_y = -near_y * bell_near
    wide_x = centre_x / (cells / 8.0)
    wide_y = centre_y / (cells / 8.0)
    bell_wide = jnp.exp(-(wide_x * wide_x + wide_y * wide_y) / 2.0)
    lift_kernel = -wide_x * bell_wide
    drag_kernel = wide_y * bell_wide

    def total(plane):
        return jnp.sum(jnp.sum(plane, axis=0, keepdims=True), axis=1, keepdims=True)

    lift_kernel = lift_kernel / jnp.sqrt(total(lift_kernel * lift_kernel))
    drag_kernel = drag_kernel / jnp.sqrt(total(drag_kernel * drag_kernel))
    return (source_x, source_y, lift_kernel, drag_kernel)


def run_substeps(vorticity, flow_x, flow_y, forcing_of, lift_kernel, drag_kernel, substeps):
    rows_across, cols_across = vorticity.shape
    lane = lax.broadcasted_iota(jnp.int32, (1, 2 * substeps), 1)
    row = jnp.zeros((1, 2 * substeps), jnp.float32)
    along_x = (TIME_STEP * 0.5) * flow_x
    along_y = (TIME_STEP * 0.5) * flow_y
    for substep in range(substeps):
        right_cell = pltpu.roll(vorticity, cols_across - 1, 1)
        left_cell = pltpu.roll(vorticity, 1, 1)
        upper_cell = pltpu.roll(vorticity, rows_across - 1, 0)
        lower_cell = pltpu.roll(vorticity, 1, 0)
        laplacian = (right_cell + left_cell) + (upper_cell + lower_cell) - 4.0 * vorticity
        step = (
            (TIME_STEP * VISCOSITY) * laplacian
            - along_x * (right_cell - left_cell)
            - along_y * (upper_cell - lower_cell)
        )
        if forcing_of is None:
            vorticity = vorticity + step
        else:
            vorticity = vorticity + step + forcing_of(substep)
        lift = jnp.sum(jnp.sum(vorticity * lift_kernel, axis=0, keepdims=True), axis=1, keepdims=True)
        drag = jnp.sum(jnp.sum(vorticity * drag_kernel, axis=0, keepdims=True), axis=1, keepdims=True)
        row = row + jnp.where(lane == substep, lift, 0.0) + jnp.where(lane == substeps + substep, drag, 0.0)
    return vorticity, row


def stencil_kernel(velocity_ref, vorticity_ref, flow_x_ref, flow_y_ref, out_ref, rows_ref, *, substeps):
    strip = pl.program_id(0)
    source_x, source_y, lift_kernel, drag_kernel = kernel_planes(vorticity_ref.shape[-1])

    def forcing_of(substep):
        return COUPLING * (
            velocity_ref[strip, substep] * source_x
            - velocity_ref[strip, substeps + substep] * source_y
        )

    vorticity, row = run_substeps(
        vorticity_ref[0, 0], flow_x_ref[0, 0], flow_y_ref[0, 0], forcing_of,
        lift_kernel, drag_kernel, substeps,
    )
    out_ref[0] = vorticity
    rows_ref[0] = row


def strip_step_kernel(strip_fields, vorticity, motion, kernels, substeps):
    strips, cells_y, cells_x = strip_fields.shape[1:]
    halves = motion.reshape(strips, 2, substeps)
    earlier = jnp.concatenate([jnp.zeros_like(halves[:, :, :1]), halves[:, :, :-1]], axis=2)
    velocity = (halves - earlier).reshape(strips, 2 * substeps)
    def field(index):
        return pl.BlockSpec((1, 1, cells_y, cells_x), lambda s: (index, s, 0, 0))

    new_vorticity, rows = pl.pallas_call(
        lambda *refs: stencil_kernel(*refs, substeps=substeps),
        grid=(strips,),
        in_specs=[
            pl.BlockSpec(memory_space=pltpu.SMEM),
            field(0), field(1), field(2),
        ],
        out_specs=[
            pl.BlockSpec((1, cells_y, cells_x), lambda s: (s, 0, 0)),
            pl.BlockSpec((1, 1, 2 * substeps), lambda s: (s, 0, 0)),
        ],
        out_shape=[
            jax.ShapeDtypeStruct((strips, cells_y, cells_x), jnp.float32),
            jax.ShapeDtypeStruct((strips, 1, 2 * substeps), jnp.float32),
        ],
        name="strip_stencil",
    )(velocity, vorticity, strip_fields, strip_fields)
    return new_vorticity, rows[:, 0, :]


def apply_block(vectors, matrix):
    return lax.dot_general(vectors, matrix, (((1,), (1,)), ((), ())), precision=EXACT_DOT)


def first_contract(left_side, right_side):
    return lax.dot_general(left_side, right_side, (((0,), (0,)), ((), ())), precision=EXACT_DOT)


def beam_solve(beam_load, pivot_inv, lower_block, upper_block):
    block_count = pivot_inv.shape[0]
    block_size = pivot_inv.shape[1]
    blocks = beam_load.reshape(beam_load.shape[0], block_count, block_size)
    carried = [blocks[:, 0]]
    for block_index in range(1, block_count):
        pivoted = apply_block(carried[-1], pivot_inv[block_index - 1])
        carried.append(blocks[:, block_index] - apply_block(pivoted, lower_block[block_index - 1]))
    solved = [apply_block(carried[-1], pivot_inv[block_count - 1])]
    for block_index in range(block_count - 2, -1, -1):
        remainder = carried[block_index] - apply_block(solved[0], upper_block[block_index])
        solved.insert(0, apply_block(remainder, pivot_inv[block_index]))
    return jnp.concatenate(solved, axis=1)


def start_kernel(owner_ref, riser_ref, node_ref, spread_ref, pivot_ref, lower_ref, upper_ref, fields_ref,
                 response_ref, vorticity_ref, sent_ref, *, substeps):
    block_count = pivot_ref.shape[1]
    block_size = pivot_ref.shape[2]
    node_count = block_count * block_size
    strips = node_ref.shape[1]
    per_device = fields_ref.shape[1]
    position = lax.axis_index("strip")
    group_position = lax.axis_index("group")

    strip_lane = lax.broadcasted_iota(jnp.int32, (1, strips), 1)
    strip_sublane = lax.broadcasted_iota(jnp.int32, (strips, 1), 0)
    owned_row = jnp.zeros((1, strips), jnp.float32)
    owned_col = jnp.zeros((strips, 1), jnp.float32)
    for strip in range(strips):
        held = jnp.where(owner_ref[0, riser_ref[strip]] == position, 1.0, 0.0)
        owned_row = jnp.where(strip_lane == strip, held, owned_row)
        owned_col = jnp.where(strip_sublane == strip, held, owned_col)
    diagonal = lax.broadcasted_iota(jnp.int32, (strips, strips), 0) == lax.broadcasted_iota(jnp.int32, (strips, strips), 1)
    node_row = node_ref[...]
    node_col = jnp.sum(jnp.where(diagonal, node_row.astype(jnp.float32), 0.0), axis=1, keepdims=True)

    def apply(matrix, vectors):
        return jnp.dot(matrix, vectors, precision=lax.Precision.HIGH, preferred_element_type=jnp.float32)

    def unit_load(block_index):
        node = block_index * block_size + lax.broadcasted_iota(jnp.int32, (block_size, strips), 0)
        return (node == node_row).astype(jnp.float32) * owned_row

    def product(left, right):
        return jnp.dot(left, right, precision=lax.Precision.HIGH, preferred_element_type=jnp.float32)

    forward = [None] + [product(lower_ref[0, i - 1], pivot_ref[0, i - 1]) for i in range(1, block_count)]
    backward = [product(pivot_ref[0, i], upper_ref[0, i]) for i in range(block_count - 1)]
    carried = [unit_load(0)]
    for block_index in range(1, block_count):
        carried.append(unit_load(block_index) - apply(forward[block_index], carried[-1]))
    pivoted = [apply(pivot_ref[0, i], carried[i]) for i in range(block_count)]
    solved = pivoted[block_count - 1]
    response_ref[(block_count - 1) * block_size:, :] = solved
    for block_index in range(block_count - 2, -1, -1):
        solved = pivoted[block_index] - apply(backward[block_index], solved)
        response_ref[block_index * block_size:(block_index + 1) * block_size, :] = solved

    _, _, lift_kernel, drag_kernel = kernel_planes(fields_ref.shape[-1])
    strip_of_row = lax.broadcasted_iota(jnp.int32, (per_device, 2 * substeps), 0)
    rows = jnp.zeros((per_device, 2 * substeps), jnp.float32)
    for strip in range(per_device):
        vorticity, row = run_substeps(
            fields_ref[0, strip], fields_ref[1, strip], fields_ref[2, strip], None,
            lift_kernel, drag_kernel, substeps,
        )
        vorticity_ref[strip] = vorticity
        rows = jnp.where(strip_of_row == strip, row, rows)

    node_onehot = (
        node_col == lax.broadcasted_iota(jnp.int32, (strips, node_count), 1).astype(jnp.float32)
    ).astype(jnp.float32)
    coupling = jnp.dot(node_onehot, response_ref[...], precision=EXACT_DOT, preferred_element_type=jnp.float32)
    coupling = coupling * owned_col
    sent_rows = sent_ref.shape[0]
    place = lax.broadcasted_iota(jnp.int32, (sent_rows, strips), 0) - group_position * strips
    pick = (place == lax.broadcasted_iota(jnp.int32, (sent_rows, strips), 1)).astype(jnp.float32)
    sent_ref[:, 0:2 * substeps] = jnp.dot(spread_ref[...], rows, precision=EXACT_DOT, preferred_element_type=jnp.float32)
    sent_ref[:, 2 * substeps:] = jnp.dot(pick, coupling, precision=EXACT_DOT, preferred_element_type=jnp.float32)


def spread_matrix(devices, per_device):
    return (
        np.arange(devices * per_device)[:, None] % per_device == np.arange(per_device)[None, :]
    ).astype(np.float32)


def start_step(riser_owner, strip_riser, strip_node, pivot_inv, lower_block, upper_block, strip_fields, devices, substeps):
    strips = strip_node.shape[0]
    node_count = pivot_inv.shape[1] * pivot_inv.shape[2]
    _, per_device, cells_y, cells_x = strip_fields.shape
    vmem = pl.BlockSpec(memory_space=pltpu.VMEM)
    return pl.pallas_call(
        lambda *refs: start_kernel(*refs, substeps=substeps),
        in_specs=[pl.BlockSpec(memory_space=pltpu.SMEM)] * 2 + [vmem] * 6,
        out_shape=[
            jax.ShapeDtypeStruct((node_count, strips), jnp.float32),
            jax.ShapeDtypeStruct((per_device, cells_y, cells_x), jnp.float32),
            jax.ShapeDtypeStruct((devices * per_device, 2 * substeps + strips), jnp.float32),
        ],
        name="start_step",
    )(
        riser_owner, strip_riser.reshape(strips), strip_node[None, :], spread_matrix(devices, per_device),
        pivot_inv, lower_block, upper_block, strip_fields,
    )


def second_kernel(received_ref, node_ref, spread_ref, gather_ref, difference_ref, fields_ref, vorticity_ref,
                  out_ref, sent_ref, *, substeps, node_count):
    position = lax.axis_index("strip")
    group_position = lax.axis_index("group")
    total_strips, _ = received_ref.shape
    strips = node_ref.shape[1]
    per_device = fields_ref.shape[1]
    every_force = received_ref[:, 0:2 * substeps]
    offset = jnp.sum(every_force, axis=0, keepdims=True) / jnp.sqrt(jnp.float32(total_strips))
    group_force = received_ref[pl.ds(group_position * strips, strips), 0:2 * substeps]
    my_coupling = jnp.dot(
        gather_ref[...], received_ref[:, 2 * substeps:], precision=EXACT_DOT, preferred_element_type=jnp.float32
    )
    motion = jnp.dot(my_coupling, group_force, precision=EXACT_DOT, preferred_element_type=jnp.float32)
    mine = (
        lax.broadcasted_iota(jnp.int32, (per_device, strips), 1)
        == position * per_device + lax.broadcasted_iota(jnp.int32, (per_device, strips), 0)
    )
    local_node = jnp.sum(jnp.where(mine, node_ref[...].astype(jnp.float32), 0.0), axis=1, keepdims=True)
    local_taper = 1.0 - local_node / node_count
    lane = lax.broadcasted_iota(jnp.int32, (per_device, 2 * substeps), 1)
    sublane = lax.broadcasted_iota(jnp.int32, (per_device, 2 * substeps), 0)
    motion = motion + jnp.where(lane >= substeps, local_taper * offset, 0.0)
    velocity = jnp.dot(motion, difference_ref[...], precision=EXACT_DOT, preferred_element_type=jnp.float32)

    source_x, source_y, lift_kernel, drag_kernel = kernel_planes(fields_ref.shape[-1])
    coupled_x = COUPLING * source_x
    coupled_y = COUPLING * source_y
    rows = jnp.zeros((per_device, 2 * substeps), jnp.float32)
    for strip in range(per_device):
        picks = [velocity[strip:strip + 1, column:column + 1] for column in range(2 * substeps)]

        def forcing_of(substep, picks=picks):
            return picks[substep] * coupled_x - picks[substeps + substep] * coupled_y

        vorticity, row = run_substeps(
            vorticity_ref[strip], fields_ref[1, strip], fields_ref[2, strip], forcing_of,
            lift_kernel, drag_kernel, substeps,
        )
        out_ref[strip] = vorticity
        rows = jnp.where(sublane == strip, row, rows)
    sent_ref[...] = jnp.dot(spread_ref[...], rows, precision=EXACT_DOT, preferred_element_type=jnp.float32)


def difference_matrix(substeps):
    columns = np.arange(2 * substeps)
    same = columns[:, None] == columns[None, :]
    before = (columns[:, None] + 1 == columns[None, :]) & (columns[None, :] % substeps != 0)
    return same.astype(np.float32) - before.astype(np.float32)


def second_step(received, strip_node, strip_fields, vorticity, devices, node_count, substeps):
    _, per_device, cells_y, cells_x = strip_fields.shape
    spread = spread_matrix(devices, per_device)
    vmem = pl.BlockSpec(memory_space=pltpu.VMEM)
    return pl.pallas_call(
        lambda *refs: second_kernel(*refs, substeps=substeps, node_count=node_count),
        in_specs=[vmem] * 7,
        out_shape=[
            jax.ShapeDtypeStruct((per_device, cells_y, cells_x), jnp.float32),
            jax.ShapeDtypeStruct((devices * per_device, 2 * substeps), jnp.float32),
        ],
        name="second_step",
    )(received, strip_node[None, :], spread, np.ascontiguousarray(spread.T), difference_matrix(substeps), strip_fields, vorticity)


def local(strip_fields, strip_riser, strip_node, riser_owner, pivot_inv, lower_block, upper_block):
    position = lax.axis_index("strip")
    group_position = lax.axis_index("group")
    group_count = lax.axis_size("group")
    devices = lax.axis_size("strip") * group_count
    per_device = strip_fields.shape[1]
    grid_cells = strip_fields.shape[2]
    node_count = pivot_inv.shape[1] * pivot_inv.shape[2]
    riser_count = riser_owner.shape[1]
    group_strips = strip_node.shape[0]
    substeps = NSUB
    total_strips = per_device * devices
    top_taper = 1.0 - jnp.arange(node_count, dtype=jnp.float32) / node_count

    unit_response, first_vorticity, first_sent = start_step(
        riser_owner, strip_riser, strip_node, pivot_inv, lower_block, upper_block, strip_fields, devices, substeps
    )

    received = lax.all_to_all(first_sent, ("group", "strip"), 0, 0, tiled=True)
    vorticity, sent = second_step(received, strip_node, strip_fields, first_vorticity, devices, node_count, substeps)
    received = lax.all_to_all(sent, ("group", "strip"), 0, 0, tiled=True)
    offset = jnp.sum(received[:, substeps:], axis=0) / jnp.sqrt(jnp.float32(total_strips))
    group_force = lax.dynamic_slice_in_dim(received, group_position * group_strips, group_strips)
    displacement = lax.dot_general(
        group_force, unit_response, (((0,), (1,)), ((), ())), precision=EXACT_DOT
    )
    displacement = displacement.at[substeps:, :].add(offset[:, None] * top_taper[None, :])
    return (vorticity, displacement[None])


def solution(mesh):
    in_specs = (
        P(None, ("group", "strip"), None, None),
        P("group", None),
        P("group"),
        P("group", None),
        P(("group", "strip"), None, None, None),
        P(("group", "strip"), None, None, None),
        P(("group", "strip"), None, None, None),
    )
    out_specs = (P(("group", "strip"), None, None), P(("group", "strip"), None, None))
    return jax.shard_map(local, mesh=mesh, in_specs=in_specs, out_specs=out_specs, check_vma=False)
```

```python
import numpy as np
import jax
import jax.numpy as jnp
from jax import lax
from jax.sharding import PartitionSpec as P
from jax.experimental import pallas as pl
from jax.experimental.pallas import tpu as pltpu

NSUB = 8
COUPLED = 2


TIME_STEP = 0.25
VISCOSITY = 0.05
COUPLING = 0.5
EXACT_DOT = lax.Precision.HIGHEST


def make_kernels(grid_cells):
    centre = jnp.arange(grid_cells, dtype=jnp.float32) - grid_cells / 2.0 + 0.5
    near_x = (centre / (grid_cells / 16.0))[None, :]
    near_y = (centre / (grid_cells / 16.0))[:, None]
    bell_near = jnp.exp(-(near_x * near_x + near_y * near_y) / 2.0)
    source_x = -near_x * bell_near
    source_y = -near_y * bell_near
    wide_x = (centre / (grid_cells / 8.0))[None, :]
    wide_y = (centre / (grid_cells / 8.0))[:, None]
    bell_wide = jnp.exp(-(wide_x * wide_x + wide_y * wide_y) / 2.0)
    lift_kernel = -wide_x * bell_wide
    drag_kernel = wide_y * bell_wide
    lift_kernel = lift_kernel / jnp.sqrt(jnp.sum(lift_kernel * lift_kernel))
    drag_kernel = drag_kernel / jnp.sqrt(jnp.sum(drag_kernel * drag_kernel))
    return (source_x, source_y, lift_kernel, drag_kernel)


def strip_step(vorticity, flow_x, flow_y, motion, kernels, substeps):
    source_x, source_y, lift_kernel, drag_kernel = kernels
    halves = motion.reshape(motion.shape[0], 2, substeps)
    earlier = jnp.concatenate([jnp.zeros_like(halves[:, :, :1]), halves[:, :, :-1]], axis=2)
    velocity = halves - earlier
    lift_rows = []
    drag_rows = []
    for substep in range(substeps):
        right_cell = jnp.roll(vorticity, -1, axis=2)
        left_cell = jnp.roll(vorticity, 1, axis=2)
        upper_cell = jnp.roll(vorticity, -1, axis=1)
        lower_cell = jnp.roll(vorticity, 1, axis=1)
        laplacian = right_cell + left_cell + upper_cell + lower_cell - 4.0 * vorticity
        tendency = (
            VISCOSITY * laplacian
            - flow_x * (0.5 * (right_cell - left_cell))
            - flow_y * (0.5 * (upper_cell - lower_cell))
        )
        forcing = (
            velocity[:, 0, substep][:, None, None] * source_x
            - velocity[:, 1, substep][:, None, None] * source_y
        )
        vorticity = vorticity + TIME_STEP * tendency + COUPLING * forcing
        lift_rows.append(jnp.sum(vorticity * lift_kernel, axis=(1, 2)))
        drag_rows.append(jnp.sum(vorticity * drag_kernel, axis=(1, 2)))
    return (vorticity, jnp.stack(lift_rows + drag_rows, axis=1))


def kernel_planes(cells):
    centre_x = lax.broadcasted_iota(jnp.int32, (cells, cells), 1).astype(jnp.float32) - cells / 2.0 + 0.5
    centre_y = lax.broadcasted_iota(jnp.int32, (cells, cells), 0).astype(jnp.float32) - cells / 2.0 + 0.5
    near_x = centre_x / (cells / 16.0)
    near_y = centre_y / (cells / 16.0)
    bell_near = jnp.exp(-(near_x * near_x + near_y * near_y) / 2.0)
    source_x = -near_x * bell_near
    source_y = -near_y * bell_near
    wide_x = centre_x / (cells / 8.0)
    wide_y = centre_y / (cells / 8.0)
    bell_wide = jnp.exp(-(wide_x * wide_x + wide_y * wide_y) / 2.0)
    lift_kernel = -wide_x * bell_wide
    drag_kernel = wide_y * bell_wide

    def total(plane):
        return jnp.sum(jnp.sum(plane, axis=0, keepdims=True), axis=1, keepdims=True)

    lift_kernel = lift_kernel / jnp.sqrt(total(lift_kernel * lift_kernel))
    drag_kernel = drag_kernel / jnp.sqrt(total(drag_kernel * drag_kernel))
    return (source_x, source_y, lift_kernel, drag_kernel)


def run_substeps(vorticity, flow_x, flow_y, forcing_of, lift_kernel, drag_kernel, substeps):
    rows_across, cols_across = vorticity.shape
    lane = lax.broadcasted_iota(jnp.int32, (1, 2 * substeps), 1)
    row = jnp.zeros((1, 2 * substeps), jnp.float32)
    along_x = (TIME_STEP * 0.5) * flow_x
    along_y = (TIME_STEP * 0.5) * flow_y
    for substep in range(substeps):
        right_cell = pltpu.roll(vorticity, cols_across - 1, 1)
        left_cell = pltpu.roll(vorticity, 1, 1)
        upper_cell = pltpu.roll(vorticity, rows_across - 1, 0)
        lower_cell = pltpu.roll(vorticity, 1, 0)
        laplacian = (right_cell + left_cell) + (upper_cell + lower_cell) - 4.0 * vorticity
        step = (
            (TIME_STEP * VISCOSITY) * laplacian
            - along_x * (right_cell - left_cell)
            - along_y * (upper_cell - lower_cell)
        )
        if forcing_of is None:
            vorticity = vorticity + step
        else:
            vorticity = vorticity + step + forcing_of(substep)
        lift = jnp.sum(jnp.sum(vorticity * lift_kernel, axis=0, keepdims=True), axis=1, keepdims=True)
        drag = jnp.sum(jnp.sum(vorticity * drag_kernel, axis=0, keepdims=True), axis=1, keepdims=True)
        row = row + jnp.where(lane == substep, lift, 0.0) + jnp.where(lane == substeps + substep, drag, 0.0)
    return vorticity, row


def stencil_kernel(velocity_ref, vorticity_ref, flow_x_ref, flow_y_ref, out_ref, rows_ref, *, substeps):
    strip = pl.program_id(0)
    source_x, source_y, lift_kernel, drag_kernel = kernel_planes(vorticity_ref.shape[-1])

    def forcing_of(substep):
        return COUPLING * (
            velocity_ref[strip, substep] * source_x
            - velocity_ref[strip, substeps + substep] * source_y
        )

    vorticity, row = run_substeps(
        vorticity_ref[0, 0], flow_x_ref[0, 0], flow_y_ref[0, 0], forcing_of,
        lift_kernel, drag_kernel, substeps,
    )
    out_ref[0] = vorticity
    rows_ref[0] = row


def strip_step_kernel(strip_fields, vorticity, motion, kernels, substeps):
    strips, cells_y, cells_x = strip_fields.shape[1:]
    halves = motion.reshape(strips, 2, substeps)
    earlier = jnp.concatenate([jnp.zeros_like(halves[:, :, :1]), halves[:, :, :-1]], axis=2)
    velocity = (halves - earlier).reshape(strips, 2 * substeps)
    def field(index):
        return pl.BlockSpec((1, 1, cells_y, cells_x), lambda s: (index, s, 0, 0))

    new_vorticity, rows = pl.pallas_call(
        lambda *refs: stencil_kernel(*refs, substeps=substeps),
        grid=(strips,),
        in_specs=[
            pl.BlockSpec(memory_space=pltpu.SMEM),
            field(0), field(1), field(2),
        ],
        out_specs=[
            pl.BlockSpec((1, cells_y, cells_x), lambda s: (s, 0, 0)),
            pl.BlockSpec((1, 1, 2 * substeps), lambda s: (s, 0, 0)),
        ],
        out_shape=[
            jax.ShapeDtypeStruct((strips, cells_y, cells_x), jnp.float32),
            jax.ShapeDtypeStruct((strips, 1, 2 * substeps), jnp.float32),
        ],
        name="strip_stencil",
    )(velocity, vorticity, strip_fields, strip_fields)
    return new_vorticity, rows[:, 0, :]


def apply_block(vectors, matrix):
    return lax.dot_general(vectors, matrix, (((1,), (1,)), ((), ())), precision=EXACT_DOT)


def first_contract(left_side, right_side):
    return lax.dot_general(left_side, right_side, (((0,), (0,)), ((), ())), precision=EXACT_DOT)


def beam_solve(beam_load, pivot_inv, lower_block, upper_block):
    block_count = pivot_inv.shape[0]
    block_size = pivot_inv.shape[1]
    blocks = beam_load.reshape(beam_load.shape[0], block_count, block_size)
    carried = [blocks[:, 0]]
    for block_index in range(1, block_count):
        pivoted = apply_block(carried[-1], pivot_inv[block_index - 1])
        carried.append(blocks[:, block_index] - apply_block(pivoted, lower_block[block_index - 1]))
    solved = [apply_block(carried[-1], pivot_inv[block_count - 1])]
    for block_index in range(block_count - 2, -1, -1):
        remainder = carried[block_index] - apply_block(solved[0], upper_block[block_index])
        solved.insert(0, apply_block(remainder, pivot_inv[block_index]))
    return jnp.concatenate(solved, axis=1)


def start_kernel(owner_ref, riser_ref, node_ref, spread_ref, pivot_ref, lower_ref, upper_ref, fields_ref,
                 response_ref, vorticity_ref, sent_ref, *, substeps):
    block_count = pivot_ref.shape[1]
    block_size = pivot_ref.shape[2]
    node_count = block_count * block_size
    strips = node_ref.shape[1]
    per_device = fields_ref.shape[1]
    position = lax.axis_index("strip")
    group_position = lax.axis_index("group")

    strip_lane = lax.broadcasted_iota(jnp.int32, (1, strips), 1)
    strip_sublane = lax.broadcasted_iota(jnp.int32, (strips, 1), 0)
    owned_row = jnp.zeros((1, strips), jnp.float32)
    owned_col = jnp.zeros((strips, 1), jnp.float32)
    for strip in range(strips):
        held = jnp.where(owner_ref[0, riser_ref[strip]] == position, 1.0, 0.0)
        owned_row = jnp.where(strip_lane == strip, held, owned_row)
        owned_col = jnp.where(strip_sublane == strip, held, owned_col)
    diagonal = lax.broadcasted_iota(jnp.int32, (strips, strips), 0) == lax.broadcasted_iota(jnp.int32, (strips, strips), 1)
    node_row = node_ref[...]
    node_col = jnp.sum(jnp.where(diagonal, node_row.astype(jnp.float32), 0.0), axis=1, keepdims=True)

    def apply(matrix, vectors):
        return jnp.dot(matrix, vectors, precision=lax.Precision.HIGH, preferred_element_type=jnp.float32)

    def unit_load(block_index):
        node = block_index * block_size + lax.broadcasted_iota(jnp.int32, (block_size, strips), 0)
        return (node == node_row).astype(jnp.float32) * owned_row

    def product(left, right):
        return jnp.dot(left, right, precision=lax.Precision.HIGH, preferred_element_type=jnp.float32)

    forward = [None] + [product(lower_ref[0, i - 1], pivot_ref[0, i - 1]) for i in range(1, block_count)]
    backward = [product(pivot_ref[0, i], upper_ref[0, i]) for i in range(block_count - 1)]
    carried = [unit_load(0)]
    for block_index in range(1, block_count):
        carried.append(unit_load(block_index) - apply(forward[block_index], carried[-1]))
    pivoted = [apply(pivot_ref[0, i], carried[i]) for i in range(block_count)]
    solved = pivoted[block_count - 1]
    response_ref[(block_count - 1) * block_size:, :] = solved
    for block_index in range(block_count - 2, -1, -1):
        solved = pivoted[block_index] - apply(backward[block_index], solved)
        response_ref[block_index * block_size:(block_index + 1) * block_size, :] = solved

    _, _, lift_kernel, drag_kernel = kernel_planes(fields_ref.shape[-1])
    strip_of_row = lax.broadcasted_iota(jnp.int32, (per_device, 2 * substeps), 0)
    rows = jnp.zeros((per_device, 2 * substeps), jnp.float32)
    for strip in range(per_device):
        vorticity, row = run_substeps(
            fields_ref[0, strip], fields_ref[1, strip], fields_ref[2, strip], None,
            lift_kernel, drag_kernel, substeps,
        )
        vorticity_ref[strip] = vorticity
        rows = jnp.where(strip_of_row == strip, row, rows)

    node_onehot = (
        node_col == lax.broadcasted_iota(jnp.int32, (strips, node_count), 1).astype(jnp.float32)
    ).astype(jnp.float32)
    coupling = jnp.dot(node_onehot, response_ref[...], precision=lax.Precision.HIGH, preferred_element_type=jnp.float32)
    coupling = coupling * owned_col
    sent_rows = sent_ref.shape[0]
    place = lax.broadcasted_iota(jnp.int32, (sent_rows, strips), 0) - group_position * strips
    pick = (place == lax.broadcasted_iota(jnp.int32, (sent_rows, strips), 1)).astype(jnp.float32)
    sent_ref[:, 0:2 * substeps] = jnp.dot(spread_ref[...], rows, precision=lax.Precision.HIGH, preferred_element_type=jnp.float32)
    sent_ref[:, 2 * substeps:] = jnp.dot(pick, coupling, precision=lax.Precision.HIGH, preferred_element_type=jnp.float32)


def spread_matrix(devices, per_device):
    return (
        np.arange(devices * per_device)[:, None] % per_device == np.arange(per_device)[None, :]
    ).astype(np.float32)


def start_step(riser_owner, strip_riser, strip_node, pivot_inv, lower_block, upper_block, strip_fields, devices, substeps):
    strips = strip_node.shape[0]
    node_count = pivot_inv.shape[1] * pivot_inv.shape[2]
    _, per_device, cells_y, cells_x = strip_fields.shape
    vmem = pl.BlockSpec(memory_space=pltpu.VMEM)
    return pl.pallas_call(
        lambda *refs: start_kernel(*refs, substeps=substeps),
        in_specs=[pl.BlockSpec(memory_space=pltpu.SMEM)] * 2 + [vmem] * 6,
        out_shape=[
            jax.ShapeDtypeStruct((node_count, strips), jnp.float32),
            jax.ShapeDtypeStruct((per_device, cells_y, cells_x), jnp.float32),
            jax.ShapeDtypeStruct((devices * per_device, 2 * substeps + strips), jnp.float32),
        ],
        name="start_step",
    )(
        riser_owner, strip_riser.reshape(strips), strip_node[None, :], spread_matrix(devices, per_device),
        pivot_inv, lower_block, upper_block, strip_fields,
    )


def second_kernel(received_ref, node_ref, spread_ref, gather_ref, difference_ref, fields_ref, vorticity_ref,
                  out_ref, sent_ref, *, substeps, node_count):
    position = lax.axis_index("strip")
    group_position = lax.axis_index("group")
    total_strips, _ = received_ref.shape
    strips = node_ref.shape[1]
    per_device = fields_ref.shape[1]
    every_force = received_ref[:, 0:2 * substeps]
    offset = jnp.sum(every_force, axis=0, keepdims=True) / jnp.sqrt(jnp.float32(total_strips))
    group_force = received_ref[pl.ds(group_position * strips, strips), 0:2 * substeps]
    my_coupling = jnp.dot(
        gather_ref[...], received_ref[:, 2 * substeps:], precision=lax.Precision.HIGH, preferred_element_type=jnp.float32
    )
    motion = jnp.dot(my_coupling, group_force, precision=lax.Precision.HIGH, preferred_element_type=jnp.float32)
    mine = (
        lax.broadcasted_iota(jnp.int32, (per_device, strips), 1)
        == position * per_device + lax.broadcasted_iota(jnp.int32, (per_device, strips), 0)
    )
    local_node = jnp.sum(jnp.where(mine, node_ref[...].astype(jnp.float32), 0.0), axis=1, keepdims=True)
    local_taper = 1.0 - local_node / node_count
    lane = lax.broadcasted_iota(jnp.int32, (per_device, 2 * substeps), 1)
    sublane = lax.broadcasted_iota(jnp.int32, (per_device, 2 * substeps), 0)
    motion = motion + jnp.where(lane >= substeps, local_taper * offset, 0.0)
    velocity = jnp.dot(motion, difference_ref[...], precision=EXACT_DOT, preferred_element_type=jnp.float32)

    source_x, source_y, lift_kernel, drag_kernel = kernel_planes(fields_ref.shape[-1])
    coupled_x = COUPLING * source_x
    coupled_y = COUPLING * source_y
    rows = jnp.zeros((per_device, 2 * substeps), jnp.float32)
    for strip in range(per_device):
        picks = [
            jnp.sum(jnp.sum(jnp.where((sublane == strip) & (lane == column), velocity, 0.0), axis=0, keepdims=True), axis=1, keepdims=True)
            for column in range(2 * substeps)
        ]

        def forcing_of(substep, picks=picks):
            return picks[substep] * coupled_x - picks[substeps + substep] * coupled_y

        vorticity, row = run_substeps(
            vorticity_ref[strip], fields_ref[1, strip], fields_ref[2, strip], forcing_of,
            lift_kernel, drag_kernel, substeps,
        )
        out_ref[strip] = vorticity
        rows = jnp.where(sublane == strip, row, rows)
    sent_ref[...] = jnp.dot(spread_ref[...], rows, precision=lax.Precision.HIGH, preferred_element_type=jnp.float32)


def difference_matrix(substeps):
    columns = np.arange(2 * substeps)
    same = columns[:, None] == columns[None, :]
    before = (columns[:, None] + 1 == columns[None, :]) & (columns[None, :] % substeps != 0)
    return same.astype(np.float32) - before.astype(np.float32)


def second_step(received, strip_node, strip_fields, vorticity, devices, node_count, substeps):
    _, per_device, cells_y, cells_x = strip_fields.shape
    spread = spread_matrix(devices, per_device)
    vmem = pl.BlockSpec(memory_space=pltpu.VMEM)
    return pl.pallas_call(
        lambda *refs: second_kernel(*refs, substeps=substeps, node_count=node_count),
        in_specs=[vmem] * 7,
        out_shape=[
            jax.ShapeDtypeStruct((per_device, cells_y, cells_x), jnp.float32),
            jax.ShapeDtypeStruct((devices * per_device, 2 * substeps), jnp.float32),
        ],
        name="second_step",
    )(received, strip_node[None, :], spread, np.ascontiguousarray(spread.T), difference_matrix(substeps), strip_fields, vorticity)


def local(strip_fields, strip_riser, strip_node, riser_owner, pivot_inv, lower_block, upper_block):
    position = lax.axis_index("strip")
    group_position = lax.axis_index("group")
    group_count = lax.axis_size("group")
    devices = lax.axis_size("strip") * group_count
    per_device = strip_fields.shape[1]
    grid_cells = strip_fields.shape[2]
    node_count = pivot_inv.shape[1] * pivot_inv.shape[2]
    riser_count = riser_owner.shape[1]
    group_strips = strip_node.shape[0]
    substeps = NSUB
    total_strips = per_device * devices
    top_taper = 1.0 - jnp.arange(node_count, dtype=jnp.float32) / node_count

    unit_response, first_vorticity, first_sent = start_step(
        riser_owner, strip_riser, strip_node, pivot_inv, lower_block, upper_block, strip_fields, devices, substeps
    )

    received = lax.all_to_all(first_sent, ("group", "strip"), 0, 0, tiled=True)
    vorticity, sent = second_step(received, strip_node, strip_fields, first_vorticity, devices, node_count, substeps)
    received = lax.all_to_all(sent, ("group", "strip"), 0, 0, tiled=True)
    offset = jnp.sum(received[:, substeps:], axis=0) / jnp.sqrt(jnp.float32(total_strips))
    group_force = lax.dynamic_slice_in_dim(received, group_position * group_strips, group_strips)
    displacement = lax.dot_general(
        group_force, unit_response, (((0,), (1,)), ((), ())), precision=EXACT_DOT
    )
    displacement = displacement.at[substeps:, :].add(offset[:, None] * top_taper[None, :])
    return (vorticity, displacement[None])


def solution(mesh):
    in_specs = (
        P(None, ("group", "strip"), None, None),
        P("group", None),
        P("group"),
        P("group", None),
        P(("group", "strip"), None, None, None),
        P(("group", "strip"), None, None, None),
        P(("group", "strip"), None, None, None),
    )
    out_specs = (P(("group", "strip"), None, None), P(("group", "strip"), None, None))
    return jax.shard_map(local, mesh=mesh, in_specs=in_specs, out_specs=out_specs, check_vma=False)
```

```python
import numpy as np
import jax
import jax.numpy as jnp
from jax import lax
from jax.sharding import PartitionSpec as P
from jax.experimental import pallas as pl
from jax.experimental.pallas import tpu as pltpu

NSUB = 8
COUPLED = 2


TIME_STEP = 0.25
VISCOSITY = 0.05
COUPLING = 0.5
EXACT_DOT = lax.Precision.HIGHEST


def make_kernels(grid_cells):
    centre = jnp.arange(grid_cells, dtype=jnp.float32) - grid_cells / 2.0 + 0.5
    near_x = (centre / (grid_cells / 16.0))[None, :]
    near_y = (centre / (grid_cells / 16.0))[:, None]
    bell_near = jnp.exp(-(near_x * near_x + near_y * near_y) / 2.0)
    source_x = -near_x * bell_near
    source_y = -near_y * bell_near
    wide_x = (centre / (grid_cells / 8.0))[None, :]
    wide_y = (centre / (grid_cells / 8.0))[:, None]
    bell_wide = jnp.exp(-(wide_x * wide_x + wide_y * wide_y) / 2.0)
    lift_kernel = -wide_x * bell_wide
    drag_kernel = wide_y * bell_wide
    lift_kernel = lift_kernel / jnp.sqrt(jnp.sum(lift_kernel * lift_kernel))
    drag_kernel = drag_kernel / jnp.sqrt(jnp.sum(drag_kernel * drag_kernel))
    return (source_x, source_y, lift_kernel, drag_kernel)


def strip_step(vorticity, flow_x, flow_y, motion, kernels, substeps):
    source_x, source_y, lift_kernel, drag_kernel = kernels
    halves = motion.reshape(motion.shape[0], 2, substeps)
    earlier = jnp.concatenate([jnp.zeros_like(halves[:, :, :1]), halves[:, :, :-1]], axis=2)
    velocity = halves - earlier
    lift_rows = []
    drag_rows = []
    for substep in range(substeps):
        right_cell = jnp.roll(vorticity, -1, axis=2)
        left_cell = jnp.roll(vorticity, 1, axis=2)
        upper_cell = jnp.roll(vorticity, -1, axis=1)
        lower_cell = jnp.roll(vorticity, 1, axis=1)
        laplacian = right_cell + left_cell + upper_cell + lower_cell - 4.0 * vorticity
        tendency = (
            VISCOSITY * laplacian
            - flow_x * (0.5 * (right_cell - left_cell))
            - flow_y * (0.5 * (upper_cell - lower_cell))
        )
        forcing = (
            velocity[:, 0, substep][:, None, None] * source_x
            - velocity[:, 1, substep][:, None, None] * source_y
        )
        vorticity = vorticity + TIME_STEP * tendency + COUPLING * forcing
        lift_rows.append(jnp.sum(vorticity * lift_kernel, axis=(1, 2)))
        drag_rows.append(jnp.sum(vorticity * drag_kernel, axis=(1, 2)))
    return (vorticity, jnp.stack(lift_rows + drag_rows, axis=1))


def kernel_planes(cells):
    centre_x = lax.broadcasted_iota(jnp.int32, (cells, cells), 1).astype(jnp.float32) - cells / 2.0 + 0.5
    centre_y = lax.broadcasted_iota(jnp.int32, (cells, cells), 0).astype(jnp.float32) - cells / 2.0 + 0.5
    near_x = centre_x / (cells / 16.0)
    near_y = centre_y / (cells / 16.0)
    bell_near = jnp.exp(-(near_x * near_x + near_y * near_y) / 2.0)
    source_x = -near_x * bell_near
    source_y = -near_y * bell_near
    wide_x = centre_x / (cells / 8.0)
    wide_y = centre_y / (cells / 8.0)
    bell_wide = jnp.exp(-(wide_x * wide_x + wide_y * wide_y) / 2.0)
    lift_kernel = -wide_x * bell_wide
    drag_kernel = wide_y * bell_wide

    def total(plane):
        return jnp.sum(jnp.sum(plane, axis=0, keepdims=True), axis=1, keepdims=True)

    lift_kernel = lift_kernel / jnp.sqrt(total(lift_kernel * lift_kernel))
    drag_kernel = drag_kernel / jnp.sqrt(total(drag_kernel * drag_kernel))
    return (source_x, source_y, lift_kernel, drag_kernel)


def run_substeps(vorticity, flow_x, flow_y, forcing_of, lift_kernel, drag_kernel, substeps):
    rows_across, cols_across = vorticity.shape
    lane = lax.broadcasted_iota(jnp.int32, (1, 2 * substeps), 1)
    row = jnp.zeros((1, 2 * substeps), jnp.float32)
    along_x = (TIME_STEP * 0.5) * flow_x
    along_y = (TIME_STEP * 0.5) * flow_y
    for substep in range(substeps):
        right_cell = pltpu.roll(vorticity, cols_across - 1, 1)
        left_cell = pltpu.roll(vorticity, 1, 1)
        upper_cell = pltpu.roll(vorticity, rows_across - 1, 0)
        lower_cell = pltpu.roll(vorticity, 1, 0)
        laplacian = (right_cell + left_cell) + (upper_cell + lower_cell) - 4.0 * vorticity
        step = (
            (TIME_STEP * VISCOSITY) * laplacian
            - along_x * (right_cell - left_cell)
            - along_y * (upper_cell - lower_cell)
        )
        if forcing_of is None:
            vorticity = vorticity + step
        else:
            vorticity = vorticity + step + forcing_of(substep)
        lift = jnp.sum(jnp.sum(vorticity * lift_kernel, axis=0, keepdims=True), axis=1, keepdims=True)
        drag = jnp.sum(jnp.sum(vorticity * drag_kernel, axis=0, keepdims=True), axis=1, keepdims=True)
        row = row + jnp.where(lane == substep, lift, 0.0) + jnp.where(lane == substeps + substep, drag, 0.0)
    return vorticity, row


def stencil_kernel(velocity_ref, vorticity_ref, flow_x_ref, flow_y_ref, out_ref, rows_ref, *, substeps):
    strip = pl.program_id(0)
    source_x, source_y, lift_kernel, drag_kernel = kernel_planes(vorticity_ref.shape[-1])

    def forcing_of(substep):
        return COUPLING * (
            velocity_ref[strip, substep] * source_x
            - velocity_ref[strip, substeps + substep] * source_y
        )

    vorticity, row = run_substeps(
        vorticity_ref[0, 0], flow_x_ref[0, 0], flow_y_ref[0, 0], forcing_of,
        lift_kernel, drag_kernel, substeps,
    )
    out_ref[0] = vorticity
    rows_ref[0] = row


def strip_step_kernel(strip_fields, vorticity, motion, kernels, substeps):
    strips, cells_y, cells_x = strip_fields.shape[1:]
    halves = motion.reshape(strips, 2, substeps)
    earlier = jnp.concatenate([jnp.zeros_like(halves[:, :, :1]), halves[:, :, :-1]], axis=2)
    velocity = (halves - earlier).reshape(strips, 2 * substeps)
    def field(index):
        return pl.BlockSpec((1, 1, cells_y, cells_x), lambda s: (index, s, 0, 0))

    new_vorticity, rows = pl.pallas_call(
        lambda *refs: stencil_kernel(*refs, substeps=substeps),
        grid=(strips,),
        in_specs=[
            pl.BlockSpec(memory_space=pltpu.SMEM),
            field(0), field(1), field(2),
        ],
        out_specs=[
            pl.BlockSpec((1, cells_y, cells_x), lambda s: (s, 0, 0)),
            pl.BlockSpec((1, 1, 2 * substeps), lambda s: (s, 0, 0)),
        ],
        out_shape=[
            jax.ShapeDtypeStruct((strips, cells_y, cells_x), jnp.float32),
            jax.ShapeDtypeStruct((strips, 1, 2 * substeps), jnp.float32),
        ],
        name="strip_stencil",
    )(velocity, vorticity, strip_fields, strip_fields)
    return new_vorticity, rows[:, 0, :]


def apply_block(vectors, matrix):
    return lax.dot_general(vectors, matrix, (((1,), (1,)), ((), ())), precision=EXACT_DOT)


def first_contract(left_side, right_side):
    return lax.dot_general(left_side, right_side, (((0,), (0,)), ((), ())), precision=EXACT_DOT)


def beam_solve(beam_load, pivot_inv, lower_block, upper_block):
    block_count = pivot_inv.shape[0]
    block_size = pivot_inv.shape[1]
    blocks = beam_load.reshape(beam_load.shape[0], block_count, block_size)
    carried = [blocks[:, 0]]
    for block_index in range(1, block_count):
        pivoted = apply_block(carried[-1], pivot_inv[block_index - 1])
        carried.append(blocks[:, block_index] - apply_block(pivoted, lower_block[block_index - 1]))
    solved = [apply_block(carried[-1], pivot_inv[block_count - 1])]
    for block_index in range(block_count - 2, -1, -1):
        remainder = carried[block_index] - apply_block(solved[0], upper_block[block_index])
        solved.insert(0, apply_block(remainder, pivot_inv[block_index]))
    return jnp.concatenate(solved, axis=1)


def start_kernel(owner_ref, riser_ref, node_ref, spread_ref, pivot_ref, lower_ref, upper_ref, fields_ref,
                 response_ref, vorticity_ref, sent_ref, *, substeps):
    block_count = pivot_ref.shape[1]
    block_size = pivot_ref.shape[2]
    node_count = block_count * block_size
    strips = node_ref.shape[1]
    per_device = fields_ref.shape[1]
    position = lax.axis_index("strip")
    group_position = lax.axis_index("group")

    strip_lane = lax.broadcasted_iota(jnp.int32, (1, strips), 1)
    strip_sublane = lax.broadcasted_iota(jnp.int32, (strips, 1), 0)
    owned_row = jnp.zeros((1, strips), jnp.float32)
    owned_col = jnp.zeros((strips, 1), jnp.float32)
    for strip in range(strips):
        held = jnp.where(owner_ref[0, riser_ref[strip]] == position, 1.0, 0.0)
        owned_row = jnp.where(strip_lane == strip, held, owned_row)
        owned_col = jnp.where(strip_sublane == strip, held, owned_col)
    diagonal = lax.broadcasted_iota(jnp.int32, (strips, strips), 0) == lax.broadcasted_iota(jnp.int32, (strips, strips), 1)
    node_row = node_ref[...]
    node_col = jnp.sum(jnp.where(diagonal, node_row.astype(jnp.float32), 0.0), axis=1, keepdims=True)

    def apply(matrix, vectors):
        return jnp.dot(matrix, vectors, precision=lax.Precision.HIGH, preferred_element_type=jnp.float32)

    def unit_load(block_index):
        node = block_index * block_size + lax.broadcasted_iota(jnp.int32, (block_size, strips), 0)
        return (node == node_row).astype(jnp.float32) * owned_row

    def product(left, right):
        return jnp.dot(left, right, precision=lax.Precision.HIGH, preferred_element_type=jnp.float32)

    forward = [None] + [product(lower_ref[0, i - 1], pivot_ref[0, i - 1]) for i in range(1, block_count)]
    backward = [product(pivot_ref[0, i], upper_ref[0, i]) for i in range(block_count - 1)]
    carried = [unit_load(0)]
    for block_index in range(1, block_count):
        carried.append(unit_load(block_index) - apply(forward[block_index], carried[-1]))
    pivoted = [apply(pivot_ref[0, i], carried[i]) for i in range(block_count)]
    solved = pivoted[block_count - 1]
    response_ref[(block_count - 1) * block_size:, :] = solved
    for block_index in range(block_count - 2, -1, -1):
        solved = pivoted[block_index] - apply(backward[block_index], solved)
        response_ref[block_index * block_size:(block_index + 1) * block_size, :] = solved

    _, _, lift_kernel, drag_kernel = kernel_planes(fields_ref.shape[-1])
    strip_of_row = lax.broadcasted_iota(jnp.int32, (per_device, 2 * substeps), 0)
    rows = jnp.zeros((per_device, 2 * substeps), jnp.float32)
    for strip in range(per_device):
        vorticity, row = run_substeps(
            fields_ref[0, strip], fields_ref[1, strip], fields_ref[2, strip], None,
            lift_kernel, drag_kernel, substeps,
        )
        vorticity_ref[strip] = vorticity
        rows = jnp.where(strip_of_row == strip, row, rows)

    node_onehot = (
        node_col == lax.broadcasted_iota(jnp.int32, (strips, node_count), 1).astype(jnp.float32)
    ).astype(jnp.float32)
    coupling = jnp.dot(node_onehot, response_ref[...], precision=EXACT_DOT, preferred_element_type=jnp.float32)
    coupling = coupling * owned_col
    sent_rows = sent_ref.shape[0]
    place = lax.broadcasted_iota(jnp.int32, (sent_rows, strips), 0) - group_position * strips
    pick = (place == lax.broadcasted_iota(jnp.int32, (sent_rows, strips), 1)).astype(jnp.float32)
    sent_ref[:, 0:2 * substeps] = jnp.dot(spread_ref[...], rows, precision=EXACT_DOT, preferred_element_type=jnp.float32)
    sent_ref[:, 2 * substeps:] = jnp.dot(pick, coupling, precision=EXACT_DOT, preferred_element_type=jnp.float32)


def spread_matrix(devices, per_device):
    return (
        np.arange(devices * per_device)[:, None] % per_device == np.arange(per_device)[None, :]
    ).astype(np.float32)


def start_step(riser_owner, strip_riser, strip_node, pivot_inv, lower_block, upper_block, strip_fields, devices, substeps):
    strips = strip_node.shape[0]
    node_count = pivot_inv.shape[1] * pivot_inv.shape[2]
    _, per_device, cells_y, cells_x = strip_fields.shape
    vmem = pl.BlockSpec(memory_space=pltpu.VMEM)
    return pl.pallas_call(
        lambda *refs: start_kernel(*refs, substeps=substeps),
        in_specs=[pl.BlockSpec(memory_space=pltpu.SMEM)] * 2 + [vmem] * 6,
        out_shape=[
            jax.ShapeDtypeStruct((node_count, strips), jnp.float32),
            jax.ShapeDtypeStruct((per_device, cells_y, cells_x), jnp.float32),
            jax.ShapeDtypeStruct((devices * per_device, 2 * substeps + strips), jnp.float32),
        ],
        name="start_step",
    )(
        riser_owner, strip_riser.reshape(strips), strip_node[None, :], spread_matrix(devices, per_device),
        pivot_inv, lower_block, upper_block, strip_fields,
    )


def second_kernel(received_ref, node_ref, spread_ref, gather_ref, difference_ref, fields_ref, vorticity_ref,
                  out_ref, sent_ref, *, substeps, node_count):
    position = lax.axis_index("strip")
    group_position = lax.axis_index("group")
    total_strips, _ = received_ref.shape
    strips = node_ref.shape[1]
    per_device = fields_ref.shape[1]
    every_force = received_ref[:, 0:2 * substeps]
    offset = jnp.sum(every_force, axis=0, keepdims=True) / jnp.sqrt(jnp.float32(total_strips))
    group_force = received_ref[pl.ds(group_position * strips, strips), 0:2 * substeps]
    my_coupling = jnp.dot(
        gather_ref[...], received_ref[:, 2 * substeps:], precision=EXACT_DOT, preferred_element_type=jnp.float32
    )
    motion = jnp.dot(my_coupling, group_force, precision=EXACT_DOT, preferred_element_type=jnp.float32)
    mine = (
        lax.broadcasted_iota(jnp.int32, (per_device, strips), 1)
        == position * per_device + lax.broadcasted_iota(jnp.int32, (per_device, strips), 0)
    )
    local_node = jnp.sum(jnp.where(mine, node_ref[...].astype(jnp.float32), 0.0), axis=1, keepdims=True)
    local_taper = 1.0 - local_node / node_count
    lane = lax.broadcasted_iota(jnp.int32, (per_device, 2 * substeps), 1)
    sublane = lax.broadcasted_iota(jnp.int32, (per_device, 2 * substeps), 0)
    motion = motion + jnp.where(lane >= substeps, local_taper * offset, 0.0)
    velocity = jnp.dot(motion, difference_ref[...], precision=EXACT_DOT, preferred_element_type=jnp.float32)

    source_x, source_y, lift_kernel, drag_kernel = kernel_planes(fields_ref.shape[-1])
    coupled_x = COUPLING * source_x
    coupled_y = COUPLING * source_y
    rows = jnp.zeros((per_device, 2 * substeps), jnp.float32)
    for strip in range(per_device):
        picks = [
            jnp.sum(jnp.sum(jnp.where((sublane == strip) & (lane == column), velocity, 0.0), axis=0, keepdims=True), axis=1, keepdims=True)
            for column in range(2 * substeps)
        ]

        def forcing_of(substep, picks=picks):
            return picks[substep] * coupled_x - picks[substeps + substep] * coupled_y

        vorticity, row = run_substeps(
            vorticity_ref[strip], fields_ref[1, strip], fields_ref[2, strip], forcing_of,
            lift_kernel, drag_kernel, substeps,
        )
        out_ref[strip] = vorticity
        rows = jnp.where(sublane == strip, row, rows)
    sent_ref[...] = jnp.dot(spread_ref[...], rows, precision=EXACT_DOT, preferred_element_type=jnp.float32)


def difference_matrix(substeps):
    columns = np.arange(2 * substeps)
    same = columns[:, None] == columns[None, :]
    before = (columns[:, None] + 1 == columns[None, :]) & (columns[None, :] % substeps != 0)
    return same.astype(np.float32) - before.astype(np.float32)


def second_step(received, strip_node, strip_fields, vorticity, devices, node_count, substeps):
    _, per_device, cells_y, cells_x = strip_fields.shape
    spread = spread_matrix(devices, per_device)
    vmem = pl.BlockSpec(memory_space=pltpu.VMEM)
    return pl.pallas_call(
        lambda *refs: second_kernel(*refs, substeps=substeps, node_count=node_count),
        in_specs=[vmem] * 7,
        out_shape=[
            jax.ShapeDtypeStruct((per_device, cells_y, cells_x), jnp.float32),
            jax.ShapeDtypeStruct((devices * per_device, 2 * substeps), jnp.float32),
        ],
        name="second_step",
    )(received, strip_node[None, :], spread, np.ascontiguousarray(spread.T), difference_matrix(substeps), strip_fields, vorticity)


def local(strip_fields, strip_riser, strip_node, riser_owner, pivot_inv, lower_block, upper_block):
    position = lax.axis_index("strip")
    group_position = lax.axis_index("group")
    group_count = lax.axis_size("group")
    devices = lax.axis_size("strip") * group_count
    per_device = strip_fields.shape[1]
    grid_cells = strip_fields.shape[2]
    node_count = pivot_inv.shape[1] * pivot_inv.shape[2]
    riser_count = riser_owner.shape[1]
    group_strips = strip_node.shape[0]
    substeps = NSUB
    total_strips = per_device * devices
    top_taper = 1.0 - jnp.arange(node_count, dtype=jnp.float32) / node_count

    unit_response, first_vorticity, first_sent = start_step(
        riser_owner, strip_riser, strip_node, pivot_inv, lower_block, upper_block, strip_fields, devices, substeps
    )

    received = lax.all_to_all(first_sent, ("group", "strip"), 0, 0, tiled=True)
    vorticity, sent = second_step(received, strip_node, strip_fields, first_vorticity, devices, node_count, substeps)
    received = lax.all_to_all(sent, ("group", "strip"), 0, 0, tiled=True)
    offset = jnp.sum(received, axis=0) / jnp.sqrt(jnp.float32(total_strips))
    group_force = lax.dynamic_slice_in_dim(received, group_position * group_strips, group_strips)
    displacement = lax.dot_general(
        group_force, unit_response, (((0,), (1,)), ((), ())), precision=EXACT_DOT
    )
    lower_half = (jnp.arange(2 * substeps) >= substeps)[:, None]
    displacement = displacement + jnp.where(lower_half, offset[:, None] * top_taper[None, :], 0.0)
    return (vorticity, displacement[None])


def solution(mesh):
    in_specs = (
        P(None, ("group", "strip"), None, None),
        P("group", None),
        P("group"),
        P("group", None),
        P(("group", "strip"), None, None, None),
        P(("group", "strip"), None, None, None),
        P(("group", "strip"), None, None, None),
    )
    out_specs = (P(("group", "strip"), None, None), P(("group", "strip"), None, None))
    return jax.shard_map(local, mesh=mesh, in_specs=in_specs, out_specs=out_specs, check_vma=False)
```

```python
import numpy as np
import jax
import jax.numpy as jnp
from jax import lax
from jax.sharding import PartitionSpec as P
from jax.experimental import pallas as pl
from jax.experimental.pallas import tpu as pltpu

NSUB = 8
COUPLED = 2


TIME_STEP = 0.25
VISCOSITY = 0.05
COUPLING = 0.5
EXACT_DOT = lax.Precision.HIGHEST


def make_kernels(grid_cells):
    centre = jnp.arange(grid_cells, dtype=jnp.float32) - grid_cells / 2.0 + 0.5
    near_x = (centre / (grid_cells / 16.0))[None, :]
    near_y = (centre / (grid_cells / 16.0))[:, None]
    bell_near = jnp.exp(-(near_x * near_x + near_y * near_y) / 2.0)
    source_x = -near_x * bell_near
    source_y = -near_y * bell_near
    wide_x = (centre / (grid_cells / 8.0))[None, :]
    wide_y = (centre / (grid_cells / 8.0))[:, None]
    bell_wide = jnp.exp(-(wide_x * wide_x + wide_y * wide_y) / 2.0)
    lift_kernel = -wide_x * bell_wide
    drag_kernel = wide_y * bell_wide
    lift_kernel = lift_kernel / jnp.sqrt(jnp.sum(lift_kernel * lift_kernel))
    drag_kernel = drag_kernel / jnp.sqrt(jnp.sum(drag_kernel * drag_kernel))
    return (source_x, source_y, lift_kernel, drag_kernel)


def strip_step(vorticity, flow_x, flow_y, motion, kernels, substeps):
    source_x, source_y, lift_kernel, drag_kernel = kernels
    halves = motion.reshape(motion.shape[0], 2, substeps)
    earlier = jnp.concatenate([jnp.zeros_like(halves[:, :, :1]), halves[:, :, :-1]], axis=2)
    velocity = halves - earlier
    lift_rows = []
    drag_rows = []
    for substep in range(substeps):
        right_cell = jnp.roll(vorticity, -1, axis=2)
        left_cell = jnp.roll(vorticity, 1, axis=2)
        upper_cell = jnp.roll(vorticity, -1, axis=1)
        lower_cell = jnp.roll(vorticity, 1, axis=1)
        laplacian = right_cell + left_cell + upper_cell + lower_cell - 4.0 * vorticity
        tendency = (
            VISCOSITY * laplacian
            - flow_x * (0.5 * (right_cell - left_cell))
            - flow_y * (0.5 * (upper_cell - lower_cell))
        )
        forcing = (
            velocity[:, 0, substep][:, None, None] * source_x
            - velocity[:, 1, substep][:, None, None] * source_y
        )
        vorticity = vorticity + TIME_STEP * tendency + COUPLING * forcing
        lift_rows.append(jnp.sum(vorticity * lift_kernel, axis=(1, 2)))
        drag_rows.append(jnp.sum(vorticity * drag_kernel, axis=(1, 2)))
    return (vorticity, jnp.stack(lift_rows + drag_rows, axis=1))


def kernel_planes(cells):
    centre_x = lax.broadcasted_iota(jnp.int32, (cells, cells), 1).astype(jnp.float32) - cells / 2.0 + 0.5
    centre_y = lax.broadcasted_iota(jnp.int32, (cells, cells), 0).astype(jnp.float32) - cells / 2.0 + 0.5
    near_x = centre_x / (cells / 16.0)
    near_y = centre_y / (cells / 16.0)
    bell_near = jnp.exp(-(near_x * near_x + near_y * near_y) / 2.0)
    source_x = -near_x * bell_near
    source_y = -near_y * bell_near
    wide_x = centre_x / (cells / 8.0)
    wide_y = centre_y / (cells / 8.0)
    bell_wide = jnp.exp(-(wide_x * wide_x + wide_y * wide_y) / 2.0)
    lift_kernel = -wide_x * bell_wide
    drag_kernel = wide_y * bell_wide

    def total(plane):
        return jnp.sum(jnp.sum(plane, axis=0, keepdims=True), axis=1, keepdims=True)

    lift_kernel = lift_kernel / jnp.sqrt(total(lift_kernel * lift_kernel))
    drag_kernel = drag_kernel / jnp.sqrt(total(drag_kernel * drag_kernel))
    return (source_x, source_y, lift_kernel, drag_kernel)


def run_substeps(vorticity, flow_x, flow_y, forcing_of, lift_kernel, drag_kernel, substeps):
    rows_across, cols_across = vorticity.shape
    sample = lax.broadcasted_iota(jnp.int32, (2 * substeps, cols_across), 0)
    partial = jnp.zeros((2 * substeps, cols_across), jnp.float32)
    along_x = (TIME_STEP * 0.5) * flow_x
    along_y = (TIME_STEP * 0.5) * flow_y
    for substep in range(substeps):
        right_cell = pltpu.roll(vorticity, cols_across - 1, 1)
        left_cell = pltpu.roll(vorticity, 1, 1)
        upper_cell = pltpu.roll(vorticity, rows_across - 1, 0)
        lower_cell = pltpu.roll(vorticity, 1, 0)
        laplacian = (right_cell + left_cell) + (upper_cell + lower_cell) - 4.0 * vorticity
        step = (
            (TIME_STEP * VISCOSITY) * laplacian
            - along_x * (right_cell - left_cell)
            - along_y * (upper_cell - lower_cell)
        )
        if forcing_of is None:
            vorticity = vorticity + step
        else:
            vorticity = vorticity + step + forcing_of(substep)
        lift = jnp.sum(vorticity * lift_kernel, axis=0, keepdims=True)
        drag = jnp.sum(vorticity * drag_kernel, axis=0, keepdims=True)
        partial = jnp.where(sample == substep, lift, partial)
        partial = jnp.where(sample == substeps + substep, drag, partial)
    column = jnp.sum(partial, axis=1, keepdims=True)
    diagonal = (
        lax.broadcasted_iota(jnp.int32, (2 * substeps, 2 * substeps), 0)
        == lax.broadcasted_iota(jnp.int32, (2 * substeps, 2 * substeps), 1)
    )
    row = jnp.sum(jnp.where(diagonal, column, 0.0), axis=0, keepdims=True)
    return vorticity, row


def stencil_kernel(velocity_ref, vorticity_ref, flow_x_ref, flow_y_ref, out_ref, rows_ref, *, substeps):
    strip = pl.program_id(0)
    source_x, source_y, lift_kernel, drag_kernel = kernel_planes(vorticity_ref.shape[-1])

    def forcing_of(substep):
        return COUPLING * (
            velocity_ref[strip, substep] * source_x
            - velocity_ref[strip, substeps + substep] * source_y
        )

    vorticity, row = run_substeps(
        vorticity_ref[0, 0], flow_x_ref[0, 0], flow_y_ref[0, 0], forcing_of,
        lift_kernel, drag_kernel, substeps,
    )
    out_ref[0] = vorticity
    rows_ref[0] = row


def strip_step_kernel(strip_fields, vorticity, motion, kernels, substeps):
    strips, cells_y, cells_x = strip_fields.shape[1:]
    halves = motion.reshape(strips, 2, substeps)
    earlier = jnp.concatenate([jnp.zeros_like(halves[:, :, :1]), halves[:, :, :-1]], axis=2)
    velocity = (halves - earlier).reshape(strips, 2 * substeps)
    def field(index):
        return pl.BlockSpec((1, 1, cells_y, cells_x), lambda s: (index, s, 0, 0))

    new_vorticity, rows = pl.pallas_call(
        lambda *refs: stencil_kernel(*refs, substeps=substeps),
        grid=(strips,),
        in_specs=[
            pl.BlockSpec(memory_space=pltpu.SMEM),
            field(0), field(1), field(2),
        ],
        out_specs=[
            pl.BlockSpec((1, cells_y, cells_x), lambda s: (s, 0, 0)),
            pl.BlockSpec((1, 1, 2 * substeps), lambda s: (s, 0, 0)),
        ],
        out_shape=[
            jax.ShapeDtypeStruct((strips, cells_y, cells_x), jnp.float32),
            jax.ShapeDtypeStruct((strips, 1, 2 * substeps), jnp.float32),
        ],
        name="strip_stencil",
    )(velocity, vorticity, strip_fields, strip_fields)
    return new_vorticity, rows[:, 0, :]


def apply_block(vectors, matrix):
    return lax.dot_general(vectors, matrix, (((1,), (1,)), ((), ())), precision=EXACT_DOT)


def first_contract(left_side, right_side):
    return lax.dot_general(left_side, right_side, (((0,), (0,)), ((), ())), precision=EXACT_DOT)


def beam_solve(beam_load, pivot_inv, lower_block, upper_block):
    block_count = pivot_inv.shape[0]
    block_size = pivot_inv.shape[1]
    blocks = beam_load.reshape(beam_load.shape[0], block_count, block_size)
    carried = [blocks[:, 0]]
    for block_index in range(1, block_count):
        pivoted = apply_block(carried[-1], pivot_inv[block_index - 1])
        carried.append(blocks[:, block_index] - apply_block(pivoted, lower_block[block_index - 1]))
    solved = [apply_block(carried[-1], pivot_inv[block_count - 1])]
    for block_index in range(block_count - 2, -1, -1):
        remainder = carried[block_index] - apply_block(solved[0], upper_block[block_index])
        solved.insert(0, apply_block(remainder, pivot_inv[block_index]))
    return jnp.concatenate(solved, axis=1)


def start_kernel(owner_ref, riser_ref, node_ref, spread_ref, pivot_ref, lower_ref, upper_ref, fields_ref,
                 response_ref, vorticity_ref, sent_ref, *, substeps):
    block_count = pivot_ref.shape[1]
    block_size = pivot_ref.shape[2]
    node_count = block_count * block_size
    strips = node_ref.shape[1]
    per_device = fields_ref.shape[1]
    position = lax.axis_index("strip")
    group_position = lax.axis_index("group")

    strip_lane = lax.broadcasted_iota(jnp.int32, (1, strips), 1)
    strip_sublane = lax.broadcasted_iota(jnp.int32, (strips, 1), 0)
    owned_row = jnp.zeros((1, strips), jnp.float32)
    owned_col = jnp.zeros((strips, 1), jnp.float32)
    for strip in range(strips):
        held = jnp.where(owner_ref[0, riser_ref[strip]] == position, 1.0, 0.0)
        owned_row = jnp.where(strip_lane == strip, held, owned_row)
        owned_col = jnp.where(strip_sublane == strip, held, owned_col)
    diagonal = lax.broadcasted_iota(jnp.int32, (strips, strips), 0) == lax.broadcasted_iota(jnp.int32, (strips, strips), 1)
    node_row = node_ref[...]
    node_col = jnp.sum(jnp.where(diagonal, node_row.astype(jnp.float32), 0.0), axis=1, keepdims=True)

    def apply(matrix, vectors):
        return jnp.dot(matrix, vectors, precision=lax.Precision.HIGH, preferred_element_type=jnp.float32)

    def unit_load(block_index):
        node = block_index * block_size + lax.broadcasted_iota(jnp.int32, (block_size, strips), 0)
        return (node == node_row).astype(jnp.float32) * owned_row

    def product(left, right):
        return jnp.dot(left, right, precision=lax.Precision.HIGH, preferred_element_type=jnp.float32)

    forward = [None] + [product(lower_ref[0, i - 1], pivot_ref[0, i - 1]) for i in range(1, block_count)]
    backward = [product(pivot_ref[0, i], upper_ref[0, i]) for i in range(block_count - 1)]
    carried = [unit_load(0)]
    for block_index in range(1, block_count):
        carried.append(unit_load(block_index) - apply(forward[block_index], carried[-1]))
    pivoted = [apply(pivot_ref[0, i], carried[i]) for i in range(block_count)]
    solved = pivoted[block_count - 1]
    response_ref[(block_count - 1) * block_size:, :] = solved
    for block_index in range(block_count - 2, -1, -1):
        solved = pivoted[block_index] - apply(backward[block_index], solved)
        response_ref[block_index * block_size:(block_index + 1) * block_size, :] = solved

    _, _, lift_kernel, drag_kernel = kernel_planes(fields_ref.shape[-1])
    strip_of_row = lax.broadcasted_iota(jnp.int32, (per_device, 2 * substeps), 0)
    rows = jnp.zeros((per_device, 2 * substeps), jnp.float32)
    for strip in range(per_device):
        vorticity, row = run_substeps(
            fields_ref[0, strip], fields_ref[1, strip], fields_ref[2, strip], None,
            lift_kernel, drag_kernel, substeps,
        )
        vorticity_ref[strip] = vorticity
        rows = jnp.where(strip_of_row == strip, row, rows)

    node_onehot = (
        node_col == lax.broadcasted_iota(jnp.int32, (strips, node_count), 1).astype(jnp.float32)
    ).astype(jnp.float32)
    coupling = jnp.dot(node_onehot, response_ref[...], precision=EXACT_DOT, preferred_element_type=jnp.float32)
    coupling = coupling * owned_col
    sent_rows = sent_ref.shape[0]
    place = lax.broadcasted_iota(jnp.int32, (sent_rows, strips), 0) - group_position * strips
    pick = (place == lax.broadcasted_iota(jnp.int32, (sent_rows, strips), 1)).astype(jnp.float32)
    sent_ref[:, 0:2 * substeps] = jnp.dot(spread_ref[...], rows, precision=EXACT_DOT, preferred_element_type=jnp.float32)
    sent_ref[:, 2 * substeps:] = jnp.dot(pick, coupling, precision=EXACT_DOT, preferred_element_type=jnp.float32)


def spread_matrix(devices, per_device):
    return (
        np.arange(devices * per_device)[:, None] % per_device == np.arange(per_device)[None, :]
    ).astype(np.float32)


def start_step(riser_owner, strip_riser, strip_node, pivot_inv, lower_block, upper_block, strip_fields, devices, substeps):
    strips = strip_node.shape[0]
    node_count = pivot_inv.shape[1] * pivot_inv.shape[2]
    _, per_device, cells_y, cells_x = strip_fields.shape
    vmem = pl.BlockSpec(memory_space=pltpu.VMEM)
    return pl.pallas_call(
        lambda *refs: start_kernel(*refs, substeps=substeps),
        in_specs=[pl.BlockSpec(memory_space=pltpu.SMEM)] * 2 + [vmem] * 6,
        out_shape=[
            jax.ShapeDtypeStruct((node_count, strips), jnp.float32),
            jax.ShapeDtypeStruct((per_device, cells_y, cells_x), jnp.float32),
            jax.ShapeDtypeStruct((devices * per_device, 2 * substeps + strips), jnp.float32),
        ],
        name="start_step",
    )(
        riser_owner, strip_riser.reshape(strips), strip_node[None, :], spread_matrix(devices, per_device),
        pivot_inv, lower_block, upper_block, strip_fields,
    )


def second_kernel(received_ref, node_ref, spread_ref, gather_ref, difference_ref, fields_ref, vorticity_ref,
                  out_ref, sent_ref, *, substeps, node_count):
    position = lax.axis_index("strip")
    group_position = lax.axis_index("group")
    total_strips, _ = received_ref.shape
    strips = node_ref.shape[1]
    per_device = fields_ref.shape[1]
    every_force = received_ref[:, 0:2 * substeps]
    offset = jnp.sum(every_force, axis=0, keepdims=True) / jnp.sqrt(jnp.float32(total_strips))
    group_force = received_ref[pl.ds(group_position * strips, strips), 0:2 * substeps]
    my_coupling = jnp.dot(
        gather_ref[...], received_ref[:, 2 * substeps:], precision=EXACT_DOT, preferred_element_type=jnp.float32
    )
    motion = jnp.dot(my_coupling, group_force, precision=EXACT_DOT, preferred_element_type=jnp.float32)
    mine = (
        lax.broadcasted_iota(jnp.int32, (per_device, strips), 1)
        == position * per_device + lax.broadcasted_iota(jnp.int32, (per_device, strips), 0)
    )
    local_node = jnp.sum(jnp.where(mine, node_ref[...].astype(jnp.float32), 0.0), axis=1, keepdims=True)
    local_taper = 1.0 - local_node / node_count
    lane = lax.broadcasted_iota(jnp.int32, (per_device, 2 * substeps), 1)
    sublane = lax.broadcasted_iota(jnp.int32, (per_device, 2 * substeps), 0)
    motion = motion + jnp.where(lane >= substeps, local_taper * offset, 0.0)
    velocity = jnp.dot(motion, difference_ref[...], precision=EXACT_DOT, preferred_element_type=jnp.float32)

    source_x, source_y, lift_kernel, drag_kernel = kernel_planes(fields_ref.shape[-1])
    coupled_x = COUPLING * source_x
    coupled_y = COUPLING * source_y
    rows = jnp.zeros((per_device, 2 * substeps), jnp.float32)
    for strip in range(per_device):
        picks = [
            jnp.sum(jnp.sum(jnp.where((sublane == strip) & (lane == column), velocity, 0.0), axis=0, keepdims=True), axis=1, keepdims=True)
            for column in range(2 * substeps)
        ]

        def forcing_of(substep, picks=picks):
            return picks[substep] * coupled_x - picks[substeps + substep] * coupled_y

        vorticity, row = run_substeps(
            vorticity_ref[strip], fields_ref[1, strip], fields_ref[2, strip], forcing_of,
            lift_kernel, drag_kernel, substeps,
        )
        out_ref[strip] = vorticity
        rows = jnp.where(sublane == strip, row, rows)
    sent_ref[...] = jnp.dot(spread_ref[...], rows, precision=EXACT_DOT, preferred_element_type=jnp.float32)


def difference_matrix(substeps):
    columns = np.arange(2 * substeps)
    same = columns[:, None] == columns[None, :]
    before = (columns[:, None] + 1 == columns[None, :]) & (columns[None, :] % substeps != 0)
    return same.astype(np.float32) - before.astype(np.float32)


def second_step(received, strip_node, strip_fields, vorticity, devices, node_count, substeps):
    _, per_device, cells_y, cells_x = strip_fields.shape
    spread = spread_matrix(devices, per_device)
    vmem = pl.BlockSpec(memory_space=pltpu.VMEM)
    return pl.pallas_call(
        lambda *refs: second_kernel(*refs, substeps=substeps, node_count=node_count),
        in_specs=[vmem] * 7,
        out_shape=[
            jax.ShapeDtypeStruct((per_device, cells_y, cells_x), jnp.float32),
            jax.ShapeDtypeStruct((devices * per_device, 2 * substeps), jnp.float32),
        ],
        name="second_step",
    )(received, strip_node[None, :], spread, np.ascontiguousarray(spread.T), difference_matrix(substeps), strip_fields, vorticity)


def local(strip_fields, strip_riser, strip_node, riser_owner, pivot_inv, lower_block, upper_block):
    position = lax.axis_index("strip")
    group_position = lax.axis_index("group")
    group_count = lax.axis_size("group")
    devices = lax.axis_size("strip") * group_count
    per_device = strip_fields.shape[1]
    grid_cells = strip_fields.shape[2]
    node_count = pivot_inv.shape[1] * pivot_inv.shape[2]
    riser_count = riser_owner.shape[1]
    group_strips = strip_node.shape[0]
    substeps = NSUB
    total_strips = per_device * devices
    top_taper = 1.0 - jnp.arange(node_count, dtype=jnp.float32) / node_count

    unit_response, first_vorticity, first_sent = start_step(
        riser_owner, strip_riser, strip_node, pivot_inv, lower_block, upper_block, strip_fields, devices, substeps
    )

    received = lax.all_to_all(first_sent, ("group", "strip"), 0, 0, tiled=True)
    vorticity, sent = second_step(received, strip_node, strip_fields, first_vorticity, devices, node_count, substeps)
    received = lax.all_to_all(sent, ("group", "strip"), 0, 0, tiled=True)
    offset = jnp.sum(received[:, substeps:], axis=0) / jnp.sqrt(jnp.float32(total_strips))
    group_force = lax.dynamic_slice_in_dim(received, group_position * group_strips, group_strips)
    displacement = lax.dot_general(
        group_force, unit_response, (((0,), (1,)), ((), ())), precision=EXACT_DOT
    )
    displacement = displacement.at[substeps:, :].add(offset[:, None] * top_taper[None, :])
    return (vorticity, displacement[None])


def solution(mesh):
    in_specs = (
        P(None, ("group", "strip"), None, None),
        P("group", None),
        P("group"),
        P("group", None),
        P(("group", "strip"), None, None, None),
        P(("group", "strip"), None, None, None),
        P(("group", "strip"), None, None, None),
    )
    out_specs = (P(("group", "strip"), None, None), P(("group", "strip"), None, None))
    return jax.shard_map(local, mesh=mesh, in_specs=in_specs, out_specs=out_specs, check_vma=False)
```

```python
import numpy as np
import jax
import jax.numpy as jnp
from jax import lax
from jax.sharding import PartitionSpec as P
from jax.experimental import pallas as pl
from jax.experimental.pallas import tpu as pltpu

NSUB = 8
COUPLED = 2


TIME_STEP = 0.25
VISCOSITY = 0.05
COUPLING = 0.5
EXACT_DOT = lax.Precision.HIGHEST


def make_kernels(grid_cells):
    centre = jnp.arange(grid_cells, dtype=jnp.float32) - grid_cells / 2.0 + 0.5
    near_x = (centre / (grid_cells / 16.0))[None, :]
    near_y = (centre / (grid_cells / 16.0))[:, None]
    bell_near = jnp.exp(-(near_x * near_x + near_y * near_y) / 2.0)
    source_x = -near_x * bell_near
    source_y = -near_y * bell_near
    wide_x = (centre / (grid_cells / 8.0))[None, :]
    wide_y = (centre / (grid_cells / 8.0))[:, None]
    bell_wide = jnp.exp(-(wide_x * wide_x + wide_y * wide_y) / 2.0)
    lift_kernel = -wide_x * bell_wide
    drag_kernel = wide_y * bell_wide
    lift_kernel = lift_kernel / jnp.sqrt(jnp.sum(lift_kernel * lift_kernel))
    drag_kernel = drag_kernel / jnp.sqrt(jnp.sum(drag_kernel * drag_kernel))
    return (source_x, source_y, lift_kernel, drag_kernel)


def strip_step(vorticity, flow_x, flow_y, motion, kernels, substeps):
    source_x, source_y, lift_kernel, drag_kernel = kernels
    halves = motion.reshape(motion.shape[0], 2, substeps)
    earlier = jnp.concatenate([jnp.zeros_like(halves[:, :, :1]), halves[:, :, :-1]], axis=2)
    velocity = halves - earlier
    lift_rows = []
    drag_rows = []
    for substep in range(substeps):
        right_cell = jnp.roll(vorticity, -1, axis=2)
        left_cell = jnp.roll(vorticity, 1, axis=2)
        upper_cell = jnp.roll(vorticity, -1, axis=1)
        lower_cell = jnp.roll(vorticity, 1, axis=1)
        laplacian = right_cell + left_cell + upper_cell + lower_cell - 4.0 * vorticity
        tendency = (
            VISCOSITY * laplacian
            - flow_x * (0.5 * (right_cell - left_cell))
            - flow_y * (0.5 * (upper_cell - lower_cell))
        )
        forcing = (
            velocity[:, 0, substep][:, None, None] * source_x
            - velocity[:, 1, substep][:, None, None] * source_y
        )
        vorticity = vorticity + TIME_STEP * tendency + COUPLING * forcing
        lift_rows.append(jnp.sum(vorticity * lift_kernel, axis=(1, 2)))
        drag_rows.append(jnp.sum(vorticity * drag_kernel, axis=(1, 2)))
    return (vorticity, jnp.stack(lift_rows + drag_rows, axis=1))


def kernel_planes(cells):
    centre_x = lax.broadcasted_iota(jnp.int32, (cells, cells), 1).astype(jnp.float32) - cells / 2.0 + 0.5
    centre_y = lax.broadcasted_iota(jnp.int32, (cells, cells), 0).astype(jnp.float32) - cells / 2.0 + 0.5
    near_x = centre_x / (cells / 16.0)
    near_y = centre_y / (cells / 16.0)
    bell_near = jnp.exp(-(near_x * near_x + near_y * near_y) / 2.0)
    source_x = -near_x * bell_near
    source_y = -near_y * bell_near
    wide_x = centre_x / (cells / 8.0)
    wide_y = centre_y / (cells / 8.0)
    bell_wide = jnp.exp(-(wide_x * wide_x + wide_y * wide_y) / 2.0)
    lift_kernel = -wide_x * bell_wide
    drag_kernel = wide_y * bell_wide

    def total(plane):
        return jnp.sum(jnp.sum(plane, axis=0, keepdims=True), axis=1, keepdims=True)

    lift_kernel = lift_kernel / jnp.sqrt(total(lift_kernel * lift_kernel))
    drag_kernel = drag_kernel / jnp.sqrt(total(drag_kernel * drag_kernel))
    return (source_x, source_y, lift_kernel, drag_kernel)


def run_substeps(vorticity, flow_x, flow_y, forcing_of, lift_kernel, drag_kernel, substeps, halo_ref=None):
    rows_across, cols_across = vorticity.shape
    lane = lax.broadcasted_iota(jnp.int32, (1, 2 * substeps), 1)
    row = jnp.zeros((1, 2 * substeps), jnp.float32)
    along_x = (TIME_STEP * 0.5) * flow_x
    along_y = (TIME_STEP * 0.5) * flow_y
    for substep in range(substeps):
        right_cell = pltpu.roll(vorticity, cols_across - 1, 1)
        left_cell = pltpu.roll(vorticity, 1, 1)
        if halo_ref is None:
            upper_cell = pltpu.roll(vorticity, rows_across - 1, 0)
            lower_cell = pltpu.roll(vorticity, 1, 0)
        else:
            halo_ref[8:8 + rows_across, :] = vorticity
            halo_ref[7:8, :] = vorticity[rows_across - 1:rows_across, :]
            halo_ref[8 + rows_across:9 + rows_across, :] = vorticity[0:1, :]
            upper_cell = halo_ref[9:9 + rows_across, :]
            lower_cell = halo_ref[7:7 + rows_across, :]
        laplacian = (right_cell + left_cell) + (upper_cell + lower_cell) - 4.0 * vorticity
        step = (
            (TIME_STEP * VISCOSITY) * laplacian
            - along_x * (right_cell - left_cell)
            - along_y * (upper_cell - lower_cell)
        )
        if forcing_of is None:
            vorticity = vorticity + step
        else:
            vorticity = vorticity + step + forcing_of(substep)
        lift = jnp.sum(jnp.sum(vorticity * lift_kernel, axis=0, keepdims=True), axis=1, keepdims=True)
        drag = jnp.sum(jnp.sum(vorticity * drag_kernel, axis=0, keepdims=True), axis=1, keepdims=True)
        row = row + jnp.where(lane == substep, lift, 0.0) + jnp.where(lane == substeps + substep, drag, 0.0)
    return vorticity, row


def stencil_kernel(velocity_ref, vorticity_ref, flow_x_ref, flow_y_ref, out_ref, rows_ref, *, substeps):
    strip = pl.program_id(0)
    source_x, source_y, lift_kernel, drag_kernel = kernel_planes(vorticity_ref.shape[-1])

    def forcing_of(substep):
        return COUPLING * (
            velocity_ref[strip, substep] * source_x
            - velocity_ref[strip, substeps + substep] * source_y
        )

    vorticity, row = run_substeps(
        vorticity_ref[0, 0], flow_x_ref[0, 0], flow_y_ref[0, 0], forcing_of,
        lift_kernel, drag_kernel, substeps,
    )
    out_ref[0] = vorticity
    rows_ref[0] = row


def strip_step_kernel(strip_fields, vorticity, motion, kernels, substeps):
    strips, cells_y, cells_x = strip_fields.shape[1:]
    halves = motion.reshape(strips, 2, substeps)
    earlier = jnp.concatenate([jnp.zeros_like(halves[:, :, :1]), halves[:, :, :-1]], axis=2)
    velocity = (halves - earlier).reshape(strips, 2 * substeps)
    def field(index):
        return pl.BlockSpec((1, 1, cells_y, cells_x), lambda s: (index, s, 0, 0))

    new_vorticity, rows = pl.pallas_call(
        lambda *refs: stencil_kernel(*refs, substeps=substeps),
        grid=(strips,),
        in_specs=[
            pl.BlockSpec(memory_space=pltpu.SMEM),
            field(0), field(1), field(2),
        ],
        out_specs=[
            pl.BlockSpec((1, cells_y, cells_x), lambda s: (s, 0, 0)),
            pl.BlockSpec((1, 1, 2 * substeps), lambda s: (s, 0, 0)),
        ],
        out_shape=[
            jax.ShapeDtypeStruct((strips, cells_y, cells_x), jnp.float32),
            jax.ShapeDtypeStruct((strips, 1, 2 * substeps), jnp.float32),
        ],
        name="strip_stencil",
    )(velocity, vorticity, strip_fields, strip_fields)
    return new_vorticity, rows[:, 0, :]


def apply_block(vectors, matrix):
    return lax.dot_general(vectors, matrix, (((1,), (1,)), ((), ())), precision=EXACT_DOT)


def first_contract(left_side, right_side):
    return lax.dot_general(left_side, right_side, (((0,), (0,)), ((), ())), precision=EXACT_DOT)


def beam_solve(beam_load, pivot_inv, lower_block, upper_block):
    block_count = pivot_inv.shape[0]
    block_size = pivot_inv.shape[1]
    blocks = beam_load.reshape(beam_load.shape[0], block_count, block_size)
    carried = [blocks[:, 0]]
    for block_index in range(1, block_count):
        pivoted = apply_block(carried[-1], pivot_inv[block_index - 1])
        carried.append(blocks[:, block_index] - apply_block(pivoted, lower_block[block_index - 1]))
    solved = [apply_block(carried[-1], pivot_inv[block_count - 1])]
    for block_index in range(block_count - 2, -1, -1):
        remainder = carried[block_index] - apply_block(solved[0], upper_block[block_index])
        solved.insert(0, apply_block(remainder, pivot_inv[block_index]))
    return jnp.concatenate(solved, axis=1)


def start_kernel(owner_ref, riser_ref, node_ref, spread_ref, pivot_ref, lower_ref, upper_ref, fields_ref,
                 response_ref, vorticity_ref, sent_ref, *, substeps):
    block_count = pivot_ref.shape[1]
    block_size = pivot_ref.shape[2]
    node_count = block_count * block_size
    strips = node_ref.shape[1]
    per_device = fields_ref.shape[1]
    position = lax.axis_index("strip")
    group_position = lax.axis_index("group")

    strip_lane = lax.broadcasted_iota(jnp.int32, (1, strips), 1)
    strip_sublane = lax.broadcasted_iota(jnp.int32, (strips, 1), 0)
    owned_row = jnp.zeros((1, strips), jnp.float32)
    owned_col = jnp.zeros((strips, 1), jnp.float32)
    for strip in range(strips):
        held = jnp.where(owner_ref[0, riser_ref[strip]] == position, 1.0, 0.0)
        owned_row = jnp.where(strip_lane == strip, held, owned_row)
        owned_col = jnp.where(strip_sublane == strip, held, owned_col)
    diagonal = lax.broadcasted_iota(jnp.int32, (strips, strips), 0) == lax.broadcasted_iota(jnp.int32, (strips, strips), 1)
    node_row = node_ref[...]
    node_col = jnp.sum(jnp.where(diagonal, node_row.astype(jnp.float32), 0.0), axis=1, keepdims=True)

    def apply(matrix, vectors):
        return jnp.dot(matrix, vectors, precision=lax.Precision.HIGH, preferred_element_type=jnp.float32)

    def unit_load(block_index):
        node = block_index * block_size + lax.broadcasted_iota(jnp.int32, (block_size, strips), 0)
        return (node == node_row).astype(jnp.float32) * owned_row

    def product(left, right):
        return jnp.dot(left, right, precision=lax.Precision.HIGH, preferred_element_type=jnp.float32)

    forward = [None] + [product(lower_ref[0, i - 1], pivot_ref[0, i - 1]) for i in range(1, block_count)]
    backward = [product(pivot_ref[0, i], upper_ref[0, i]) for i in range(block_count - 1)]
    carried = [unit_load(0)]
    for block_index in range(1, block_count):
        carried.append(unit_load(block_index) - apply(forward[block_index], carried[-1]))
    pivoted = [apply(pivot_ref[0, i], carried[i]) for i in range(block_count)]
    solved = pivoted[block_count - 1]
    response_ref[(block_count - 1) * block_size:, :] = solved
    for block_index in range(block_count - 2, -1, -1):
        solved = pivoted[block_index] - apply(backward[block_index], solved)
        response_ref[block_index * block_size:(block_index + 1) * block_size, :] = solved

    _, _, lift_kernel, drag_kernel = kernel_planes(fields_ref.shape[-1])
    strip_of_row = lax.broadcasted_iota(jnp.int32, (per_device, 2 * substeps), 0)
    rows = jnp.zeros((per_device, 2 * substeps), jnp.float32)
    for strip in range(per_device):
        vorticity, row = run_substeps(
            fields_ref[0, strip], fields_ref[1, strip], fields_ref[2, strip], None,
            lift_kernel, drag_kernel, substeps,
        )
        vorticity_ref[strip] = vorticity
        rows = jnp.where(strip_of_row == strip, row, rows)

    node_onehot = (
        node_col == lax.broadcasted_iota(jnp.int32, (strips, node_count), 1).astype(jnp.float32)
    ).astype(jnp.float32)
    coupling = jnp.dot(node_onehot, response_ref[...], precision=EXACT_DOT, preferred_element_type=jnp.float32)
    coupling = coupling * owned_col
    sent_rows = sent_ref.shape[0]
    place = lax.broadcasted_iota(jnp.int32, (sent_rows, strips), 0) - group_position * strips
    pick = (place == lax.broadcasted_iota(jnp.int32, (sent_rows, strips), 1)).astype(jnp.float32)
    sent_ref[:, 0:2 * substeps] = jnp.dot(spread_ref[...], rows, precision=EXACT_DOT, preferred_element_type=jnp.float32)
    sent_ref[:, 2 * substeps:] = jnp.dot(pick, coupling, precision=EXACT_DOT, preferred_element_type=jnp.float32)


def spread_matrix(devices, per_device):
    return (
        np.arange(devices * per_device)[:, None] % per_device == np.arange(per_device)[None, :]
    ).astype(np.float32)


def start_step(riser_owner, strip_riser, strip_node, pivot_inv, lower_block, upper_block, strip_fields, devices, substeps):
    strips = strip_node.shape[0]
    node_count = pivot_inv.shape[1] * pivot_inv.shape[2]
    _, per_device, cells_y, cells_x = strip_fields.shape
    vmem = pl.BlockSpec(memory_space=pltpu.VMEM)
    return pl.pallas_call(
        lambda *refs: start_kernel(*refs, substeps=substeps),
        in_specs=[pl.BlockSpec(memory_space=pltpu.SMEM)] * 2 + [vmem] * 6,
        out_shape=[
            jax.ShapeDtypeStruct((node_count, strips), jnp.float32),
            jax.ShapeDtypeStruct((per_device, cells_y, cells_x), jnp.float32),
            jax.ShapeDtypeStruct((devices * per_device, 2 * substeps + strips), jnp.float32),
        ],
        name="start_step",
    )(
        riser_owner, strip_riser.reshape(strips), strip_node[None, :], spread_matrix(devices, per_device),
        pivot_inv, lower_block, upper_block, strip_fields,
    )


def second_kernel(received_ref, node_ref, spread_ref, gather_ref, difference_ref, fields_ref, vorticity_ref,
                  out_ref, sent_ref, halo_ref, *, substeps, node_count):
    position = lax.axis_index("strip")
    group_position = lax.axis_index("group")
    total_strips, _ = received_ref.shape
    strips = node_ref.shape[1]
    per_device = fields_ref.shape[1]
    every_force = received_ref[:, 0:2 * substeps]
    offset = jnp.sum(every_force, axis=0, keepdims=True) / jnp.sqrt(jnp.float32(total_strips))
    group_force = received_ref[pl.ds(group_position * strips, strips), 0:2 * substeps]
    my_coupling = jnp.dot(
        gather_ref[...], received_ref[:, 2 * substeps:], precision=EXACT_DOT, preferred_element_type=jnp.float32
    )
    motion = jnp.dot(my_coupling, group_force, precision=EXACT_DOT, preferred_element_type=jnp.float32)
    mine = (
        lax.broadcasted_iota(jnp.int32, (per_device, strips), 1)
        == position * per_device + lax.broadcasted_iota(jnp.int32, (per_device, strips), 0)
    )
    local_node = jnp.sum(jnp.where(mine, node_ref[...].astype(jnp.float32), 0.0), axis=1, keepdims=True)
    local_taper = 1.0 - local_node / node_count
    lane = lax.broadcasted_iota(jnp.int32, (per_device, 2 * substeps), 1)
    sublane = lax.broadcasted_iota(jnp.int32, (per_device, 2 * substeps), 0)
    motion = motion + jnp.where(lane >= substeps, local_taper * offset, 0.0)
    velocity = jnp.dot(motion, difference_ref[...], precision=EXACT_DOT, preferred_element_type=jnp.float32)

    source_x, source_y, lift_kernel, drag_kernel = kernel_planes(fields_ref.shape[-1])
    coupled_x = COUPLING * source_x
    coupled_y = COUPLING * source_y
    rows = jnp.zeros((per_device, 2 * substeps), jnp.float32)
    for strip in range(per_device):
        picks = [
            jnp.sum(jnp.sum(jnp.where((sublane == strip) & (lane == column), velocity, 0.0), axis=0, keepdims=True), axis=1, keepdims=True)
            for column in range(2 * substeps)
        ]

        def forcing_of(substep, picks=picks):
            return picks[substep] * coupled_x - picks[substeps + substep] * coupled_y

        vorticity, row = run_substeps(
            vorticity_ref[strip], fields_ref[1, strip], fields_ref[2, strip], forcing_of,
            lift_kernel, drag_kernel, substeps, halo_ref.at[strip],
        )
        out_ref[strip] = vorticity
        rows = jnp.where(sublane == strip, row, rows)
    sent_ref[...] = jnp.dot(spread_ref[...], rows, precision=EXACT_DOT, preferred_element_type=jnp.float32)


def difference_matrix(substeps):
    columns = np.arange(2 * substeps)
    same = columns[:, None] == columns[None, :]
    before = (columns[:, None] + 1 == columns[None, :]) & (columns[None, :] % substeps != 0)
    return same.astype(np.float32) - before.astype(np.float32)


def second_step(received, strip_node, strip_fields, vorticity, devices, node_count, substeps):
    _, per_device, cells_y, cells_x = strip_fields.shape
    spread = spread_matrix(devices, per_device)
    vmem = pl.BlockSpec(memory_space=pltpu.VMEM)
    return pl.pallas_call(
        lambda *refs: second_kernel(*refs, substeps=substeps, node_count=node_count),
        in_specs=[vmem] * 7,
        out_shape=[
            jax.ShapeDtypeStruct((per_device, cells_y, cells_x), jnp.float32),
            jax.ShapeDtypeStruct((devices * per_device, 2 * substeps), jnp.float32),
        ],
        scratch_shapes=[pltpu.VMEM((per_device, cells_y + 16, cells_x), jnp.float32)],
        name="second_step",
    )(received, strip_node[None, :], spread, np.ascontiguousarray(spread.T), difference_matrix(substeps), strip_fields, vorticity)


def local(strip_fields, strip_riser, strip_node, riser_owner, pivot_inv, lower_block, upper_block):
    position = lax.axis_index("strip")
    group_position = lax.axis_index("group")
    group_count = lax.axis_size("group")
    devices = lax.axis_size("strip") * group_count
    per_device = strip_fields.shape[1]
    grid_cells = strip_fields.shape[2]
    node_count = pivot_inv.shape[1] * pivot_inv.shape[2]
    riser_count = riser_owner.shape[1]
    group_strips = strip_node.shape[0]
    substeps = NSUB
    total_strips = per_device * devices
    top_taper = 1.0 - jnp.arange(node_count, dtype=jnp.float32) / node_count

    unit_response, first_vorticity, first_sent = start_step(
        riser_owner, strip_riser, strip_node, pivot_inv, lower_block, upper_block, strip_fields, devices, substeps
    )

    received = lax.all_to_all(first_sent, ("group", "strip"), 0, 0, tiled=True)
    vorticity, sent = second_step(received, strip_node, strip_fields, first_vorticity, devices, node_count, substeps)
    received = lax.all_to_all(sent, ("group", "strip"), 0, 0, tiled=True)
    offset = jnp.sum(received[:, substeps:], axis=0) / jnp.sqrt(jnp.float32(total_strips))
    group_force = lax.dynamic_slice_in_dim(received, group_position * group_strips, group_strips)
    displacement = lax.dot_general(
        group_force, unit_response, (((0,), (1,)), ((), ())), precision=EXACT_DOT
    )
    displacement = displacement.at[substeps:, :].add(offset[:, None] * top_taper[None, :])
    return (vorticity, displacement[None])


def solution(mesh):
    in_specs = (
        P(None, ("group", "strip"), None, None),
        P("group", None),
        P("group"),
        P("group", None),
        P(("group", "strip"), None, None, None),
        P(("group", "strip"), None, None, None),
        P(("group", "strip"), None, None, None),
    )
    out_specs = (P(("group", "strip"), None, None), P(("group", "strip"), None, None))
    return jax.shard_map(local, mesh=mesh, in_specs=in_specs, out_specs=out_specs, check_vma=False)
```

```python
import numpy as np
import jax
import jax.numpy as jnp
from jax import lax
from jax.sharding import PartitionSpec as P
from jax.experimental import pallas as pl
from jax.experimental.pallas import tpu as pltpu

NSUB = 8
COUPLED = 2


TIME_STEP = 0.25
VISCOSITY = 0.05
COUPLING = 0.5
EXACT_DOT = lax.Precision.HIGHEST


def make_kernels(grid_cells):
    centre = jnp.arange(grid_cells, dtype=jnp.float32) - grid_cells / 2.0 + 0.5
    near_x = (centre / (grid_cells / 16.0))[None, :]
    near_y = (centre / (grid_cells / 16.0))[:, None]
    bell_near = jnp.exp(-(near_x * near_x + near_y * near_y) / 2.0)
    source_x = -near_x * bell_near
    source_y = -near_y * bell_near
    wide_x = (centre / (grid_cells / 8.0))[None, :]
    wide_y = (centre / (grid_cells / 8.0))[:, None]
    bell_wide = jnp.exp(-(wide_x * wide_x + wide_y * wide_y) / 2.0)
    lift_kernel = -wide_x * bell_wide
    drag_kernel = wide_y * bell_wide
    lift_kernel = lift_kernel / jnp.sqrt(jnp.sum(lift_kernel * lift_kernel))
    drag_kernel = drag_kernel / jnp.sqrt(jnp.sum(drag_kernel * drag_kernel))
    return (source_x, source_y, lift_kernel, drag_kernel)


def strip_step(vorticity, flow_x, flow_y, motion, kernels, substeps):
    source_x, source_y, lift_kernel, drag_kernel = kernels
    halves = motion.reshape(motion.shape[0], 2, substeps)
    earlier = jnp.concatenate([jnp.zeros_like(halves[:, :, :1]), halves[:, :, :-1]], axis=2)
    velocity = halves - earlier
    lift_rows = []
    drag_rows = []
    for substep in range(substeps):
        right_cell = jnp.roll(vorticity, -1, axis=2)
        left_cell = jnp.roll(vorticity, 1, axis=2)
        upper_cell = jnp.roll(vorticity, -1, axis=1)
        lower_cell = jnp.roll(vorticity, 1, axis=1)
        laplacian = right_cell + left_cell + upper_cell + lower_cell - 4.0 * vorticity
        tendency = (
            VISCOSITY * laplacian
            - flow_x * (0.5 * (right_cell - left_cell))
            - flow_y * (0.5 * (upper_cell - lower_cell))
        )
        forcing = (
            velocity[:, 0, substep][:, None, None] * source_x
            - velocity[:, 1, substep][:, None, None] * source_y
        )
        vorticity = vorticity + TIME_STEP * tendency + COUPLING * forcing
        lift_rows.append(jnp.sum(vorticity * lift_kernel, axis=(1, 2)))
        drag_rows.append(jnp.sum(vorticity * drag_kernel, axis=(1, 2)))
    return (vorticity, jnp.stack(lift_rows + drag_rows, axis=1))


def kernel_planes(cells):
    centre_x = lax.broadcasted_iota(jnp.int32, (cells, cells), 1).astype(jnp.float32) - cells / 2.0 + 0.5
    centre_y = lax.broadcasted_iota(jnp.int32, (cells, cells), 0).astype(jnp.float32) - cells / 2.0 + 0.5
    near_x = centre_x / (cells / 16.0)
    near_y = centre_y / (cells / 16.0)
    bell_near = jnp.exp(-(near_x * near_x + near_y * near_y) / 2.0)
    source_x = -near_x * bell_near
    source_y = -near_y * bell_near
    wide_x = centre_x / (cells / 8.0)
    wide_y = centre_y / (cells / 8.0)
    bell_wide = jnp.exp(-(wide_x * wide_x + wide_y * wide_y) / 2.0)
    lift_kernel = -wide_x * bell_wide
    drag_kernel = wide_y * bell_wide

    def total(plane):
        return jnp.sum(jnp.sum(plane, axis=0, keepdims=True), axis=1, keepdims=True)

    lift_kernel = lift_kernel / jnp.sqrt(total(lift_kernel * lift_kernel))
    drag_kernel = drag_kernel / jnp.sqrt(total(drag_kernel * drag_kernel))
    return (source_x, source_y, lift_kernel, drag_kernel)


def run_substeps(vorticity, flow_x, flow_y, forcing_of, lift_kernel, drag_kernel, substeps):
    rows_across, cols_across = vorticity.shape
    lane = lax.broadcasted_iota(jnp.int32, (1, 2 * substeps), 1)
    row = jnp.zeros((1, 2 * substeps), jnp.float32)
    along_x = (TIME_STEP * 0.5) * flow_x
    along_y = (TIME_STEP * 0.5) * flow_y
    for substep in range(substeps):
        right_cell = pltpu.roll(vorticity, cols_across - 1, 1)
        left_cell = pltpu.roll(vorticity, 1, 1)
        upper_cell = pltpu.roll(vorticity, rows_across - 1, 0)
        lower_cell = pltpu.roll(vorticity, 1, 0)
        laplacian = (right_cell + left_cell) + (upper_cell + lower_cell) - 4.0 * vorticity
        step = (
            (TIME_STEP * VISCOSITY) * laplacian
            - along_x * (right_cell - left_cell)
            - along_y * (upper_cell - lower_cell)
        )
        if forcing_of is None:
            vorticity = vorticity + step
        else:
            vorticity = vorticity + step + forcing_of(substep)
        lift = jnp.sum(jnp.sum(vorticity * lift_kernel, axis=0, keepdims=True), axis=1, keepdims=True)
        drag = jnp.sum(jnp.sum(vorticity * drag_kernel, axis=0, keepdims=True), axis=1, keepdims=True)
        row = row + jnp.where(lane == substep, lift, 0.0) + jnp.where(lane == substeps + substep, drag, 0.0)
    return vorticity, row


def stencil_kernel(velocity_ref, vorticity_ref, flow_x_ref, flow_y_ref, out_ref, rows_ref, *, substeps):
    strip = pl.program_id(0)
    source_x, source_y, lift_kernel, drag_kernel = kernel_planes(vorticity_ref.shape[-1])

    def forcing_of(substep):
        return COUPLING * (
            velocity_ref[strip, substep] * source_x
            - velocity_ref[strip, substeps + substep] * source_y
        )

    vorticity, row = run_substeps(
        vorticity_ref[0, 0], flow_x_ref[0, 0], flow_y_ref[0, 0], forcing_of,
        lift_kernel, drag_kernel, substeps,
    )
    out_ref[0] = vorticity
    rows_ref[0] = row


def strip_step_kernel(strip_fields, vorticity, motion, kernels, substeps):
    strips, cells_y, cells_x = strip_fields.shape[1:]
    halves = motion.reshape(strips, 2, substeps)
    earlier = jnp.concatenate([jnp.zeros_like(halves[:, :, :1]), halves[:, :, :-1]], axis=2)
    velocity = (halves - earlier).reshape(strips, 2 * substeps)
    def field(index):
        return pl.BlockSpec((1, 1, cells_y, cells_x), lambda s: (index, s, 0, 0))

    new_vorticity, rows = pl.pallas_call(
        lambda *refs: stencil_kernel(*refs, substeps=substeps),
        grid=(strips,),
        in_specs=[
            pl.BlockSpec(memory_space=pltpu.SMEM),
            field(0), field(1), field(2),
        ],
        out_specs=[
            pl.BlockSpec((1, cells_y, cells_x), lambda s: (s, 0, 0)),
            pl.BlockSpec((1, 1, 2 * substeps), lambda s: (s, 0, 0)),
        ],
        out_shape=[
            jax.ShapeDtypeStruct((strips, cells_y, cells_x), jnp.float32),
            jax.ShapeDtypeStruct((strips, 1, 2 * substeps), jnp.float32),
        ],
        name="strip_stencil",
    )(velocity, vorticity, strip_fields, strip_fields)
    return new_vorticity, rows[:, 0, :]


def apply_block(vectors, matrix):
    return lax.dot_general(vectors, matrix, (((1,), (1,)), ((), ())), precision=EXACT_DOT)


def first_contract(left_side, right_side):
    return lax.dot_general(left_side, right_side, (((0,), (0,)), ((), ())), precision=EXACT_DOT)


def beam_solve(beam_load, pivot_inv, lower_block, upper_block):
    block_count = pivot_inv.shape[0]
    block_size = pivot_inv.shape[1]
    blocks = beam_load.reshape(beam_load.shape[0], block_count, block_size)
    carried = [blocks[:, 0]]
    for block_index in range(1, block_count):
        pivoted = apply_block(carried[-1], pivot_inv[block_index - 1])
        carried.append(blocks[:, block_index] - apply_block(pivoted, lower_block[block_index - 1]))
    solved = [apply_block(carried[-1], pivot_inv[block_count - 1])]
    for block_index in range(block_count - 2, -1, -1):
        remainder = carried[block_index] - apply_block(solved[0], upper_block[block_index])
        solved.insert(0, apply_block(remainder, pivot_inv[block_index]))
    return jnp.concatenate(solved, axis=1)


def start_kernel(owner_ref, riser_ref, node_ref, spread_ref, pivot_ref, lower_ref, upper_ref, fields_ref,
                 response_ref, vorticity_ref, sent_ref, *, substeps):
    block_count = pivot_ref.shape[1]
    block_size = pivot_ref.shape[2]
    node_count = block_count * block_size
    strips = node_ref.shape[1]
    per_device = fields_ref.shape[1]
    position = lax.axis_index("strip")
    group_position = lax.axis_index("group")

    strip_lane = lax.broadcasted_iota(jnp.int32, (1, strips), 1)
    strip_sublane = lax.broadcasted_iota(jnp.int32, (strips, 1), 0)
    owned_row = jnp.zeros((1, strips), jnp.float32)
    owned_col = jnp.zeros((strips, 1), jnp.float32)
    for strip in range(strips):
        held = jnp.where(owner_ref[0, riser_ref[strip]] == position, 1.0, 0.0)
        owned_row = jnp.where(strip_lane == strip, held, owned_row)
        owned_col = jnp.where(strip_sublane == strip, held, owned_col)
    diagonal = lax.broadcasted_iota(jnp.int32, (strips, strips), 0) == lax.broadcasted_iota(jnp.int32, (strips, strips), 1)
    node_row = node_ref[...]
    node_col = jnp.sum(jnp.where(diagonal, node_row.astype(jnp.float32), 0.0), axis=1, keepdims=True)

    def apply(matrix, vectors):
        return jnp.dot(matrix, vectors, precision=lax.Precision.HIGH, preferred_element_type=jnp.float32)

    def unit_load(block_index):
        node = block_index * block_size + lax.broadcasted_iota(jnp.int32, (block_size, strips), 0)
        return (node == node_row).astype(jnp.float32) * owned_row

    def product(left, right):
        return jnp.dot(left, right, precision=lax.Precision.HIGH, preferred_element_type=jnp.float32)

    forward = [None] + [product(lower_ref[0, i - 1], pivot_ref[0, i - 1]) for i in range(1, block_count)]
    backward = [product(pivot_ref[0, i], upper_ref[0, i]) for i in range(block_count - 1)]
    carried = [unit_load(0)]
    for block_index in range(1, block_count):
        carried.append(unit_load(block_index) - apply(forward[block_index], carried[-1]))
    pivoted = [apply(pivot_ref[0, i], carried[i]) for i in range(block_count)]
    solved = pivoted[block_count - 1]
    response_ref[(block_count - 1) * block_size:, :] = solved
    for block_index in range(block_count - 2, -1, -1):
        solved = pivoted[block_index] - apply(backward[block_index], solved)
        response_ref[block_index * block_size:(block_index + 1) * block_size, :] = solved

    _, _, lift_kernel, drag_kernel = kernel_planes(fields_ref.shape[-1])
    strip_of_row = lax.broadcasted_iota(jnp.int32, (per_device, 2 * substeps), 0)
    rows = jnp.zeros((per_device, 2 * substeps), jnp.float32)
    for strip in range(per_device):
        vorticity, row = run_substeps(
            fields_ref[0, strip], fields_ref[1, strip], fields_ref[2, strip], None,
            lift_kernel, drag_kernel, substeps,
        )
        vorticity_ref[strip] = vorticity
        rows = jnp.where(strip_of_row == strip, row, rows)

    node_onehot = (
        node_col == lax.broadcasted_iota(jnp.int32, (strips, node_count), 1).astype(jnp.float32)
    ).astype(jnp.float32)
    coupling = jnp.dot(node_onehot, response_ref[...], precision=EXACT_DOT, preferred_element_type=jnp.float32)
    coupling = coupling * owned_col
    sent_rows = sent_ref.shape[0]
    place = lax.broadcasted_iota(jnp.int32, (sent_rows, strips), 0) - group_position * strips
    pick = (place == lax.broadcasted_iota(jnp.int32, (sent_rows, strips), 1)).astype(jnp.float32)
    sent_ref[:, 0:2 * substeps] = jnp.dot(spread_ref[...], rows, precision=EXACT_DOT, preferred_element_type=jnp.float32)
    sent_ref[:, 2 * substeps:] = jnp.dot(pick, coupling, precision=EXACT_DOT, preferred_element_type=jnp.float32)


def spread_matrix(devices, per_device):
    return (
        np.arange(devices * per_device)[:, None] % per_device == np.arange(per_device)[None, :]
    ).astype(np.float32)


def start_step(riser_owner, strip_riser, strip_node, pivot_inv, lower_block, upper_block, strip_fields, devices, substeps):
    strips = strip_node.shape[0]
    node_count = pivot_inv.shape[1] * pivot_inv.shape[2]
    _, per_device, cells_y, cells_x = strip_fields.shape
    vmem = pl.BlockSpec(memory_space=pltpu.VMEM)
    return pl.pallas_call(
        lambda *refs: start_kernel(*refs, substeps=substeps),
        in_specs=[pl.BlockSpec(memory_space=pltpu.SMEM)] * 2 + [vmem] * 6,
        out_shape=[
            jax.ShapeDtypeStruct((node_count, strips), jnp.float32),
            jax.ShapeDtypeStruct((per_device, cells_y, cells_x), jnp.float32),
            jax.ShapeDtypeStruct((devices * per_device, 2 * substeps + strips), jnp.float32),
        ],
        name="start_step",
    )(
        riser_owner, strip_riser.reshape(strips), strip_node[None, :], spread_matrix(devices, per_device),
        pivot_inv, lower_block, upper_block, strip_fields,
    )


def second_kernel(received_ref, node_ref, spread_ref, gather_ref, difference_ref, flow_x_ref, flow_y_ref, vorticity_ref,
                  out_ref, sent_ref, *, substeps, node_count):
    position = lax.axis_index("strip")
    group_position = lax.axis_index("group")
    total_strips, _ = received_ref.shape
    strips = node_ref.shape[1]
    per_device = flow_x_ref.shape[1]
    every_force = received_ref[:, 0:2 * substeps]
    offset = jnp.sum(every_force, axis=0, keepdims=True) / jnp.sqrt(jnp.float32(total_strips))
    group_force = received_ref[pl.ds(group_position * strips, strips), 0:2 * substeps]
    my_coupling = jnp.dot(
        gather_ref[...], received_ref[:, 2 * substeps:], precision=EXACT_DOT, preferred_element_type=jnp.float32
    )
    motion = jnp.dot(my_coupling, group_force, precision=EXACT_DOT, preferred_element_type=jnp.float32)
    mine = (
        lax.broadcasted_iota(jnp.int32, (per_device, strips), 1)
        == position * per_device + lax.broadcasted_iota(jnp.int32, (per_device, strips), 0)
    )
    local_node = jnp.sum(jnp.where(mine, node_ref[...].astype(jnp.float32), 0.0), axis=1, keepdims=True)
    local_taper = 1.0 - local_node / node_count
    lane = lax.broadcasted_iota(jnp.int32, (per_device, 2 * substeps), 1)
    sublane = lax.broadcasted_iota(jnp.int32, (per_device, 2 * substeps), 0)
    motion = motion + jnp.where(lane >= substeps, local_taper * offset, 0.0)
    velocity = jnp.dot(motion, difference_ref[...], precision=EXACT_DOT, preferred_element_type=jnp.float32)

    source_x, source_y, lift_kernel, drag_kernel = kernel_planes(flow_x_ref.shape[-1])
    coupled_x = COUPLING * source_x
    coupled_y = COUPLING * source_y
    rows = jnp.zeros((per_device, 2 * substeps), jnp.float32)
    for strip in range(per_device):
        picks = [
            jnp.sum(jnp.sum(jnp.where((sublane == strip) & (lane == column), velocity, 0.0), axis=0, keepdims=True), axis=1, keepdims=True)
            for column in range(2 * substeps)
        ]

        def forcing_of(substep, picks=picks):
            return picks[substep] * coupled_x - picks[substeps + substep] * coupled_y

        vorticity, row = run_substeps(
            vorticity_ref[strip], flow_x_ref[0, strip], flow_y_ref[0, strip], forcing_of,
            lift_kernel, drag_kernel, substeps,
        )
        out_ref[strip] = vorticity
        rows = jnp.where(sublane == strip, row, rows)
    sent_ref[...] = jnp.dot(spread_ref[...], rows, precision=EXACT_DOT, preferred_element_type=jnp.float32)


def difference_matrix(substeps):
    columns = np.arange(2 * substeps)
    same = columns[:, None] == columns[None, :]
    before = (columns[:, None] + 1 == columns[None, :]) & (columns[None, :] % substeps != 0)
    return same.astype(np.float32) - before.astype(np.float32)


def second_step(received, strip_node, strip_fields, vorticity, devices, node_count, substeps):
    _, per_device, cells_y, cells_x = strip_fields.shape
    spread = spread_matrix(devices, per_device)
    vmem = pl.BlockSpec(memory_space=pltpu.VMEM)
    return pl.pallas_call(
        lambda *refs: second_kernel(*refs, substeps=substeps, node_count=node_count),
        grid=(1,),
        in_specs=[vmem] * 5 + [
            pl.BlockSpec((1, per_device, cells_y, cells_x), lambda step: (1, 0, 0, 0)),
            pl.BlockSpec((1, per_device, cells_y, cells_x), lambda step: (2, 0, 0, 0)),
            vmem,
        ],
        out_shape=[
            jax.ShapeDtypeStruct((per_device, cells_y, cells_x), jnp.float32),
            jax.ShapeDtypeStruct((devices * per_device, 2 * substeps), jnp.float32),
        ],
        name="second_step",
    )(received, strip_node[None, :], spread, np.ascontiguousarray(spread.T), difference_matrix(substeps), strip_fields, strip_fields, vorticity)


def local(strip_fields, strip_riser, strip_node, riser_owner, pivot_inv, lower_block, upper_block):
    position = lax.axis_index("strip")
    group_position = lax.axis_index("group")
    group_count = lax.axis_size("group")
    devices = lax.axis_size("strip") * group_count
    per_device = strip_fields.shape[1]
    grid_cells = strip_fields.shape[2]
    node_count = pivot_inv.shape[1] * pivot_inv.shape[2]
    riser_count = riser_owner.shape[1]
    group_strips = strip_node.shape[0]
    substeps = NSUB
    total_strips = per_device * devices
    top_taper = 1.0 - jnp.arange(node_count, dtype=jnp.float32) / node_count

    unit_response, first_vorticity, first_sent = start_step(
        riser_owner, strip_riser, strip_node, pivot_inv, lower_block, upper_block, strip_fields, devices, substeps
    )

    received = lax.all_to_all(first_sent, ("group", "strip"), 0, 0, tiled=True)
    vorticity, sent = second_step(received, strip_node, strip_fields, first_vorticity, devices, node_count, substeps)
    received = lax.all_to_all(sent, ("group", "strip"), 0, 0, tiled=True)
    offset = jnp.sum(received[:, substeps:], axis=0) / jnp.sqrt(jnp.float32(total_strips))
    group_force = lax.dynamic_slice_in_dim(received, group_position * group_strips, group_strips)
    displacement = lax.dot_general(
        group_force, unit_response, (((0,), (1,)), ((), ())), precision=EXACT_DOT
    )
    displacement = displacement.at[substeps:, :].add(offset[:, None] * top_taper[None, :])
    return (vorticity, displacement[None])


def solution(mesh):
    in_specs = (
        P(None, ("group", "strip"), None, None),
        P("group", None),
        P("group"),
        P("group", None),
        P(("group", "strip"), None, None, None),
        P(("group", "strip"), None, None, None),
        P(("group", "strip"), None, None, None),
    )
    out_specs = (P(("group", "strip"), None, None), P(("group", "strip"), None, None))
    return jax.shard_map(local, mesh=mesh, in_specs=in_specs, out_specs=out_specs, check_vma=False)
```

```python
import numpy as np
import jax
import jax.numpy as jnp
from jax import lax
from jax.sharding import PartitionSpec as P
from jax.experimental import pallas as pl
from jax.experimental.pallas import tpu as pltpu

NSUB = 8
COUPLED = 2


TIME_STEP = 0.25
VISCOSITY = 0.05
COUPLING = 0.5
EXACT_DOT = lax.Precision.HIGHEST


def make_kernels(grid_cells):
    centre = jnp.arange(grid_cells, dtype=jnp.float32) - grid_cells / 2.0 + 0.5
    near_x = (centre / (grid_cells / 16.0))[None, :]
    near_y = (centre / (grid_cells / 16.0))[:, None]
    bell_near = jnp.exp(-(near_x * near_x + near_y * near_y) / 2.0)
    source_x = -near_x * bell_near
    source_y = -near_y * bell_near
    wide_x = (centre / (grid_cells / 8.0))[None, :]
    wide_y = (centre / (grid_cells / 8.0))[:, None]
    bell_wide = jnp.exp(-(wide_x * wide_x + wide_y * wide_y) / 2.0)
    lift_kernel = -wide_x * bell_wide
    drag_kernel = wide_y * bell_wide
    lift_kernel = lift_kernel / jnp.sqrt(jnp.sum(lift_kernel * lift_kernel))
    drag_kernel = drag_kernel / jnp.sqrt(jnp.sum(drag_kernel * drag_kernel))
    return (source_x, source_y, lift_kernel, drag_kernel)


def strip_step(vorticity, flow_x, flow_y, motion, kernels, substeps):
    source_x, source_y, lift_kernel, drag_kernel = kernels
    halves = motion.reshape(motion.shape[0], 2, substeps)
    earlier = jnp.concatenate([jnp.zeros_like(halves[:, :, :1]), halves[:, :, :-1]], axis=2)
    velocity = halves - earlier
    lift_rows = []
    drag_rows = []
    for substep in range(substeps):
        right_cell = jnp.roll(vorticity, -1, axis=2)
        left_cell = jnp.roll(vorticity, 1, axis=2)
        upper_cell = jnp.roll(vorticity, -1, axis=1)
        lower_cell = jnp.roll(vorticity, 1, axis=1)
        laplacian = right_cell + left_cell + upper_cell + lower_cell - 4.0 * vorticity
        tendency = (
            VISCOSITY * laplacian
            - flow_x * (0.5 * (right_cell - left_cell))
            - flow_y * (0.5 * (upper_cell - lower_cell))
        )
        forcing = (
            velocity[:, 0, substep][:, None, None] * source_x
            - velocity[:, 1, substep][:, None, None] * source_y
        )
        vorticity = vorticity + TIME_STEP * tendency + COUPLING * forcing
        lift_rows.append(jnp.sum(vorticity * lift_kernel, axis=(1, 2)))
        drag_rows.append(jnp.sum(vorticity * drag_kernel, axis=(1, 2)))
    return (vorticity, jnp.stack(lift_rows + drag_rows, axis=1))


def kernel_planes(cells):
    centre_x = lax.broadcasted_iota(jnp.int32, (cells, cells), 1).astype(jnp.float32) - cells / 2.0 + 0.5
    centre_y = lax.broadcasted_iota(jnp.int32, (cells, cells), 0).astype(jnp.float32) - cells / 2.0 + 0.5
    near_x = centre_x / (cells / 16.0)
    near_y = centre_y / (cells / 16.0)
    bell_near = jnp.exp(-(near_x * near_x + near_y * near_y) / 2.0)
    source_x = -near_x * bell_near
    source_y = -near_y * bell_near
    wide_x = centre_x / (cells / 8.0)
    wide_y = centre_y / (cells / 8.0)
    bell_wide = jnp.exp(-(wide_x * wide_x + wide_y * wide_y) / 2.0)
    lift_kernel = -wide_x * bell_wide
    drag_kernel = wide_y * bell_wide

    def total(plane):
        return jnp.sum(jnp.sum(plane, axis=0, keepdims=True), axis=1, keepdims=True)

    lift_kernel = lift_kernel / jnp.sqrt(total(lift_kernel * lift_kernel))
    drag_kernel = drag_kernel / jnp.sqrt(total(drag_kernel * drag_kernel))
    return (source_x, source_y, lift_kernel, drag_kernel)


def run_substeps(vorticity, flow_x, flow_y, forcing_of, lift_kernel, drag_kernel, substeps):
    rows_across, cols_across = vorticity.shape
    lane = lax.broadcasted_iota(jnp.int32, (1, 2 * substeps), 1)
    row = jnp.zeros((1, 2 * substeps), jnp.float32)
    along_x = (TIME_STEP * 0.5) * flow_x
    along_y = (TIME_STEP * 0.5) * flow_y
    for substep in range(substeps):
        right_cell = pltpu.roll(vorticity, cols_across - 1, 1)
        left_cell = pltpu.roll(vorticity, 1, 1)
        upper_cell = pltpu.roll(vorticity, rows_across - 1, 0)
        lower_cell = pltpu.roll(vorticity, 1, 0)
        laplacian = (right_cell + left_cell) + (upper_cell + lower_cell) - 4.0 * vorticity
        step = (
            (TIME_STEP * VISCOSITY) * laplacian
            - along_x * (right_cell - left_cell)
            - along_y * (upper_cell - lower_cell)
        )
        if forcing_of is None:
            vorticity = vorticity + step
        else:
            vorticity = vorticity + step + forcing_of(substep)
        lift = jnp.sum(jnp.sum(vorticity * lift_kernel, axis=0, keepdims=True), axis=1, keepdims=True)
        drag = jnp.sum(jnp.sum(vorticity * drag_kernel, axis=0, keepdims=True), axis=1, keepdims=True)
        row = row + jnp.where(lane == substep, lift, 0.0) + jnp.where(lane == substeps + substep, drag, 0.0)
    return vorticity, row


def stencil_kernel(velocity_ref, vorticity_ref, flow_x_ref, flow_y_ref, out_ref, rows_ref, *, substeps):
    strip = pl.program_id(0)
    source_x, source_y, lift_kernel, drag_kernel = kernel_planes(vorticity_ref.shape[-1])

    def forcing_of(substep):
        return COUPLING * (
            velocity_ref[strip, substep] * source_x
            - velocity_ref[strip, substeps + substep] * source_y
        )

    vorticity, row = run_substeps(
        vorticity_ref[0, 0], flow_x_ref[0, 0], flow_y_ref[0, 0], forcing_of,
        lift_kernel, drag_kernel, substeps,
    )
    out_ref[0] = vorticity
    rows_ref[0] = row


def strip_step_kernel(strip_fields, vorticity, motion, kernels, substeps):
    strips, cells_y, cells_x = strip_fields.shape[1:]
    halves = motion.reshape(strips, 2, substeps)
    earlier = jnp.concatenate([jnp.zeros_like(halves[:, :, :1]), halves[:, :, :-1]], axis=2)
    velocity = (halves - earlier).reshape(strips, 2 * substeps)
    def field(index):
        return pl.BlockSpec((1, 1, cells_y, cells_x), lambda s: (index, s, 0, 0))

    new_vorticity, rows = pl.pallas_call(
        lambda *refs: stencil_kernel(*refs, substeps=substeps),
        grid=(strips,),
        in_specs=[
            pl.BlockSpec(memory_space=pltpu.SMEM),
            field(0), field(1), field(2),
        ],
        out_specs=[
            pl.BlockSpec((1, cells_y, cells_x), lambda s: (s, 0, 0)),
            pl.BlockSpec((1, 1, 2 * substeps), lambda s: (s, 0, 0)),
        ],
        out_shape=[
            jax.ShapeDtypeStruct((strips, cells_y, cells_x), jnp.float32),
            jax.ShapeDtypeStruct((strips, 1, 2 * substeps), jnp.float32),
        ],
        name="strip_stencil",
    )(velocity, vorticity, strip_fields, strip_fields)
    return new_vorticity, rows[:, 0, :]


def apply_block(vectors, matrix):
    return lax.dot_general(vectors, matrix, (((1,), (1,)), ((), ())), precision=EXACT_DOT)


def first_contract(left_side, right_side):
    return lax.dot_general(left_side, right_side, (((0,), (0,)), ((), ())), precision=EXACT_DOT)


def beam_solve(beam_load, pivot_inv, lower_block, upper_block):
    block_count = pivot_inv.shape[0]
    block_size = pivot_inv.shape[1]
    blocks = beam_load.reshape(beam_load.shape[0], block_count, block_size)
    carried = [blocks[:, 0]]
    for block_index in range(1, block_count):
        pivoted = apply_block(carried[-1], pivot_inv[block_index - 1])
        carried.append(blocks[:, block_index] - apply_block(pivoted, lower_block[block_index - 1]))
    solved = [apply_block(carried[-1], pivot_inv[block_count - 1])]
    for block_index in range(block_count - 2, -1, -1):
        remainder = carried[block_index] - apply_block(solved[0], upper_block[block_index])
        solved.insert(0, apply_block(remainder, pivot_inv[block_index]))
    return jnp.concatenate(solved, axis=1)


def start_kernel(owner_ref, riser_ref, node_ref, spread_ref, pivot_ref, lower_ref, upper_ref, fields_ref,
                 response_ref, vorticity_ref, sent_ref, *, substeps):
    block_count = pivot_ref.shape[1]
    block_size = pivot_ref.shape[2]
    node_count = block_count * block_size
    strips = node_ref.shape[1]
    per_device = fields_ref.shape[1]
    position = lax.axis_index("strip")
    group_position = lax.axis_index("group")

    strip_lane = lax.broadcasted_iota(jnp.int32, (1, strips), 1)
    strip_sublane = lax.broadcasted_iota(jnp.int32, (strips, 1), 0)
    owned_row = jnp.zeros((1, strips), jnp.float32)
    owned_col = jnp.zeros((strips, 1), jnp.float32)
    for strip in range(strips):
        held = jnp.where(owner_ref[0, riser_ref[strip]] == position, 1.0, 0.0)
        owned_row = jnp.where(strip_lane == strip, held, owned_row)
        owned_col = jnp.where(strip_sublane == strip, held, owned_col)
    diagonal = lax.broadcasted_iota(jnp.int32, (strips, strips), 0) == lax.broadcasted_iota(jnp.int32, (strips, strips), 1)
    node_row = node_ref[...]
    node_col = jnp.sum(jnp.where(diagonal, node_row.astype(jnp.float32), 0.0), axis=1, keepdims=True)

    def apply(matrix, vectors):
        return jnp.dot(matrix, vectors, precision=lax.Precision.HIGH, preferred_element_type=jnp.float32)

    def unit_load(block_index):
        node = block_index * block_size + lax.broadcasted_iota(jnp.int32, (block_size, strips), 0)
        return (node == node_row).astype(jnp.float32) * owned_row

    def product(left, right):
        return jnp.dot(left, right, precision=lax.Precision.HIGH, preferred_element_type=jnp.float32)

    forward = [None] + [product(lower_ref[0, i - 1], pivot_ref[0, i - 1]) for i in range(1, block_count)]
    backward = [product(pivot_ref[0, i], upper_ref[0, i]) for i in range(block_count - 1)]
    carried = [unit_load(0)]
    for block_index in range(1, block_count):
        carried.append(unit_load(block_index) - apply(forward[block_index], carried[-1]))
    pivoted = [apply(pivot_ref[0, i], carried[i]) for i in range(block_count)]
    solved = pivoted[block_count - 1]
    response_ref[(block_count - 1) * block_size:, :] = solved
    for block_index in range(block_count - 2, -1, -1):
        solved = pivoted[block_index] - apply(backward[block_index], solved)
        response_ref[block_index * block_size:(block_index + 1) * block_size, :] = solved

    _, _, lift_kernel, drag_kernel = kernel_planes(fields_ref.shape[-1])
    strip_of_row = lax.broadcasted_iota(jnp.int32, (per_device, 2 * substeps), 0)
    rows = jnp.zeros((per_device, 2 * substeps), jnp.float32)
    for strip in range(per_device):
        vorticity, row = run_substeps(
            fields_ref[0, strip], fields_ref[1, strip], fields_ref[2, strip], None,
            lift_kernel, drag_kernel, substeps,
        )
        vorticity_ref[strip] = vorticity
        rows = jnp.where(strip_of_row == strip, row, rows)

    node_onehot = (
        node_col == lax.broadcasted_iota(jnp.int32, (strips, node_count), 1).astype(jnp.float32)
    ).astype(jnp.float32)
    coupling = jnp.dot(node_onehot, response_ref[...], precision=EXACT_DOT, preferred_element_type=jnp.float32)
    coupling = coupling * owned_col
    sent_rows = sent_ref.shape[0]
    place = lax.broadcasted_iota(jnp.int32, (sent_rows, strips), 0) - group_position * strips
    pick = (place == lax.broadcasted_iota(jnp.int32, (sent_rows, strips), 1)).astype(jnp.float32)
    sent_ref[:, 0:2 * substeps] = jnp.dot(spread_ref[...], rows, precision=EXACT_DOT, preferred_element_type=jnp.float32)
    sent_ref[:, 2 * substeps:] = jnp.dot(pick, coupling, precision=EXACT_DOT, preferred_element_type=jnp.float32)


def spread_matrix(devices, per_device):
    return (
        np.arange(devices * per_device)[:, None] % per_device == np.arange(per_device)[None, :]
    ).astype(np.float32)


def start_step(riser_owner, strip_riser, strip_node, pivot_inv, lower_block, upper_block, strip_fields, devices, substeps):
    strips = strip_node.shape[0]
    node_count = pivot_inv.shape[1] * pivot_inv.shape[2]
    _, per_device, cells_y, cells_x = strip_fields.shape
    vmem = pl.BlockSpec(memory_space=pltpu.VMEM)
    return pl.pallas_call(
        lambda *refs: start_kernel(*refs, substeps=substeps),
        in_specs=[pl.BlockSpec(memory_space=pltpu.SMEM)] * 2 + [vmem] * 6,
        out_shape=[
            jax.ShapeDtypeStruct((node_count, strips), jnp.float32),
            jax.ShapeDtypeStruct((per_device, cells_y, cells_x), jnp.float32),
            jax.ShapeDtypeStruct((devices * per_device, 2 * substeps + strips), jnp.float32),
        ],
        name="start_step",
    )(
        riser_owner, strip_riser.reshape(strips), strip_node[None, :], spread_matrix(devices, per_device),
        pivot_inv, lower_block, upper_block, strip_fields,
    )


def second_kernel(received_ref, node_ref, flow_x_ref, flow_y_ref, vorticity_ref,
                  out_ref, sent_ref, *, substeps, node_count):
    position = lax.axis_index("strip")
    group_position = lax.axis_index("group")
    total_strips, _ = received_ref.shape
    strips = node_ref.shape[1]
    per_device = flow_x_ref.shape[1]
    sent_rows = received_ref.shape[0]
    spread = (
        lax.rem(lax.broadcasted_iota(jnp.int32, (sent_rows, per_device), 0), per_device)
        == lax.broadcasted_iota(jnp.int32, (sent_rows, per_device), 1)
    ).astype(jnp.float32)
    gather = (
        lax.rem(lax.broadcasted_iota(jnp.int32, (per_device, sent_rows), 1), per_device)
        == lax.broadcasted_iota(jnp.int32, (per_device, sent_rows), 0)
    ).astype(jnp.float32)
    column_in = lax.broadcasted_iota(jnp.int32, (2 * substeps, 2 * substeps), 0)
    column_out = lax.broadcasted_iota(jnp.int32, (2 * substeps, 2 * substeps), 1)
    difference = (column_in == column_out).astype(jnp.float32) - (
        (column_in + 1 == column_out) & (column_out != substeps)
    ).astype(jnp.float32)
    every_force = received_ref[:, 0:2 * substeps]
    offset = jnp.sum(every_force, axis=0, keepdims=True) / jnp.sqrt(jnp.float32(total_strips))
    group_force = received_ref[pl.ds(group_position * strips, strips), 0:2 * substeps]
    my_coupling = jnp.dot(
        gather, received_ref[:, 2 * substeps:], precision=EXACT_DOT, preferred_element_type=jnp.float32
    )
    motion = jnp.dot(my_coupling, group_force, precision=EXACT_DOT, preferred_element_type=jnp.float32)
    mine = (
        lax.broadcasted_iota(jnp.int32, (per_device, strips), 1)
        == position * per_device + lax.broadcasted_iota(jnp.int32, (per_device, strips), 0)
    )
    local_node = jnp.sum(jnp.where(mine, node_ref[...].astype(jnp.float32), 0.0), axis=1, keepdims=True)
    local_taper = 1.0 - local_node / node_count
    lane = lax.broadcasted_iota(jnp.int32, (per_device, 2 * substeps), 1)
    sublane = lax.broadcasted_iota(jnp.int32, (per_device, 2 * substeps), 0)
    motion = motion + jnp.where(lane >= substeps, local_taper * offset, 0.0)
    velocity = jnp.dot(motion, difference, precision=EXACT_DOT, preferred_element_type=jnp.float32)

    source_x, source_y, lift_kernel, drag_kernel = kernel_planes(flow_x_ref.shape[-1])
    coupled_x = COUPLING * source_x
    coupled_y = COUPLING * source_y
    rows = jnp.zeros((per_device, 2 * substeps), jnp.float32)
    for strip in range(per_device):
        picks = [
            jnp.sum(jnp.sum(jnp.where((sublane == strip) & (lane == column), velocity, 0.0), axis=0, keepdims=True), axis=1, keepdims=True)
            for column in range(2 * substeps)
        ]

        def forcing_of(substep, picks=picks):
            return picks[substep] * coupled_x - picks[substeps + substep] * coupled_y

        vorticity, row = run_substeps(
            vorticity_ref[strip], flow_x_ref[0, strip], flow_y_ref[0, strip], forcing_of,
            lift_kernel, drag_kernel, substeps,
        )
        out_ref[strip] = vorticity
        rows = jnp.where(sublane == strip, row, rows)
    sent_ref[...] = jnp.dot(spread, rows, precision=EXACT_DOT, preferred_element_type=jnp.float32)


def difference_matrix(substeps):
    columns = np.arange(2 * substeps)
    same = columns[:, None] == columns[None, :]
    before = (columns[:, None] + 1 == columns[None, :]) & (columns[None, :] % substeps != 0)
    return same.astype(np.float32) - before.astype(np.float32)


def second_step(received, strip_node, strip_fields, vorticity, devices, node_count, substeps):
    _, per_device, cells_y, cells_x = strip_fields.shape
    spread = spread_matrix(devices, per_device)
    vmem = pl.BlockSpec(memory_space=pltpu.VMEM)
    return pl.pallas_call(
        lambda *refs: second_kernel(*refs, substeps=substeps, node_count=node_count),
        grid=(1,),
        in_specs=[vmem] * 2 + [
            pl.BlockSpec((1, per_device, cells_y, cells_x), lambda step: (1, 0, 0, 0)),
            pl.BlockSpec((1, per_device, cells_y, cells_x), lambda step: (2, 0, 0, 0)),
            vmem,
        ],
        out_shape=[
            jax.ShapeDtypeStruct((per_device, cells_y, cells_x), jnp.float32),
            jax.ShapeDtypeStruct((devices * per_device, 2 * substeps), jnp.float32),
        ],
        name="second_step",
    )(received, strip_node[None, :], strip_fields, strip_fields, vorticity)


def local(strip_fields, strip_riser, strip_node, riser_owner, pivot_inv, lower_block, upper_block):
    position = lax.axis_index("strip")
    group_position = lax.axis_index("group")
    group_count = lax.axis_size("group")
    devices = lax.axis_size("strip") * group_count
    per_device = strip_fields.shape[1]
    grid_cells = strip_fields.shape[2]
    node_count = pivot_inv.shape[1] * pivot_inv.shape[2]
    riser_count = riser_owner.shape[1]
    group_strips = strip_node.shape[0]
    substeps = NSUB
    total_strips = per_device * devices
    top_taper = 1.0 - jnp.arange(node_count, dtype=jnp.float32) / node_count

    unit_response, first_vorticity, first_sent = start_step(
        riser_owner, strip_riser, strip_node, pivot_inv, lower_block, upper_block, strip_fields, devices, substeps
    )

    received = lax.all_to_all(first_sent, ("group", "strip"), 0, 0, tiled=True)
    vorticity, sent = second_step(received, strip_node, strip_fields, first_vorticity, devices, node_count, substeps)
    received = lax.all_to_all(sent, ("group", "strip"), 0, 0, tiled=True)
    offset = jnp.sum(received[:, substeps:], axis=0) / jnp.sqrt(jnp.float32(total_strips))
    group_force = lax.dynamic_slice_in_dim(received, group_position * group_strips, group_strips)
    displacement = lax.dot_general(
        group_force, unit_response, (((0,), (1,)), ((), ())), precision=EXACT_DOT
    )
    displacement = displacement.at[substeps:, :].add(offset[:, None] * top_taper[None, :])
    return (vorticity, displacement[None])


def solution(mesh):
    in_specs = (
        P(None, ("group", "strip"), None, None),
        P("group", None),
        P("group"),
        P("group", None),
        P(("group", "strip"), None, None, None),
        P(("group", "strip"), None, None, None),
        P(("group", "strip"), None, None, None),
    )
    out_specs = (P(("group", "strip"), None, None), P(("group", "strip"), None, None))
    return jax.shard_map(local, mesh=mesh, in_specs=in_specs, out_specs=out_specs, check_vma=False)
```

```python
import numpy as np
import jax
import jax.numpy as jnp
from jax import lax
from jax.sharding import PartitionSpec as P
from jax.experimental import pallas as pl
from jax.experimental.pallas import tpu as pltpu

NSUB = 8
COUPLED = 2


TIME_STEP = 0.25
VISCOSITY = 0.05
COUPLING = 0.5
EXACT_DOT = lax.Precision.HIGHEST


def make_kernels(grid_cells):
    centre = jnp.arange(grid_cells, dtype=jnp.float32) - grid_cells / 2.0 + 0.5
    near_x = (centre / (grid_cells / 16.0))[None, :]
    near_y = (centre / (grid_cells / 16.0))[:, None]
    bell_near = jnp.exp(-(near_x * near_x + near_y * near_y) / 2.0)
    source_x = -near_x * bell_near
    source_y = -near_y * bell_near
    wide_x = (centre / (grid_cells / 8.0))[None, :]
    wide_y = (centre / (grid_cells / 8.0))[:, None]
    bell_wide = jnp.exp(-(wide_x * wide_x + wide_y * wide_y) / 2.0)
    lift_kernel = -wide_x * bell_wide
    drag_kernel = wide_y * bell_wide
    lift_kernel = lift_kernel / jnp.sqrt(jnp.sum(lift_kernel * lift_kernel))
    drag_kernel = drag_kernel / jnp.sqrt(jnp.sum(drag_kernel * drag_kernel))
    return (source_x, source_y, lift_kernel, drag_kernel)


def strip_step(vorticity, flow_x, flow_y, motion, kernels, substeps):
    source_x, source_y, lift_kernel, drag_kernel = kernels
    halves = motion.reshape(motion.shape[0], 2, substeps)
    earlier = jnp.concatenate([jnp.zeros_like(halves[:, :, :1]), halves[:, :, :-1]], axis=2)
    velocity = halves - earlier
    lift_rows = []
    drag_rows = []
    for substep in range(substeps):
        right_cell = jnp.roll(vorticity, -1, axis=2)
        left_cell = jnp.roll(vorticity, 1, axis=2)
        upper_cell = jnp.roll(vorticity, -1, axis=1)
        lower_cell = jnp.roll(vorticity, 1, axis=1)
        laplacian = right_cell + left_cell + upper_cell + lower_cell - 4.0 * vorticity
        tendency = (
            VISCOSITY * laplacian
            - flow_x * (0.5 * (right_cell - left_cell))
            - flow_y * (0.5 * (upper_cell - lower_cell))
        )
        forcing = (
            velocity[:, 0, substep][:, None, None] * source_x
            - velocity[:, 1, substep][:, None, None] * source_y
        )
        vorticity = vorticity + TIME_STEP * tendency + COUPLING * forcing
        lift_rows.append(jnp.sum(vorticity * lift_kernel, axis=(1, 2)))
        drag_rows.append(jnp.sum(vorticity * drag_kernel, axis=(1, 2)))
    return (vorticity, jnp.stack(lift_rows + drag_rows, axis=1))


def kernel_planes(cells):
    centre_x = lax.broadcasted_iota(jnp.int32, (cells, cells), 1).astype(jnp.float32) - cells / 2.0 + 0.5
    centre_y = lax.broadcasted_iota(jnp.int32, (cells, cells), 0).astype(jnp.float32) - cells / 2.0 + 0.5
    near_x = centre_x / (cells / 16.0)
    near_y = centre_y / (cells / 16.0)
    bell_near = jnp.exp(-(near_x * near_x + near_y * near_y) / 2.0)
    source_x = -near_x * bell_near
    source_y = -near_y * bell_near
    wide_x = centre_x / (cells / 8.0)
    wide_y = centre_y / (cells / 8.0)
    bell_wide = jnp.exp(-(wide_x * wide_x + wide_y * wide_y) / 2.0)
    lift_kernel = -wide_x * bell_wide
    drag_kernel = wide_y * bell_wide

    def total(plane):
        return jnp.sum(jnp.sum(plane, axis=0, keepdims=True), axis=1, keepdims=True)

    lift_kernel = lift_kernel / jnp.sqrt(total(lift_kernel * lift_kernel))
    drag_kernel = drag_kernel / jnp.sqrt(total(drag_kernel * drag_kernel))
    return (source_x, source_y, lift_kernel, drag_kernel)


def run_substeps(vorticity, flow_x, flow_y, forcing_of, lift_kernel, drag_kernel, substeps):
    rows_across, cols_across = vorticity.shape
    lane = lax.broadcasted_iota(jnp.int32, (1, 2 * substeps), 1)
    row = jnp.zeros((1, 2 * substeps), jnp.float32)
    along_x = (TIME_STEP * 0.5) * flow_x
    along_y = (TIME_STEP * 0.5) * flow_y
    for substep in range(substeps):
        right_cell = pltpu.roll(vorticity, cols_across - 1, 1)
        left_cell = pltpu.roll(vorticity, 1, 1)
        upper_cell = pltpu.roll(vorticity, rows_across - 1, 0)
        lower_cell = pltpu.roll(vorticity, 1, 0)
        laplacian = (right_cell + left_cell) + (upper_cell + lower_cell) - 4.0 * vorticity
        step = (
            (TIME_STEP * VISCOSITY) * laplacian
            - along_x * (right_cell - left_cell)
            - along_y * (upper_cell - lower_cell)
        )
        if forcing_of is None:
            vorticity = vorticity + step
        else:
            vorticity = vorticity + step + forcing_of(substep)
        lift = jnp.sum(jnp.sum(vorticity * lift_kernel, axis=0, keepdims=True), axis=1, keepdims=True)
        drag = jnp.sum(jnp.sum(vorticity * drag_kernel, axis=0, keepdims=True), axis=1, keepdims=True)
        row = row + jnp.where(lane == substep, lift, 0.0) + jnp.where(lane == substeps + substep, drag, 0.0)
    return vorticity, row


def stencil_kernel(velocity_ref, vorticity_ref, flow_x_ref, flow_y_ref, out_ref, rows_ref, *, substeps):
    strip = pl.program_id(0)
    source_x, source_y, lift_kernel, drag_kernel = kernel_planes(vorticity_ref.shape[-1])

    def forcing_of(substep):
        return COUPLING * (
            velocity_ref[strip, substep] * source_x
            - velocity_ref[strip, substeps + substep] * source_y
        )

    vorticity, row = run_substeps(
        vorticity_ref[0, 0], flow_x_ref[0, 0], flow_y_ref[0, 0], forcing_of,
        lift_kernel, drag_kernel, substeps,
    )
    out_ref[0] = vorticity
    rows_ref[0] = row


def strip_step_kernel(strip_fields, vorticity, motion, kernels, substeps):
    strips, cells_y, cells_x = strip_fields.shape[1:]
    halves = motion.reshape(strips, 2, substeps)
    earlier = jnp.concatenate([jnp.zeros_like(halves[:, :, :1]), halves[:, :, :-1]], axis=2)
    velocity = (halves - earlier).reshape(strips, 2 * substeps)
    def field(index):
        return pl.BlockSpec((1, 1, cells_y, cells_x), lambda s: (index, s, 0, 0))

    new_vorticity, rows = pl.pallas_call(
        lambda *refs: stencil_kernel(*refs, substeps=substeps),
        grid=(strips,),
        in_specs=[
            pl.BlockSpec(memory_space=pltpu.SMEM),
            field(0), field(1), field(2),
        ],
        out_specs=[
            pl.BlockSpec((1, cells_y, cells_x), lambda s: (s, 0, 0)),
            pl.BlockSpec((1, 1, 2 * substeps), lambda s: (s, 0, 0)),
        ],
        out_shape=[
            jax.ShapeDtypeStruct((strips, cells_y, cells_x), jnp.float32),
            jax.ShapeDtypeStruct((strips, 1, 2 * substeps), jnp.float32),
        ],
        name="strip_stencil",
    )(velocity, vorticity, strip_fields, strip_fields)
    return new_vorticity, rows[:, 0, :]


def apply_block(vectors, matrix):
    return lax.dot_general(vectors, matrix, (((1,), (1,)), ((), ())), precision=EXACT_DOT)


def first_contract(left_side, right_side):
    return lax.dot_general(left_side, right_side, (((0,), (0,)), ((), ())), precision=EXACT_DOT)


def beam_solve(beam_load, pivot_inv, lower_block, upper_block):
    block_count = pivot_inv.shape[0]
    block_size = pivot_inv.shape[1]
    blocks = beam_load.reshape(beam_load.shape[0], block_count, block_size)
    carried = [blocks[:, 0]]
    for block_index in range(1, block_count):
        pivoted = apply_block(carried[-1], pivot_inv[block_index - 1])
        carried.append(blocks[:, block_index] - apply_block(pivoted, lower_block[block_index - 1]))
    solved = [apply_block(carried[-1], pivot_inv[block_count - 1])]
    for block_index in range(block_count - 2, -1, -1):
        remainder = carried[block_index] - apply_block(solved[0], upper_block[block_index])
        solved.insert(0, apply_block(remainder, pivot_inv[block_index]))
    return jnp.concatenate(solved, axis=1)


def start_kernel(owner_ref, riser_ref, node_ref, pivot_ref, lower_ref, upper_ref, fields_ref,
                 response_ref, vorticity_ref, sent_ref, *, substeps):
    block_count = pivot_ref.shape[1]
    block_size = pivot_ref.shape[2]
    node_count = block_count * block_size
    strips = node_ref.shape[1]
    per_device = fields_ref.shape[1]
    position = lax.axis_index("strip")
    group_position = lax.axis_index("group")

    strip_lane = lax.broadcasted_iota(jnp.int32, (1, strips), 1)
    strip_sublane = lax.broadcasted_iota(jnp.int32, (strips, 1), 0)
    owned_row = jnp.zeros((1, strips), jnp.float32)
    owned_col = jnp.zeros((strips, 1), jnp.float32)
    for strip in range(strips):
        held = jnp.where(owner_ref[0, riser_ref[strip]] == position, 1.0, 0.0)
        owned_row = jnp.where(strip_lane == strip, held, owned_row)
        owned_col = jnp.where(strip_sublane == strip, held, owned_col)
    diagonal = lax.broadcasted_iota(jnp.int32, (strips, strips), 0) == lax.broadcasted_iota(jnp.int32, (strips, strips), 1)
    node_row = node_ref[...]
    node_col = jnp.sum(jnp.where(diagonal, node_row.astype(jnp.float32), 0.0), axis=1, keepdims=True)

    def apply(matrix, vectors):
        return jnp.dot(matrix, vectors, precision=lax.Precision.HIGH, preferred_element_type=jnp.float32)

    def unit_load(block_index):
        node = block_index * block_size + lax.broadcasted_iota(jnp.int32, (block_size, strips), 0)
        return (node == node_row).astype(jnp.float32) * owned_row

    def product(left, right):
        return jnp.dot(left, right, precision=lax.Precision.HIGH, preferred_element_type=jnp.float32)

    forward = [None] + [product(lower_ref[0, i - 1], pivot_ref[0, i - 1]) for i in range(1, block_count)]
    backward = [product(pivot_ref[0, i], upper_ref[0, i]) for i in range(block_count - 1)]
    carried = [unit_load(0)]
    for block_index in range(1, block_count):
        carried.append(unit_load(block_index) - apply(forward[block_index], carried[-1]))
    pivoted = [apply(pivot_ref[0, i], carried[i]) for i in range(block_count)]
    solved = pivoted[block_count - 1]
    response_ref[(block_count - 1) * block_size:, :] = solved
    for block_index in range(block_count - 2, -1, -1):
        solved = pivoted[block_index] - apply(backward[block_index], solved)
        response_ref[block_index * block_size:(block_index + 1) * block_size, :] = solved

    _, _, lift_kernel, drag_kernel = kernel_planes(fields_ref.shape[-1])
    strip_of_row = lax.broadcasted_iota(jnp.int32, (per_device, 2 * substeps), 0)
    rows = jnp.zeros((per_device, 2 * substeps), jnp.float32)
    for strip in range(per_device):
        vorticity, row = run_substeps(
            fields_ref[0, strip], fields_ref[1, strip], fields_ref[2, strip], None,
            lift_kernel, drag_kernel, substeps,
        )
        vorticity_ref[strip] = vorticity
        rows = jnp.where(strip_of_row == strip, row, rows)

    node_onehot = (
        node_col == lax.broadcasted_iota(jnp.int32, (strips, node_count), 1).astype(jnp.float32)
    ).astype(jnp.float32)
    coupling = jnp.dot(node_onehot, response_ref[...], precision=EXACT_DOT, preferred_element_type=jnp.float32)
    coupling = coupling * owned_col
    sent_rows = sent_ref.shape[0]
    place = lax.broadcasted_iota(jnp.int32, (sent_rows, strips), 0) - group_position * strips
    pick = (place == lax.broadcasted_iota(jnp.int32, (sent_rows, strips), 1)).astype(jnp.float32)
    spread = (
        lax.rem(lax.broadcasted_iota(jnp.int32, (sent_rows, per_device), 0), per_device)
        == lax.broadcasted_iota(jnp.int32, (sent_rows, per_device), 1)
    ).astype(jnp.float32)
    sent_ref[:, 0:2 * substeps] = jnp.dot(spread, rows, precision=EXACT_DOT, preferred_element_type=jnp.float32)
    sent_ref[:, 2 * substeps:] = jnp.dot(pick, coupling, precision=EXACT_DOT, preferred_element_type=jnp.float32)


def spread_matrix(devices, per_device):
    return (
        np.arange(devices * per_device)[:, None] % per_device == np.arange(per_device)[None, :]
    ).astype(np.float32)


def start_step(riser_owner, strip_riser, strip_node, pivot_inv, lower_block, upper_block, strip_fields, devices, substeps):
    strips = strip_node.shape[0]
    node_count = pivot_inv.shape[1] * pivot_inv.shape[2]
    _, per_device, cells_y, cells_x = strip_fields.shape
    vmem = pl.BlockSpec(memory_space=pltpu.VMEM)
    return pl.pallas_call(
        lambda *refs: start_kernel(*refs, substeps=substeps),
        in_specs=[pl.BlockSpec(memory_space=pltpu.SMEM)] * 2 + [vmem] * 5,
        out_shape=[
            jax.ShapeDtypeStruct((node_count, strips), jnp.float32),
            jax.ShapeDtypeStruct((per_device, cells_y, cells_x), jnp.float32),
            jax.ShapeDtypeStruct((devices * per_device, 2 * substeps + strips), jnp.float32),
        ],
        name="start_step",
    )(
        riser_owner, strip_riser.reshape(strips), strip_node[None, :],
        pivot_inv, lower_block, upper_block, strip_fields,
    )


def second_kernel(received_ref, node_ref, spread_ref, gather_ref, difference_ref, flow_x_ref, flow_y_ref, vorticity_ref,
                  out_ref, sent_ref, *, substeps, node_count):
    position = lax.axis_index("strip")
    group_position = lax.axis_index("group")
    total_strips, _ = received_ref.shape
    strips = node_ref.shape[1]
    per_device = flow_x_ref.shape[1]
    every_force = received_ref[:, 0:2 * substeps]
    offset = jnp.sum(every_force, axis=0, keepdims=True) / jnp.sqrt(jnp.float32(total_strips))
    group_force = received_ref[pl.ds(group_position * strips, strips), 0:2 * substeps]
    my_coupling = jnp.dot(
        gather_ref[...], received_ref[:, 2 * substeps:], precision=EXACT_DOT, preferred_element_type=jnp.float32
    )
    motion = jnp.dot(my_coupling, group_force, precision=EXACT_DOT, preferred_element_type=jnp.float32)
    mine = (
        lax.broadcasted_iota(jnp.int32, (per_device, strips), 1)
        == position * per_device + lax.broadcasted_iota(jnp.int32, (per_device, strips), 0)
    )
    local_node = jnp.sum(jnp.where(mine, node_ref[...].astype(jnp.float32), 0.0), axis=1, keepdims=True)
    local_taper = 1.0 - local_node / node_count
    lane = lax.broadcasted_iota(jnp.int32, (per_device, 2 * substeps), 1)
    sublane = lax.broadcasted_iota(jnp.int32, (per_device, 2 * substeps), 0)
    motion = motion + jnp.where(lane >= substeps, local_taper * offset, 0.0)
    velocity = jnp.dot(motion, difference_ref[...], precision=EXACT_DOT, preferred_element_type=jnp.float32)

    source_x, source_y, lift_kernel, drag_kernel = kernel_planes(flow_x_ref.shape[-1])
    coupled_x = COUPLING * source_x
    coupled_y = COUPLING * source_y
    rows = jnp.zeros((per_device, 2 * substeps), jnp.float32)
    for strip in range(per_device):
        picks = [
            jnp.sum(jnp.sum(jnp.where((sublane == strip) & (lane == column), velocity, 0.0), axis=0, keepdims=True), axis=1, keepdims=True)
            for column in range(2 * substeps)
        ]

        def forcing_of(substep, picks=picks):
            return picks[substep] * coupled_x - picks[substeps + substep] * coupled_y

        vorticity, row = run_substeps(
            vorticity_ref[strip], flow_x_ref[0, strip], flow_y_ref[0, strip], forcing_of,
            lift_kernel, drag_kernel, substeps,
        )
        out_ref[strip] = vorticity
        rows = jnp.where(sublane == strip, row, rows)
    sent_ref[...] = jnp.dot(spread_ref[...], rows, precision=EXACT_DOT, preferred_element_type=jnp.float32)


def difference_matrix(substeps):
    columns = np.arange(2 * substeps)
    same = columns[:, None] == columns[None, :]
    before = (columns[:, None] + 1 == columns[None, :]) & (columns[None, :] % substeps != 0)
    return same.astype(np.float32) - before.astype(np.float32)


def second_step(received, strip_node, strip_fields, vorticity, devices, node_count, substeps):
    _, per_device, cells_y, cells_x = strip_fields.shape
    spread = spread_matrix(devices, per_device)
    vmem = pl.BlockSpec(memory_space=pltpu.VMEM)
    return pl.pallas_call(
        lambda *refs: second_kernel(*refs, substeps=substeps, node_count=node_count),
        grid=(1,),
        in_specs=[vmem] * 5 + [
            pl.BlockSpec((1, per_device, cells_y, cells_x), lambda step: (1, 0, 0, 0)),
            pl.BlockSpec((1, per_device, cells_y, cells_x), lambda step: (2, 0, 0, 0)),
            vmem,
        ],
        out_shape=[
            jax.ShapeDtypeStruct((per_device, cells_y, cells_x), jnp.float32),
            jax.ShapeDtypeStruct((devices * per_device, 2 * substeps), jnp.float32),
        ],
        name="second_step",
    )(received, strip_node[None, :], spread, np.ascontiguousarray(spread.T), difference_matrix(substeps), strip_fields, strip_fields, vorticity)


def local(strip_fields, strip_riser, strip_node, riser_owner, pivot_inv, lower_block, upper_block):
    position = lax.axis_index("strip")
    group_position = lax.axis_index("group")
    group_count = lax.axis_size("group")
    devices = lax.axis_size("strip") * group_count
    per_device = strip_fields.shape[1]
    grid_cells = strip_fields.shape[2]
    node_count = pivot_inv.shape[1] * pivot_inv.shape[2]
    riser_count = riser_owner.shape[1]
    group_strips = strip_node.shape[0]
    substeps = NSUB
    total_strips = per_device * devices
    top_taper = 1.0 - jnp.arange(node_count, dtype=jnp.float32) / node_count

    unit_response, first_vorticity, first_sent = start_step(
        riser_owner, strip_riser, strip_node, pivot_inv, lower_block, upper_block, strip_fields, devices, substeps
    )

    received = lax.all_to_all(first_sent, ("group", "strip"), 0, 0, tiled=True)
    vorticity, sent = second_step(received, strip_node, strip_fields, first_vorticity, devices, node_count, substeps)
    received = lax.all_to_all(sent, ("group", "strip"), 0, 0, tiled=True)
    offset = jnp.sum(received[:, substeps:], axis=0) / jnp.sqrt(jnp.float32(total_strips))
    group_force = lax.dynamic_slice_in_dim(received, group_position * group_strips, group_strips)
    displacement = lax.dot_general(
        group_force, unit_response, (((0,), (1,)), ((), ())), precision=EXACT_DOT
    )
    displacement = displacement.at[substeps:, :].add(offset[:, None] * top_taper[None, :])
    return (vorticity, displacement[None])


def solution(mesh):
    in_specs = (
        P(None, ("group", "strip"), None, None),
        P("group", None),
        P("group"),
        P("group", None),
        P(("group", "strip"), None, None, None),
        P(("group", "strip"), None, None, None),
        P(("group", "strip"), None, None, None),
    )
    out_specs = (P(("group", "strip"), None, None), P(("group", "strip"), None, None))
    return jax.shard_map(local, mesh=mesh, in_specs=in_specs, out_specs=out_specs, check_vma=False)
```
